32 devices in a mesh: grp: 2 (over y), seq: 4 (over z), head: 4 (over x, core).
Axes of the slice: x: 2, y: 2, z: 4, core: 2. Of those that a mesh axis runs over, the one named last changes fastest.
Arguments:
- inner_input: bfloat16 [8192, 4096], P(('grp', 'seq'), 'head'), parts along dimension 0, may hold values from -6 to 6
- state_input: bfloat16 [2, 8192, 512], P(None, ('grp', 'seq'), 'head'), parts along dimension 1, may hold values from -6 to 6
- conv_inner: bfloat16 [4, 4096], P(None, 'head'), may hold values from -3 to 3
- bias_inner: float32 [4096], P('head'), may hold values from -3 to 3
- conv_state: bfloat16 [2, 4, 512], P(None, None, 'head'), may hold values from -3 to 3
- bias_state: float32 [2, 512], P(None, 'head'), may hold values from -3 to 3
- step_size: float32 [64, 8192], P('head', ('grp', 'seq')), parts along dimension 1, may hold values from 0.005 to 0.045
- decay_rate: float32 [64], P('head'), may hold values from 0.0048828125 to 2.5
- skip_gain: float32 [64], P('head'), may hold values from -4 to 5
- lengths: int32 [6], P('grp'), parts along dimension 0, may hold values from 1 to 2048, 4096 in all
Outputs:
- mixed: bfloat16 [8192, 4096], P(('grp', 'seq'), 'head'), parts along dimension 0
The draws below stay inside these ranges and needn't reach their ends.
There are 2 independent parts, one for each index of `grp`. The reference program is written for one: setup_inputs(seed, part) draws one part's arguments, and reference() takes and returns one part's arrays. A program takes and returns all parts, laid end to end along the dimension named above; an argument that names none is the same for every part. Nothing has to cross between parts.
All inputs are finite; a program needn't handle non-finite values.
Results may differ from the reference program's by a relative error of at most 0.0034.
Values may be sent and summed in bfloat16 or wider, within the bound.
No kernel may reach another device: no remote copies, remote signals or barrier semaphores. Data moves between devices by JAX's collectives and lax.ppermute only.
A program may use at most 64 MiB of HBM per device.

```python
import math
import jax
import jax.numpy as jnp
import numpy as np
from jax import lax

P_SIZE = 64
N = 256
BLOCK = 128
HEADS = 64
GROUPS = 2
D_INNER = 4096
TOKENS = 4096
REQS = 3


def draw_decay_rate(key, part):
    key_pick, key_level = jax.random.split(key)
    share = 0.5
    quick = jax.random.uniform(key_pick, (HEADS,), jnp.float32) < share
    level = jax.random.uniform(key_level, (HEADS,), jnp.float32)
    quick_rate = jnp.exp(level * jnp.log(2.5))
    slow_rate = 20.0 / TOKENS * jnp.exp(level * jnp.log(5.0))
    return jnp.where(quick, quick_rate, slow_rate).astype(jnp.float32)


def draw_skip_gain(key, part):
    values = 0.5 + 1.5 * jax.random.normal(key, (HEADS,), jnp.float32)
    values = jnp.clip(values, -4.0, 5.0)
    return values.astype(jnp.float32)


def levels(key, shape, cuts, least, top_value):
    factor_of = 1.0
    for axis_at, shards_of in cuts:
        heights = jax.random.uniform(jax.random.fold_in(jax.random.fold_in(key, 6), axis_at), (shards_of,), jnp.float32, least / len(cuts), top_value / len(cuts))
        factor_of = factor_of * jnp.repeat(jnp.exp(heights), shape[axis_at] // shards_of).reshape((-1,) + (1,) * (len(shape) - 1 - axis_at))
    return factor_of


def split_up(count, total, bound, slope):
    portions = [(1 << 20) // math.isqrt(grade ** slope) + 1 for grade in range(2, count + 1)]
    rest, counts = total - bound - (count - 1), [1] * (count - 1)
    while rest > 0:
        movable = [i for i in range(count - 1) if counts[i] < bound]
        whole, left = sum([portions[i] for i in movable]), rest
        for i in movable:
            extra = min(bound - counts[i], max(1, left * portions[i] // whole), rest)
            counts[i] = counts[i] + extra
            rest = rest - extra
    return np.array([bound] + counts)


def uneven_parts(rng, amount, total, limit, lean):
    if amount == 2:
        one = jax.random.randint(rng, (), max(1, total - limit), min(limit, total - 1) + 1)
        return jnp.stack([one, total - one])
    tallies = jnp.asarray(split_up(amount, total, limit, lean), jnp.int32)
    couples = (amount - 1) // 2
    donor, receiver = tallies[1:1 + 2 * couples:2], tallies[2:2 + 2 * couples:2]
    room = jnp.minimum(donor - 1, limit - receiver)
    moved = jax.random.randint(jax.random.fold_in(rng, 1), (couples,), 0, 1 << 20) % (room + 1)
    tallies = tallies.at[1:1 + 2 * couples:2].set(donor - moved).at[2:2 + 2 * couples:2].set(receiver + moved)
    return tallies[jax.random.permutation(jax.random.fold_in(rng, 2), amount)]


def normal_values(key, dims, scale, reach, shards=(), held_as=jnp.bfloat16):
    values = scale * jax.random.normal(key, dims, jnp.float32)
    if shards:
        values = values * levels(key, dims, shards, -0.22, 0.18)
    return jnp.clip(values, -reach, reach).astype(held_as)


def setup_inputs(seed: int = 0, part: int = 0) -> dict:
    keys = jax.random.split(jax.random.key(seed), 11)
    part_splits = jax.random.split(jax.random.fold_in(keys[10], part), 11)
    inner_input = normal_values(part_splits[0], (TOKENS, D_INNER), 1.0, 6.0, ((0, 4), (1, 4)))
    state_input = normal_values(part_splits[1], (2, TOKENS, GROUPS * N), 1.0, 6.0, ((1, 4), (2, 4)))
    conv_inner = normal_values(keys[2], (4, D_INNER), 4 ** -0.5, 3.0, ((1, 4),))
    bias_inner = normal_values(keys[3], (D_INNER,), 0.5, 3.0, ((0, 4),), jnp.float32)
    conv_state = normal_values(keys[4], (2, 4, GROUPS * N), 4 ** -0.5, 3.0, ((2, 4),))
    bias_state = normal_values(keys[5], (2, GROUPS * N), 0.5, 3.0, ((1, 4),), jnp.float32)
    step_size = jnp.clip(jnp.exp(math.log(0.045) - 2.1972246 * jax.random.uniform(part_splits[6], (HEADS, TOKENS), jnp.float32) ** levels(part_splits[6], (HEADS, TOKENS), ((0, 4), (1, 4)), -0.2, 0.2)), 0.005, 0.045)
    decay_rate = draw_decay_rate(jax.random.fold_in(keys[10], 71), part)
    skip_gain = draw_skip_gain(jax.random.fold_in(keys[10], 71), part)
    lengths = uneven_parts(part_splits[9], REQS, TOKENS, TOKENS // 2, 2).astype(jnp.int32)
    return {"inner_input": inner_input, "state_input": state_input, "conv_inner": conv_inner, "bias_inner": bias_inner, "conv_state": conv_state, "bias_state": bias_state, "step_size": step_size, "decay_rate": decay_rate, "skip_gain": skip_gain, "lengths": lengths}


def segment_of(lengths, positions):
    starts = jnp.cumsum(lengths, dtype=jnp.int32) - lengths
    covered = (starts[None, :] <= positions[:, None]).astype(jnp.int32)
    return jnp.sum(covered, axis=1, dtype=jnp.int32) - 1


def convolve(extended, weight, bias_row, seg_ext, row_count):
    own_seg = seg_ext[3:]
    summed = jnp.zeros(extended.shape[:-2] + (row_count, extended.shape[-1]), jnp.float32) + bias_row.astype(jnp.float32)
    for offset in range(4):
        kept_mask = (seg_ext[offset:offset + row_count] == own_seg).astype(jnp.float32)[:, None]
        window = extended[..., offset:offset + row_count, :].astype(jnp.float32)
        summed = summed + weight[offset].astype(jnp.float32) * window * kept_mask
    return jax.nn.silu(summed).astype(jnp.bfloat16)


def ssd_block(inner_conv, state_conv, steps_dt, log_decay, own_seg, prev_seg, skip_gain, carry_state):
    precise = lax.Precision.HIGHEST
    row_count = inner_conv.shape[0]
    per_group = HEADS // GROUPS
    inner_heads = inner_conv.reshape(row_count, GROUPS, per_group, P_SIZE).astype(jnp.float32)
    b_float = state_conv[0].reshape(row_count, GROUPS, N).astype(jnp.float32)
    c_float = state_conv[1].reshape(row_count, GROUPS, N).astype(jnp.float32)
    scores = jnp.einsum('tgn,sgn->gts', c_float, b_float, precision=precise)
    places = jnp.arange(row_count, dtype=jnp.int32)
    allowed = (places[:, None] >= places[None, :]) & (own_seg[:, None] == own_seg[None, :])
    decay_grid = jnp.exp(log_decay[:, :, None] - log_decay[:, None, :]) * steps_dt[:, None, :]
    decay_grid = decay_grid.reshape(GROUPS, per_group, row_count, row_count)
    weights = jnp.where(allowed[None, None], decay_grid * scores[:, None], 0.0).astype(jnp.bfloat16)
    intra_out = jnp.einsum('gkts,sgkp->tgkp', weights.astype(jnp.float32), inner_heads, precision=precise)
    ending = jnp.exp(log_decay[:, -1:] - log_decay) * steps_dt * (own_seg == own_seg[-1]).astype(jnp.float32)[None, :]
    ending = jnp.transpose(ending).reshape(row_count, GROUPS, per_group, 1)
    weighted = (inner_heads * ending).astype(jnp.bfloat16).astype(jnp.float32)
    block_state = jnp.einsum('sgkp,sgn->gkpn', weighted, b_float, precision=precise).reshape(HEADS, P_SIZE, N)
    entry_coef = jnp.exp(log_decay) * (own_seg == prev_seg).astype(jnp.float32)[None, :]
    entry_coef = jnp.transpose(entry_coef).reshape(row_count, GROUPS, per_group, 1)
    inter_out = jnp.einsum('tgn,gkpn->tgkp', c_float, carry_state.reshape(GROUPS, per_group, P_SIZE, N), precision=precise) * entry_coef
    block_decay = jnp.exp(log_decay[:, -1]) * (own_seg[-1] == prev_seg).astype(jnp.float32)
    new_state = block_decay[:, None, None] * carry_state + block_state
    skip_heads = skip_gain.reshape(GROUPS, per_group)[None, :, :, None]
    mixed_out = (intra_out + inter_out + skip_heads * inner_heads).astype(jnp.bfloat16).reshape(row_count, HEADS * P_SIZE)
    return new_state, mixed_out


def reference(inner_input, state_input, conv_inner, bias_inner, conv_state, bias_state, step_size, decay_rate, skip_gain, lengths):
    block_count = TOKENS // BLOCK
    positions = jnp.arange(TOKENS + 3, dtype=jnp.int32) - 3
    seg_pad = segment_of(lengths, positions)
    inner_pad = jnp.concatenate([jnp.zeros((3, inner_input.shape[1]), inner_input.dtype), inner_input], 0)
    state_pad = jnp.concatenate([jnp.zeros((2, 3, state_input.shape[2]), state_input.dtype), state_input], 1)
    weight_state = jnp.swapaxes(conv_state, 0, 1)[:, :, None, :]
    bias_pair = bias_state[:, None, :]

    def advance(carry_state, block_index):
        start_row = (block_index * BLOCK).astype(jnp.int32)
        seg_ext = lax.dynamic_slice_in_dim(seg_pad, start_row, BLOCK + 3)
        inner_conv = convolve(lax.dynamic_slice_in_dim(inner_pad, start_row, BLOCK + 3, 0), conv_inner, bias_inner, seg_ext, BLOCK)
        state_conv = convolve(lax.dynamic_slice_in_dim(state_pad, start_row, BLOCK + 3, 1), weight_state, bias_pair, seg_ext, BLOCK)
        steps_dt = lax.dynamic_slice_in_dim(step_size, start_row, BLOCK, 1)
        log_decay = jnp.cumsum(-steps_dt * decay_rate[:, None], axis=1)
        return ssd_block(inner_conv, state_conv, steps_dt, log_decay, seg_ext[3:], seg_ext[2], skip_gain, carry_state)

    initial = jnp.zeros((HEADS, P_SIZE, N), jnp.float32)
    final_state, outputs = lax.scan(advance, initial, jnp.arange(block_count, dtype=jnp.int32))
    return outputs.reshape(TOKENS, HEADS * P_SIZE)
```

```python
import functools

import jax
import jax.numpy as jnp
from jax import lax
from jax.experimental import pallas as pl
from jax.experimental.pallas import tpu as pltpu
from jax.sharding import PartitionSpec as P

BLOCK = 128


def shifted(value, axis, steps):
    count = lax.axis_size(axis)
    initial, last = (max(0, -steps), min(count, count - steps))
    return lax.ppermute(value, axis, [(source, source + steps) for source in range(initial, last)])


def from_partner(block, axis, stride):
    count = lax.axis_size(axis)
    route = []
    for low in range(count):
        high = low | 1 << stride
        if high != low and high < count:
            route += [(low, high), (high, low)]
    return lax.ppermute(block, axis, route)


def segment_of(lengths, positions):
    starts = jnp.cumsum(lengths, dtype=jnp.int32) - lengths
    covered = (starts[None, :] <= positions[:, None]).astype(jnp.int32)
    return jnp.sum(covered, axis=1, dtype=jnp.int32) - 1


def convolve(extended, weight, bias_row, seg_ext, row_count):
    own_seg = seg_ext[3:]
    summed = (
        jnp.zeros(extended.shape[:-2] + (row_count, extended.shape[-1]), jnp.float32) + bias_row
    )
    for offset in range(4):
        kept_mask = (seg_ext[offset : offset + row_count] == own_seg).astype(jnp.float32)[:, None]
        window = extended[..., offset : offset + row_count, :].astype(jnp.float32)
        summed = summed + weight[offset].astype(jnp.float32) * window * kept_mask
    return jax.nn.silu(summed).astype(jnp.bfloat16)


def split_dot_nt(lhs, value):
    high = value.astype(jnp.bfloat16)
    low = (value - high.astype(jnp.float32)).astype(jnp.bfloat16)
    dims = (((1,), (1,)), ((), ()))
    return lax.dot_general(lhs, high, dims, preferred_element_type=jnp.float32) + lax.dot_general(
        lhs, low, dims, preferred_element_type=jnp.float32
    )


def block_kernel(with_y, head_count, head_width, *refs):
    if with_y:
        (decay_ref, skip_ref, x_ref, b_ref, c_ref, l_ref, lt_ref, dt_ref, dtt_ref, segr_ref,
         segc_ref, entry_ref, ein_ref, out_ref, state_ref) = refs
    else:
        (decay_ref, x_ref, b_ref, l_ref, lt_ref, dtt_ref, segc_ref, state_ref) = refs
    blk = pl.program_id(0)

    @pl.when(blk == 0)
    def _():
        if with_y:
            state_ref[...] = ein_ref[...]
        else:
            state_ref[...] = jnp.zeros(state_ref.shape, jnp.float32)

    b_mat = b_ref[...]
    seg_col = segc_ref[...]
    end_col = (seg_col == seg_col[BLOCK - 1 : BLOCK, :]).astype(jnp.float32)
    if with_y:
        c_mat = c_ref[...]
        seg_row = segr_ref[...]
        scores = lax.dot_general(
            c_mat, b_mat, (((1,), (1,)), ((), ())), preferred_element_type=jnp.float32
        )
        rows = lax.broadcasted_iota(jnp.int32, (BLOCK, BLOCK), 0)
        cols = lax.broadcasted_iota(jnp.int32, (BLOCK, BLOCK), 1)
        allowed = (rows >= cols) & (seg_col == seg_row)
        entry_col = entry_ref[...]
    for h in range(head_count):
        lanes = slice(h * head_width, (h + 1) * head_width)
        l_col = lt_ref[:, h : h + 1]
        dt_col = dtt_ref[:, h : h + 1]
        x_h = x_ref[:, lanes]
        state_h = state_ref[h]
        if with_y:
            l_row = l_ref[h : h + 1, :]
            dt_row = dt_ref[h : h + 1, :]
            weights = jnp.where(allowed, jnp.exp(l_col - l_row) * dt_row * scores, 0.0)
            intra = jnp.dot(weights.astype(jnp.bfloat16), x_h, preferred_element_type=jnp.float32)
            inter = split_dot_nt(c_mat, state_h) * (jnp.exp(l_col) * entry_col)
            mixed = intra + inter + skip_ref[h] * x_h.astype(jnp.float32)
            out_ref[:, lanes] = mixed.astype(jnp.bfloat16)
        ending = jnp.exp(l_col[BLOCK - 1 : BLOCK, :] - l_col) * dt_col * end_col
        weighted = (x_h.astype(jnp.float32) * ending).astype(jnp.bfloat16)
        block_state = lax.dot_general(
            weighted, b_mat, (((0,), (0,)), ((), ())), preferred_element_type=jnp.float32
        )
        state_ref[h] = decay_ref[blk * head_count + h] * state_h + block_state


def run_blocks(with_y, decay_flat, skip_gain, x, b_full, c_full, l, lt, dt, dtt, seg_row, seg_col,
               entry_col, entering):
    rows, width = x.shape
    head_count = l.shape[0]
    head_width = width // head_count
    n_size = b_full.shape[1]
    block_count = rows // BLOCK
    smem = pl.BlockSpec(memory_space=pltpu.SMEM)
    row_block = lambda cols: pl.BlockSpec((BLOCK, cols), lambda b: (b, 0))
    head_block = pl.BlockSpec((head_count, BLOCK), lambda b: (0, b))
    state_spec = pl.BlockSpec((head_count, head_width, n_size), lambda b: (0, 0, 0))
    state_shape = (head_count, head_width, n_size)
    kernel = functools.partial(block_kernel, with_y, head_count, head_width)
    params = pltpu.CompilerParams(dimension_semantics=("arbitrary",))
    if with_y:
        return pl.pallas_call(
            kernel,
            grid=(block_count,),
            in_specs=[smem, smem, row_block(width), row_block(n_size), row_block(n_size), head_block,
                      row_block(head_count), head_block, row_block(head_count),
                      pl.BlockSpec((1, BLOCK), lambda b: (0, b)), row_block(1), row_block(1),
                      state_spec],
            out_specs=row_block(width),
            out_shape=jax.ShapeDtypeStruct((rows, width), jnp.bfloat16),
            scratch_shapes=[pltpu.VMEM(state_shape, jnp.float32)],
            compiler_params=params,
        )(decay_flat, skip_gain, x, b_full, c_full, l, lt, dt, dtt, seg_row, seg_col, entry_col,
          entering)
    return pl.pallas_call(
        kernel,
        grid=(block_count,),
        in_specs=[smem, row_block(width), row_block(n_size), head_block, row_block(head_count),
                  row_block(head_count), row_block(1)],
        out_specs=state_spec,
        out_shape=jax.ShapeDtypeStruct(state_shape, jnp.float32),
        compiler_params=params,
    )(decay_flat, x, b_full, l, lt, dtt, seg_col)


def body(
    inner_input,
    state_input,
    conv_inner,
    bias_inner,
    conv_state,
    bias_state,
    step_size,
    decay_rate,
    skip_gain,
    lengths,
):
    precise = lax.Precision.HIGHEST
    own_rows = inner_input.shape[0]
    head_count = decay_rate.shape[0]
    group_half = state_input.shape[2]
    block_count = own_rows // BLOCK
    positions = lax.axis_index("seq") * own_rows + jnp.arange(own_rows + 3, dtype=jnp.int32) - 3
    seg_ext = segment_of(lengths, positions)
    inner_tail, state_tail = shifted((inner_input[-3:], state_input[:, -3:]), "seq", 1)
    weight_state = jnp.swapaxes(conv_state, 0, 1)[:, :, None, :]
    state_half = convolve(
        jnp.concatenate([state_tail, state_input], 1),
        weight_state,
        bias_state[:, None, :],
        seg_ext,
        own_rows,
    )
    partner = from_partner(state_half, "head", 0)
    inner_conv = convolve(
        jnp.concatenate([inner_tail, inner_input], 0), conv_inner, bias_inner, seg_ext, own_rows
    )
    lower_half = lax.axis_index("head") % 2 == 0
    state_full = jnp.where(
        lower_half,
        jnp.concatenate([state_half, partner], 2),
        jnp.concatenate([partner, state_half], 2),
    )
    b_full = state_full[0]
    c_full = state_full[1]
    steps_dt = step_size.reshape(head_count, block_count, BLOCK)
    upper = (
        lax.broadcasted_iota(jnp.int32, (BLOCK, BLOCK), 0)
        <= lax.broadcasted_iota(jnp.int32, (BLOCK, BLOCK), 1)
    ).astype(jnp.float32)
    log_decay = jnp.einsum(
        "hbs,st->hbt", -steps_dt * decay_rate[:, None, None], upper, precision=precise
    )
    seg_own = seg_ext[3:].reshape(block_count, BLOCK)
    seg_prev = seg_ext[2 : 2 + own_rows].reshape(block_count, BLOCK)[:, 0]
    block_decay = jnp.exp(log_decay[:, :, -1]) * (seg_own[:, -1] == seg_prev).astype(jnp.float32)[
        None
    ]
    decay_flat = jnp.transpose(block_decay).reshape(-1)
    l_flat = log_decay.reshape(head_count, own_rows)
    l_t = jnp.transpose(l_flat)
    dt_t = jnp.transpose(step_size)
    seg_row = seg_ext[3:].reshape(1, own_rows)
    seg_col = seg_ext[3:].reshape(own_rows, 1)
    entry_col = (seg_own == seg_prev[:, None]).astype(jnp.float32).reshape(own_rows, 1)

    local_end = run_blocks(
        False, decay_flat, None, inner_conv, b_full, None, l_flat, l_t, None, dt_t, None, seg_col,
        None, None
    )
    total_decay = jnp.prod(block_decay, axis=1)

    def relay(step_num, incoming):
        return shifted(
            (total_decay[:, None, None] * incoming + local_end).astype(jnp.bfloat16), "seq", 1
        ).astype(jnp.float32)

    incoming = lax.fori_loop(0, lax.axis_size("seq") - 1, relay, jnp.zeros_like(local_end))
    return run_blocks(
        True, decay_flat, skip_gain, inner_conv, b_full, c_full, l_flat, l_t, step_size, dt_t,
        seg_row, seg_col, entry_col, incoming
    )


def solution(mesh):
    return jax.shard_map(
        body,
        mesh=mesh,
        in_specs=(
            P(("grp", "seq"), "head"),
            P(None, ("grp", "seq"), "head"),
            P(None, "head"),
            P("head"),
            P(None, None, "head"),
            P(None, "head"),
            P("head", ("grp", "seq")),
            P("head"),
            P("head"),
            P("grp"),
        ),
        out_specs=P(("grp", "seq"), "head"),
        check_vma=False,
    )
```

```python
import functools

import jax
import jax.numpy as jnp
from jax import lax
from jax.experimental import pallas as pl
from jax.experimental.pallas import tpu as pltpu
from jax.sharding import PartitionSpec as P

BLOCK = 128


def shifted(value, axis, steps):
    count = lax.axis_size(axis)
    initial, last = (max(0, -steps), min(count, count - steps))
    return lax.ppermute(value, axis, [(source, source + steps) for source in range(initial, last)])


def from_partner(block, axis, stride):
    count = lax.axis_size(axis)
    route = []
    for low in range(count):
        high = low | 1 << stride
        if high != low and high < count:
            route += [(low, high), (high, low)]
    return lax.ppermute(block, axis, route)


def segment_of(lengths, positions):
    starts = jnp.cumsum(lengths, dtype=jnp.int32) - lengths
    covered = (starts[None, :] <= positions[:, None]).astype(jnp.int32)
    return jnp.sum(covered, axis=1, dtype=jnp.int32) - 1


def convolve(extended, weight, bias_row, seg_ext, row_count):
    own_seg = seg_ext[3:]
    summed = (
        jnp.zeros(extended.shape[:-2] + (row_count, extended.shape[-1]), jnp.float32) + bias_row
    )
    for offset in range(4):
        kept_mask = (seg_ext[offset : offset + row_count] == own_seg).astype(jnp.float32)[:, None]
        window = extended[..., offset : offset + row_count, :].astype(jnp.float32)
        summed = summed + weight[offset].astype(jnp.float32) * window * kept_mask
    return jax.nn.silu(summed).astype(jnp.bfloat16)


def split_dot(lhs, value):
    high = value.astype(jnp.bfloat16)
    low = (value - high.astype(jnp.float32)).astype(jnp.bfloat16)
    return jnp.dot(lhs, high, preferred_element_type=jnp.float32) + jnp.dot(
        lhs, low, preferred_element_type=jnp.float32
    )


def expand_heads(small, head_width):
    rows, heads = small.shape
    per_tile = 128 // head_width
    lane = lax.broadcasted_iota(jnp.int32, (rows, 128), 1) // head_width
    tiles = []
    for tile in range(heads // per_tile):
        picked = jnp.broadcast_to(small[:, tile * per_tile : tile * per_tile + 1], (rows, 128))
        for k in range(1, per_tile):
            column = small[:, tile * per_tile + k : tile * per_tile + k + 1]
            picked = jnp.where(lane == k, jnp.broadcast_to(column, (rows, 128)), picked)
        tiles.append(picked)
    return jnp.concatenate(tiles, axis=1)


def block_kernel(with_y, head_width, *refs):
    if with_y:
        (x_ref, bt_ref, b_ref, c_ref, l_ref, dt_ref, segr_ref, segc_ref, entry_ref, decay_ref,
         skip_ref, ein_ref, out_ref, state_ref) = refs
    else:
        (x_ref, bt_ref, l_ref, dt_ref, segc_ref, decay_ref, state_ref) = refs
    blk = pl.program_id(0)

    @pl.when(blk == 0)
    def _():
        if with_y:
            state_ref[...] = ein_ref[...]
        else:
            state_ref[...] = jnp.zeros(state_ref.shape, jnp.float32)

    seg_col = segc_ref[...]
    end_col = (seg_col == seg_col[BLOCK - 1 : BLOCK, :]).astype(jnp.float32)
    l_small = l_ref[...]
    dt_small = dt_ref[...]
    x = x_ref[...].astype(jnp.float32)
    state = state_ref[...]
    if with_y:
        c_mat = c_ref[...]
        seg_row = segr_ref[...]
        scores = lax.dot_general(
            c_mat, b_ref[...], (((1,), (1,)), ((), ())), preferred_element_type=jnp.float32
        )
        rows = lax.broadcasted_iota(jnp.int32, (BLOCK, BLOCK), 0)
        cols = lax.broadcasted_iota(jnp.int32, (BLOCK, BLOCK), 1)
        allowed = (rows >= cols) & (seg_col == seg_row)
        masked = jnp.where(allowed, scores, 0.0).astype(jnp.bfloat16)
        rising = expand_heads(jnp.exp(l_small), head_width)
        falling = expand_heads(jnp.exp(-l_small) * dt_small, head_width)
        intra = split_dot(masked, x * falling) * rising
        inter = split_dot(c_mat, state) * (rising * entry_ref[...])
        out_ref[...] = (intra + inter + skip_ref[...] * x).astype(jnp.bfloat16)
    ending = expand_heads(
        jnp.exp(l_small[BLOCK - 1 : BLOCK, :] - l_small) * dt_small * end_col, head_width
    )
    weighted = (x * ending).astype(jnp.bfloat16)
    state_ref[...] = decay_ref[0] * state + jnp.dot(
        bt_ref[...], weighted, preferred_element_type=jnp.float32
    )


def run_blocks(with_y, x, b_t, b_full, c_full, l_t, dt_t, seg_row, seg_col, entry_col, decay_x,
               skip_x, entering):
    rows, width = x.shape
    head_count = l_t.shape[1]
    head_width = width // head_count
    n_size = b_t.shape[0]
    block_count = rows // BLOCK
    row_block = lambda cols: pl.BlockSpec((BLOCK, cols), lambda b: (b, 0))
    bt_spec = pl.BlockSpec((n_size, BLOCK), lambda b: (0, b))
    decay_spec = pl.BlockSpec((1, 1, width), lambda b: (b, 0, 0))
    state_spec = pl.BlockSpec((n_size, width), lambda b: (0, 0))
    state_shape = jax.ShapeDtypeStruct((n_size, width), jnp.float32)
    kernel = functools.partial(block_kernel, with_y, head_width)
    params = pltpu.CompilerParams(dimension_semantics=("arbitrary",))
    if with_y:
        return pl.pallas_call(
            kernel,
            grid=(block_count,),
            in_specs=[row_block(width), bt_spec, row_block(n_size), row_block(n_size),
                      row_block(head_count), row_block(head_count),
                      pl.BlockSpec((1, BLOCK), lambda b: (0, b)), row_block(1), row_block(1),
                      decay_spec, pl.BlockSpec((1, width), lambda b: (0, 0)), state_spec],
            out_specs=row_block(width),
            out_shape=jax.ShapeDtypeStruct((rows, width), jnp.bfloat16),
            scratch_shapes=[pltpu.VMEM((n_size, width), jnp.float32)],
            compiler_params=params,
        )(x, b_t, b_full, c_full, l_t, dt_t, seg_row, seg_col, entry_col, decay_x, skip_x,
          entering)
    return pl.pallas_call(
        kernel,
        grid=(block_count,),
        in_specs=[row_block(width), bt_spec, row_block(head_count), row_block(head_count),
                  row_block(1), decay_spec],
        out_specs=state_spec,
        out_shape=state_shape,
        compiler_params=params,
    )(x, b_t, l_t, dt_t, seg_col, decay_x)


def body(
    inner_input,
    state_input,
    conv_inner,
    bias_inner,
    conv_state,
    bias_state,
    step_size,
    decay_rate,
    skip_gain,
    lengths,
):
    precise = lax.Precision.HIGHEST
    own_rows = inner_input.shape[0]
    head_count = decay_rate.shape[0]
    group_half = state_input.shape[2]
    block_count = own_rows // BLOCK
    positions = lax.axis_index("seq") * own_rows + jnp.arange(own_rows + 3, dtype=jnp.int32) - 3
    seg_ext = segment_of(lengths, positions)
    inner_tail, state_tail = shifted((inner_input[-3:], state_input[:, -3:]), "seq", 1)
    weight_state = jnp.swapaxes(conv_state, 0, 1)[:, :, None, :]
    state_half = convolve(
        jnp.concatenate([state_tail, state_input], 1),
        weight_state,
        bias_state[:, None, :],
        seg_ext,
        own_rows,
    )
    partner = from_partner(state_half, "head", 0)
    inner_conv = convolve(
        jnp.concatenate([inner_tail, inner_input], 0), conv_inner, bias_inner, seg_ext, own_rows
    )
    lower_half = lax.axis_index("head") % 2 == 0
    state_full = jnp.where(
        lower_half,
        jnp.concatenate([state_half, partner], 2),
        jnp.concatenate([partner, state_half], 2),
    )
    b_full = state_full[0]
    c_full = state_full[1]
    steps_dt = step_size.reshape(head_count, block_count, BLOCK)
    upper = (
        lax.broadcasted_iota(jnp.int32, (BLOCK, BLOCK), 0)
        <= lax.broadcasted_iota(jnp.int32, (BLOCK, BLOCK), 1)
    ).astype(jnp.float32)
    log_decay = jnp.einsum(
        "hbs,st->hbt", -steps_dt * decay_rate[:, None, None], upper, precision=precise
    )
    seg_own = seg_ext[3:].reshape(block_count, BLOCK)
    seg_prev = seg_ext[2 : 2 + own_rows].reshape(block_count, BLOCK)[:, 0]
    block_decay = jnp.exp(log_decay[:, :, -1]) * (seg_own[:, -1] == seg_prev).astype(jnp.float32)[
        None
    ]
    head_width = inner_input.shape[1] // head_count
    spread = lambda v: jnp.repeat(v, head_width, axis=-1)
    decay_x = spread(jnp.transpose(block_decay)).reshape(block_count, 1, -1)
    skip_x = spread(skip_gain).reshape(1, -1)
    l_t = jnp.transpose(log_decay.reshape(head_count, own_rows))
    dt_t = jnp.transpose(step_size)
    seg_row = seg_ext[3:].reshape(1, own_rows)
    seg_col = seg_ext[3:].reshape(own_rows, 1)
    entry_col = (seg_own == seg_prev[:, None]).astype(jnp.float32).reshape(own_rows, 1)
    b_t = jnp.transpose(b_full)

    local_end = run_blocks(
        False, inner_conv, b_t, None, None, l_t, dt_t, None, seg_col, None, decay_x, None, None
    )
    total_decay = spread(jnp.prod(block_decay, axis=1))[None, :]

    def relay(step_num, incoming):
        return shifted((total_decay * incoming + local_end).astype(jnp.bfloat16), "seq", 1).astype(
            jnp.float32
        )

    incoming = lax.fori_loop(0, lax.axis_size("seq") - 1, relay, jnp.zeros_like(local_end))
    return run_blocks(
        True, inner_conv, b_t, b_full, c_full, l_t, dt_t, seg_row, seg_col, entry_col, decay_x,
        skip_x, incoming
    )


def solution(mesh):
    return jax.shard_map(
        body,
        mesh=mesh,
        in_specs=(
            P(("grp", "seq"), "head"),
            P(None, ("grp", "seq"), "head"),
            P(None, "head"),
            P("head"),
            P(None, None, "head"),
            P(None, "head"),
            P("head", ("grp", "seq")),
            P("head"),
            P("head"),
            P("grp"),
        ),
        out_specs=P(("grp", "seq"), "head"),
        check_vma=False,
    )
```

```python
import functools

import jax
import jax.numpy as jnp
from jax import lax
from jax.experimental import pallas as pl
from jax.experimental.pallas import tpu as pltpu
from jax.sharding import PartitionSpec as P

BLOCK = 128


def shifted(value, axis, steps):
    count = lax.axis_size(axis)
    initial, last = (max(0, -steps), min(count, count - steps))
    return lax.ppermute(value, axis, [(source, source + steps) for source in range(initial, last)])


def from_partner(block, axis, stride):
    count = lax.axis_size(axis)
    route = []
    for low in range(count):
        high = low | 1 << stride
        if high != low and high < count:
            route += [(low, high), (high, low)]
    return lax.ppermute(block, axis, route)


def segment_of(lengths, positions):
    starts = jnp.cumsum(lengths, dtype=jnp.int32) - lengths
    covered = (starts[None, :] <= positions[:, None]).astype(jnp.int32)
    return jnp.sum(covered, axis=1, dtype=jnp.int32) - 1


def convolve(extended, weight, bias_row, seg_ext, row_count):
    own_seg = seg_ext[3:]
    summed = (
        jnp.zeros(extended.shape[:-2] + (row_count, extended.shape[-1]), jnp.float32) + bias_row
    )
    for offset in range(4):
        kept_mask = (seg_ext[offset : offset + row_count] == own_seg).astype(jnp.float32)[:, None]
        window = extended[..., offset : offset + row_count, :].astype(jnp.float32)
        summed = summed + weight[offset].astype(jnp.float32) * window * kept_mask
    return jax.nn.silu(summed).astype(jnp.bfloat16)


def split_dot(lhs, value):
    high = value.astype(jnp.bfloat16)
    low = (value - high.astype(jnp.float32)).astype(jnp.bfloat16)
    return jnp.dot(lhs, high, preferred_element_type=jnp.float32) + jnp.dot(
        lhs, low, preferred_element_type=jnp.float32
    )


def expand_heads(small, head_width):
    rows, heads = small.shape
    per_tile = 128 // head_width
    lane = lax.broadcasted_iota(jnp.int32, (rows, 128), 1) // head_width
    tiles = []
    for tile in range(heads // per_tile):
        picked = jnp.broadcast_to(small[:, tile * per_tile : tile * per_tile + 1], (rows, 128))
        for k in range(1, per_tile):
            column = small[:, tile * per_tile + k : tile * per_tile + k + 1]
            picked = jnp.where(lane == k, jnp.broadcast_to(column, (rows, 128)), picked)
        tiles.append(picked)
    return jnp.concatenate(tiles, axis=1)


def block_kernel(with_y, head_width, *refs):
    if with_y:
        (x_ref, bt_ref, b_ref, c_ref, l_ref, dt_ref, segr_ref, segc_ref, entry_ref, decay_ref,
         skip_ref, ein_ref, out_ref, state_ref) = refs
    else:
        (x_ref, bt_ref, l_ref, dt_ref, segc_ref, decay_ref, state_ref) = refs
    blk = pl.program_id(0)

    @pl.when(blk == 0)
    def _():
        if with_y:
            state_ref[...] = ein_ref[...]
        else:
            state_ref[...] = jnp.zeros(state_ref.shape, jnp.float32)

    seg_col = segc_ref[...]
    end_col = (seg_col == seg_col[BLOCK - 1 : BLOCK, :]).astype(jnp.float32)
    l_small = l_ref[...]
    dt_small = dt_ref[...]
    x = x_ref[...].astype(jnp.float32)
    state = state_ref[...]
    if with_y:
        c_mat = c_ref[...]
        seg_row = segr_ref[...]
        scores = lax.dot_general(
            c_mat, b_ref[...], (((1,), (1,)), ((), ())), preferred_element_type=jnp.float32
        )
        rows = lax.broadcasted_iota(jnp.int32, (BLOCK, BLOCK), 0)
        cols = lax.broadcasted_iota(jnp.int32, (BLOCK, BLOCK), 1)
        allowed = (rows >= cols) & (seg_col == seg_row)
        masked = jnp.where(allowed, scores, 0.0).astype(jnp.bfloat16)
        rising = expand_heads(jnp.exp(l_small), head_width)
        falling = expand_heads(jnp.exp(-l_small) * dt_small, head_width)
        intra = split_dot(masked, x * falling) * rising
        inter = split_dot(c_mat, state) * (rising * entry_ref[...])
        out_ref[...] = (intra + inter + skip_ref[...] * x).astype(jnp.bfloat16)
    ending = expand_heads(
        jnp.exp(l_small[BLOCK - 1 : BLOCK, :] - l_small) * dt_small * end_col, head_width
    )
    weighted = (x * ending).astype(jnp.bfloat16)
    state_ref[...] = decay_ref[0] * state + jnp.dot(
        bt_ref[...], weighted, preferred_element_type=jnp.float32
    )


def run_blocks(with_y, x, b_t, b_full, c_full, l_t, dt_t, seg_row, seg_col, entry_col, decay_x,
               skip_x, entering):
    rows, width = x.shape
    head_count = l_t.shape[1]
    head_width = width // head_count
    n_size = b_t.shape[0]
    block_count = rows // BLOCK
    row_block = lambda cols: pl.BlockSpec((BLOCK, cols), lambda b: (b, 0))
    bt_spec = pl.BlockSpec((n_size, BLOCK), lambda b: (0, b))
    decay_spec = pl.BlockSpec((1, 1, width), lambda b: (b, 0, 0))
    state_spec = pl.BlockSpec((n_size, width), lambda b: (0, 0))
    state_shape = jax.ShapeDtypeStruct((n_size, width), jnp.float32)
    kernel = functools.partial(block_kernel, with_y, head_width)
    params = pltpu.CompilerParams(dimension_semantics=("arbitrary",))
    if with_y:
        return pl.pallas_call(
            kernel,
            grid=(block_count,),
            in_specs=[row_block(width), bt_spec, row_block(n_size), row_block(n_size),
                      row_block(head_count), row_block(head_count),
                      pl.BlockSpec((1, BLOCK), lambda b: (0, b)), row_block(1), row_block(1),
                      decay_spec, pl.BlockSpec((1, width), lambda b: (0, 0)), state_spec],
            out_specs=row_block(width),
            out_shape=jax.ShapeDtypeStruct((rows, width), jnp.bfloat16),
            scratch_shapes=[pltpu.VMEM((n_size, width), jnp.float32)],
            compiler_params=params,
        )(x, b_t, b_full, c_full, l_t, dt_t, seg_row, seg_col, entry_col, decay_x, skip_x,
          entering)
    return pl.pallas_call(
        kernel,
        grid=(block_count,),
        in_specs=[row_block(width), bt_spec, row_block(head_count), row_block(head_count),
                  row_block(1), decay_spec],
        out_specs=state_spec,
        out_shape=state_shape,
        compiler_params=params,
    )(x, b_t, l_t, dt_t, seg_col, decay_x)


def body(
    inner_input,
    state_input,
    conv_inner,
    bias_inner,
    conv_state,
    bias_state,
    step_size,
    decay_rate,
    skip_gain,
    lengths,
):
    precise = lax.Precision.HIGHEST
    own_rows = inner_input.shape[0]
    head_count = decay_rate.shape[0]
    group_half = state_input.shape[2]
    block_count = own_rows // BLOCK
    positions = lax.axis_index("seq") * own_rows + jnp.arange(own_rows + 3, dtype=jnp.int32) - 3
    seg_ext = segment_of(lengths, positions)
    inner_tail, state_tail = shifted((inner_input[-3:], state_input[:, -3:]), "seq", 1)
    weight_state = jnp.swapaxes(conv_state, 0, 1)[:, :, None, :]
    state_half = convolve(
        jnp.concatenate([state_tail, state_input], 1),
        weight_state,
        bias_state[:, None, :],
        seg_ext,
        own_rows,
    )
    partner = from_partner(state_half, "head", 0)
    inner_conv = convolve(
        jnp.concatenate([inner_tail, inner_input], 0), conv_inner, bias_inner, seg_ext, own_rows
    )
    lower_half = lax.axis_index("head") % 2 == 0
    state_full = jnp.where(
        lower_half,
        jnp.concatenate([state_half, partner], 2),
        jnp.concatenate([partner, state_half], 2),
    )
    b_full = state_full[0]
    c_full = state_full[1]
    steps_dt = step_size.reshape(head_count, block_count, BLOCK)
    upper = (
        lax.broadcasted_iota(jnp.int32, (BLOCK, BLOCK), 0)
        <= lax.broadcasted_iota(jnp.int32, (BLOCK, BLOCK), 1)
    ).astype(jnp.float32)
    log_decay = jnp.einsum(
        "hbs,st->hbt", -steps_dt * decay_rate[:, None, None], upper, precision=precise
    )
    seg_own = seg_ext[3:].reshape(block_count, BLOCK)
    seg_prev = seg_ext[2 : 2 + own_rows].reshape(block_count, BLOCK)[:, 0]
    block_decay = jnp.exp(log_decay[:, :, -1]) * (seg_own[:, -1] == seg_prev).astype(jnp.float32)[
        None
    ]
    head_width = inner_input.shape[1] // head_count
    spread = lambda v: jnp.repeat(v, head_width, axis=-1)
    decay_x = spread(jnp.transpose(block_decay)).reshape(block_count, 1, -1)
    skip_x = spread(skip_gain).reshape(1, -1)
    l_t = jnp.transpose(log_decay.reshape(head_count, own_rows))
    dt_t = jnp.transpose(step_size)
    seg_row = seg_ext[3:].reshape(1, own_rows)
    seg_col = seg_ext[3:].reshape(own_rows, 1)
    entry_col = (seg_own == seg_prev[:, None]).astype(jnp.float32).reshape(own_rows, 1)
    b_t = jnp.transpose(b_full)

    local_end = run_blocks(
        False, inner_conv, b_t, None, None, l_t, dt_t, None, seg_col, None, decay_x, None, None
    )
    total_decay = spread(jnp.prod(block_decay, axis=1))[None, :]

    def relay(step_num, incoming):
        return shifted((total_decay * incoming + local_end).astype(jnp.bfloat16), "seq", 1).astype(
            jnp.float32
        )

    part_rows = own_rows * lax.axis_size("seq")
    hops = min(lax.axis_size("seq") - 1, -(-(part_rows // 2) // own_rows))
    incoming = jnp.zeros_like(local_end)
    for step_num in range(hops):
        incoming = relay(step_num, incoming)
    return run_blocks(
        True, inner_conv, b_t, b_full, c_full, l_t, dt_t, seg_row, seg_col, entry_col, decay_x,
        skip_x, incoming
    )


def solution(mesh):
    return jax.shard_map(
        body,
        mesh=mesh,
        in_specs=(
            P(("grp", "seq"), "head"),
            P(None, ("grp", "seq"), "head"),
            P(None, "head"),
            P("head"),
            P(None, None, "head"),
            P(None, "head"),
            P("head", ("grp", "seq")),
            P("head"),
            P("head"),
            P("grp"),
        ),
        out_specs=P(("grp", "seq"), "head"),
        check_vma=False,
    )
```

```python
import functools

import jax
import jax.numpy as jnp
from jax import lax
from jax.experimental import pallas as pl
from jax.experimental.pallas import tpu as pltpu
from jax.sharding import PartitionSpec as P

BLOCK = 128


def shifted(value, axis, steps):
    count = lax.axis_size(axis)
    initial, last = (max(0, -steps), min(count, count - steps))
    return lax.ppermute(value, axis, [(source, source + steps) for source in range(initial, last)])


def from_partner(block, axis, stride):
    count = lax.axis_size(axis)
    route = []
    for low in range(count):
        high = low | 1 << stride
        if high != low and high < count:
            route += [(low, high), (high, low)]
    return lax.ppermute(block, axis, route)


def segment_of(lengths, positions):
    starts = jnp.cumsum(lengths, dtype=jnp.int32) - lengths
    covered = (starts[None, :] <= positions[:, None]).astype(jnp.int32)
    return jnp.sum(covered, axis=1, dtype=jnp.int32) - 1


def convolve(extended, weight, bias_row, seg_ext, row_count):
    own_seg = seg_ext[3:]
    summed = (
        jnp.zeros(extended.shape[:-2] + (row_count, extended.shape[-1]), jnp.float32) + bias_row
    )
    for offset in range(4):
        kept_mask = (seg_ext[offset : offset + row_count] == own_seg).astype(jnp.float32)[:, None]
        window = extended[..., offset : offset + row_count, :].astype(jnp.float32)
        summed = summed + weight[offset].astype(jnp.float32) * window * kept_mask
    return jax.nn.silu(summed).astype(jnp.bfloat16)


def split_dot(lhs, value):
    high = value.astype(jnp.bfloat16)
    low = (value - high.astype(jnp.float32)).astype(jnp.bfloat16)
    return jnp.dot(lhs, high, preferred_element_type=jnp.float32) + jnp.dot(
        lhs, low, preferred_element_type=jnp.float32
    )


def expand_heads(small, head_width):
    rows, heads = small.shape
    per_tile = 128 // head_width
    lane = lax.broadcasted_iota(jnp.int32, (rows, 128), 1) // head_width
    tiles = []
    for tile in range(heads // per_tile):
        picked = jnp.broadcast_to(small[:, tile * per_tile : tile * per_tile + 1], (rows, 128))
        for k in range(1, per_tile):
            column = small[:, tile * per_tile + k : tile * per_tile + k + 1]
            picked = jnp.where(lane == k, jnp.broadcast_to(column, (rows, 128)), picked)
        tiles.append(picked)
    return jnp.concatenate(tiles, axis=1)


def block_kernel(with_y, head_width, *refs):
    if with_y:
        (x_ref, bt_ref, b_ref, c_ref, l_ref, dt_ref, segr_ref, segc_ref, entry_ref, decay_ref,
         skip_ref, out_ref, state_ref) = refs
    else:
        (x_ref, bt_ref, l_ref, dt_ref, segc_ref, decay_ref, state_ref) = refs
    blk = pl.program_id(0)

    @pl.when(blk == 0)
    def _():
        state_ref[...] = jnp.zeros(state_ref.shape, jnp.float32)

    seg_col = segc_ref[...]
    end_col = (seg_col == seg_col[BLOCK - 1 : BLOCK, :]).astype(jnp.float32)
    l_small = l_ref[...]
    dt_small = dt_ref[...]
    x = x_ref[...].astype(jnp.float32)
    state = state_ref[...]
    if with_y:
        c_mat = c_ref[...]
        seg_row = segr_ref[...]
        scores = lax.dot_general(
            c_mat, b_ref[...], (((1,), (1,)), ((), ())), preferred_element_type=jnp.float32
        )
        rows = lax.broadcasted_iota(jnp.int32, (BLOCK, BLOCK), 0)
        cols = lax.broadcasted_iota(jnp.int32, (BLOCK, BLOCK), 1)
        allowed = (rows >= cols) & (seg_col == seg_row)
        masked = jnp.where(allowed, scores, 0.0).astype(jnp.bfloat16)
        rising = expand_heads(jnp.exp(l_small), head_width)
        falling = expand_heads(jnp.exp(-l_small) * dt_small, head_width)
        intra = split_dot(masked, x * falling) * rising
        inter = split_dot(c_mat, state) * (rising * entry_ref[...])
        out_ref[...] = intra + inter + skip_ref[...] * x
    ending = expand_heads(
        jnp.exp(l_small[BLOCK - 1 : BLOCK, :] - l_small) * dt_small * end_col, head_width
    )
    weighted = (x * ending).astype(jnp.bfloat16)
    state_ref[...] = decay_ref[0] * state + jnp.dot(
        bt_ref[...], weighted, preferred_element_type=jnp.float32
    )


def correct_kernel(head_width, y_ref, c_ref, l_ref, entry_ref, prefix_ref, ein_ref, out_ref):
    rising = expand_heads(jnp.exp(l_ref[...]), head_width)
    carried = jnp.dot(c_ref[...], ein_ref[...], preferred_element_type=jnp.float32)
    out_ref[...] = (y_ref[...] + carried * (rising * entry_ref[...] * prefix_ref[0])).astype(
        jnp.bfloat16
    )


def run_correct(partial, c_full, l_t, entry_col, prefix_x, entering):
    rows, width = partial.shape
    head_count = l_t.shape[1]
    n_size = c_full.shape[1]
    row_block = lambda cols: pl.BlockSpec((BLOCK, cols), lambda b: (b, 0))
    return pl.pallas_call(
        functools.partial(correct_kernel, width // head_count),
        grid=(rows // BLOCK,),
        in_specs=[row_block(width), row_block(n_size), row_block(head_count), row_block(1),
                  pl.BlockSpec((1, 1, width), lambda b: (b, 0, 0)),
                  pl.BlockSpec((n_size, width), lambda b: (0, 0))],
        out_specs=row_block(width),
        out_shape=jax.ShapeDtypeStruct((rows, width), jnp.bfloat16),
        compiler_params=pltpu.CompilerParams(dimension_semantics=("arbitrary",)),
    )(partial, c_full, l_t, entry_col, prefix_x, entering)


def run_blocks(with_y, x, b_t, b_full, c_full, l_t, dt_t, seg_row, seg_col, entry_col, decay_x,
               skip_x):
    rows, width = x.shape
    head_count = l_t.shape[1]
    head_width = width // head_count
    n_size = b_t.shape[0]
    block_count = rows // BLOCK
    row_block = lambda cols: pl.BlockSpec((BLOCK, cols), lambda b: (b, 0))
    bt_spec = pl.BlockSpec((n_size, BLOCK), lambda b: (0, b))
    decay_spec = pl.BlockSpec((1, 1, width), lambda b: (b, 0, 0))
    state_spec = pl.BlockSpec((n_size, width), lambda b: (0, 0))
    state_shape = jax.ShapeDtypeStruct((n_size, width), jnp.float32)
    kernel = functools.partial(block_kernel, with_y, head_width)
    params = pltpu.CompilerParams(dimension_semantics=("arbitrary",))
    if with_y:
        return pl.pallas_call(
            kernel,
            grid=(block_count,),
            in_specs=[row_block(width), bt_spec, row_block(n_size), row_block(n_size),
                      row_block(head_count), row_block(head_count),
                      pl.BlockSpec((1, BLOCK), lambda b: (0, b)), row_block(1), row_block(1),
                      decay_spec, pl.BlockSpec((1, width), lambda b: (0, 0))],
            out_specs=row_block(width),
            out_shape=jax.ShapeDtypeStruct((rows, width), jnp.float32),
            scratch_shapes=[pltpu.VMEM((n_size, width), jnp.float32)],
            compiler_params=params,
        )(x, b_t, b_full, c_full, l_t, dt_t, seg_row, seg_col, entry_col, decay_x, skip_x)
    return pl.pallas_call(
        kernel,
        grid=(block_count,),
        in_specs=[row_block(width), bt_spec, row_block(head_count), row_block(head_count),
                  row_block(1), decay_spec],
        out_specs=state_spec,
        out_shape=state_shape,
        compiler_params=params,
    )(x, b_t, l_t, dt_t, seg_col, decay_x)


def body(
    inner_input,
    state_input,
    conv_inner,
    bias_inner,
    conv_state,
    bias_state,
    step_size,
    decay_rate,
    skip_gain,
    lengths,
):
    precise = lax.Precision.HIGHEST
    own_rows = inner_input.shape[0]
    head_count = decay_rate.shape[0]
    group_half = state_input.shape[2]
    block_count = own_rows // BLOCK
    positions = lax.axis_index("seq") * own_rows + jnp.arange(own_rows + 3, dtype=jnp.int32) - 3
    seg_ext = segment_of(lengths, positions)
    inner_tail, state_tail = shifted((inner_input[-3:], state_input[:, -3:]), "seq", 1)
    weight_state = jnp.swapaxes(conv_state, 0, 1)[:, :, None, :]
    state_half = convolve(
        jnp.concatenate([state_tail, state_input], 1),
        weight_state,
        bias_state[:, None, :],
        seg_ext,
        own_rows,
    )
    partner = from_partner(state_half, "head", 0)
    inner_conv = convolve(
        jnp.concatenate([inner_tail, inner_input], 0), conv_inner, bias_inner, seg_ext, own_rows
    )
    lower_half = lax.axis_index("head") % 2 == 0
    state_full = jnp.where(
        lower_half,
        jnp.concatenate([state_half, partner], 2),
        jnp.concatenate([partner, state_half], 2),
    )
    b_full = state_full[0]
    c_full = state_full[1]
    steps_dt = step_size.reshape(head_count, block_count, BLOCK)
    upper = (
        lax.broadcasted_iota(jnp.int32, (BLOCK, BLOCK), 0)
        <= lax.broadcasted_iota(jnp.int32, (BLOCK, BLOCK), 1)
    ).astype(jnp.float32)
    log_decay = jnp.einsum(
        "hbs,st->hbt", -steps_dt * decay_rate[:, None, None], upper, precision=precise
    )
    seg_own = seg_ext[3:].reshape(block_count, BLOCK)
    seg_prev = seg_ext[2 : 2 + own_rows].reshape(block_count, BLOCK)[:, 0]
    block_decay = jnp.exp(log_decay[:, :, -1]) * (seg_own[:, -1] == seg_prev).astype(jnp.float32)[
        None
    ]
    head_width = inner_input.shape[1] // head_count
    spread = lambda v: jnp.repeat(v, head_width, axis=-1)
    decay_x = spread(jnp.transpose(block_decay)).reshape(block_count, 1, -1)
    skip_x = spread(skip_gain).reshape(1, -1)
    l_t = jnp.transpose(log_decay.reshape(head_count, own_rows))
    dt_t = jnp.transpose(step_size)
    seg_row = seg_ext[3:].reshape(1, own_rows)
    seg_col = seg_ext[3:].reshape(own_rows, 1)
    entry_col = (seg_own == seg_prev[:, None]).astype(jnp.float32).reshape(own_rows, 1)
    b_t = jnp.transpose(b_full)

    local_end = run_blocks(
        False, inner_conv, b_t, None, None, l_t, dt_t, None, seg_col, None, decay_x, None
    )
    partial = run_blocks(
        True, inner_conv, b_t, b_full, c_full, l_t, dt_t, seg_row, seg_col, entry_col, decay_x,
        skip_x
    )
    prefix = [jnp.ones((head_count,), jnp.float32)]
    for blk in range(block_count - 1):
        prefix.append(prefix[-1] * block_decay[:, blk])
    prefix_x = spread(jnp.stack(prefix)).reshape(block_count, 1, -1)
    total_decay = spread(jnp.prod(block_decay, axis=1))[None, :]

    def relay(step_num, incoming):
        return shifted((total_decay * incoming.astype(jnp.float32) + local_end).astype(jnp.bfloat16),
                       "seq", 1)

    part_rows = own_rows * lax.axis_size("seq")
    hops = min(lax.axis_size("seq") - 1, -(-(part_rows // 2) // own_rows))
    incoming = jnp.zeros(local_end.shape, jnp.bfloat16)
    for step_num in range(hops):
        incoming = relay(step_num, incoming)
    return run_correct(partial, c_full, l_t, entry_col, prefix_x, incoming)


def solution(mesh):
    return jax.shard_map(
        body,
        mesh=mesh,
        in_specs=(
            P(("grp", "seq"), "head"),
            P(None, ("grp", "seq"), "head"),
            P(None, "head"),
            P("head"),
            P(None, None, "head"),
            P(None, "head"),
            P("head", ("grp", "seq")),
            P("head"),
            P("head"),
            P("grp"),
        ),
        out_specs=P(("grp", "seq"), "head"),
        check_vma=False,
    )
```

```python
import functools

import jax
import jax.numpy as jnp
from jax import lax
from jax.experimental import pallas as pl
from jax.experimental.pallas import tpu as pltpu
from jax.sharding import PartitionSpec as P

BLOCK = 128


def shifted(value, axis, steps):
    count = lax.axis_size(axis)
    initial, last = (max(0, -steps), min(count, count - steps))
    return lax.ppermute(value, axis, [(source, source + steps) for source in range(initial, last)])


def from_partner(block, axis, stride):
    count = lax.axis_size(axis)
    route = []
    for low in range(count):
        high = low | 1 << stride
        if high != low and high < count:
            route += [(low, high), (high, low)]
    return lax.ppermute(block, axis, route)


def segment_of(lengths, positions):
    starts = jnp.cumsum(lengths, dtype=jnp.int32) - lengths
    covered = (starts[None, :] <= positions[:, None]).astype(jnp.int32)
    return jnp.sum(covered, axis=1, dtype=jnp.int32) - 1


def convolve(extended, weight, bias_row, seg_ext, row_count):
    own_seg = seg_ext[3:]
    summed = (
        jnp.zeros(extended.shape[:-2] + (row_count, extended.shape[-1]), jnp.float32) + bias_row
    )
    for offset in range(4):
        kept_mask = (seg_ext[offset : offset + row_count] == own_seg).astype(jnp.float32)[:, None]
        window = extended[..., offset : offset + row_count, :].astype(jnp.float32)
        summed = summed + weight[offset].astype(jnp.float32) * window * kept_mask
    return jax.nn.silu(summed).astype(jnp.bfloat16)


def split_dot(lhs, value):
    high = value.astype(jnp.bfloat16)
    low = (value - high.astype(jnp.float32)).astype(jnp.bfloat16)
    return jnp.dot(lhs, high, preferred_element_type=jnp.float32) + jnp.dot(
        lhs, low, preferred_element_type=jnp.float32
    )


def expand_heads(small, head_width):
    rows, heads = small.shape
    per_tile = 128 // head_width
    lane = lax.broadcasted_iota(jnp.int32, (rows, 128), 1) // head_width
    tiles = []
    for tile in range(heads // per_tile):
        picked = jnp.broadcast_to(small[:, tile * per_tile : tile * per_tile + 1], (rows, 128))
        for k in range(1, per_tile):
            column = small[:, tile * per_tile + k : tile * per_tile + k + 1]
            picked = jnp.where(lane == k, jnp.broadcast_to(column, (rows, 128)), picked)
        tiles.append(picked)
    return jnp.concatenate(tiles, axis=1)


def block_kernel(with_y, head_width, *refs):
    if with_y:
        (x_ref, b_ref, c_ref, l_ref, dt_ref, segr_ref, segc_ref, entry_ref, decay_ref,
         skip_ref, ein_ref, out_ref, state_ref) = refs
    else:
        (x_ref, b_ref, l_ref, dt_ref, segc_ref, decay_ref, state_ref) = refs
    blk = pl.program_id(0)

    @pl.when(blk == 0)
    def _():
        if with_y:
            state_ref[...] = ein_ref[...]
        else:
            state_ref[...] = jnp.zeros(state_ref.shape, jnp.float32)

    seg_col = segc_ref[...]
    end_col = (seg_col == seg_col[BLOCK - 1 : BLOCK, :]).astype(jnp.float32)
    l_small = l_ref[...]
    dt_small = dt_ref[...]
    x = x_ref[...].astype(jnp.float32)
    state = state_ref[...]
    if with_y:
        c_mat = c_ref[...]
        seg_row = segr_ref[...]
        scores = lax.dot_general(
            c_mat, b_ref[...], (((1,), (1,)), ((), ())), preferred_element_type=jnp.float32
        )
        rows = lax.broadcasted_iota(jnp.int32, (BLOCK, BLOCK), 0)
        cols = lax.broadcasted_iota(jnp.int32, (BLOCK, BLOCK), 1)
        allowed = (rows >= cols) & (seg_col == seg_row)
        masked = jnp.where(allowed, scores, 0.0).astype(jnp.bfloat16)
        rising = expand_heads(jnp.exp(l_small), head_width)
        falling = expand_heads(jnp.exp(-l_small) * dt_small, head_width)
        intra = split_dot(masked, x * falling) * rising
        inter = split_dot(c_mat, state) * (rising * entry_ref[...])
        out_ref[...] = (intra + inter + skip_ref[...] * x).astype(jnp.bfloat16)
    ending = expand_heads(
        jnp.exp(l_small[BLOCK - 1 : BLOCK, :] - l_small) * dt_small * end_col, head_width
    )
    weighted = (x * ending).astype(jnp.bfloat16)
    state_ref[...] = decay_ref[0] * state + lax.dot_general(
        b_ref[...], weighted, (((0,), (0,)), ((), ())), preferred_element_type=jnp.float32
    )


def state_kernel(head_width, x_ref, b_ref, dt_ref, rate_ref, segc_ref, entry_ref, state_ref, l_ref,
                 dtt_ref, decay_ref, total_ref):
    blk = pl.program_id(0)

    @pl.when(blk == 0)
    def _():
        state_ref[...] = jnp.zeros(state_ref.shape, jnp.float32)
        total_ref[...] = jnp.ones(total_ref.shape, jnp.float32)

    rows = lax.broadcasted_iota(jnp.int32, (2 * BLOCK, BLOCK), 0)
    cols = lax.broadcasted_iota(jnp.int32, (2 * BLOCK, BLOCK), 1)
    picker = jnp.where(
        ((rows < BLOCK) & (rows >= cols)) | (rows - BLOCK == cols), 1.0, 0.0
    ).astype(jnp.bfloat16)
    rest = dt_ref[...]
    summed = None
    for _ in range(3):
        piece = rest.astype(jnp.bfloat16)
        part = lax.dot_general(
            picker, piece, (((1,), (1,)), ((), ())), preferred_element_type=jnp.float32
        )
        summed = part if summed is None else summed + part
        rest = rest - piece.astype(jnp.float32)
    l_small = -summed[:BLOCK] * rate_ref[...]
    dt_small = summed[BLOCK:]
    l_ref[...] = l_small
    dtt_ref[...] = dt_small
    seg_col = segc_ref[...]
    end_col = (seg_col == seg_col[BLOCK - 1 : BLOCK, :]).astype(jnp.float32)
    decay_x = expand_heads(
        jnp.exp(l_small[BLOCK - 1 : BLOCK, :]) * entry_ref[BLOCK - 1 : BLOCK, :], head_width
    )
    decay_ref[0] = decay_x
    total_ref[...] = total_ref[...] * decay_x
    ending = expand_heads(
        jnp.exp(l_small[BLOCK - 1 : BLOCK, :] - l_small) * dt_small * end_col, head_width
    )
    weighted = (x_ref[...].astype(jnp.float32) * ending).astype(jnp.bfloat16)
    state_ref[...] = decay_x * state_ref[...] + lax.dot_general(
        b_ref[...], weighted, (((0,), (0,)), ((), ())), preferred_element_type=jnp.float32
    )


def run_state(x, b_full, step_size, rate_row, seg_col, entry_col):
    rows, width = x.shape
    head_count = step_size.shape[0]
    n_size = b_full.shape[1]
    block_count = rows // BLOCK
    row_block = lambda cols: pl.BlockSpec((BLOCK, cols), lambda b: (b, 0))
    whole = lambda shape: pl.BlockSpec(shape, lambda b: (0,) * len(shape))
    return pl.pallas_call(
        functools.partial(state_kernel, width // head_count),
        grid=(block_count,),
        in_specs=[row_block(width), row_block(n_size),
                  pl.BlockSpec((head_count, BLOCK), lambda b: (0, b)), whole((1, head_count)),
                  row_block(1), row_block(1)],
        out_specs=[whole((n_size, width)), row_block(head_count), row_block(head_count),
                   pl.BlockSpec((1, 1, width), lambda b: (b, 0, 0)), whole((1, width))],
        out_shape=[jax.ShapeDtypeStruct((n_size, width), jnp.float32),
                   jax.ShapeDtypeStruct((rows, head_count), jnp.float32),
                   jax.ShapeDtypeStruct((rows, head_count), jnp.float32),
                   jax.ShapeDtypeStruct((block_count, 1, width), jnp.float32),
                   jax.ShapeDtypeStruct((1, width), jnp.float32)],
        compiler_params=pltpu.CompilerParams(dimension_semantics=("arbitrary",)),
    )(x, b_full, step_size, rate_row, seg_col, entry_col)


def run_blocks(with_y, x, b_full, c_full, l_t, dt_t, seg_row, seg_col, entry_col, decay_x,
               skip_x, entering):
    rows, width = x.shape
    head_count = l_t.shape[1]
    head_width = width // head_count
    n_size = b_full.shape[1]
    block_count = rows // BLOCK
    row_block = lambda cols: pl.BlockSpec((BLOCK, cols), lambda b: (b, 0))
    bt_spec = pl.BlockSpec((n_size, BLOCK), lambda b: (0, b))
    decay_spec = pl.BlockSpec((1, 1, width), lambda b: (b, 0, 0))
    state_spec = pl.BlockSpec((n_size, width), lambda b: (0, 0))
    state_shape = jax.ShapeDtypeStruct((n_size, width), jnp.float32)
    kernel = functools.partial(block_kernel, with_y, head_width)
    params = pltpu.CompilerParams(dimension_semantics=("arbitrary",))
    if with_y:
        return pl.pallas_call(
            kernel,
            grid=(block_count,),
            in_specs=[row_block(width), row_block(n_size), row_block(n_size),
                      row_block(head_count), row_block(head_count),
                      pl.BlockSpec((1, BLOCK), lambda b: (0, b)), row_block(1), row_block(1),
                      decay_spec, pl.BlockSpec((1, width), lambda b: (0, 0)), state_spec],
            out_specs=row_block(width),
            out_shape=jax.ShapeDtypeStruct((rows, width), jnp.bfloat16),
            scratch_shapes=[pltpu.VMEM((n_size, width), jnp.float32)],
            compiler_params=params,
        )(x, b_full, c_full, l_t, dt_t, seg_row, seg_col, entry_col, decay_x, skip_x,
          entering)
    return pl.pallas_call(
        kernel,
        grid=(block_count,),
        in_specs=[row_block(width), bt_spec, row_block(head_count), row_block(head_count),
                  row_block(1), decay_spec],
        out_specs=state_spec,
        out_shape=state_shape,
        compiler_params=params,
    )(x, b_t, l_t, dt_t, seg_col, decay_x)


def body(
    inner_input,
    state_input,
    conv_inner,
    bias_inner,
    conv_state,
    bias_state,
    step_size,
    decay_rate,
    skip_gain,
    lengths,
):
    own_rows = inner_input.shape[0]
    head_count = decay_rate.shape[0]
    group_half = state_input.shape[2]
    block_count = own_rows // BLOCK
    positions = lax.axis_index("seq") * own_rows + jnp.arange(own_rows + 3, dtype=jnp.int32) - 3
    seg_ext = segment_of(lengths, positions)
    width = inner_input.shape[1]
    tails = jnp.concatenate(
        [inner_input[-3:], jnp.transpose(state_input[:, -3:], (1, 0, 2)).reshape(3, -1)], 1
    )
    tails = shifted(tails, "seq", 1)
    inner_tail = tails[:, :width]
    state_tail = jnp.transpose(tails[:, width:].reshape(3, 2, group_half), (1, 0, 2))
    weight_state = jnp.swapaxes(conv_state, 0, 1)[:, :, None, :]
    state_half = convolve(
        jnp.concatenate([state_tail, state_input], 1),
        weight_state,
        bias_state[:, None, :],
        seg_ext,
        own_rows,
    )
    partner = from_partner(state_half, "head", 0)
    inner_conv = convolve(
        jnp.concatenate([inner_tail, inner_input], 0), conv_inner, bias_inner, seg_ext, own_rows
    )
    lower_half = lax.axis_index("head") % 2 == 0
    state_full = jnp.where(
        lower_half,
        jnp.concatenate([state_half, partner], 2),
        jnp.concatenate([partner, state_half], 2),
    )
    b_full = state_full[0]
    c_full = state_full[1]
    head_width = inner_input.shape[1] // head_count
    spread = lambda v: jnp.repeat(v, head_width, axis=-1)
    skip_x = spread(skip_gain).reshape(1, -1)
    seg_own = seg_ext[3:].reshape(block_count, BLOCK)
    seg_prev = seg_ext[2 : 2 + own_rows].reshape(block_count, BLOCK)[:, 0]
    seg_row = seg_ext[3:].reshape(1, own_rows)
    seg_col = seg_ext[3:].reshape(own_rows, 1)
    entry_col = (seg_own == seg_prev[:, None]).astype(jnp.float32).reshape(own_rows, 1)

    local_end, l_t, dt_t, decay_x, total_decay = run_state(
        inner_conv, b_full, step_size, decay_rate.reshape(1, -1), seg_col, entry_col
    )

    def relay(step_num, incoming):
        return shifted((total_decay * incoming + local_end).astype(jnp.bfloat16), "seq", 1).astype(
            jnp.float32
        )

    part_rows = own_rows * lax.axis_size("seq")
    hops = min(lax.axis_size("seq") - 1, -(-(part_rows // 2) // own_rows))
    incoming = jnp.zeros_like(local_end)
    for step_num in range(hops):
        incoming = relay(step_num, incoming)
    return run_blocks(
        True, inner_conv, b_full, c_full, l_t, dt_t, seg_row, seg_col, entry_col, decay_x,
        skip_x, incoming
    )


def solution(mesh):
    return jax.shard_map(
        body,
        mesh=mesh,
        in_specs=(
            P(("grp", "seq"), "head"),
            P(None, ("grp", "seq"), "head"),
            P(None, "head"),
            P("head"),
            P(None, None, "head"),
            P(None, "head"),
            P("head", ("grp", "seq")),
            P("head"),
            P("head"),
            P("grp"),
        ),
        out_specs=P(("grp", "seq"), "head"),
        check_vma=False,
    )
```

```python
import functools

import jax
import jax.numpy as jnp
from jax import lax
from jax.experimental import pallas as pl
from jax.experimental.pallas import tpu as pltpu
from jax.sharding import PartitionSpec as P

BLOCK = 128


def shifted(value, axis, steps):
    count = lax.axis_size(axis)
    initial, last = (max(0, -steps), min(count, count - steps))
    return lax.ppermute(value, axis, [(source, source + steps) for source in range(initial, last)])


def from_partner(block, axis, stride):
    count = lax.axis_size(axis)
    route = []
    for low in range(count):
        high = low | 1 << stride
        if high != low and high < count:
            route += [(low, high), (high, low)]
    return lax.ppermute(block, axis, route)


def segment_of(lengths, positions):
    starts = jnp.cumsum(lengths, dtype=jnp.int32) - lengths
    covered = (starts[None, :] <= positions[:, None]).astype(jnp.int32)
    return jnp.sum(covered, axis=1, dtype=jnp.int32) - 1


def convolve(extended, weight, bias_row, seg_ext, row_count):
    own_seg = seg_ext[3:]
    summed = (
        jnp.zeros(extended.shape[:-2] + (row_count, extended.shape[-1]), jnp.float32) + bias_row
    )
    for offset in range(4):
        kept_mask = (seg_ext[offset : offset + row_count] == own_seg).astype(jnp.float32)[:, None]
        window = extended[..., offset : offset + row_count, :].astype(jnp.float32)
        summed = summed + weight[offset].astype(jnp.float32) * window * kept_mask
    return jax.nn.silu(summed).astype(jnp.bfloat16)


def split_dot(lhs, value):
    high = value.astype(jnp.bfloat16)
    low = (value - high.astype(jnp.float32)).astype(jnp.bfloat16)
    return jnp.dot(lhs, high, preferred_element_type=jnp.float32) + jnp.dot(
        lhs, low, preferred_element_type=jnp.float32
    )


def expand_heads(small, head_width):
    rows, heads = small.shape
    per_tile = 128 // head_width
    lane = lax.broadcasted_iota(jnp.int32, (rows, 128), 1) // head_width
    tiles = []
    for tile in range(heads // per_tile):
        picked = jnp.broadcast_to(small[:, tile * per_tile : tile * per_tile + 1], (rows, 128))
        for k in range(1, per_tile):
            column = small[:, tile * per_tile + k : tile * per_tile + k + 1]
            picked = jnp.where(lane == k, jnp.broadcast_to(column, (rows, 128)), picked)
        tiles.append(picked)
    return jnp.concatenate(tiles, axis=1)


def block_kernel(with_y, head_width, *refs):
    if with_y:
        (x_ref, b_ref, c_ref, l_ref, dt_ref, segr_ref, segc_ref, entry_ref, decay_ref,
         skip_ref, out_ref, state_ref) = refs
    else:
        (x_ref, b_ref, l_ref, dt_ref, segc_ref, decay_ref, state_ref) = refs
    blk = pl.program_id(0)

    @pl.when(blk == 0)
    def _():
        state_ref[...] = jnp.zeros(state_ref.shape, jnp.float32)

    seg_col = segc_ref[...]
    end_col = (seg_col == seg_col[BLOCK - 1 : BLOCK, :]).astype(jnp.float32)
    l_small = l_ref[...]
    dt_small = dt_ref[...]
    x = x_ref[...].astype(jnp.float32)
    state = state_ref[...]
    if with_y:
        c_mat = c_ref[...]
        seg_row = segr_ref[...]
        scores = lax.dot_general(
            c_mat, b_ref[...], (((1,), (1,)), ((), ())), preferred_element_type=jnp.float32
        )
        rows = lax.broadcasted_iota(jnp.int32, (BLOCK, BLOCK), 0)
        cols = lax.broadcasted_iota(jnp.int32, (BLOCK, BLOCK), 1)
        allowed = (rows >= cols) & (seg_col == seg_row)
        masked = jnp.where(allowed, scores, 0.0).astype(jnp.bfloat16)
        rising = expand_heads(jnp.exp(l_small), head_width)
        falling = expand_heads(jnp.exp(-l_small) * dt_small, head_width)
        intra = split_dot(masked, x * falling) * rising
        inter = split_dot(c_mat, state) * (rising * entry_ref[...])
        out_ref[...] = intra + inter + skip_ref[...] * x
    ending = expand_heads(
        jnp.exp(l_small[BLOCK - 1 : BLOCK, :] - l_small) * dt_small * end_col, head_width
    )
    weighted = (x * ending).astype(jnp.bfloat16)
    state_ref[...] = decay_ref[0] * state + lax.dot_general(
        b_ref[...], weighted, (((0,), (0,)), ((), ())), preferred_element_type=jnp.float32
    )


def state_kernel(head_width, x_ref, b_ref, dt_ref, rate_ref, segc_ref, entry_ref, state_ref, l_ref,
                 dtt_ref, decay_ref, total_ref):
    blk = pl.program_id(0)

    @pl.when(blk == 0)
    def _():
        state_ref[...] = jnp.zeros(state_ref.shape, jnp.float32)
        total_ref[...] = jnp.ones(total_ref.shape, jnp.float32)

    rows = lax.broadcasted_iota(jnp.int32, (2 * BLOCK, BLOCK), 0)
    cols = lax.broadcasted_iota(jnp.int32, (2 * BLOCK, BLOCK), 1)
    picker = jnp.where(
        ((rows < BLOCK) & (rows >= cols)) | (rows - BLOCK == cols), 1.0, 0.0
    ).astype(jnp.bfloat16)
    rest = dt_ref[...]
    summed = None
    for _ in range(3):
        piece = rest.astype(jnp.bfloat16)
        part = lax.dot_general(
            picker, piece, (((1,), (1,)), ((), ())), preferred_element_type=jnp.float32
        )
        summed = part if summed is None else summed + part
        rest = rest - piece.astype(jnp.float32)
    l_small = -summed[:BLOCK] * rate_ref[...]
    dt_small = summed[BLOCK:]
    l_ref[...] = l_small
    dtt_ref[...] = dt_small
    seg_col = segc_ref[...]
    end_col = (seg_col == seg_col[BLOCK - 1 : BLOCK, :]).astype(jnp.float32)
    decay_x = expand_heads(
        jnp.exp(l_small[BLOCK - 1 : BLOCK, :]) * entry_ref[BLOCK - 1 : BLOCK, :], head_width
    )
    decay_ref[0] = decay_x
    total_ref[...] = total_ref[...] * decay_x
    ending = expand_heads(
        jnp.exp(l_small[BLOCK - 1 : BLOCK, :] - l_small) * dt_small * end_col, head_width
    )
    weighted = (x_ref[...].astype(jnp.float32) * ending).astype(jnp.bfloat16)
    state_ref[...] = decay_x * state_ref[...] + lax.dot_general(
        b_ref[...], weighted, (((0,), (0,)), ((), ())), preferred_element_type=jnp.float32
    )


def run_state(x, b_full, step_size, rate_row, seg_col, entry_col):
    rows, width = x.shape
    head_count = step_size.shape[0]
    n_size = b_full.shape[1]
    block_count = rows // BLOCK
    row_block = lambda cols: pl.BlockSpec((BLOCK, cols), lambda b: (b, 0))
    whole = lambda shape: pl.BlockSpec(shape, lambda b: (0,) * len(shape))
    return pl.pallas_call(
        functools.partial(state_kernel, width // head_count),
        grid=(block_count,),
        in_specs=[row_block(width), row_block(n_size),
                  pl.BlockSpec((head_count, BLOCK), lambda b: (0, b)), whole((1, head_count)),
                  row_block(1), row_block(1)],
        out_specs=[whole((n_size, width)), row_block(head_count), row_block(head_count),
                   pl.BlockSpec((1, 1, width), lambda b: (b, 0, 0)), whole((1, width))],
        out_shape=[jax.ShapeDtypeStruct((n_size, width), jnp.float32),
                   jax.ShapeDtypeStruct((rows, head_count), jnp.float32),
                   jax.ShapeDtypeStruct((rows, head_count), jnp.float32),
                   jax.ShapeDtypeStruct((block_count, 1, width), jnp.float32),
                   jax.ShapeDtypeStruct((1, width), jnp.float32)],
        compiler_params=pltpu.CompilerParams(dimension_semantics=("arbitrary",)),
    )(x, b_full, step_size, rate_row, seg_col, entry_col)


def correct_kernel(head_width, y_ref, c_ref, l_ref, entry_ref, prefix_ref, ein_ref, out_ref):
    rows, cols = y_ref.shape
    rising = expand_heads(jnp.exp(l_ref[0]), head_width)
    blocks = prefix_ref.shape[0]
    prefix = jnp.broadcast_to(prefix_ref[...], (blocks, BLOCK, cols)).reshape(rows, cols)
    carried = jnp.dot(c_ref[...], ein_ref[...], preferred_element_type=jnp.float32)
    out_ref[...] = (y_ref[...] + carried * (rising * entry_ref[...] * prefix)).astype(jnp.bfloat16)


def run_correct(partial, c_full, l_t, entry_col, prefix_x, entering):
    rows, width = partial.shape
    head_count = l_t.shape[1]
    head_width = width // head_count
    n_size = c_full.shape[1]
    tile = 256
    tiles = width // tile
    heads_per = tile // head_width
    l_tiles = jnp.transpose(l_t.reshape(rows, tiles, heads_per), (1, 0, 2))
    block_count = prefix_x.shape[0]
    return pl.pallas_call(
        functools.partial(correct_kernel, head_width),
        grid=(tiles,),
        in_specs=[pl.BlockSpec((rows, tile), lambda j: (0, j)),
                  pl.BlockSpec((rows, n_size), lambda j: (0, 0)),
                  pl.BlockSpec((1, rows, heads_per), lambda j: (j, 0, 0)),
                  pl.BlockSpec((rows, 1), lambda j: (0, 0)),
                  pl.BlockSpec((block_count, 1, tile), lambda j: (0, 0, j)),
                  pl.BlockSpec((n_size, tile), lambda j: (0, j))],
        out_specs=pl.BlockSpec((rows, tile), lambda j: (0, j)),
        out_shape=jax.ShapeDtypeStruct((rows, width), jnp.bfloat16),
        compiler_params=pltpu.CompilerParams(dimension_semantics=("arbitrary",)),
    )(partial, c_full, l_tiles, entry_col, prefix_x, entering)


def run_blocks(with_y, x, b_full, c_full, l_t, dt_t, seg_row, seg_col, entry_col, decay_x,
               skip_x):
    rows, width = x.shape
    head_count = l_t.shape[1]
    head_width = width // head_count
    n_size = b_full.shape[1]
    block_count = rows // BLOCK
    row_block = lambda cols: pl.BlockSpec((BLOCK, cols), lambda b: (b, 0))
    bt_spec = pl.BlockSpec((n_size, BLOCK), lambda b: (0, b))
    decay_spec = pl.BlockSpec((1, 1, width), lambda b: (b, 0, 0))
    state_spec = pl.BlockSpec((n_size, width), lambda b: (0, 0))
    state_shape = jax.ShapeDtypeStruct((n_size, width), jnp.float32)
    kernel = functools.partial(block_kernel, with_y, head_width)
    params = pltpu.CompilerParams(dimension_semantics=("arbitrary",))
    if with_y:
        return pl.pallas_call(
            kernel,
            grid=(block_count,),
            in_specs=[row_block(width), row_block(n_size), row_block(n_size),
                      row_block(head_count), row_block(head_count),
                      pl.BlockSpec((1, BLOCK), lambda b: (0, b)), row_block(1), row_block(1),
                      decay_spec, pl.BlockSpec((1, width), lambda b: (0, 0))],
            out_specs=row_block(width),
            out_shape=jax.ShapeDtypeStruct((rows, width), jnp.float32),
            scratch_shapes=[pltpu.VMEM((n_size, width), jnp.float32)],
            compiler_params=params,
        )(x, b_full, c_full, l_t, dt_t, seg_row, seg_col, entry_col, decay_x, skip_x)
    return pl.pallas_call(
        kernel,
        grid=(block_count,),
        in_specs=[row_block(width), bt_spec, row_block(head_count), row_block(head_count),
                  row_block(1), decay_spec],
        out_specs=state_spec,
        out_shape=state_shape,
        compiler_params=params,
    )(x, b_t, l_t, dt_t, seg_col, decay_x)


def body(
    inner_input,
    state_input,
    conv_inner,
    bias_inner,
    conv_state,
    bias_state,
    step_size,
    decay_rate,
    skip_gain,
    lengths,
):
    own_rows = inner_input.shape[0]
    head_count = decay_rate.shape[0]
    group_half = state_input.shape[2]
    block_count = own_rows // BLOCK
    positions = lax.axis_index("seq") * own_rows + jnp.arange(own_rows + 3, dtype=jnp.int32) - 3
    seg_ext = segment_of(lengths, positions)
    width = inner_input.shape[1]
    tails = jnp.concatenate(
        [inner_input[-3:], jnp.transpose(state_input[:, -3:], (1, 0, 2)).reshape(3, -1)], 1
    )
    tails = shifted(tails, "seq", 1)
    inner_tail = tails[:, :width]
    state_tail = jnp.transpose(tails[:, width:].reshape(3, 2, group_half), (1, 0, 2))
    weight_state = jnp.swapaxes(conv_state, 0, 1)[:, :, None, :]
    state_half = convolve(
        jnp.concatenate([state_tail, state_input], 1),
        weight_state,
        bias_state[:, None, :],
        seg_ext,
        own_rows,
    )
    partner = from_partner(state_half, "head", 0)
    inner_conv = convolve(
        jnp.concatenate([inner_tail, inner_input], 0), conv_inner, bias_inner, seg_ext, own_rows
    )
    lower_half = lax.axis_index("head") % 2 == 0
    state_full = jnp.where(
        lower_half,
        jnp.concatenate([state_half, partner], 2),
        jnp.concatenate([partner, state_half], 2),
    )
    b_full = state_full[0]
    c_full = state_full[1]
    head_width = inner_input.shape[1] // head_count
    spread = lambda v: jnp.repeat(v, head_width, axis=-1)
    skip_x = spread(skip_gain).reshape(1, -1)
    seg_own = seg_ext[3:].reshape(block_count, BLOCK)
    seg_prev = seg_ext[2 : 2 + own_rows].reshape(block_count, BLOCK)[:, 0]
    seg_row = seg_ext[3:].reshape(1, own_rows)
    seg_col = seg_ext[3:].reshape(own_rows, 1)
    entry_col = (seg_own == seg_prev[:, None]).astype(jnp.float32).reshape(own_rows, 1)

    local_end, l_t, dt_t, decay_x, total_decay = run_state(
        inner_conv, b_full, step_size, decay_rate.reshape(1, -1), seg_col, entry_col
    )

    partial = run_blocks(
        True, inner_conv, b_full, c_full, l_t, dt_t, seg_row, seg_col, entry_col, decay_x, skip_x
    )
    prefix = [jnp.ones((1, 1, decay_x.shape[2]), jnp.float32)]
    for blk in range(block_count - 1):
        prefix.append(prefix[-1] * decay_x[blk : blk + 1])
    prefix_x = jnp.concatenate(prefix, 0)

    def relay(step_num, incoming):
        return shifted((total_decay * incoming.astype(jnp.float32) + local_end).astype(jnp.bfloat16),
                       "seq", 1)

    part_rows = own_rows * lax.axis_size("seq")
    hops = min(lax.axis_size("seq") - 1, -(-(part_rows // 2) // own_rows))
    incoming = jnp.zeros(local_end.shape, jnp.bfloat16)
    for step_num in range(hops):
        incoming = relay(step_num, incoming)
        if step_num == 0:
            incoming, partial = lax.optimization_barrier((incoming, partial))
    return run_correct(partial, c_full, l_t, entry_col, prefix_x, incoming)


def solution(mesh):
    return jax.shard_map(
        body,
        mesh=mesh,
        in_specs=(
            P(("grp", "seq"), "head"),
            P(None, ("grp", "seq"), "head"),
            P(None, "head"),
            P("head"),
            P(None, None, "head"),
            P(None, "head"),
            P("head", ("grp", "seq")),
            P("head"),
            P("head"),
            P("grp"),
        ),
        out_specs=P(("grp", "seq"), "head"),
        check_vma=False,
    )
```

```python
import functools

import jax
import jax.numpy as jnp
from jax import lax
from jax.experimental import pallas as pl
from jax.experimental.pallas import tpu as pltpu
from jax.sharding import PartitionSpec as P

BLOCK = 128


def shifted(value, axis, steps):
    count = lax.axis_size(axis)
    initial, last = (max(0, -steps), min(count, count - steps))
    return lax.ppermute(value, axis, [(source, source + steps) for source in range(initial, last)])


def from_partner(block, axis, stride):
    count = lax.axis_size(axis)
    route = []
    for low in range(count):
        high = low | 1 << stride
        if high != low and high < count:
            route += [(low, high), (high, low)]
    return lax.ppermute(block, axis, route)


def segment_of(lengths, positions):
    starts = jnp.cumsum(lengths, dtype=jnp.int32) - lengths
    covered = (starts[None, :] <= positions[:, None]).astype(jnp.int32)
    return jnp.sum(covered, axis=1, dtype=jnp.int32) - 1


def convolve(extended, weight, bias_row, seg_ext, row_count):
    own_seg = seg_ext[3:]
    summed = (
        jnp.zeros(extended.shape[:-2] + (row_count, extended.shape[-1]), jnp.float32) + bias_row
    )
    for offset in range(4):
        kept_mask = (seg_ext[offset : offset + row_count] == own_seg).astype(jnp.float32)[:, None]
        window = extended[..., offset : offset + row_count, :].astype(jnp.float32)
        summed = summed + weight[offset].astype(jnp.float32) * window * kept_mask
    return jax.nn.silu(summed).astype(jnp.bfloat16)


def split_dot(lhs, value):
    high = value.astype(jnp.bfloat16)
    low = (value - high.astype(jnp.float32)).astype(jnp.bfloat16)
    return jnp.dot(lhs, high, preferred_element_type=jnp.float32) + jnp.dot(
        lhs, low, preferred_element_type=jnp.float32
    )


def expand_heads(small, head_width):
    rows, heads = small.shape
    per_tile = 128 // head_width
    lane = lax.broadcasted_iota(jnp.int32, (rows, 128), 1) // head_width
    tiles = []
    for tile in range(heads // per_tile):
        picked = jnp.broadcast_to(small[:, tile * per_tile : tile * per_tile + 1], (rows, 128))
        for k in range(1, per_tile):
            column = small[:, tile * per_tile + k : tile * per_tile + k + 1]
            picked = jnp.where(lane == k, jnp.broadcast_to(column, (rows, 128)), picked)
        tiles.append(picked)
    return jnp.concatenate(tiles, axis=1)


def block_kernel(with_y, head_width, *refs):
    if with_y:
        (x_ref, b_ref, c_ref, l_ref, dt_ref, segr_ref, info_ref, decay_ref,
         skip_ref, ein_ref, out_ref, state_ref) = refs
    else:
        (x_ref, b_ref, l_ref, dt_ref, segc_ref, decay_ref, state_ref) = refs
    blk = pl.program_id(0)

    @pl.when(blk == 0)
    def _():
        if with_y:
            state_ref[...] = ein_ref[...]
        else:
            state_ref[...] = jnp.zeros(state_ref.shape, jnp.float32)

    info = info_ref[...]
    seg_col = info[:, 0:1]
    end_col = (seg_col == seg_col[BLOCK - 1 : BLOCK, :]).astype(jnp.float32)
    l_small = l_ref[...]
    dt_small = dt_ref[...]
    x = x_ref[...].astype(jnp.float32)
    state = state_ref[...]
    if with_y:
        c_mat = c_ref[...]
        seg_row = segr_ref[...]
        scores = lax.dot_general(
            c_mat, b_ref[...], (((1,), (1,)), ((), ())), preferred_element_type=jnp.float32
        )
        rows = lax.broadcasted_iota(jnp.int32, (BLOCK, BLOCK), 0)
        cols = lax.broadcasted_iota(jnp.int32, (BLOCK, BLOCK), 1)
        allowed = (rows >= cols) & (seg_col == seg_row)
        masked = jnp.where(allowed, scores, 0.0).astype(jnp.bfloat16)
        rising = expand_heads(jnp.exp(l_small), head_width)
        falling = expand_heads(jnp.exp(-l_small) * dt_small, head_width)
        intra = split_dot(masked, x * falling) * rising
        inter = split_dot(c_mat, state) * (rising * info[:, 1:2])
        out_ref[...] = (intra + inter + skip_ref[...] * x).astype(jnp.bfloat16)
    ending = expand_heads(
        jnp.exp(l_small[BLOCK - 1 : BLOCK, :] - l_small) * dt_small * end_col, head_width
    )
    weighted = (x * ending).astype(jnp.bfloat16)
    state_ref[...] = decay_ref[0] * state + lax.dot_general(
        b_ref[...], weighted, (((0,), (0,)), ((), ())), preferred_element_type=jnp.float32
    )


def state_kernel(head_width, x_ref, tail_ref, wconv_ref, bias_ref, b_ref, dt_ref, rate_ref,
                 info_ref, state_ref, l_ref, dtt_ref, decay_ref, total_ref, xc_ref, prev_ref):
    blk = pl.program_id(0)

    @pl.when(blk == 0)
    def _():
        state_ref[...] = jnp.zeros(state_ref.shape, jnp.float32)
        total_ref[...] = jnp.ones(total_ref.shape, jnp.float32)
        prev_ref[...] = tail_ref[...].astype(jnp.float32)

    info = info_ref[...]
    raw = x_ref[...].astype(jnp.float32)
    prev = prev_ref[...]
    top_row = lax.broadcasted_iota(jnp.int32, prev.shape, 0)
    summed = jnp.zeros(raw.shape, jnp.float32) + bias_ref[...]
    for offset in range(4):
        back = 3 - offset
        if back == 0:
            window = raw
        else:
            rolled = pltpu.roll(raw, back, 0)
            top = jnp.where(top_row < back, pltpu.roll(prev, back, 0), rolled[:8])
            window = jnp.concatenate([top, rolled[8:]], 0) * info[:, 1 + back : 2 + back]
        summed = summed + wconv_ref[offset : offset + 1, :] * window
    prev_ref[...] = raw[BLOCK - 8 :]
    xc = jax.nn.silu(summed).astype(jnp.bfloat16)
    xc_ref[...] = xc

    rows = lax.broadcasted_iota(jnp.int32, (2 * BLOCK, BLOCK), 0)
    cols = lax.broadcasted_iota(jnp.int32, (2 * BLOCK, BLOCK), 1)
    picker = jnp.where(
        ((rows < BLOCK) & (rows >= cols)) | (rows - BLOCK == cols), 1.0, 0.0
    ).astype(jnp.bfloat16)
    rest = dt_ref[...]
    cum = None
    for _ in range(3):
        piece = rest.astype(jnp.bfloat16)
        part = lax.dot_general(
            picker, piece, (((1,), (1,)), ((), ())), preferred_element_type=jnp.float32
        )
        cum = part if cum is None else cum + part
        rest = rest - piece.astype(jnp.float32)
    l_small = -cum[:BLOCK] * rate_ref[...]
    dt_small = cum[BLOCK:]
    l_ref[...] = l_small
    dtt_ref[...] = dt_small
    seg_col = info[:, 0:1]
    end_col = (seg_col == seg_col[BLOCK - 1 : BLOCK, :]).astype(jnp.float32)
    decay_x = expand_heads(
        jnp.exp(l_small[BLOCK - 1 : BLOCK, :]) * info[BLOCK - 1 : BLOCK, 1:2], head_width
    )
    decay_ref[0] = decay_x
    total_ref[...] = total_ref[...] * decay_x
    ending = expand_heads(
        jnp.exp(l_small[BLOCK - 1 : BLOCK, :] - l_small) * dt_small * end_col, head_width
    )
    weighted = (xc.astype(jnp.float32) * ending).astype(jnp.bfloat16)
    state_ref[...] = decay_x * state_ref[...] + lax.dot_general(
        b_ref[...], weighted, (((0,), (0,)), ((), ())), preferred_element_type=jnp.float32
    )


def run_state(x, tail8, wconv, bias_row, b_full, step_size, rate_row, info):
    rows, width = x.shape
    head_count = step_size.shape[0]
    n_size = b_full.shape[1]
    block_count = rows // BLOCK
    row_block = lambda cols: pl.BlockSpec((BLOCK, cols), lambda b: (b, 0))
    whole = lambda shape: pl.BlockSpec(shape, lambda b: (0,) * len(shape))
    return pl.pallas_call(
        functools.partial(state_kernel, width // head_count),
        grid=(block_count,),
        in_specs=[row_block(width), whole((8, width)), whole((4, width)), whole((1, width)),
                  row_block(n_size), pl.BlockSpec((head_count, BLOCK), lambda b: (0, b)),
                  whole((1, head_count)), row_block(info.shape[1])],
        out_specs=[whole((n_size, width)), row_block(head_count), row_block(head_count),
                   pl.BlockSpec((1, 1, width), lambda b: (b, 0, 0)), whole((1, width)),
                   row_block(width)],
        out_shape=[jax.ShapeDtypeStruct((n_size, width), jnp.float32),
                   jax.ShapeDtypeStruct((rows, head_count), jnp.float32),
                   jax.ShapeDtypeStruct((rows, head_count), jnp.float32),
                   jax.ShapeDtypeStruct((block_count, 1, width), jnp.float32),
                   jax.ShapeDtypeStruct((1, width), jnp.float32),
                   jax.ShapeDtypeStruct((rows, width), jnp.bfloat16)],
        scratch_shapes=[pltpu.VMEM((8, width), jnp.float32)],
        compiler_params=pltpu.CompilerParams(dimension_semantics=("arbitrary",)),
    )(x, tail8, wconv, bias_row, b_full, step_size, rate_row, info)


def run_blocks(with_y, x, b_full, c_full, l_t, dt_t, seg_row, seg_col, entry_col, decay_x,
               skip_x, entering):
    rows, width = x.shape
    head_count = l_t.shape[1]
    head_width = width // head_count
    n_size = b_full.shape[1]
    block_count = rows // BLOCK
    row_block = lambda cols: pl.BlockSpec((BLOCK, cols), lambda b: (b, 0))
    bt_spec = pl.BlockSpec((n_size, BLOCK), lambda b: (0, b))
    decay_spec = pl.BlockSpec((1, 1, width), lambda b: (b, 0, 0))
    state_spec = pl.BlockSpec((n_size, width), lambda b: (0, 0))
    state_shape = jax.ShapeDtypeStruct((n_size, width), jnp.float32)
    kernel = functools.partial(block_kernel, with_y, head_width)
    params = pltpu.CompilerParams(dimension_semantics=("arbitrary",))
    if with_y:
        return pl.pallas_call(
            kernel,
            grid=(block_count,),
            in_specs=[row_block(width), row_block(n_size), row_block(n_size),
                      row_block(head_count), row_block(head_count),
                      pl.BlockSpec((1, BLOCK), lambda b: (0, b)), row_block(seg_col.shape[1]),
                      decay_spec, pl.BlockSpec((1, width), lambda b: (0, 0)), state_spec],
            out_specs=row_block(width),
            out_shape=jax.ShapeDtypeStruct((rows, width), jnp.bfloat16),
            scratch_shapes=[pltpu.VMEM((n_size, width), jnp.float32)],
            compiler_params=params,
        )(x, b_full, c_full, l_t, dt_t, seg_row, seg_col, decay_x, skip_x, entering)
    return pl.pallas_call(
        kernel,
        grid=(block_count,),
        in_specs=[row_block(width), bt_spec, row_block(head_count), row_block(head_count),
                  row_block(1), decay_spec],
        out_specs=state_spec,
        out_shape=state_shape,
        compiler_params=params,
    )(x, b_t, l_t, dt_t, seg_col, decay_x)


def body(
    inner_input,
    state_input,
    conv_inner,
    bias_inner,
    conv_state,
    bias_state,
    step_size,
    decay_rate,
    skip_gain,
    lengths,
):
    own_rows = inner_input.shape[0]
    head_count = decay_rate.shape[0]
    group_half = state_input.shape[2]
    block_count = own_rows // BLOCK
    positions = lax.axis_index("seq") * own_rows + jnp.arange(own_rows + 3, dtype=jnp.int32) - 3
    seg_ext = segment_of(lengths, positions)
    width = inner_input.shape[1]
    tails = jnp.concatenate(
        [inner_input[-3:], jnp.transpose(state_input[:, -3:], (1, 0, 2)).reshape(3, -1)], 1
    )
    tails = shifted(tails, "seq", 1)
    inner_tail = tails[:, :width]
    state_tail = jnp.transpose(tails[:, width:].reshape(3, 2, group_half), (1, 0, 2))
    weight_state = jnp.swapaxes(conv_state, 0, 1)[:, :, None, :]
    state_half = convolve(
        jnp.concatenate([state_tail, state_input], 1),
        weight_state,
        bias_state[:, None, :],
        seg_ext,
        own_rows,
    )
    partner = from_partner(state_half, "head", 0)
    lower_half = lax.axis_index("head") % 2 == 0
    state_full = jnp.where(
        lower_half,
        jnp.concatenate([state_half, partner], 2),
        jnp.concatenate([partner, state_half], 2),
    )
    b_full = state_full[0]
    c_full = state_full[1]
    head_width = inner_input.shape[1] // head_count
    spread = lambda v: jnp.repeat(v, head_width, axis=-1)
    skip_x = spread(skip_gain).reshape(1, -1)
    seg_own = seg_ext[3:].reshape(block_count, BLOCK)
    seg_prev = seg_ext[2 : 2 + own_rows].reshape(block_count, BLOCK)[:, 0]
    seg_row = seg_ext[3:].reshape(1, own_rows).astype(jnp.float32)
    own_seg = seg_ext[3:]
    entry_col = (seg_own == seg_prev[:, None]).reshape(own_rows)
    keeps = [(seg_ext[3 - back : 3 - back + own_rows] == own_seg) for back in (1, 2, 3)]
    info = jnp.stack(
        [own_seg.astype(jnp.float32), entry_col.astype(jnp.float32)]
        + [keep.astype(jnp.float32) for keep in keeps]
        + [jnp.zeros((own_rows,), jnp.float32)] * 3,
        1,
    )
    tail8 = jnp.concatenate([jnp.zeros((5, inner_tail.shape[1]), inner_tail.dtype), inner_tail], 0)

    local_end, l_t, dt_t, decay_x, total_decay, inner_conv = run_state(
        inner_input, tail8, conv_inner.astype(jnp.float32), bias_inner.reshape(1, -1), b_full,
        step_size, decay_rate.reshape(1, -1), info
    )

    def relay(step_num, incoming):
        return shifted((total_decay * incoming + local_end).astype(jnp.bfloat16), "seq", 1).astype(
            jnp.float32
        )

    part_rows = own_rows * lax.axis_size("seq")
    hops = min(lax.axis_size("seq") - 1, -(-(part_rows // 2) // own_rows))
    incoming = jnp.zeros_like(local_end)
    for step_num in range(hops):
        incoming = relay(step_num, incoming)
    return run_blocks(
        True, inner_conv, b_full, c_full, l_t, dt_t, seg_row, info, None, decay_x, skip_x,
        incoming
    )


def solution(mesh):
    return jax.shard_map(
        body,
        mesh=mesh,
        in_specs=(
            P(("grp", "seq"), "head"),
            P(None, ("grp", "seq"), "head"),
            P(None, "head"),
            P("head"),
            P(None, None, "head"),
            P(None, "head"),
            P("head", ("grp", "seq")),
            P("head"),
            P("head"),
            P("grp"),
        ),
        out_specs=P(("grp", "seq"), "head"),
        check_vma=False,
    )
```

```python
import functools

import jax
import jax.numpy as jnp
from jax import lax
from jax.experimental import pallas as pl
from jax.experimental.pallas import tpu as pltpu
from jax.sharding import PartitionSpec as P

BLOCK = 128


def shifted(value, axis, steps):
    count = lax.axis_size(axis)
    initial, last = (max(0, -steps), min(count, count - steps))
    return lax.ppermute(value, axis, [(source, source + steps) for source in range(initial, last)])


def from_partner(block, axis, stride):
    count = lax.axis_size(axis)
    route = []
    for low in range(count):
        high = low | 1 << stride
        if high != low and high < count:
            route += [(low, high), (high, low)]
    return lax.ppermute(block, axis, route)


def segment_of(lengths, positions):
    starts = jnp.cumsum(lengths, dtype=jnp.int32) - lengths
    covered = (starts[None, :] <= positions[:, None]).astype(jnp.int32)
    return jnp.sum(covered, axis=1, dtype=jnp.int32) - 1


def convolve(extended, weight, bias_row, seg_ext, row_count):
    own_seg = seg_ext[3:]
    summed = (
        jnp.zeros(extended.shape[:-2] + (row_count, extended.shape[-1]), jnp.float32) + bias_row
    )
    for offset in range(4):
        kept_mask = (seg_ext[offset : offset + row_count] == own_seg).astype(jnp.float32)[:, None]
        window = extended[..., offset : offset + row_count, :].astype(jnp.float32)
        summed = summed + weight[offset].astype(jnp.float32) * window * kept_mask
    return jax.nn.silu(summed).astype(jnp.bfloat16)


def split_dot(lhs, value):
    high = value.astype(jnp.bfloat16)
    low = (value - high.astype(jnp.float32)).astype(jnp.bfloat16)
    return jnp.dot(lhs, high, preferred_element_type=jnp.float32) + jnp.dot(
        lhs, low, preferred_element_type=jnp.float32
    )


def expand_heads(small, head_width):
    rows, heads = small.shape
    per_tile = 128 // head_width
    lane = lax.broadcasted_iota(jnp.int32, (rows, 128), 1) // head_width
    tiles = []
    for tile in range(heads // per_tile):
        picked = jnp.broadcast_to(small[:, tile * per_tile : tile * per_tile + 1], (rows, 128))
        for k in range(1, per_tile):
            column = small[:, tile * per_tile + k : tile * per_tile + k + 1]
            picked = jnp.where(lane == k, jnp.broadcast_to(column, (rows, 128)), picked)
        tiles.append(picked)
    return jnp.concatenate(tiles, axis=1)


def block_kernel(with_y, head_width, *refs):
    if with_y:
        (x_ref, b_ref, c_ref, l_ref, dt_ref, segr_ref, info_ref, decay_ref,
         skip_ref, ein_ref, out_ref, state_ref) = refs
    else:
        (x_ref, b_ref, l_ref, dt_ref, segc_ref, decay_ref, state_ref) = refs
    blk = pl.program_id(0)

    @pl.when(blk == 0)
    def _():
        if with_y:
            state_ref[...] = ein_ref[...].astype(jnp.float32)
        else:
            state_ref[...] = jnp.zeros(state_ref.shape, jnp.float32)

    info = info_ref[...]
    seg_col = info[:, 0:1]
    end_col = (seg_col == seg_col[BLOCK - 1 : BLOCK, :]).astype(jnp.float32)
    l_small = l_ref[...]
    dt_small = dt_ref[...]
    x = x_ref[...].astype(jnp.float32)
    state = state_ref[...]
    if with_y:
        c_mat = c_ref[...]
        seg_row = segr_ref[...]
        scores = lax.dot_general(
            c_mat, b_ref[...], (((1,), (1,)), ((), ())), preferred_element_type=jnp.float32
        )
        rows = lax.broadcasted_iota(jnp.int32, (BLOCK, BLOCK), 0)
        cols = lax.broadcasted_iota(jnp.int32, (BLOCK, BLOCK), 1)
        allowed = (rows >= cols) & (seg_col == seg_row)
        masked = jnp.where(allowed, scores, 0.0).astype(jnp.bfloat16)
        rising = expand_heads(jnp.exp(l_small), head_width)
        falling = expand_heads(jnp.exp(-l_small) * dt_small, head_width)
        intra = split_dot(masked, x * falling) * rising
        inter = split_dot(c_mat, state) * (rising * info[:, 1:2])
        out_ref[...] = (intra + inter + skip_ref[...] * x).astype(jnp.bfloat16)
    ending = expand_heads(
        jnp.exp(l_small[BLOCK - 1 : BLOCK, :] - l_small) * dt_small * end_col, head_width
    )
    weighted = (x * ending).astype(jnp.bfloat16)
    state_ref[...] = decay_ref[0] * state + lax.dot_general(
        b_ref[...], weighted, (((0,), (0,)), ((), ())), preferred_element_type=jnp.float32
    )


def state_kernel(head_width, x_ref, tail_ref, wconv_ref, bias_ref, b_ref, dt_ref, rate_ref,
                 info_ref, state_ref, l_ref, dtt_ref, decay_ref, total_ref, xc_ref, sent_ref,
                 prev_ref):
    blk = pl.program_id(0)

    @pl.when(blk == 0)
    def _():
        state_ref[...] = jnp.zeros(state_ref.shape, jnp.float32)
        total_ref[...] = jnp.ones(total_ref.shape, jnp.float32)
        prev_ref[...] = tail_ref[...].astype(jnp.float32)

    info = info_ref[...]
    raw = x_ref[...].astype(jnp.float32)
    prev = prev_ref[...]
    top_row = lax.broadcasted_iota(jnp.int32, prev.shape, 0)
    taps = wconv_ref[...].astype(jnp.float32)
    summed = jnp.zeros(raw.shape, jnp.float32) + bias_ref[...]
    for offset in range(4):
        back = 3 - offset
        if back == 0:
            window = raw
        else:
            rolled = pltpu.roll(raw, back, 0)
            top = jnp.where(top_row < back, pltpu.roll(prev, back, 0), rolled[:8])
            window = jnp.concatenate([top, rolled[8:]], 0) * info[:, 1 + back : 2 + back]
        summed = summed + taps[offset : offset + 1, :] * window
    prev_ref[...] = raw[BLOCK - 8 :]
    xc = jax.nn.silu(summed).astype(jnp.bfloat16)
    xc_ref[...] = xc

    rows = lax.broadcasted_iota(jnp.int32, (2 * BLOCK, BLOCK), 0)
    cols = lax.broadcasted_iota(jnp.int32, (2 * BLOCK, BLOCK), 1)
    picker = jnp.where(
        ((rows < BLOCK) & (rows >= cols)) | (rows - BLOCK == cols), 1.0, 0.0
    ).astype(jnp.bfloat16)
    rest = dt_ref[...]
    cum = None
    for _ in range(3):
        piece = rest.astype(jnp.bfloat16)
        part = lax.dot_general(
            picker, piece, (((1,), (1,)), ((), ())), preferred_element_type=jnp.float32
        )
        cum = part if cum is None else cum + part
        rest = rest - piece.astype(jnp.float32)
    l_small = -cum[:BLOCK] * rate_ref[...]
    dt_small = cum[BLOCK:]
    l_ref[...] = l_small
    dtt_ref[...] = dt_small
    seg_col = info[:, 0:1]
    end_col = (seg_col == seg_col[BLOCK - 1 : BLOCK, :]).astype(jnp.float32)
    decay_x = expand_heads(
        jnp.exp(l_small[BLOCK - 1 : BLOCK, :]) * info[BLOCK - 1 : BLOCK, 1:2], head_width
    )
    decay_ref[0] = decay_x
    total_ref[...] = total_ref[...] * decay_x
    ending = expand_heads(
        jnp.exp(l_small[BLOCK - 1 : BLOCK, :] - l_small) * dt_small * end_col, head_width
    )
    weighted = (xc.astype(jnp.float32) * ending).astype(jnp.bfloat16)
    new_state = decay_x * state_ref[...] + lax.dot_general(
        b_ref[...], weighted, (((0,), (0,)), ((), ())), preferred_element_type=jnp.float32
    )
    state_ref[...] = new_state

    @pl.when(blk == pl.num_programs(0) - 1)
    def _():
        sent_ref[...] = new_state.astype(jnp.bfloat16)


def run_state(x, tail8, wconv, bias_row, b_full, step_size, rate_row, info):
    rows, width = x.shape
    head_count = step_size.shape[0]
    n_size = b_full.shape[1]
    block_count = rows // BLOCK
    row_block = lambda cols: pl.BlockSpec((BLOCK, cols), lambda b: (b, 0))
    whole = lambda shape: pl.BlockSpec(shape, lambda b: (0,) * len(shape))
    return pl.pallas_call(
        functools.partial(state_kernel, width // head_count),
        grid=(block_count,),
        in_specs=[row_block(width), whole((8, width)), whole((4, width)), whole((1, width)),
                  row_block(n_size), pl.BlockSpec((head_count, BLOCK), lambda b: (0, b)),
                  whole((1, head_count)), row_block(info.shape[1])],
        out_specs=[whole((n_size, width)), row_block(head_count), row_block(head_count),
                   pl.BlockSpec((1, 1, width), lambda b: (b, 0, 0)), whole((1, width)),
                   row_block(width), whole((n_size, width))],
        out_shape=[jax.ShapeDtypeStruct((n_size, width), jnp.float32),
                   jax.ShapeDtypeStruct((rows, head_count), jnp.float32),
                   jax.ShapeDtypeStruct((rows, head_count), jnp.float32),
                   jax.ShapeDtypeStruct((block_count, 1, width), jnp.float32),
                   jax.ShapeDtypeStruct((1, width), jnp.float32),
                   jax.ShapeDtypeStruct((rows, width), jnp.bfloat16),
                   jax.ShapeDtypeStruct((n_size, width), jnp.bfloat16)],
        scratch_shapes=[pltpu.VMEM((8, width), jnp.float32)],
        compiler_params=pltpu.CompilerParams(dimension_semantics=("arbitrary",)),
    )(x, tail8, wconv, bias_row, b_full, step_size, rate_row, info)


def run_blocks(with_y, x, b_full, c_full, l_t, dt_t, seg_row, seg_col, entry_col, decay_x,
               skip_x, entering):
    rows, width = x.shape
    head_count = l_t.shape[1]
    head_width = width // head_count
    n_size = b_full.shape[1]
    block_count = rows // BLOCK
    row_block = lambda cols: pl.BlockSpec((BLOCK, cols), lambda b: (b, 0))
    bt_spec = pl.BlockSpec((n_size, BLOCK), lambda b: (0, b))
    decay_spec = pl.BlockSpec((1, 1, width), lambda b: (b, 0, 0))
    state_spec = pl.BlockSpec((n_size, width), lambda b: (0, 0))
    state_shape = jax.ShapeDtypeStruct((n_size, width), jnp.float32)
    kernel = functools.partial(block_kernel, with_y, head_width)
    params = pltpu.CompilerParams(dimension_semantics=("arbitrary",))
    if with_y:
        return pl.pallas_call(
            kernel,
            grid=(block_count,),
            in_specs=[row_block(width), row_block(n_size), row_block(n_size),
                      row_block(head_count), row_block(head_count),
                      pl.BlockSpec((1, BLOCK), lambda b: (0, b)), row_block(seg_col.shape[1]),
                      decay_spec, pl.BlockSpec((1, width), lambda b: (0, 0)), state_spec],
            out_specs=row_block(width),
            out_shape=jax.ShapeDtypeStruct((rows, width), jnp.bfloat16),
            scratch_shapes=[pltpu.VMEM((n_size, width), jnp.float32)],
            compiler_params=params,
        )(x, b_full, c_full, l_t, dt_t, seg_row, seg_col, decay_x, skip_x, entering)
    return pl.pallas_call(
        kernel,
        grid=(block_count,),
        in_specs=[row_block(width), bt_spec, row_block(head_count), row_block(head_count),
                  row_block(1), decay_spec],
        out_specs=state_spec,
        out_shape=state_shape,
        compiler_params=params,
    )(x, b_t, l_t, dt_t, seg_col, decay_x)


def body(
    inner_input,
    state_input,
    conv_inner,
    bias_inner,
    conv_state,
    bias_state,
    step_size,
    decay_rate,
    skip_gain,
    lengths,
):
    own_rows = inner_input.shape[0]
    head_count = decay_rate.shape[0]
    group_half = state_input.shape[2]
    block_count = own_rows // BLOCK
    positions = lax.axis_index("seq") * own_rows + jnp.arange(own_rows + 3, dtype=jnp.int32) - 3
    seg_ext = segment_of(lengths, positions)
    width = inner_input.shape[1]
    tails = jnp.concatenate(
        [inner_input[-8:], jnp.transpose(state_input[:, -8:], (1, 0, 2)).reshape(8, -1)], 1
    )
    tails = shifted(tails, "seq", 1)
    tail8 = tails[:, :width]
    state_tail = jnp.transpose(tails[5:, width:].reshape(3, 2, group_half), (1, 0, 2))
    weight_state = jnp.swapaxes(conv_state, 0, 1)[:, :, None, :]
    state_half = convolve(
        jnp.concatenate([state_tail, state_input], 1),
        weight_state,
        bias_state[:, None, :],
        seg_ext,
        own_rows,
    )
    partner = from_partner(state_half, "head", 0)
    lower_half = lax.axis_index("head") % 2 == 0
    state_full = jnp.where(
        lower_half,
        jnp.concatenate([state_half, partner], 2),
        jnp.concatenate([partner, state_half], 2),
    )
    b_full = state_full[0]
    c_full = state_full[1]
    head_width = inner_input.shape[1] // head_count
    spread = lambda v: jnp.repeat(v, head_width, axis=-1)
    skip_x = spread(skip_gain).reshape(1, -1)
    seg_own = seg_ext[3:].reshape(block_count, BLOCK)
    seg_prev = seg_ext[2 : 2 + own_rows].reshape(block_count, BLOCK)[:, 0]
    seg_row = seg_ext[3:].reshape(1, own_rows).astype(jnp.float32)
    own_seg = seg_ext[3:]
    entry_col = (seg_own == seg_prev[:, None]).reshape(own_rows)
    keeps = [(seg_ext[3 - back : 3 - back + own_rows] == own_seg) for back in (1, 2, 3)]
    info = jnp.stack(
        [own_seg.astype(jnp.float32), entry_col.astype(jnp.float32)]
        + [keep.astype(jnp.float32) for keep in keeps]
        + [jnp.zeros((own_rows,), jnp.float32)] * 3,
        1,
    )

    local_end, l_t, dt_t, decay_x, total_decay, inner_conv, end_sent = run_state(
        inner_input, tail8, conv_inner, bias_inner.reshape(1, -1), b_full,
        step_size, decay_rate.reshape(1, -1), info
    )

    def relay(step_num, incoming):
        return shifted(
            (total_decay * incoming.astype(jnp.float32) + local_end).astype(jnp.bfloat16), "seq", 1
        )

    part_rows = own_rows * lax.axis_size("seq")
    hops = min(lax.axis_size("seq") - 1, -(-(part_rows // 2) // own_rows))
    incoming = shifted(end_sent, "seq", 1)
    for step_num in range(1, hops):
        incoming = relay(step_num, incoming)
    return run_blocks(
        True, inner_conv, b_full, c_full, l_t, dt_t, seg_row, info, None, decay_x, skip_x,
        incoming
    )


def solution(mesh):
    return jax.shard_map(
        body,
        mesh=mesh,
        in_specs=(
            P(("grp", "seq"), "head"),
            P(None, ("grp", "seq"), "head"),
            P(None, "head"),
            P("head"),
            P(None, None, "head"),
            P(None, "head"),
            P("head", ("grp", "seq")),
            P("head"),
            P("head"),
            P("grp"),
        ),
        out_specs=P(("grp", "seq"), "head"),
        check_vma=False,
    )
```

```python
import functools

import jax
import jax.numpy as jnp
from jax import lax
from jax.experimental import pallas as pl
from jax.experimental.pallas import tpu as pltpu
from jax.sharding import PartitionSpec as P

BLOCK = 128


def shifted(value, axis, steps):
    count = lax.axis_size(axis)
    initial, last = (max(0, -steps), min(count, count - steps))
    return lax.ppermute(value, axis, [(source, source + steps) for source in range(initial, last)])


def from_partner(block, axis, stride):
    count = lax.axis_size(axis)
    route = []
    for low in range(count):
        high = low | 1 << stride
        if high != low and high < count:
            route += [(low, high), (high, low)]
    return lax.ppermute(block, axis, route)


def segment_of(lengths, positions):
    starts = jnp.cumsum(lengths, dtype=jnp.int32) - lengths
    covered = (starts[None, :] <= positions[:, None]).astype(jnp.int32)
    return jnp.sum(covered, axis=1, dtype=jnp.int32) - 1


def convolve(extended, weight, bias_row, seg_ext, row_count):
    own_seg = seg_ext[3:]
    summed = (
        jnp.zeros(extended.shape[:-2] + (row_count, extended.shape[-1]), jnp.float32) + bias_row
    )
    for offset in range(4):
        kept_mask = (seg_ext[offset : offset + row_count] == own_seg).astype(jnp.float32)[:, None]
        window = extended[..., offset : offset + row_count, :].astype(jnp.float32)
        summed = summed + weight[offset].astype(jnp.float32) * window * kept_mask
    return jax.nn.silu(summed).astype(jnp.bfloat16)


def split_dot(lhs, value):
    high = value.astype(jnp.bfloat16)
    low = (value - high.astype(jnp.float32)).astype(jnp.bfloat16)
    return jnp.dot(lhs, high, preferred_element_type=jnp.float32) + jnp.dot(
        lhs, low, preferred_element_type=jnp.float32
    )


def expand_heads(small, head_width):
    rows, heads = small.shape
    per_tile = 128 // head_width
    lane = lax.broadcasted_iota(jnp.int32, (rows, 128), 1) // head_width
    tiles = []
    for tile in range(heads // per_tile):
        picked = jnp.broadcast_to(small[:, tile * per_tile : tile * per_tile + 1], (rows, 128))
        for k in range(1, per_tile):
            column = small[:, tile * per_tile + k : tile * per_tile + k + 1]
            picked = jnp.where(lane == k, jnp.broadcast_to(column, (rows, 128)), picked)
        tiles.append(picked)
    return jnp.concatenate(tiles, axis=1)


def block_kernel(with_y, head_width, *refs):
    if with_y:
        (x_ref, b_ref, c_ref, l_ref, dt_ref, segr_ref, info_ref, decay_ref,
         skip_ref, ein_ref, out_ref, state_ref) = refs
    else:
        (x_ref, b_ref, l_ref, dt_ref, segc_ref, decay_ref, state_ref) = refs
    blk = pl.program_id(0)

    @pl.when(blk == 0)
    def _():
        if with_y:
            state_ref[...] = ein_ref[...].astype(jnp.float32)
        else:
            state_ref[...] = jnp.zeros(state_ref.shape, jnp.float32)

    info = info_ref[...]
    seg_col = info[:, 0:1]
    end_col = (seg_col == seg_col[BLOCK - 1 : BLOCK, :]).astype(jnp.float32)
    l_small = l_ref[...]
    dt_small = dt_ref[...]
    x = x_ref[...].astype(jnp.float32)
    state = state_ref[...]
    if with_y:
        c_mat = c_ref[...]
        seg_row = segr_ref[...]
        scores = lax.dot_general(
            c_mat, b_ref[...], (((1,), (1,)), ((), ())), preferred_element_type=jnp.float32
        )
        rows = lax.broadcasted_iota(jnp.int32, (BLOCK, BLOCK), 0)
        cols = lax.broadcasted_iota(jnp.int32, (BLOCK, BLOCK), 1)
        allowed = (rows >= cols) & (seg_col == seg_row)
        masked = jnp.where(allowed, scores, 0.0).astype(jnp.bfloat16)
        rising = expand_heads(jnp.exp(l_small), head_width)
        falling = expand_heads(jnp.exp(-l_small) * dt_small, head_width)
        scaled = (x * falling).astype(jnp.bfloat16)
        intra = jnp.dot(masked, scaled, preferred_element_type=jnp.float32) * rising
        inter = split_dot(c_mat, state) * (rising * info[:, 1:2])
        out_ref[...] = (intra + inter + skip_ref[...] * x).astype(jnp.bfloat16)
    ending = expand_heads(
        jnp.exp(l_small[BLOCK - 1 : BLOCK, :] - l_small) * dt_small * end_col, head_width
    )
    weighted = (x * ending).astype(jnp.bfloat16)
    state_ref[...] = decay_ref[0] * state + lax.dot_general(
        b_ref[...], weighted, (((0,), (0,)), ((), ())), preferred_element_type=jnp.float32
    )


def state_kernel(head_width, x_ref, tail_ref, wconv_ref, bias_ref, b_ref, dt_ref, rate_ref,
                 info_ref, state_ref, l_ref, dtt_ref, decay_ref, total_ref, xc_ref, sent_ref,
                 prev_ref):
    blk = pl.program_id(0)

    @pl.when(blk == 0)
    def _():
        state_ref[...] = jnp.zeros(state_ref.shape, jnp.float32)
        total_ref[...] = jnp.ones(total_ref.shape, jnp.float32)
        prev_ref[...] = tail_ref[...].astype(jnp.float32)

    info = info_ref[...]
    raw = x_ref[...].astype(jnp.float32)
    prev = prev_ref[...]
    top_row = lax.broadcasted_iota(jnp.int32, prev.shape, 0)
    taps = wconv_ref[...].astype(jnp.float32)
    summed = jnp.zeros(raw.shape, jnp.float32) + bias_ref[...]
    for offset in range(4):
        back = 3 - offset
        if back == 0:
            window = raw
        else:
            rolled = pltpu.roll(raw, back, 0)
            top = jnp.where(top_row < back, pltpu.roll(prev, back, 0), rolled[:8])
            window = jnp.concatenate([top, rolled[8:]], 0) * info[:, 1 + back : 2 + back]
        summed = summed + taps[offset : offset + 1, :] * window
    prev_ref[...] = raw[BLOCK - 8 :]
    xc = jax.nn.silu(summed).astype(jnp.bfloat16)
    xc_ref[...] = xc

    rows = lax.broadcasted_iota(jnp.int32, (2 * BLOCK, BLOCK), 0)
    cols = lax.broadcasted_iota(jnp.int32, (2 * BLOCK, BLOCK), 1)
    picker = jnp.where(
        ((rows < BLOCK) & (rows >= cols)) | (rows - BLOCK == cols), 1.0, 0.0
    ).astype(jnp.bfloat16)
    rest = dt_ref[...]
    cum = None
    for _ in range(3):
        piece = rest.astype(jnp.bfloat16)
        part = lax.dot_general(
            picker, piece, (((1,), (1,)), ((), ())), preferred_element_type=jnp.float32
        )
        cum = part if cum is None else cum + part
        rest = rest - piece.astype(jnp.float32)
    l_small = -cum[:BLOCK] * rate_ref[...]
    dt_small = cum[BLOCK:]
    l_ref[...] = l_small
    dtt_ref[...] = dt_small
    seg_col = info[:, 0:1]
    end_col = (seg_col == seg_col[BLOCK - 1 : BLOCK, :]).astype(jnp.float32)
    decay_x = expand_heads(
        jnp.exp(l_small[BLOCK - 1 : BLOCK, :]) * info[BLOCK - 1 : BLOCK, 1:2], head_width
    )
    decay_ref[0] = decay_x
    total_ref[...] = total_ref[...] * decay_x
    ending = expand_heads(
        jnp.exp(l_small[BLOCK - 1 : BLOCK, :] - l_small) * dt_small * end_col, head_width
    )
    weighted = (xc.astype(jnp.float32) * ending).astype(jnp.bfloat16)
    new_state = decay_x * state_ref[...] + lax.dot_general(
        b_ref[...], weighted, (((0,), (0,)), ((), ())), preferred_element_type=jnp.float32
    )
    state_ref[...] = new_state

    @pl.when(blk == pl.num_programs(0) - 1)
    def _():
        sent_ref[...] = new_state.astype(jnp.bfloat16)


def run_state(x, tail8, wconv, bias_row, b_full, step_size, rate_row, info):
    rows, width = x.shape
    head_count = step_size.shape[0]
    n_size = b_full.shape[1]
    block_count = rows // BLOCK
    row_block = lambda cols: pl.BlockSpec((BLOCK, cols), lambda b: (b, 0))
    whole = lambda shape: pl.BlockSpec(shape, lambda b: (0,) * len(shape))
    return pl.pallas_call(
        functools.partial(state_kernel, width // head_count),
        grid=(block_count,),
        in_specs=[row_block(width), whole((8, width)), whole((4, width)), whole((1, width)),
                  row_block(n_size), pl.BlockSpec((head_count, BLOCK), lambda b: (0, b)),
                  whole((1, head_count)), row_block(info.shape[1])],
        out_specs=[whole((n_size, width)), row_block(head_count), row_block(head_count),
                   pl.BlockSpec((1, 1, width), lambda b: (b, 0, 0)), whole((1, width)),
                   row_block(width), whole((n_size, width))],
        out_shape=[jax.ShapeDtypeStruct((n_size, width), jnp.float32),
                   jax.ShapeDtypeStruct((rows, head_count), jnp.float32),
                   jax.ShapeDtypeStruct((rows, head_count), jnp.float32),
                   jax.ShapeDtypeStruct((block_count, 1, width), jnp.float32),
                   jax.ShapeDtypeStruct((1, width), jnp.float32),
                   jax.ShapeDtypeStruct((rows, width), jnp.bfloat16),
                   jax.ShapeDtypeStruct((n_size, width), jnp.bfloat16)],
        scratch_shapes=[pltpu.VMEM((8, width), jnp.float32)],
        compiler_params=pltpu.CompilerParams(dimension_semantics=("arbitrary",)),
    )(x, tail8, wconv, bias_row, b_full, step_size, rate_row, info)


def run_blocks(with_y, x, b_full, c_full, l_t, dt_t, seg_row, seg_col, entry_col, decay_x,
               skip_x, entering):
    rows, width = x.shape
    head_count = l_t.shape[1]
    head_width = width // head_count
    n_size = b_full.shape[1]
    block_count = rows // BLOCK
    row_block = lambda cols: pl.BlockSpec((BLOCK, cols), lambda b: (b, 0))
    bt_spec = pl.BlockSpec((n_size, BLOCK), lambda b: (0, b))
    decay_spec = pl.BlockSpec((1, 1, width), lambda b: (b, 0, 0))
    state_spec = pl.BlockSpec((n_size, width), lambda b: (0, 0))
    state_shape = jax.ShapeDtypeStruct((n_size, width), jnp.float32)
    kernel = functools.partial(block_kernel, with_y, head_width)
    params = pltpu.CompilerParams(dimension_semantics=("arbitrary",))
    if with_y:
        return pl.pallas_call(
            kernel,
            grid=(block_count,),
            in_specs=[row_block(width), row_block(n_size), row_block(n_size),
                      row_block(head_count), row_block(head_count),
                      pl.BlockSpec((1, BLOCK), lambda b: (0, b)), row_block(seg_col.shape[1]),
                      decay_spec, pl.BlockSpec((1, width), lambda b: (0, 0)), state_spec],
            out_specs=row_block(width),
            out_shape=jax.ShapeDtypeStruct((rows, width), jnp.bfloat16),
            scratch_shapes=[pltpu.VMEM((n_size, width), jnp.float32)],
            compiler_params=params,
        )(x, b_full, c_full, l_t, dt_t, seg_row, seg_col, decay_x, skip_x, entering)
    return pl.pallas_call(
        kernel,
        grid=(block_count,),
        in_specs=[row_block(width), bt_spec, row_block(head_count), row_block(head_count),
                  row_block(1), decay_spec],
        out_specs=state_spec,
        out_shape=state_shape,
        compiler_params=params,
    )(x, b_t, l_t, dt_t, seg_col, decay_x)


def body(
    inner_input,
    state_input,
    conv_inner,
    bias_inner,
    conv_state,
    bias_state,
    step_size,
    decay_rate,
    skip_gain,
    lengths,
):
    own_rows = inner_input.shape[0]
    head_count = decay_rate.shape[0]
    group_half = state_input.shape[2]
    block_count = own_rows // BLOCK
    positions = lax.axis_index("seq") * own_rows + jnp.arange(own_rows + 3, dtype=jnp.int32) - 3
    seg_ext = segment_of(lengths, positions)
    width = inner_input.shape[1]
    tails = jnp.concatenate(
        [inner_input[-8:], jnp.transpose(state_input[:, -8:], (1, 0, 2)).reshape(8, -1)], 1
    )
    tails = shifted(tails, "seq", 1)
    tail8 = tails[:, :width]
    state_tail = jnp.transpose(tails[5:, width:].reshape(3, 2, group_half), (1, 0, 2))
    weight_state = jnp.swapaxes(conv_state, 0, 1)[:, :, None, :]
    state_half = convolve(
        jnp.concatenate([state_tail, state_input], 1),
        weight_state,
        bias_state[:, None, :],
        seg_ext,
        own_rows,
    )
    partner = from_partner(state_half, "head", 0)
    lower_half = lax.axis_index("head") % 2 == 0
    state_full = jnp.where(
        lower_half,
        jnp.concatenate([state_half, partner], 2),
        jnp.concatenate([partner, state_half], 2),
    )
    b_full = state_full[0]
    c_full = state_full[1]
    head_width = inner_input.shape[1] // head_count
    spread = lambda v: jnp.repeat(v, head_width, axis=-1)
    skip_x = spread(skip_gain).reshape(1, -1)
    seg_own = seg_ext[3:].reshape(block_count, BLOCK)
    seg_prev = seg_ext[2 : 2 + own_rows].reshape(block_count, BLOCK)[:, 0]
    seg_row = seg_ext[3:].reshape(1, own_rows).astype(jnp.float32)
    own_seg = seg_ext[3:]
    entry_col = (seg_own == seg_prev[:, None]).reshape(own_rows)
    keeps = [(seg_ext[3 - back : 3 - back + own_rows] == own_seg) for back in (1, 2, 3)]
    info = jnp.stack(
        [own_seg.astype(jnp.float32), entry_col.astype(jnp.float32)]
        + [keep.astype(jnp.float32) for keep in keeps]
        + [jnp.zeros((own_rows,), jnp.float32)] * 3,
        1,
    )

    local_end, l_t, dt_t, decay_x, total_decay, inner_conv, end_sent = run_state(
        inner_input, tail8, conv_inner, bias_inner.reshape(1, -1), b_full,
        step_size, decay_rate.reshape(1, -1), info
    )

    def relay(step_num, incoming):
        return shifted(
            (total_decay * incoming.astype(jnp.float32) + local_end).astype(jnp.bfloat16), "seq", 1
        )

    part_rows = own_rows * lax.axis_size("seq")
    hops = min(lax.axis_size("seq") - 1, -(-(part_rows // 2) // own_rows))
    incoming = shifted(end_sent, "seq", 1)
    for step_num in range(1, hops):
        incoming = relay(step_num, incoming)
    return run_blocks(
        True, inner_conv, b_full, c_full, l_t, dt_t, seg_row, info, None, decay_x, skip_x,
        incoming
    )


def solution(mesh):
    return jax.shard_map(
        body,
        mesh=mesh,
        in_specs=(
            P(("grp", "seq"), "head"),
            P(None, ("grp", "seq"), "head"),
            P(None, "head"),
            P("head"),
            P(None, None, "head"),
            P(None, "head"),
            P("head", ("grp", "seq")),
            P("head"),
            P("head"),
            P("grp"),
        ),
        out_specs=P(("grp", "seq"), "head"),
        check_vma=False,
    )
```

```python
import functools

import jax
import jax.numpy as jnp
from jax import lax
from jax.experimental import pallas as pl
from jax.experimental.pallas import tpu as pltpu
from jax.sharding import PartitionSpec as P

BLOCK = 128


def shifted(value, axis, steps):
    count = lax.axis_size(axis)
    initial, last = (max(0, -steps), min(count, count - steps))
    return lax.ppermute(value, axis, [(source, source + steps) for source in range(initial, last)])


def from_partner(block, axis, stride):
    count = lax.axis_size(axis)
    route = []
    for low in range(count):
        high = low | 1 << stride
        if high != low and high < count:
            route += [(low, high), (high, low)]
    return lax.ppermute(block, axis, route)


def segment_of(lengths, positions):
    starts = jnp.cumsum(lengths, dtype=jnp.int32) - lengths
    covered = (starts[None, :] <= positions[:, None]).astype(jnp.int32)
    return jnp.sum(covered, axis=1, dtype=jnp.int32) - 1


def convolve(extended, weight, bias_row, seg_ext, row_count):
    own_seg = seg_ext[3:]
    summed = (
        jnp.zeros(extended.shape[:-2] + (row_count, extended.shape[-1]), jnp.float32) + bias_row
    )
    for offset in range(4):
        kept_mask = (seg_ext[offset : offset + row_count] == own_seg).astype(jnp.float32)[:, None]
        window = extended[..., offset : offset + row_count, :].astype(jnp.float32)
        summed = summed + weight[offset].astype(jnp.float32) * window * kept_mask
    return jax.nn.silu(summed).astype(jnp.bfloat16)


def split_dot(lhs, value):
    high = value.astype(jnp.bfloat16)
    low = (value - high.astype(jnp.float32)).astype(jnp.bfloat16)
    return jnp.dot(lhs, high, preferred_element_type=jnp.float32) + jnp.dot(
        lhs, low, preferred_element_type=jnp.float32
    )


def expand_heads(small, head_width):
    rows, heads = small.shape
    per_tile = 128 // head_width
    lane = lax.broadcasted_iota(jnp.int32, (rows, 128), 1) // head_width
    tiles = []
    for tile in range(heads // per_tile):
        picked = jnp.broadcast_to(small[:, tile * per_tile : tile * per_tile + 1], (rows, 128))
        for k in range(1, per_tile):
            column = small[:, tile * per_tile + k : tile * per_tile + k + 1]
            picked = jnp.where(lane == k, jnp.broadcast_to(column, (rows, 128)), picked)
        tiles.append(picked)
    return jnp.concatenate(tiles, axis=1)


def block_kernel(with_y, head_width, *refs):
    if with_y:
        (x_ref, b_ref, c_ref, l_ref, dt_ref, segr_ref, info_ref, decay_ref,
         skip_ref, ein_ref, out_ref, state_ref) = refs
    else:
        (x_ref, b_ref, l_ref, dt_ref, segc_ref, decay_ref, state_ref) = refs
    blk = pl.program_id(0)

    @pl.when(blk == 0)
    def _():
        if with_y:
            state_ref[...] = ein_ref[...].astype(jnp.float32)
        else:
            state_ref[...] = jnp.zeros(state_ref.shape, jnp.float32)

    info = info_ref[...]
    seg_col = info[:, 0:1]
    end_col = (seg_col == seg_col[BLOCK - 1 : BLOCK, :]).astype(jnp.float32)
    l_small = l_ref[...]
    dt_small = dt_ref[...]
    x = x_ref[...].astype(jnp.float32)
    state = state_ref[...]
    if with_y:
        c_mat = c_ref[...]
        seg_row = segr_ref[...]
        scores = lax.dot_general(
            c_mat, b_ref[...], (((1,), (1,)), ((), ())), preferred_element_type=jnp.float32
        )
        rows = lax.broadcasted_iota(jnp.int32, (BLOCK, BLOCK), 0)
        cols = lax.broadcasted_iota(jnp.int32, (BLOCK, BLOCK), 1)
        allowed = (rows >= cols) & (seg_col == seg_row)
        masked = jnp.where(allowed, scores, 0.0).astype(jnp.bfloat16)
        rising = expand_heads(jnp.exp(l_small), head_width)
        falling = expand_heads(jnp.exp(-l_small) * dt_small, head_width)
        intra = split_dot(masked, x * falling) * rising
        inter = split_dot(c_mat, state) * (rising * info[:, 1:2])
        out_ref[...] = (intra + inter + skip_ref[...] * x).astype(jnp.bfloat16)
    ending = expand_heads(
        jnp.exp(l_small[BLOCK - 1 : BLOCK, :] - l_small) * dt_small * end_col, head_width
    )
    weighted = (x * ending).astype(jnp.bfloat16)
    state_ref[...] = decay_ref[0] * state + lax.dot_general(
        b_ref[...], weighted, (((0,), (0,)), ((), ())), preferred_element_type=jnp.float32
    )


def causal_conv(raw, prev, taps, bias, info):
    top_row = lax.broadcasted_iota(jnp.int32, prev.shape, 0)
    summed = jnp.zeros(raw.shape, jnp.float32) + bias
    for offset in range(4):
        back = 3 - offset
        if back == 0:
            window = raw
        else:
            rolled = pltpu.roll(raw, back, 0)
            top = jnp.where(top_row < back, pltpu.roll(prev, back, 0), rolled[:8])
            window = jnp.concatenate([top, rolled[8:]], 0) * info[:, 1 + back : 2 + back]
        summed = summed + taps[offset : offset + 1, :] * window
    return jax.nn.silu(summed).astype(jnp.bfloat16)


def state_kernel(head_width, x_ref, tail_ref, wconv_ref, bias_ref, bc_ref, bcx_ref, dt_ref,
                 rate_ref, info_ref, state_ref, l_ref, dtt_ref, decay_ref, total_ref, xc_ref,
                 bo_ref, co_ref, sent_ref, prev_ref, bcprev_ref):
    blk = pl.program_id(0)

    @pl.when(blk == 0)
    def _():
        state_ref[...] = jnp.zeros(state_ref.shape, jnp.float32)
        total_ref[...] = jnp.ones(total_ref.shape, jnp.float32)
        prev_ref[...] = tail_ref[...].astype(jnp.float32)
        bcprev_ref[...] = bcx_ref[:, 0:8, :]

    info = info_ref[...]
    raw = x_ref[...].astype(jnp.float32)
    xc = causal_conv(raw, prev_ref[...], wconv_ref[...].astype(jnp.float32), bias_ref[...], info)
    prev_ref[...] = raw[BLOCK - 8 :]
    xc_ref[...] = xc
    convolved = []
    for which in range(2):
        raw_bc = bc_ref[which].astype(jnp.float32)
        extra = bcx_ref[which]
        convolved.append(causal_conv(raw_bc, bcprev_ref[which], extra[8:12], extra[12:13], info))
        bcprev_ref[which] = raw_bc[BLOCK - 8 :]
    b_mat, c_mat = convolved
    bo_ref[...] = b_mat
    co_ref[...] = c_mat

    rows = lax.broadcasted_iota(jnp.int32, (2 * BLOCK, BLOCK), 0)
    cols = lax.broadcasted_iota(jnp.int32, (2 * BLOCK, BLOCK), 1)
    picker = jnp.where(
        ((rows < BLOCK) & (rows >= cols)) | (rows - BLOCK == cols), 1.0, 0.0
    ).astype(jnp.bfloat16)
    rest = dt_ref[...]
    cum = None
    for _ in range(3):
        piece = rest.astype(jnp.bfloat16)
        part = lax.dot_general(
            picker, piece, (((1,), (1,)), ((), ())), preferred_element_type=jnp.float32
        )
        cum = part if cum is None else cum + part
        rest = rest - piece.astype(jnp.float32)
    l_small = -cum[:BLOCK] * rate_ref[...]
    dt_small = cum[BLOCK:]
    l_ref[...] = l_small
    dtt_ref[...] = dt_small
    seg_col = info[:, 0:1]
    end_col = (seg_col == seg_col[BLOCK - 1 : BLOCK, :]).astype(jnp.float32)
    decay_x = expand_heads(
        jnp.exp(l_small[BLOCK - 1 : BLOCK, :]) * info[BLOCK - 1 : BLOCK, 1:2], head_width
    )
    decay_ref[0] = decay_x
    total_ref[...] = total_ref[...] * decay_x
    ending = expand_heads(
        jnp.exp(l_small[BLOCK - 1 : BLOCK, :] - l_small) * dt_small * end_col, head_width
    )
    weighted = (xc.astype(jnp.float32) * ending).astype(jnp.bfloat16)
    new_state = decay_x * state_ref[...] + lax.dot_general(
        b_mat, weighted, (((0,), (0,)), ((), ())), preferred_element_type=jnp.float32
    )
    state_ref[...] = new_state

    @pl.when(blk == pl.num_programs(0) - 1)
    def _():
        sent_ref[...] = new_state.astype(jnp.bfloat16)


def run_state(x, tail8, wconv, bias_row, bc_raw, bc_extra, step_size, rate_row, info):
    rows, width = x.shape
    head_count = step_size.shape[0]
    n_size = bc_raw.shape[2]
    block_count = rows // BLOCK
    row_block = lambda cols: pl.BlockSpec((BLOCK, cols), lambda b: (b, 0))
    whole = lambda shape: pl.BlockSpec(shape, lambda b: (0,) * len(shape))
    return pl.pallas_call(
        functools.partial(state_kernel, width // head_count),
        grid=(block_count,),
        in_specs=[row_block(width), whole((8, width)), whole((4, width)), whole((1, width)),
                  pl.BlockSpec((2, BLOCK, n_size), lambda b: (0, b, 0)), whole(bc_extra.shape),
                  pl.BlockSpec((head_count, BLOCK), lambda b: (0, b)),
                  whole((1, head_count)), row_block(info.shape[1])],
        out_specs=[whole((n_size, width)), row_block(head_count), row_block(head_count),
                   pl.BlockSpec((1, 1, width), lambda b: (b, 0, 0)), whole((1, width)),
                   row_block(width), row_block(n_size), row_block(n_size),
                   whole((n_size, width))],
        out_shape=[jax.ShapeDtypeStruct((n_size, width), jnp.float32),
                   jax.ShapeDtypeStruct((rows, head_count), jnp.float32),
                   jax.ShapeDtypeStruct((rows, head_count), jnp.float32),
                   jax.ShapeDtypeStruct((block_count, 1, width), jnp.float32),
                   jax.ShapeDtypeStruct((1, width), jnp.float32),
                   jax.ShapeDtypeStruct((rows, width), jnp.bfloat16),
                   jax.ShapeDtypeStruct((rows, n_size), jnp.bfloat16),
                   jax.ShapeDtypeStruct((rows, n_size), jnp.bfloat16),
                   jax.ShapeDtypeStruct((n_size, width), jnp.bfloat16)],
        scratch_shapes=[pltpu.VMEM((8, width), jnp.float32),
                        pltpu.VMEM((2, 8, n_size), jnp.float32)],
        compiler_params=pltpu.CompilerParams(dimension_semantics=("arbitrary",)),
    )(x, tail8, wconv, bias_row, bc_raw, bc_extra, step_size, rate_row, info)


def run_blocks(with_y, x, b_full, c_full, l_t, dt_t, seg_row, seg_col, entry_col, decay_x,
               skip_x, entering):
    rows, width = x.shape
    head_count = l_t.shape[1]
    head_width = width // head_count
    n_size = b_full.shape[1]
    block_count = rows // BLOCK
    row_block = lambda cols: pl.BlockSpec((BLOCK, cols), lambda b: (b, 0))
    bt_spec = pl.BlockSpec((n_size, BLOCK), lambda b: (0, b))
    decay_spec = pl.BlockSpec((1, 1, width), lambda b: (b, 0, 0))
    state_spec = pl.BlockSpec((n_size, width), lambda b: (0, 0))
    state_shape = jax.ShapeDtypeStruct((n_size, width), jnp.float32)
    kernel = functools.partial(block_kernel, with_y, head_width)
    params = pltpu.CompilerParams(dimension_semantics=("arbitrary",))
    if with_y:
        return pl.pallas_call(
            kernel,
            grid=(block_count,),
            in_specs=[row_block(width), row_block(n_size), row_block(n_size),
                      row_block(head_count), row_block(head_count),
                      pl.BlockSpec((1, BLOCK), lambda b: (0, b)), row_block(seg_col.shape[1]),
                      decay_spec, pl.BlockSpec((1, width), lambda b: (0, 0)), state_spec],
            out_specs=row_block(width),
            out_shape=jax.ShapeDtypeStruct((rows, width), jnp.bfloat16),
            scratch_shapes=[pltpu.VMEM((n_size, width), jnp.float32)],
            compiler_params=params,
        )(x, b_full, c_full, l_t, dt_t, seg_row, seg_col, decay_x, skip_x, entering)
    return pl.pallas_call(
        kernel,
        grid=(block_count,),
        in_specs=[row_block(width), bt_spec, row_block(head_count), row_block(head_count),
                  row_block(1), decay_spec],
        out_specs=state_spec,
        out_shape=state_shape,
        compiler_params=params,
    )(x, b_t, l_t, dt_t, seg_col, decay_x)


def body(
    inner_input,
    state_input,
    conv_inner,
    bias_inner,
    conv_state,
    bias_state,
    step_size,
    decay_rate,
    skip_gain,
    lengths,
):
    own_rows = inner_input.shape[0]
    head_count = decay_rate.shape[0]
    group_half = state_input.shape[2]
    block_count = own_rows // BLOCK
    positions = lax.axis_index("seq") * own_rows + jnp.arange(own_rows + 3, dtype=jnp.int32) - 3
    seg_ext = segment_of(lengths, positions)
    width = inner_input.shape[1]
    tails = jnp.concatenate(
        [inner_input[-8:], jnp.transpose(state_input[:, -8:], (1, 0, 2)).reshape(8, -1)], 1
    )
    tails = shifted(tails, "seq", 1)
    tail8 = tails[:, :width]
    state_tail = tails[:, width:].reshape(8, 2, group_half)
    extra = jnp.concatenate(
        [jnp.transpose(state_tail, (1, 0, 2)).astype(jnp.float32),
         conv_state.astype(jnp.float32), bias_state[:, None, :]],
        1,
    )
    partner_raw, partner_extra = from_partner((state_input, extra), "head", 0)
    lower_half = lax.axis_index("head") % 2 == 0
    pair = lambda own, other: jnp.where(
        lower_half, jnp.concatenate([own, other], 2), jnp.concatenate([other, own], 2)
    )
    bc_raw = pair(state_input, partner_raw)
    bc_extra = pair(extra, partner_extra)
    head_width = inner_input.shape[1] // head_count
    spread = lambda v: jnp.repeat(v, head_width, axis=-1)
    skip_x = spread(skip_gain).reshape(1, -1)
    seg_own = seg_ext[3:].reshape(block_count, BLOCK)
    seg_prev = seg_ext[2 : 2 + own_rows].reshape(block_count, BLOCK)[:, 0]
    seg_row = seg_ext[3:].reshape(1, own_rows).astype(jnp.float32)
    own_seg = seg_ext[3:]
    entry_col = (seg_own == seg_prev[:, None]).reshape(own_rows)
    keeps = [(seg_ext[3 - back : 3 - back + own_rows] == own_seg) for back in (1, 2, 3)]
    info = jnp.stack(
        [own_seg.astype(jnp.float32), entry_col.astype(jnp.float32)]
        + [keep.astype(jnp.float32) for keep in keeps]
        + [jnp.zeros((own_rows,), jnp.float32)] * 3,
        1,
    )

    local_end, l_t, dt_t, decay_x, total_decay, inner_conv, b_full, c_full, end_sent = run_state(
        inner_input, tail8, conv_inner, bias_inner.reshape(1, -1), bc_raw, bc_extra,
        step_size, decay_rate.reshape(1, -1), info
    )

    def relay(step_num, incoming):
        return shifted(
            (total_decay * incoming.astype(jnp.float32) + local_end).astype(jnp.bfloat16), "seq", 1
        )

    part_rows = own_rows * lax.axis_size("seq")
    hops = min(lax.axis_size("seq") - 1, -(-(part_rows // 2) // own_rows))
    incoming = shifted(end_sent, "seq", 1)
    for step_num in range(1, hops):
        incoming = relay(step_num, incoming)
    return run_blocks(
        True, inner_conv, b_full, c_full, l_t, dt_t, seg_row, info, None, decay_x, skip_x,
        incoming
    )


def solution(mesh):
    return jax.shard_map(
        body,
        mesh=mesh,
        in_specs=(
            P(("grp", "seq"), "head"),
            P(None, ("grp", "seq"), "head"),
            P(None, "head"),
            P("head"),
            P(None, None, "head"),
            P(None, "head"),
            P("head", ("grp", "seq")),
            P("head"),
            P("head"),
            P("grp"),
        ),
        out_specs=P(("grp", "seq"), "head"),
        check_vma=False,
    )
```

```python
import functools

import jax
import jax.numpy as jnp
from jax import lax
from jax.experimental import pallas as pl
from jax.experimental.pallas import tpu as pltpu
from jax.sharding import PartitionSpec as P

BLOCK = 128


def shifted(value, axis, steps):
    count = lax.axis_size(axis)
    initial, last = (max(0, -steps), min(count, count - steps))
    return lax.ppermute(value, axis, [(source, source + steps) for source in range(initial, last)])


def from_partner(block, axis, stride):
    count = lax.axis_size(axis)
    route = []
    for low in range(count):
        high = low | 1 << stride
        if high != low and high < count:
            route += [(low, high), (high, low)]
    return lax.ppermute(block, axis, route)


def segment_of(lengths, positions):
    starts = jnp.cumsum(lengths, dtype=jnp.int32) - lengths
    covered = (starts[None, :] <= positions[:, None]).astype(jnp.int32)
    return jnp.sum(covered, axis=1, dtype=jnp.int32) - 1


def convolve(extended, weight, bias_row, seg_ext, row_count):
    own_seg = seg_ext[3:]
    summed = (
        jnp.zeros(extended.shape[:-2] + (row_count, extended.shape[-1]), jnp.float32) + bias_row
    )
    for offset in range(4):
        kept_mask = (seg_ext[offset : offset + row_count] == own_seg).astype(jnp.float32)[:, None]
        window = extended[..., offset : offset + row_count, :].astype(jnp.float32)
        summed = summed + weight[offset].astype(jnp.float32) * window * kept_mask
    return jax.nn.silu(summed).astype(jnp.bfloat16)


def split_dot(lhs, value):
    high = value.astype(jnp.bfloat16)
    low = (value - high.astype(jnp.float32)).astype(jnp.bfloat16)
    return jnp.dot(lhs, high, preferred_element_type=jnp.float32) + jnp.dot(
        lhs, low, preferred_element_type=jnp.float32
    )


def expand_heads(small, head_width):
    rows, heads = small.shape
    per_tile = 128 // head_width
    lane = lax.broadcasted_iota(jnp.int32, (rows, 128), 1) // head_width
    tiles = []
    for tile in range(heads // per_tile):
        picked = jnp.broadcast_to(small[:, tile * per_tile : tile * per_tile + 1], (rows, 128))
        for k in range(1, per_tile):
            column = small[:, tile * per_tile + k : tile * per_tile + k + 1]
            picked = jnp.where(lane == k, jnp.broadcast_to(column, (rows, 128)), picked)
        tiles.append(picked)
    return jnp.concatenate(tiles, axis=1)


def block_kernel(with_y, head_width, *refs):
    if with_y:
        (x_ref, b_ref, c_ref, l_ref, dt_ref, segr_ref, info_ref, decay_ref,
         skip_ref, ein_ref, out_ref, state_ref) = refs
    else:
        (x_ref, b_ref, l_ref, dt_ref, segc_ref, decay_ref, state_ref) = refs
    blk = pl.program_id(0)

    @pl.when(blk == 0)
    def _():
        if with_y:
            state_ref[...] = ein_ref[...].astype(jnp.float32)
        else:
            state_ref[...] = jnp.zeros(state_ref.shape, jnp.float32)

    info = info_ref[...]
    seg_col = info[:, 0:1]
    end_col = (seg_col == seg_col[BLOCK - 1 : BLOCK, :]).astype(jnp.float32)
    l_small = l_ref[...]
    dt_small = dt_ref[...]
    x = x_ref[...].astype(jnp.float32)
    state = state_ref[...]
    if with_y:
        c_mat = c_ref[...]
        seg_row = segr_ref[...]
        scores = lax.dot_general(
            c_mat, b_ref[...], (((1,), (1,)), ((), ())), preferred_element_type=jnp.float32
        )
        rows = lax.broadcasted_iota(jnp.int32, (BLOCK, BLOCK), 0)
        cols = lax.broadcasted_iota(jnp.int32, (BLOCK, BLOCK), 1)
        allowed = (rows >= cols) & (seg_col == seg_row)
        masked = jnp.where(allowed, scores, 0.0).astype(jnp.bfloat16)
        rising = expand_heads(jnp.exp(l_small), head_width)
        falling = expand_heads(jnp.exp(-l_small) * dt_small, head_width)
        intra = split_dot(masked, x * falling) * rising
        inter = split_dot(c_mat, state) * (rising * info[:, 1:2])
        out_ref[...] = (intra + inter + skip_ref[...] * x).astype(jnp.bfloat16)
    ending = expand_heads(
        jnp.exp(l_small[BLOCK - 1 : BLOCK, :] - l_small) * dt_small * end_col, head_width
    )
    weighted = (x * ending).astype(jnp.bfloat16)
    state_ref[...] = decay_ref[0] * state + lax.dot_general(
        b_ref[...], weighted, (((0,), (0,)), ((), ())), preferred_element_type=jnp.float32
    )


def causal_conv(raw, prev, taps, bias, info):
    top_row = lax.broadcasted_iota(jnp.int32, prev.shape, 0)
    summed = jnp.zeros(raw.shape, jnp.float32) + bias
    for offset in range(4):
        back = 3 - offset
        if back == 0:
            window = raw
        else:
            rolled = pltpu.roll(raw, back, 0)
            top = jnp.where(top_row < back, pltpu.roll(prev, back, 0), rolled[:8])
            window = jnp.concatenate([top, rolled[8:]], 0) * info[:, 1 + back : 2 + back]
        summed = summed + taps[offset : offset + 1, :] * window
    return jax.nn.silu(summed).astype(jnp.bfloat16)


def state_kernel(head_width, x_ref, tail_ref, wconv_ref, bias_ref, own_ref, other_ref, ownx_ref,
                 otherx_ref, flag_ref, dt_ref, rate_ref, info_ref, state_ref, l_ref, dtt_ref,
                 decay_ref, total_ref, xc_ref, bo_ref, co_ref, sent_ref, prev_ref, bcprev_ref):
    blk = pl.program_id(0)

    @pl.when(blk == 0)
    def _():
        state_ref[...] = jnp.zeros(state_ref.shape, jnp.float32)
        total_ref[...] = jnp.ones(total_ref.shape, jnp.float32)
        prev_ref[...] = tail_ref[...].astype(jnp.float32)
        bcprev_ref[0] = ownx_ref[:, 0:8, :]
        bcprev_ref[1] = otherx_ref[:, 0:8, :]

    info = info_ref[...]
    raw = x_ref[...].astype(jnp.float32)
    xc = causal_conv(raw, prev_ref[...], wconv_ref[...].astype(jnp.float32), bias_ref[...], info)
    prev_ref[...] = raw[BLOCK - 8 :]
    xc_ref[...] = xc
    lower = flag_ref[...][:, 0:1] > 0.5
    convolved = []
    for which in range(2):
        halves = []
        for side, (raw_ref, extra_ref) in enumerate(((own_ref, ownx_ref), (other_ref, otherx_ref))):
            raw_bc = raw_ref[which].astype(jnp.float32)
            extra = extra_ref[which]
            halves.append(
                causal_conv(raw_bc, bcprev_ref[side, which], extra[8:12], extra[12:13], info)
            )
            bcprev_ref[side, which] = raw_bc[BLOCK - 8 :]
        convolved.append(jnp.where(
            lower, jnp.concatenate(halves, 1), jnp.concatenate(halves[::-1], 1)
        ))
    b_mat, c_mat = convolved
    bo_ref[...] = b_mat
    co_ref[...] = c_mat

    rows = lax.broadcasted_iota(jnp.int32, (2 * BLOCK, BLOCK), 0)
    cols = lax.broadcasted_iota(jnp.int32, (2 * BLOCK, BLOCK), 1)
    picker = jnp.where(
        ((rows < BLOCK) & (rows >= cols)) | (rows - BLOCK == cols), 1.0, 0.0
    ).astype(jnp.bfloat16)
    rest = dt_ref[...]
    cum = None
    for _ in range(3):
        piece = rest.astype(jnp.bfloat16)
        part = lax.dot_general(
            picker, piece, (((1,), (1,)), ((), ())), preferred_element_type=jnp.float32
        )
        cum = part if cum is None else cum + part
        rest = rest - piece.astype(jnp.float32)
    l_small = -cum[:BLOCK] * rate_ref[...]
    dt_small = cum[BLOCK:]
    l_ref[...] = l_small
    dtt_ref[...] = dt_small
    seg_col = info[:, 0:1]
    end_col = (seg_col == seg_col[BLOCK - 1 : BLOCK, :]).astype(jnp.float32)
    decay_x = expand_heads(
        jnp.exp(l_small[BLOCK - 1 : BLOCK, :]) * info[BLOCK - 1 : BLOCK, 1:2], head_width
    )
    decay_ref[0] = decay_x
    total_ref[...] = total_ref[...] * decay_x
    ending = expand_heads(
        jnp.exp(l_small[BLOCK - 1 : BLOCK, :] - l_small) * dt_small * end_col, head_width
    )
    weighted = (xc.astype(jnp.float32) * ending).astype(jnp.bfloat16)
    new_state = decay_x * state_ref[...] + lax.dot_general(
        b_mat, weighted, (((0,), (0,)), ((), ())), preferred_element_type=jnp.float32
    )
    state_ref[...] = new_state

    @pl.when(blk == pl.num_programs(0) - 1)
    def _():
        sent_ref[...] = new_state.astype(jnp.bfloat16)


def run_state(x, tail8, wconv, bias_row, own_raw, other_raw, own_extra, other_extra, flag,
              step_size, rate_row, info):
    rows, width = x.shape
    head_count = step_size.shape[0]
    half = own_raw.shape[2]
    n_size = 2 * half
    block_count = rows // BLOCK
    row_block = lambda cols: pl.BlockSpec((BLOCK, cols), lambda b: (b, 0))
    whole = lambda shape: pl.BlockSpec(shape, lambda b: (0,) * len(shape))
    return pl.pallas_call(
        functools.partial(state_kernel, width // head_count),
        grid=(block_count,),
        in_specs=[row_block(width), whole((8, width)), whole((4, width)), whole((1, width)),
                  pl.BlockSpec((2, BLOCK, half), lambda b: (0, b, 0)),
                  pl.BlockSpec((2, BLOCK, half), lambda b: (0, b, 0)),
                  whole(own_extra.shape), whole(own_extra.shape), whole(flag.shape),
                  pl.BlockSpec((head_count, BLOCK), lambda b: (0, b)),
                  whole((1, head_count)), row_block(info.shape[1])],
        out_specs=[whole((n_size, width)), row_block(head_count), row_block(head_count),
                   pl.BlockSpec((1, 1, width), lambda b: (b, 0, 0)), whole((1, width)),
                   row_block(width), row_block(n_size), row_block(n_size),
                   whole((n_size, width))],
        out_shape=[jax.ShapeDtypeStruct((n_size, width), jnp.float32),
                   jax.ShapeDtypeStruct((rows, head_count), jnp.float32),
                   jax.ShapeDtypeStruct((rows, head_count), jnp.float32),
                   jax.ShapeDtypeStruct((block_count, 1, width), jnp.float32),
                   jax.ShapeDtypeStruct((1, width), jnp.float32),
                   jax.ShapeDtypeStruct((rows, width), jnp.bfloat16),
                   jax.ShapeDtypeStruct((rows, n_size), jnp.bfloat16),
                   jax.ShapeDtypeStruct((rows, n_size), jnp.bfloat16),
                   jax.ShapeDtypeStruct((n_size, width), jnp.bfloat16)],
        scratch_shapes=[pltpu.VMEM((8, width), jnp.float32),
                        pltpu.VMEM((2, 2, 8, half), jnp.float32)],
        compiler_params=pltpu.CompilerParams(dimension_semantics=("arbitrary",)),
    )(x, tail8, wconv, bias_row, own_raw, other_raw, own_extra, other_extra, flag, step_size,
      rate_row, info)


def run_blocks(with_y, x, b_full, c_full, l_t, dt_t, seg_row, seg_col, entry_col, decay_x,
               skip_x, entering):
    rows, width = x.shape
    head_count = l_t.shape[1]
    head_width = width // head_count
    n_size = b_full.shape[1]
    block_count = rows // BLOCK
    row_block = lambda cols: pl.BlockSpec((BLOCK, cols), lambda b: (b, 0))
    bt_spec = pl.BlockSpec((n_size, BLOCK), lambda b: (0, b))
    decay_spec = pl.BlockSpec((1, 1, width), lambda b: (b, 0, 0))
    state_spec = pl.BlockSpec((n_size, width), lambda b: (0, 0))
    state_shape = jax.ShapeDtypeStruct((n_size, width), jnp.float32)
    kernel = functools.partial(block_kernel, with_y, head_width)
    params = pltpu.CompilerParams(dimension_semantics=("arbitrary",))
    if with_y:
        return pl.pallas_call(
            kernel,
            grid=(block_count,),
            in_specs=[row_block(width), row_block(n_size), row_block(n_size),
                      row_block(head_count), row_block(head_count),
                      pl.BlockSpec((1, BLOCK), lambda b: (0, b)), row_block(seg_col.shape[1]),
                      decay_spec, pl.BlockSpec((1, width), lambda b: (0, 0)), state_spec],
            out_specs=row_block(width),
            out_shape=jax.ShapeDtypeStruct((rows, width), jnp.bfloat16),
            scratch_shapes=[pltpu.VMEM((n_size, width), jnp.float32)],
            compiler_params=params,
        )(x, b_full, c_full, l_t, dt_t, seg_row, seg_col, decay_x, skip_x, entering)
    return pl.pallas_call(
        kernel,
        grid=(block_count,),
        in_specs=[row_block(width), bt_spec, row_block(head_count), row_block(head_count),
                  row_block(1), decay_spec],
        out_specs=state_spec,
        out_shape=state_shape,
        compiler_params=params,
    )(x, b_t, l_t, dt_t, seg_col, decay_x)


def body(
    inner_input,
    state_input,
    conv_inner,
    bias_inner,
    conv_state,
    bias_state,
    step_size,
    decay_rate,
    skip_gain,
    lengths,
):
    own_rows = inner_input.shape[0]
    head_count = decay_rate.shape[0]
    group_half = state_input.shape[2]
    block_count = own_rows // BLOCK
    positions = lax.axis_index("seq") * own_rows + jnp.arange(own_rows + 3, dtype=jnp.int32) - 3
    seg_ext = segment_of(lengths, positions)
    width = inner_input.shape[1]
    tails = jnp.concatenate(
        [inner_input[-8:], jnp.transpose(state_input[:, -8:], (1, 0, 2)).reshape(8, -1)], 1
    )
    tails = shifted(tails, "seq", 1)
    tail8 = tails[:, :width]
    state_tail = tails[:, width:].reshape(8, 2, group_half)
    extra = jnp.concatenate(
        [jnp.transpose(state_tail, (1, 0, 2)).astype(jnp.float32),
         conv_state.astype(jnp.float32), bias_state[:, None, :]],
        1,
    )
    partner_raw, partner_extra = from_partner((state_input, extra), "head", 0)
    lower_half = (lax.axis_index("head") % 2 == 0).astype(jnp.float32)
    flag = jnp.full((1, 128), lower_half, jnp.float32)
    head_width = inner_input.shape[1] // head_count
    spread = lambda v: jnp.repeat(v, head_width, axis=-1)
    skip_x = spread(skip_gain).reshape(1, -1)
    seg_own = seg_ext[3:].reshape(block_count, BLOCK)
    seg_prev = seg_ext[2 : 2 + own_rows].reshape(block_count, BLOCK)[:, 0]
    seg_row = seg_ext[3:].reshape(1, own_rows).astype(jnp.float32)
    own_seg = seg_ext[3:]
    entry_col = (seg_own == seg_prev[:, None]).reshape(own_rows)
    keeps = [(seg_ext[3 - back : 3 - back + own_rows] == own_seg) for back in (1, 2, 3)]
    info = jnp.stack(
        [own_seg.astype(jnp.float32), entry_col.astype(jnp.float32)]
        + [keep.astype(jnp.float32) for keep in keeps]
        + [jnp.zeros((own_rows,), jnp.float32)] * 3,
        1,
    )

    local_end, l_t, dt_t, decay_x, total_decay, inner_conv, b_full, c_full, end_sent = run_state(
        inner_input, tail8, conv_inner, bias_inner.reshape(1, -1), state_input, partner_raw,
        extra, partner_extra, flag,
        step_size, decay_rate.reshape(1, -1), info
    )

    def relay(step_num, incoming):
        return shifted(
            (total_decay * incoming.astype(jnp.float32) + local_end).astype(jnp.bfloat16), "seq", 1
        )

    part_rows = own_rows * lax.axis_size("seq")
    hops = min(lax.axis_size("seq") - 1, -(-(part_rows // 2) // own_rows))
    incoming = shifted(end_sent, "seq", 1)
    for step_num in range(1, hops):
        incoming = relay(step_num, incoming)
    return run_blocks(
        True, inner_conv, b_full, c_full, l_t, dt_t, seg_row, info, None, decay_x, skip_x,
        incoming
    )


def solution(mesh):
    return jax.shard_map(
        body,
        mesh=mesh,
        in_specs=(
            P(("grp", "seq"), "head"),
            P(None, ("grp", "seq"), "head"),
            P(None, "head"),
            P("head"),
            P(None, None, "head"),
            P(None, "head"),
            P("head", ("grp", "seq")),
            P("head"),
            P("head"),
            P("grp"),
        ),
        out_specs=P(("grp", "seq"), "head"),
        check_vma=False,
    )
```

```python
import functools

import jax
import jax.numpy as jnp
from jax import lax
from jax.experimental import pallas as pl
from jax.experimental.pallas import tpu as pltpu
from jax.sharding import PartitionSpec as P

BLOCK = 128


def shifted(value, axis, steps):
    count = lax.axis_size(axis)
    initial, last = (max(0, -steps), min(count, count - steps))
    return lax.ppermute(value, axis, [(source, source + steps) for source in range(initial, last)])


def from_partner(block, axis, stride):
    count = lax.axis_size(axis)
    route = []
    for low in range(count):
        high = low | 1 << stride
        if high != low and high < count:
            route += [(low, high), (high, low)]
    return lax.ppermute(block, axis, route)


def segment_of(lengths, positions):
    starts = jnp.cumsum(lengths, dtype=jnp.int32) - lengths
    covered = (starts[None, :] <= positions[:, None]).astype(jnp.int32)
    return jnp.sum(covered, axis=1, dtype=jnp.int32) - 1


def convolve(extended, weight, bias_row, seg_ext, row_count):
    own_seg = seg_ext[3:]
    summed = (
        jnp.zeros(extended.shape[:-2] + (row_count, extended.shape[-1]), jnp.float32) + bias_row
    )
    for offset in range(4):
        kept_mask = (seg_ext[offset : offset + row_count] == own_seg).astype(jnp.float32)[:, None]
        window = extended[..., offset : offset + row_count, :].astype(jnp.float32)
        summed = summed + weight[offset].astype(jnp.float32) * window * kept_mask
    return jax.nn.silu(summed).astype(jnp.bfloat16)


def split_dot(lhs, value):
    high = value.astype(jnp.bfloat16)
    low = (value - high.astype(jnp.float32)).astype(jnp.bfloat16)
    return jnp.dot(lhs, high, preferred_element_type=jnp.float32) + jnp.dot(
        lhs, low, preferred_element_type=jnp.float32
    )


def expand_heads(small, head_width):
    rows, heads = small.shape
    per_tile = 128 // head_width
    lane = lax.broadcasted_iota(jnp.int32, (rows, 128), 1) // head_width
    tiles = []
    for tile in range(heads // per_tile):
        picked = jnp.broadcast_to(small[:, tile * per_tile : tile * per_tile + 1], (rows, 128))
        for k in range(1, per_tile):
            column = small[:, tile * per_tile + k : tile * per_tile + k + 1]
            picked = jnp.where(lane == k, jnp.broadcast_to(column, (rows, 128)), picked)
        tiles.append(picked)
    return jnp.concatenate(tiles, axis=1)


def block_kernel(with_y, head_width, *refs):
    if with_y:
        (x_ref, b_ref, c_ref, l_ref, dt_ref, segr_ref, info_ref, decay_ref,
         skip_ref, ein_ref, out_ref, state_ref) = refs
    else:
        (x_ref, b_ref, l_ref, dt_ref, segc_ref, decay_ref, state_ref) = refs
    blk = pl.program_id(0)

    @pl.when(blk == 0)
    def _():
        if with_y:
            state_ref[...] = ein_ref[...].astype(jnp.float32)
        else:
            state_ref[...] = jnp.zeros(state_ref.shape, jnp.float32)

    info = info_ref[...]
    seg_col = info[:, 0:1]
    end_col = (seg_col == seg_col[BLOCK - 1 : BLOCK, :]).astype(jnp.float32)
    l_small = l_ref[...]
    dt_small = dt_ref[...]
    x = x_ref[...].astype(jnp.float32)
    state = state_ref[...]
    if with_y:
        c_mat = c_ref[...]
        seg_row = segr_ref[...]
        scores = lax.dot_general(
            c_mat, b_ref[...], (((1,), (1,)), ((), ())), preferred_element_type=jnp.float32
        )
        rows = lax.broadcasted_iota(jnp.int32, (BLOCK, BLOCK), 0)
        cols = lax.broadcasted_iota(jnp.int32, (BLOCK, BLOCK), 1)
        allowed = (rows >= cols) & (seg_col == seg_row)
        masked = jnp.where(allowed, scores, 0.0).astype(jnp.bfloat16)
        rising = expand_heads(jnp.exp(l_small), head_width)
        falling = expand_heads(jnp.exp(-l_small) * dt_small, head_width)
        intra = split_dot(masked, x * falling) * rising
        inter = split_dot(c_mat, state) * (rising * info[:, 1:2])
        out_ref[...] = (intra + inter + skip_ref[...] * x).astype(jnp.bfloat16)
    ending = expand_heads(
        jnp.exp(l_small[BLOCK - 1 : BLOCK, :] - l_small) * dt_small * end_col, head_width
    )
    weighted = (x * ending).astype(jnp.bfloat16)
    state_ref[...] = decay_ref[0] * state + lax.dot_general(
        b_ref[...], weighted, (((0,), (0,)), ((), ())), preferred_element_type=jnp.float32
    )


def causal_conv(raw, prev, taps, bias, info):
    top_row = lax.broadcasted_iota(jnp.int32, prev.shape, 0)
    summed = jnp.zeros(raw.shape, jnp.float32) + bias
    for offset in range(4):
        back = 3 - offset
        if back == 0:
            window = raw
        else:
            rolled = pltpu.roll(raw, back, 0)
            top = jnp.where(top_row < back, pltpu.roll(prev, back, 0), rolled[:8])
            window = jnp.concatenate([top, rolled[8:]], 0) * info[:, 1 + back : 2 + back]
        summed = summed + taps[offset : offset + 1, :] * window
    return jax.nn.silu(summed).astype(jnp.bfloat16)


def state_kernel(head_width, x_ref, tail_ref, wconv_ref, bias_ref, own_ref, other_ref, ownx_ref,
                 otherx_ref, flag_ref, dt_ref, rate_ref, info_ref, state_ref, l_ref, dtt_ref,
                 decay_ref, total_ref, xc_ref, bo_ref, co_ref, sent_ref, prefix_ref, prev_ref,
                 bcprev_ref):
    blk = pl.program_id(0)

    @pl.when(blk == 0)
    def _():
        state_ref[...] = jnp.zeros(state_ref.shape, jnp.float32)
        total_ref[...] = jnp.ones(total_ref.shape, jnp.float32)
        prev_ref[...] = tail_ref[...].astype(jnp.float32)
        bcprev_ref[0] = ownx_ref[:, 0:8, :]
        bcprev_ref[1] = otherx_ref[:, 0:8, :]

    info = info_ref[...]
    raw = x_ref[...].astype(jnp.float32)
    xc = causal_conv(raw, prev_ref[...], wconv_ref[...].astype(jnp.float32), bias_ref[...], info)
    prev_ref[...] = raw[BLOCK - 8 :]
    xc_ref[...] = xc
    lower = flag_ref[...][:, 0:1] > 0.5
    convolved = []
    for which in range(2):
        halves = []
        for side, (raw_ref, extra_ref) in enumerate(((own_ref, ownx_ref), (other_ref, otherx_ref))):
            raw_bc = raw_ref[which].astype(jnp.float32)
            extra = extra_ref[which]
            halves.append(
                causal_conv(raw_bc, bcprev_ref[side, which], extra[8:12], extra[12:13], info)
            )
            bcprev_ref[side, which] = raw_bc[BLOCK - 8 :]
        convolved.append(jnp.where(
            lower, jnp.concatenate(halves, 1), jnp.concatenate(halves[::-1], 1)
        ))
    b_mat, c_mat = convolved
    bo_ref[...] = b_mat
    co_ref[...] = c_mat

    rows = lax.broadcasted_iota(jnp.int32, (2 * BLOCK, BLOCK), 0)
    cols = lax.broadcasted_iota(jnp.int32, (2 * BLOCK, BLOCK), 1)
    picker = jnp.where(
        ((rows < BLOCK) & (rows >= cols)) | (rows - BLOCK == cols), 1.0, 0.0
    ).astype(jnp.bfloat16)
    rest = dt_ref[...]
    cum = None
    for _ in range(3):
        piece = rest.astype(jnp.bfloat16)
        part = lax.dot_general(
            picker, piece, (((1,), (1,)), ((), ())), preferred_element_type=jnp.float32
        )
        cum = part if cum is None else cum + part
        rest = rest - piece.astype(jnp.float32)
    l_small = -cum[:BLOCK] * rate_ref[...]
    dt_small = cum[BLOCK:]
    l_ref[...] = l_small
    dtt_ref[...] = dt_small
    seg_col = info[:, 0:1]
    end_col = (seg_col == seg_col[BLOCK - 1 : BLOCK, :]).astype(jnp.float32)
    decay_x = expand_heads(
        jnp.exp(l_small[BLOCK - 1 : BLOCK, :]) * info[BLOCK - 1 : BLOCK, 1:2], head_width
    )
    decay_ref[0] = decay_x
    prefix_ref[0] = total_ref[...]
    total_ref[...] = total_ref[...] * decay_x
    ending = expand_heads(
        jnp.exp(l_small[BLOCK - 1 : BLOCK, :] - l_small) * dt_small * end_col, head_width
    )
    weighted = (xc.astype(jnp.float32) * ending).astype(jnp.bfloat16)
    new_state = decay_x * state_ref[...] + lax.dot_general(
        b_mat, weighted, (((0,), (0,)), ((), ())), preferred_element_type=jnp.float32
    )
    state_ref[...] = new_state

    @pl.when(blk == pl.num_programs(0) - 1)
    def _():
        sent_ref[...] = new_state.astype(jnp.bfloat16)


def run_state(x, tail8, wconv, bias_row, own_raw, other_raw, own_extra, other_extra, flag,
              step_size, rate_row, info):
    rows, width = x.shape
    head_count = step_size.shape[0]
    half = own_raw.shape[2]
    n_size = 2 * half
    block_count = rows // BLOCK
    row_block = lambda cols: pl.BlockSpec((BLOCK, cols), lambda b: (b, 0))
    whole = lambda shape: pl.BlockSpec(shape, lambda b: (0,) * len(shape))
    return pl.pallas_call(
        functools.partial(state_kernel, width // head_count),
        grid=(block_count,),
        in_specs=[row_block(width), whole((8, width)), whole((4, width)), whole((1, width)),
                  pl.BlockSpec((2, BLOCK, half), lambda b: (0, b, 0)),
                  pl.BlockSpec((2, BLOCK, half), lambda b: (0, b, 0)),
                  whole(own_extra.shape), whole(own_extra.shape), whole(flag.shape),
                  pl.BlockSpec((head_count, BLOCK), lambda b: (0, b)),
                  whole((1, head_count)), row_block(info.shape[1])],
        out_specs=[whole((n_size, width)), row_block(head_count), row_block(head_count),
                   pl.BlockSpec((1, 1, width), lambda b: (b, 0, 0)), whole((1, width)),
                   row_block(width), row_block(n_size), row_block(n_size),
                   whole((n_size, width)), pl.BlockSpec((1, 1, width), lambda b: (b, 0, 0))],
        out_shape=[jax.ShapeDtypeStruct((n_size, width), jnp.float32),
                   jax.ShapeDtypeStruct((rows, head_count), jnp.float32),
                   jax.ShapeDtypeStruct((rows, head_count), jnp.float32),
                   jax.ShapeDtypeStruct((block_count, 1, width), jnp.float32),
                   jax.ShapeDtypeStruct((1, width), jnp.float32),
                   jax.ShapeDtypeStruct((rows, width), jnp.bfloat16),
                   jax.ShapeDtypeStruct((rows, n_size), jnp.bfloat16),
                   jax.ShapeDtypeStruct((rows, n_size), jnp.bfloat16),
                   jax.ShapeDtypeStruct((n_size, width), jnp.bfloat16),
                   jax.ShapeDtypeStruct((block_count, 1, width), jnp.float32)],
        scratch_shapes=[pltpu.VMEM((8, width), jnp.float32),
                        pltpu.VMEM((2, 2, 8, half), jnp.float32)],
        compiler_params=pltpu.CompilerParams(dimension_semantics=("arbitrary",)),
    )(x, tail8, wconv, bias_row, own_raw, other_raw, own_extra, other_extra, flag, step_size,
      rate_row, info)


def partial_kernel(head_width, from_zero, *refs):
    if from_zero:
        (x_ref, b_ref, c_ref, l_ref, dt_ref, segr_ref, info_ref, decay_ref, skip_ref, out_ref,
         end_ref, state_ref) = refs
    else:
        (x_ref, b_ref, c_ref, l_ref, dt_ref, segr_ref, info_ref, decay_ref, skip_ref, init_ref,
         after_ref, buf_ref, out_ref, end_ref, state_ref) = refs
    blk = pl.program_id(0)

    @pl.when(blk == 0)
    def _():
        if from_zero:
            state_ref[...] = jnp.zeros(state_ref.shape, jnp.float32)
        else:
            state_ref[...] = init_ref[...]

    info = info_ref[...]
    seg_col = info[:, 0:1]
    end_col = (seg_col == seg_col[BLOCK - 1 : BLOCK, :]).astype(jnp.float32)
    l_small = l_ref[...]
    dt_small = dt_ref[...]
    x = x_ref[...].astype(jnp.float32)
    state = state_ref[...]
    c_mat = c_ref[...]
    b_mat = b_ref[...]
    scores = lax.dot_general(
        c_mat, b_mat, (((1,), (1,)), ((), ())), preferred_element_type=jnp.float32
    )
    rows = lax.broadcasted_iota(jnp.int32, (BLOCK, BLOCK), 0)
    cols = lax.broadcasted_iota(jnp.int32, (BLOCK, BLOCK), 1)
    allowed = (rows >= cols) & (seg_col == segr_ref[...])
    masked = jnp.where(allowed, scores, 0.0).astype(jnp.bfloat16)
    rising = expand_heads(jnp.exp(l_small), head_width)
    falling = expand_heads(jnp.exp(-l_small) * dt_small, head_width)
    intra = split_dot(masked, x * falling) * rising
    inter = split_dot(c_mat, state) * (rising * info[:, 1:2])
    out_ref[...] = intra + inter + skip_ref[...] * x
    ending = expand_heads(
        jnp.exp(l_small[BLOCK - 1 : BLOCK, :] - l_small) * dt_small * end_col, head_width
    )
    weighted = (x * ending).astype(jnp.bfloat16)
    new_state = decay_ref[0] * state + lax.dot_general(
        b_mat, weighted, (((0,), (0,)), ((), ())), preferred_element_type=jnp.float32
    )
    state_ref[...] = new_state

    @pl.when(blk == pl.num_programs(0) - 1)
    def _():
        end_ref[...] = new_state


def run_partial(first, count, x, b_full, c_full, l_t, dt_t, seg_row, info, decay_x, skip_x,
                init=None, after=None, buf=None):
    rows, width = x.shape
    head_count = l_t.shape[1]
    n_size = b_full.shape[1]
    row_block = lambda cols: pl.BlockSpec((BLOCK, cols), lambda b: (b + first, 0))
    whole = lambda shape: pl.BlockSpec(shape, lambda b: (0,) * len(shape))
    from_zero = init is None
    in_specs = [row_block(width), row_block(n_size), row_block(n_size), row_block(head_count),
                row_block(head_count), pl.BlockSpec((1, BLOCK), lambda b: (0, b + first)),
                row_block(info.shape[1]), pl.BlockSpec((1, 1, width), lambda b: (b + first, 0, 0)),
                whole((1, width))]
    args = [x, b_full, c_full, l_t, dt_t, seg_row, info, decay_x, skip_x]
    aliases = {}
    if not from_zero:
        any_spec = pl.BlockSpec(memory_space=pl.ANY)
        in_specs += [whole((n_size, width)), any_spec, any_spec]
        args += [init, after, buf]
        aliases = {len(args) - 1: 0}
    return pl.pallas_call(
        functools.partial(partial_kernel, width // head_count, from_zero),
        grid=(count,),
        in_specs=in_specs,
        out_specs=[row_block(width), whole((n_size, width))],
        out_shape=[jax.ShapeDtypeStruct((rows, width), jnp.float32),
                   jax.ShapeDtypeStruct((n_size, width), jnp.float32)],
        scratch_shapes=[pltpu.VMEM((n_size, width), jnp.float32)],
        input_output_aliases=aliases,
        compiler_params=pltpu.CompilerParams(dimension_semantics=("arbitrary",)),
    )(*args)


def correct_kernel(head_width, y_ref, c_ref, l_ref, info_ref, prefix_ref, ein_ref, out_ref):
    rows, cols = y_ref.shape
    rising = expand_heads(jnp.exp(l_ref[0]), head_width)
    blocks = prefix_ref.shape[0]
    prefix = jnp.broadcast_to(prefix_ref[...], (blocks, BLOCK, cols)).reshape(rows, cols)
    carried = jnp.dot(c_ref[...], ein_ref[...], preferred_element_type=jnp.float32)
    factor = rising * info_ref[...][:, 1:2] * prefix
    out_ref[...] = (y_ref[...] + carried * factor).astype(jnp.bfloat16)


def run_correct(partial, c_full, l_t, info, prefix_x, entering):
    rows, width = partial.shape
    head_count = l_t.shape[1]
    head_width = width // head_count
    n_size = c_full.shape[1]
    tile = 256
    tiles = width // tile
    heads_per = tile // head_width
    l_tiles = jnp.transpose(l_t.reshape(rows, tiles, heads_per), (1, 0, 2))
    block_count = prefix_x.shape[0]
    return pl.pallas_call(
        functools.partial(correct_kernel, head_width),
        grid=(tiles,),
        in_specs=[pl.BlockSpec((rows, tile), lambda j: (0, j)),
                  pl.BlockSpec((rows, n_size), lambda j: (0, 0)),
                  pl.BlockSpec((1, rows, heads_per), lambda j: (j, 0, 0)),
                  pl.BlockSpec((rows, info.shape[1]), lambda j: (0, 0)),
                  pl.BlockSpec((block_count, 1, tile), lambda j: (0, 0, j)),
                  pl.BlockSpec((n_size, tile), lambda j: (0, j))],
        out_specs=pl.BlockSpec((rows, tile), lambda j: (0, j)),
        out_shape=jax.ShapeDtypeStruct((rows, width), jnp.bfloat16),
        compiler_params=pltpu.CompilerParams(dimension_semantics=("arbitrary",)),
    )(partial, c_full, l_tiles, info, prefix_x, entering)


def run_blocks(with_y, x, b_full, c_full, l_t, dt_t, seg_row, seg_col, entry_col, decay_x,
               skip_x, entering):
    rows, width = x.shape
    head_count = l_t.shape[1]
    head_width = width // head_count
    n_size = b_full.shape[1]
    block_count = rows // BLOCK
    row_block = lambda cols: pl.BlockSpec((BLOCK, cols), lambda b: (b, 0))
    bt_spec = pl.BlockSpec((n_size, BLOCK), lambda b: (0, b))
    decay_spec = pl.BlockSpec((1, 1, width), lambda b: (b, 0, 0))
    state_spec = pl.BlockSpec((n_size, width), lambda b: (0, 0))
    state_shape = jax.ShapeDtypeStruct((n_size, width), jnp.float32)
    kernel = functools.partial(block_kernel, with_y, head_width)
    params = pltpu.CompilerParams(dimension_semantics=("arbitrary",))
    if with_y:
        return pl.pallas_call(
            kernel,
            grid=(block_count,),
            in_specs=[row_block(width), row_block(n_size), row_block(n_size),
                      row_block(head_count), row_block(head_count),
                      pl.BlockSpec((1, BLOCK), lambda b: (0, b)), row_block(seg_col.shape[1]),
                      decay_spec, pl.BlockSpec((1, width), lambda b: (0, 0)), state_spec],
            out_specs=row_block(width),
            out_shape=jax.ShapeDtypeStruct((rows, width), jnp.bfloat16),
            scratch_shapes=[pltpu.VMEM((n_size, width), jnp.float32)],
            compiler_params=params,
        )(x, b_full, c_full, l_t, dt_t, seg_row, seg_col, decay_x, skip_x, entering)
    return pl.pallas_call(
        kernel,
        grid=(block_count,),
        in_specs=[row_block(width), bt_spec, row_block(head_count), row_block(head_count),
                  row_block(1), decay_spec],
        out_specs=state_spec,
        out_shape=state_shape,
        compiler_params=params,
    )(x, b_t, l_t, dt_t, seg_col, decay_x)


def body(
    inner_input,
    state_input,
    conv_inner,
    bias_inner,
    conv_state,
    bias_state,
    step_size,
    decay_rate,
    skip_gain,
    lengths,
):
    own_rows = inner_input.shape[0]
    head_count = decay_rate.shape[0]
    group_half = state_input.shape[2]
    block_count = own_rows // BLOCK
    positions = lax.axis_index("seq") * own_rows + jnp.arange(own_rows + 3, dtype=jnp.int32) - 3
    seg_ext = segment_of(lengths, positions)
    width = inner_input.shape[1]
    tails = jnp.concatenate(
        [inner_input[-8:], jnp.transpose(state_input[:, -8:], (1, 0, 2)).reshape(8, -1)], 1
    )
    tails = shifted(tails, "seq", 1)
    tail8 = tails[:, :width]
    state_tail = tails[:, width:].reshape(8, 2, group_half)
    extra = jnp.concatenate(
        [jnp.transpose(state_tail, (1, 0, 2)).astype(jnp.float32),
         conv_state.astype(jnp.float32), bias_state[:, None, :]],
        1,
    )
    partner_raw, partner_extra = from_partner((state_input, extra), "head", 0)
    lower_half = (lax.axis_index("head") % 2 == 0).astype(jnp.float32)
    flag = jnp.full((1, 128), lower_half, jnp.float32)
    head_width = inner_input.shape[1] // head_count
    spread = lambda v: jnp.repeat(v, head_width, axis=-1)
    skip_x = spread(skip_gain).reshape(1, -1)
    seg_own = seg_ext[3:].reshape(block_count, BLOCK)
    seg_prev = seg_ext[2 : 2 + own_rows].reshape(block_count, BLOCK)[:, 0]
    seg_row = seg_ext[3:].reshape(1, own_rows).astype(jnp.float32)
    own_seg = seg_ext[3:]
    entry_col = (seg_own == seg_prev[:, None]).reshape(own_rows)
    keeps = [(seg_ext[3 - back : 3 - back + own_rows] == own_seg) for back in (1, 2, 3)]
    info = jnp.stack(
        [own_seg.astype(jnp.float32), entry_col.astype(jnp.float32)]
        + [keep.astype(jnp.float32) for keep in keeps]
        + [jnp.zeros((own_rows,), jnp.float32)] * 3,
        1,
    )

    (local_end, l_t, dt_t, decay_x, total_decay, inner_conv, b_full, c_full, end_sent,
     prefix_x) = run_state(
        inner_input, tail8, conv_inner, bias_inner.reshape(1, -1), state_input, partner_raw,
        extra, partner_extra, flag,
        step_size, decay_rate.reshape(1, -1), info
    )

    def relay(step_num, incoming):
        return shifted(
            (total_decay * incoming.astype(jnp.float32) + local_end).astype(jnp.bfloat16), "seq", 1
        )

    part_rows = own_rows * lax.axis_size("seq")
    hops = min(lax.axis_size("seq") - 1, -(-(part_rows // 2) // own_rows))
    half_blocks = block_count // 2
    operands = (inner_conv, b_full, c_full, l_t, dt_t, seg_row, info, decay_x, skip_x)
    incoming = shifted(end_sent, "seq", 1)
    partial, middle = run_partial(0, half_blocks, *operands)
    incoming, partial, middle = lax.optimization_barrier((incoming, partial, middle))
    first_hop = incoming
    for step_num in range(1, hops):
        incoming = relay(step_num, incoming)
    partial, _ = run_partial(
        half_blocks, block_count - half_blocks, *operands, init=middle, after=first_hop,
        buf=partial
    )
    return run_correct(partial, c_full, l_t, info, prefix_x, incoming)


def solution(mesh):
    return jax.shard_map(
        body,
        mesh=mesh,
        in_specs=(
            P(("grp", "seq"), "head"),
            P(None, ("grp", "seq"), "head"),
            P(None, "head"),
            P("head"),
            P(None, None, "head"),
            P(None, "head"),
            P("head", ("grp", "seq")),
            P("head"),
            P("head"),
            P("grp"),
        ),
        out_specs=P(("grp", "seq"), "head"),
        check_vma=False,
    )
```

```python
import functools

import jax
import jax.numpy as jnp
from jax import lax
from jax.experimental import pallas as pl
from jax.experimental.pallas import tpu as pltpu
from jax.sharding import PartitionSpec as P

BLOCK = 128
CORRECT_TILE = 256


def shifted(value, axis, steps):
    count = lax.axis_size(axis)
    initial, last = (max(0, -steps), min(count, count - steps))
    return lax.ppermute(value, axis, [(source, source + steps) for source in range(initial, last)])


def from_partner(block, axis, stride):
    count = lax.axis_size(axis)
    route = []
    for low in range(count):
        high = low | 1 << stride
        if high != low and high < count:
            route += [(low, high), (high, low)]
    return lax.ppermute(block, axis, route)


def segment_of(lengths, positions):
    starts = jnp.cumsum(lengths, dtype=jnp.int32) - lengths
    covered = (starts[None, :] <= positions[:, None]).astype(jnp.int32)
    return jnp.sum(covered, axis=1, dtype=jnp.int32) - 1


def convolve(extended, weight, bias_row, seg_ext, row_count):
    own_seg = seg_ext[3:]
    summed = (
        jnp.zeros(extended.shape[:-2] + (row_count, extended.shape[-1]), jnp.float32) + bias_row
    )
    for offset in range(4):
        kept_mask = (seg_ext[offset : offset + row_count] == own_seg).astype(jnp.float32)[:, None]
        window = extended[..., offset : offset + row_count, :].astype(jnp.float32)
        summed = summed + weight[offset].astype(jnp.float32) * window * kept_mask
    return jax.nn.silu(summed).astype(jnp.bfloat16)


def split_dot(lhs, value):
    high = value.astype(jnp.bfloat16)
    low = (value - high.astype(jnp.float32)).astype(jnp.bfloat16)
    return jnp.dot(lhs, high, preferred_element_type=jnp.float32) + jnp.dot(
        lhs, low, preferred_element_type=jnp.float32
    )


def expand_heads(small, head_width):
    rows, heads = small.shape
    per_tile = 128 // head_width
    lane = lax.broadcasted_iota(jnp.int32, (rows, 128), 1) // head_width
    tiles = []
    for tile in range(heads // per_tile):
        picked = jnp.broadcast_to(small[:, tile * per_tile : tile * per_tile + 1], (rows, 128))
        for k in range(1, per_tile):
            column = small[:, tile * per_tile + k : tile * per_tile + k + 1]
            picked = jnp.where(lane == k, jnp.broadcast_to(column, (rows, 128)), picked)
        tiles.append(picked)
    return jnp.concatenate(tiles, axis=1)


def block_kernel(with_y, head_width, *refs):
    if with_y:
        (x_ref, b_ref, c_ref, l_ref, dt_ref, segr_ref, info_ref, decay_ref,
         skip_ref, ein_ref, out_ref, state_ref) = refs
    else:
        (x_ref, b_ref, l_ref, dt_ref, segc_ref, decay_ref, state_ref) = refs
    blk = pl.program_id(0)

    @pl.when(blk == 0)
    def _():
        if with_y:
            state_ref[...] = ein_ref[...].astype(jnp.float32)
        else:
            state_ref[...] = jnp.zeros(state_ref.shape, jnp.float32)

    info = info_ref[...]
    seg_col = info[:, 0:1]
    end_col = (seg_col == seg_col[BLOCK - 1 : BLOCK, :]).astype(jnp.float32)
    l_small = l_ref[...]
    dt_small = dt_ref[...]
    x = x_ref[...].astype(jnp.float32)
    state = state_ref[...]
    if with_y:
        c_mat = c_ref[...]
        seg_row = segr_ref[...]
        scores = lax.dot_general(
            c_mat, b_ref[...], (((1,), (1,)), ((), ())), preferred_element_type=jnp.float32
        )
        rows = lax.broadcasted_iota(jnp.int32, (BLOCK, BLOCK), 0)
        cols = lax.broadcasted_iota(jnp.int32, (BLOCK, BLOCK), 1)
        allowed = (rows >= cols) & (seg_col == seg_row)
        masked = jnp.where(allowed, scores, 0.0).astype(jnp.bfloat16)
        rising = expand_heads(jnp.exp(l_small), head_width)
        falling = expand_heads(jnp.exp(-l_small) * dt_small, head_width)
        intra = split_dot(masked, x * falling) * rising
        inter = split_dot(c_mat, state) * (rising * info[:, 1:2])
        out_ref[...] = (intra + inter + skip_ref[...] * x).astype(jnp.bfloat16)
    ending = expand_heads(
        jnp.exp(l_small[BLOCK - 1 : BLOCK, :] - l_small) * dt_small * end_col, head_width
    )
    weighted = (x * ending).astype(jnp.bfloat16)
    state_ref[...] = decay_ref[0] * state + lax.dot_general(
        b_ref[...], weighted, (((0,), (0,)), ((), ())), preferred_element_type=jnp.float32
    )


def causal_conv(raw, prev, taps, bias, info):
    top_row = lax.broadcasted_iota(jnp.int32, prev.shape, 0)
    summed = jnp.zeros(raw.shape, jnp.float32) + bias
    for offset in range(4):
        back = 3 - offset
        if back == 0:
            window = raw
        else:
            rolled = pltpu.roll(raw, back, 0)
            top = jnp.where(top_row < back, pltpu.roll(prev, back, 0), rolled[:8])
            window = jnp.concatenate([top, rolled[8:]], 0) * info[:, 1 + back : 2 + back]
        summed = summed + taps[offset : offset + 1, :] * window
    return jax.nn.silu(summed).astype(jnp.bfloat16)


def state_kernel(head_width, x_ref, tail_ref, wconv_ref, bias_ref, own_ref, other_ref, ownx_ref,
                 otherx_ref, flag_ref, dt_ref, rate_ref, info_ref, state_ref, l_ref, dtt_ref,
                 decay_ref, total_ref, xc_ref, bo_ref, co_ref, sent_ref, prefix_ref, ltile_ref,
                 prev_ref, bcprev_ref):
    blk = pl.program_id(0)

    @pl.when(blk == 0)
    def _():
        state_ref[...] = jnp.zeros(state_ref.shape, jnp.float32)
        total_ref[...] = jnp.ones(total_ref.shape, jnp.float32)
        prev_ref[...] = tail_ref[...].astype(jnp.float32)
        bcprev_ref[0] = ownx_ref[:, 0:8, :]
        bcprev_ref[1] = otherx_ref[:, 0:8, :]

    info = info_ref[...]
    raw = x_ref[...].astype(jnp.float32)
    xc = causal_conv(raw, prev_ref[...], wconv_ref[...].astype(jnp.float32), bias_ref[...], info)
    prev_ref[...] = raw[BLOCK - 8 :]
    xc_ref[...] = xc
    lower = flag_ref[...][:, 0:1] > 0.5
    convolved = []
    for which in range(2):
        halves = []
        for side, (raw_ref, extra_ref) in enumerate(((own_ref, ownx_ref), (other_ref, otherx_ref))):
            raw_bc = raw_ref[which].astype(jnp.float32)
            extra = extra_ref[which]
            halves.append(
                causal_conv(raw_bc, bcprev_ref[side, which], extra[8:12], extra[12:13], info)
            )
            bcprev_ref[side, which] = raw_bc[BLOCK - 8 :]
        convolved.append(jnp.where(
            lower, jnp.concatenate(halves, 1), jnp.concatenate(halves[::-1], 1)
        ))
    b_mat, c_mat = convolved
    bo_ref[...] = b_mat
    co_ref[...] = c_mat

    rows = lax.broadcasted_iota(jnp.int32, (2 * BLOCK, BLOCK), 0)
    cols = lax.broadcasted_iota(jnp.int32, (2 * BLOCK, BLOCK), 1)
    picker = jnp.where(
        ((rows < BLOCK) & (rows >= cols)) | (rows - BLOCK == cols), 1.0, 0.0
    ).astype(jnp.bfloat16)
    rest = dt_ref[...]
    cum = None
    for _ in range(3):
        piece = rest.astype(jnp.bfloat16)
        part = lax.dot_general(
            picker, piece, (((1,), (1,)), ((), ())), preferred_element_type=jnp.float32
        )
        cum = part if cum is None else cum + part
        rest = rest - piece.astype(jnp.float32)
    l_small = -cum[:BLOCK] * rate_ref[...]
    dt_small = cum[BLOCK:]
    l_ref[...] = l_small
    dtt_ref[...] = dt_small
    tile_heads = ltile_ref.shape[2]
    for tile in range(ltile_ref.shape[0]):
        ltile_ref[tile] = l_small[:, tile * tile_heads : (tile + 1) * tile_heads]
    seg_col = info[:, 0:1]
    end_col = (seg_col == seg_col[BLOCK - 1 : BLOCK, :]).astype(jnp.float32)
    decay_x = expand_heads(
        jnp.exp(l_small[BLOCK - 1 : BLOCK, :]) * info[BLOCK - 1 : BLOCK, 1:2], head_width
    )
    decay_ref[0] = decay_x
    prefix_ref[0] = total_ref[...]
    total_ref[...] = total_ref[...] * decay_x
    ending = expand_heads(
        jnp.exp(l_small[BLOCK - 1 : BLOCK, :] - l_small) * dt_small * end_col, head_width
    )
    weighted = (xc.astype(jnp.float32) * ending).astype(jnp.bfloat16)
    new_state = decay_x * state_ref[...] + lax.dot_general(
        b_mat, weighted, (((0,), (0,)), ((), ())), preferred_element_type=jnp.float32
    )
    state_ref[...] = new_state

    @pl.when(blk == pl.num_programs(0) - 1)
    def _():
        sent_ref[...] = new_state.astype(jnp.bfloat16)


def run_state(x, tail8, wconv, bias_row, own_raw, other_raw, own_extra, other_extra, flag,
              step_size, rate_row, info):
    rows, width = x.shape
    head_count = step_size.shape[0]
    half = own_raw.shape[2]
    n_size = 2 * half
    block_count = rows // BLOCK
    tiles = width // CORRECT_TILE
    tile_heads = head_count // tiles
    row_block = lambda cols: pl.BlockSpec((BLOCK, cols), lambda b: (b, 0))
    whole = lambda shape: pl.BlockSpec(shape, lambda b: (0,) * len(shape))
    return pl.pallas_call(
        functools.partial(state_kernel, width // head_count),
        grid=(block_count,),
        in_specs=[row_block(width), whole((8, width)), whole((4, width)), whole((1, width)),
                  pl.BlockSpec((2, BLOCK, half), lambda b: (0, b, 0)),
                  pl.BlockSpec((2, BLOCK, half), lambda b: (0, b, 0)),
                  whole(own_extra.shape), whole(own_extra.shape), whole(flag.shape),
                  pl.BlockSpec((head_count, BLOCK), lambda b: (0, b)),
                  whole((1, head_count)), row_block(info.shape[1])],
        out_specs=[whole((n_size, width)), row_block(head_count), row_block(head_count),
                   pl.BlockSpec((1, 1, width), lambda b: (b, 0, 0)), whole((1, width)),
                   row_block(width), row_block(n_size), row_block(n_size),
                   whole((n_size, width)), pl.BlockSpec((1, 1, width), lambda b: (b, 0, 0)),
                   pl.BlockSpec((tiles, BLOCK, tile_heads), lambda b: (0, b, 0))],
        out_shape=[jax.ShapeDtypeStruct((n_size, width), jnp.float32),
                   jax.ShapeDtypeStruct((rows, head_count), jnp.float32),
                   jax.ShapeDtypeStruct((rows, head_count), jnp.float32),
                   jax.ShapeDtypeStruct((block_count, 1, width), jnp.float32),
                   jax.ShapeDtypeStruct((1, width), jnp.float32),
                   jax.ShapeDtypeStruct((rows, width), jnp.bfloat16),
                   jax.ShapeDtypeStruct((rows, n_size), jnp.bfloat16),
                   jax.ShapeDtypeStruct((rows, n_size), jnp.bfloat16),
                   jax.ShapeDtypeStruct((n_size, width), jnp.bfloat16),
                   jax.ShapeDtypeStruct((block_count, 1, width), jnp.float32),
                   jax.ShapeDtypeStruct((tiles, rows, tile_heads), jnp.float32)],
        scratch_shapes=[pltpu.VMEM((8, width), jnp.float32),
                        pltpu.VMEM((2, 2, 8, half), jnp.float32)],
        compiler_params=pltpu.CompilerParams(dimension_semantics=("arbitrary",)),
    )(x, tail8, wconv, bias_row, own_raw, other_raw, own_extra, other_extra, flag, step_size,
      rate_row, info)


def partial_kernel(head_width, from_zero, *refs):
    if from_zero:
        (x_ref, b_ref, c_ref, l_ref, dt_ref, segr_ref, info_ref, decay_ref, skip_ref, out_ref,
         end_ref, state_ref) = refs
    else:
        (x_ref, b_ref, c_ref, l_ref, dt_ref, segr_ref, info_ref, decay_ref, skip_ref, init_ref,
         after_ref, out_ref, end_ref, state_ref) = refs
    blk = pl.program_id(0)

    @pl.when(blk == 0)
    def _():
        if from_zero:
            state_ref[...] = jnp.zeros(state_ref.shape, jnp.float32)
        else:
            state_ref[...] = init_ref[...]

    info = info_ref[...]
    seg_col = info[:, 0:1]
    end_col = (seg_col == seg_col[BLOCK - 1 : BLOCK, :]).astype(jnp.float32)
    l_small = l_ref[...]
    dt_small = dt_ref[...]
    x = x_ref[...].astype(jnp.float32)
    state = state_ref[...]
    c_mat = c_ref[...]
    b_mat = b_ref[...]
    scores = lax.dot_general(
        c_mat, b_mat, (((1,), (1,)), ((), ())), preferred_element_type=jnp.float32
    )
    rows = lax.broadcasted_iota(jnp.int32, (BLOCK, BLOCK), 0)
    cols = lax.broadcasted_iota(jnp.int32, (BLOCK, BLOCK), 1)
    allowed = (rows >= cols) & (seg_col == segr_ref[...])
    masked = jnp.where(allowed, scores, 0.0).astype(jnp.bfloat16)
    rising = expand_heads(jnp.exp(l_small), head_width)
    falling = expand_heads(jnp.exp(-l_small) * dt_small, head_width)
    intra = split_dot(masked, x * falling) * rising
    inter = split_dot(c_mat, state) * (rising * info[:, 1:2])
    out_ref[...] = intra + inter + skip_ref[...] * x
    ending = expand_heads(
        jnp.exp(l_small[BLOCK - 1 : BLOCK, :] - l_small) * dt_small * end_col, head_width
    )
    weighted = (x * ending).astype(jnp.bfloat16)
    new_state = decay_ref[0] * state + lax.dot_general(
        b_mat, weighted, (((0,), (0,)), ((), ())), preferred_element_type=jnp.float32
    )
    state_ref[...] = new_state

    @pl.when(blk == pl.num_programs(0) - 1)
    def _():
        end_ref[...] = new_state


def run_partial(first, count, x, b_full, c_full, l_t, dt_t, seg_row, info, decay_x, skip_x,
                init=None, after=None):
    rows, width = x.shape
    head_count = l_t.shape[1]
    n_size = b_full.shape[1]
    row_block = lambda cols: pl.BlockSpec((BLOCK, cols), lambda b: (b + first, 0))
    whole = lambda shape: pl.BlockSpec(shape, lambda b: (0,) * len(shape))
    from_zero = init is None
    in_specs = [row_block(width), row_block(n_size), row_block(n_size), row_block(head_count),
                row_block(head_count), pl.BlockSpec((1, BLOCK), lambda b: (0, b + first)),
                row_block(info.shape[1]), pl.BlockSpec((1, 1, width), lambda b: (b + first, 0, 0)),
                whole((1, width))]
    args = [x, b_full, c_full, l_t, dt_t, seg_row, info, decay_x, skip_x]
    if not from_zero:
        in_specs += [whole((n_size, width)), pl.BlockSpec(memory_space=pl.ANY)]
        args += [init, after]
    return pl.pallas_call(
        functools.partial(partial_kernel, width // head_count, from_zero),
        grid=(count,),
        in_specs=in_specs,
        out_specs=[pl.BlockSpec((BLOCK, width), lambda b: (b, 0)), whole((n_size, width))],
        out_shape=[jax.ShapeDtypeStruct((count * BLOCK, width), jnp.float32),
                   jax.ShapeDtypeStruct((n_size, width), jnp.float32)],
        scratch_shapes=[pltpu.VMEM((n_size, width), jnp.float32)],
        compiler_params=pltpu.CompilerParams(dimension_semantics=("arbitrary",)),
    )(*args)


def correct_kernel(head_width, y_ref, z_ref, c_ref, l_ref, info_ref, prefix_ref, ein_ref, out_ref):
    rows, cols = out_ref.shape
    rising = expand_heads(jnp.exp(l_ref[0]), head_width)
    blocks = prefix_ref.shape[0]
    prefix = jnp.broadcast_to(prefix_ref[...], (blocks, BLOCK, cols)).reshape(rows, cols)
    carried = jnp.dot(c_ref[...], ein_ref[...], preferred_element_type=jnp.float32)
    factor = rising * info_ref[...][:, 1:2] * prefix
    partial = jnp.concatenate([y_ref[...], z_ref[...]], 0)
    out_ref[...] = (partial + carried * factor).astype(jnp.bfloat16)


def run_correct(first, second, c_full, l_tiles, info, prefix_x, entering):
    rows = first.shape[0] + second.shape[0]
    width = first.shape[1]
    tiles, _, heads_per = l_tiles.shape
    tile = CORRECT_TILE
    head_width = tile // heads_per
    n_size = c_full.shape[1]
    block_count = prefix_x.shape[0]
    return pl.pallas_call(
        functools.partial(correct_kernel, head_width),
        grid=(tiles,),
        in_specs=[pl.BlockSpec((first.shape[0], tile), lambda j: (0, j)),
                  pl.BlockSpec((second.shape[0], tile), lambda j: (0, j)),
                  pl.BlockSpec((rows, n_size), lambda j: (0, 0)),
                  pl.BlockSpec((1, rows, heads_per), lambda j: (j, 0, 0)),
                  pl.BlockSpec((rows, info.shape[1]), lambda j: (0, 0)),
                  pl.BlockSpec((block_count, 1, tile), lambda j: (0, 0, j)),
                  pl.BlockSpec((n_size, tile), lambda j: (0, j))],
        out_specs=pl.BlockSpec((rows, tile), lambda j: (0, j)),
        out_shape=jax.ShapeDtypeStruct((rows, width), jnp.bfloat16),
        compiler_params=pltpu.CompilerParams(dimension_semantics=("arbitrary",)),
    )(first, second, c_full, l_tiles, info, prefix_x, entering)


def run_blocks(with_y, x, b_full, c_full, l_t, dt_t, seg_row, seg_col, entry_col, decay_x,
               skip_x, entering):
    rows, width = x.shape
    head_count = l_t.shape[1]
    head_width = width // head_count
    n_size = b_full.shape[1]
    block_count = rows // BLOCK
    row_block = lambda cols: pl.BlockSpec((BLOCK, cols), lambda b: (b, 0))
    bt_spec = pl.BlockSpec((n_size, BLOCK), lambda b: (0, b))
    decay_spec = pl.BlockSpec((1, 1, width), lambda b: (b, 0, 0))
    state_spec = pl.BlockSpec((n_size, width), lambda b: (0, 0))
    state_shape = jax.ShapeDtypeStruct((n_size, width), jnp.float32)
    kernel = functools.partial(block_kernel, with_y, head_width)
    params = pltpu.CompilerParams(dimension_semantics=("arbitrary",))
    if with_y:
        return pl.pallas_call(
            kernel,
            grid=(block_count,),
            in_specs=[row_block(width), row_block(n_size), row_block(n_size),
                      row_block(head_count), row_block(head_count),
                      pl.BlockSpec((1, BLOCK), lambda b: (0, b)), row_block(seg_col.shape[1]),
                      decay_spec, pl.BlockSpec((1, width), lambda b: (0, 0)), state_spec],
            out_specs=row_block(width),
            out_shape=jax.ShapeDtypeStruct((rows, width), jnp.bfloat16),
            scratch_shapes=[pltpu.VMEM((n_size, width), jnp.float32)],
            compiler_params=params,
        )(x, b_full, c_full, l_t, dt_t, seg_row, seg_col, decay_x, skip_x, entering)
    return pl.pallas_call(
        kernel,
        grid=(block_count,),
        in_specs=[row_block(width), bt_spec, row_block(head_count), row_block(head_count),
                  row_block(1), decay_spec],
        out_specs=state_spec,
        out_shape=state_shape,
        compiler_params=params,
    )(x, b_t, l_t, dt_t, seg_col, decay_x)


def body(
    inner_input,
    state_input,
    conv_inner,
    bias_inner,
    conv_state,
    bias_state,
    step_size,
    decay_rate,
    skip_gain,
    lengths,
):
    own_rows = inner_input.shape[0]
    head_count = decay_rate.shape[0]
    group_half = state_input.shape[2]
    block_count = own_rows // BLOCK
    positions = lax.axis_index("seq") * own_rows + jnp.arange(own_rows + 3, dtype=jnp.int32) - 3
    seg_ext = segment_of(lengths, positions)
    width = inner_input.shape[1]
    tails = jnp.concatenate(
        [inner_input[-8:], jnp.transpose(state_input[:, -8:], (1, 0, 2)).reshape(8, -1)], 1
    )
    tails = shifted(tails, "seq", 1)
    tail8 = tails[:, :width]
    state_tail = tails[:, width:].reshape(8, 2, group_half)
    extra = jnp.concatenate(
        [jnp.transpose(state_tail, (1, 0, 2)).astype(jnp.float32),
         conv_state.astype(jnp.float32), bias_state[:, None, :]],
        1,
    )
    partner_raw, partner_extra = from_partner((state_input, extra), "head", 0)
    lower_half = (lax.axis_index("head") % 2 == 0).astype(jnp.float32)
    flag = jnp.full((1, 128), lower_half, jnp.float32)
    head_width = inner_input.shape[1] // head_count
    spread = lambda v: jnp.repeat(v, head_width, axis=-1)
    skip_x = spread(skip_gain).reshape(1, -1)
    seg_own = seg_ext[3:].reshape(block_count, BLOCK)
    seg_prev = seg_ext[2 : 2 + own_rows].reshape(block_count, BLOCK)[:, 0]
    seg_row = seg_ext[3:].reshape(1, own_rows).astype(jnp.float32)
    own_seg = seg_ext[3:]
    entry_col = (seg_own == seg_prev[:, None]).reshape(own_rows)
    keeps = [(seg_ext[3 - back : 3 - back + own_rows] == own_seg) for back in (1, 2, 3)]
    info = jnp.stack(
        [own_seg.astype(jnp.float32), entry_col.astype(jnp.float32)]
        + [keep.astype(jnp.float32) for keep in keeps]
        + [jnp.zeros((own_rows,), jnp.float32)] * 3,
        1,
    )

    (local_end, l_t, dt_t, decay_x, total_decay, inner_conv, b_full, c_full, end_sent,
     prefix_x, l_tiles) = run_state(
        inner_input, tail8, conv_inner, bias_inner.reshape(1, -1), state_input, partner_raw,
        extra, partner_extra, flag,
        step_size, decay_rate.reshape(1, -1), info
    )

    def relay(step_num, incoming):
        return shifted(
            (total_decay * incoming.astype(jnp.float32) + local_end).astype(jnp.bfloat16), "seq", 1
        )

    part_rows = own_rows * lax.axis_size("seq")
    hops = min(lax.axis_size("seq") - 1, -(-(part_rows // 2) // own_rows))
    half_blocks = block_count // 2
    operands = (inner_conv, b_full, c_full, l_t, dt_t, seg_row, info, decay_x, skip_x)
    incoming = shifted(end_sent, "seq", 1)
    partial, middle = run_partial(0, half_blocks, *operands)
    incoming, partial, middle = lax.optimization_barrier((incoming, partial, middle))
    first_hop = incoming
    for step_num in range(1, hops):
        incoming = relay(step_num, incoming)
    second, _ = run_partial(
        half_blocks, block_count - half_blocks, *operands, init=middle, after=first_hop
    )
    return run_correct(partial, second, c_full, l_tiles, info, prefix_x, incoming)


def solution(mesh):
    return jax.shard_map(
        body,
        mesh=mesh,
        in_specs=(
            P(("grp", "seq"), "head"),
            P(None, ("grp", "seq"), "head"),
            P(None, "head"),
            P("head"),
            P(None, None, "head"),
            P(None, "head"),
            P("head", ("grp", "seq")),
            P("head"),
            P("head"),
            P("grp"),
        ),
        out_specs=P(("grp", "seq"), "head"),
        check_vma=False,
    )
```

```python
import functools

import jax
import jax.numpy as jnp
from jax import lax
from jax.experimental import pallas as pl
from jax.experimental.pallas import tpu as pltpu
from jax.sharding import PartitionSpec as P

BLOCK = 128
CORRECT_TILE = 256


def shifted(value, axis, steps):
    count = lax.axis_size(axis)
    initial, last = (max(0, -steps), min(count, count - steps))
    return lax.ppermute(value, axis, [(source, source + steps) for source in range(initial, last)])


def from_partner(block, axis, stride):
    count = lax.axis_size(axis)
    route = []
    for low in range(count):
        high = low | 1 << stride
        if high != low and high < count:
            route += [(low, high), (high, low)]
    return lax.ppermute(block, axis, route)


def segment_of(lengths, positions):
    starts = jnp.cumsum(lengths, dtype=jnp.int32) - lengths
    covered = (starts[None, :] <= positions[:, None]).astype(jnp.int32)
    return jnp.sum(covered, axis=1, dtype=jnp.int32) - 1


def convolve(extended, weight, bias_row, seg_ext, row_count):
    own_seg = seg_ext[3:]
    summed = (
        jnp.zeros(extended.shape[:-2] + (row_count, extended.shape[-1]), jnp.float32) + bias_row
    )
    for offset in range(4):
        kept_mask = (seg_ext[offset : offset + row_count] == own_seg).astype(jnp.float32)[:, None]
        window = extended[..., offset : offset + row_count, :].astype(jnp.float32)
        summed = summed + weight[offset].astype(jnp.float32) * window * kept_mask
    return jax.nn.silu(summed).astype(jnp.bfloat16)


def split_dot(lhs, value):
    high = value.astype(jnp.bfloat16)
    low = (value - high.astype(jnp.float32)).astype(jnp.bfloat16)
    return jnp.dot(lhs, high, preferred_element_type=jnp.float32) + jnp.dot(
        lhs, low, preferred_element_type=jnp.float32
    )


def expand_heads(small, head_width):
    rows, heads = small.shape
    per_tile = 128 // head_width
    lane = lax.broadcasted_iota(jnp.int32, (rows, 128), 1) // head_width
    tiles = []
    for tile in range(heads // per_tile):
        picked = jnp.broadcast_to(small[:, tile * per_tile : tile * per_tile + 1], (rows, 128))
        for k in range(1, per_tile):
            column = small[:, tile * per_tile + k : tile * per_tile + k + 1]
            picked = jnp.where(lane == k, jnp.broadcast_to(column, (rows, 128)), picked)
        tiles.append(picked)
    return jnp.concatenate(tiles, axis=1)


def block_kernel(with_y, head_width, *refs):
    if with_y:
        (x_ref, b_ref, c_ref, l_ref, dt_ref, segr_ref, info_ref, decay_ref,
         skip_ref, ein_ref, out_ref, state_ref) = refs
    else:
        (x_ref, b_ref, l_ref, dt_ref, segc_ref, decay_ref, state_ref) = refs
    blk = pl.program_id(0)

    @pl.when(blk == 0)
    def _():
        if with_y:
            state_ref[...] = ein_ref[...].astype(jnp.float32)
        else:
            state_ref[...] = jnp.zeros(state_ref.shape, jnp.float32)

    info = info_ref[...]
    seg_col = info[:, 0:1]
    end_col = (seg_col == seg_col[BLOCK - 1 : BLOCK, :]).astype(jnp.float32)
    l_small = l_ref[...]
    dt_small = dt_ref[...]
    x = x_ref[...].astype(jnp.float32)
    state = state_ref[...]
    if with_y:
        c_mat = c_ref[...]
        seg_row = segr_ref[...]
        scores = lax.dot_general(
            c_mat, b_ref[...], (((1,), (1,)), ((), ())), preferred_element_type=jnp.float32
        )
        rows = lax.broadcasted_iota(jnp.int32, (BLOCK, BLOCK), 0)
        cols = lax.broadcasted_iota(jnp.int32, (BLOCK, BLOCK), 1)
        allowed = (rows >= cols) & (seg_col == seg_row)
        masked = jnp.where(allowed, scores, 0.0).astype(jnp.bfloat16)
        rising = expand_heads(jnp.exp(l_small), head_width)
        falling = expand_heads(jnp.exp(-l_small) * dt_small, head_width)
        intra = split_dot(masked, x * falling) * rising
        inter = split_dot(c_mat, state) * (rising * info[:, 1:2])
        out_ref[...] = (intra + inter + skip_ref[...] * x).astype(jnp.bfloat16)
    ending = expand_heads(
        jnp.exp(l_small[BLOCK - 1 : BLOCK, :] - l_small) * dt_small * end_col, head_width
    )
    weighted = (x * ending).astype(jnp.bfloat16)
    state_ref[...] = decay_ref[0] * state + lax.dot_general(
        b_ref[...], weighted, (((0,), (0,)), ((), ())), preferred_element_type=jnp.float32
    )


def causal_conv(raw, prev, taps, bias, info):
    top_row = lax.broadcasted_iota(jnp.int32, prev.shape, 0)
    summed = jnp.zeros(raw.shape, jnp.float32) + bias
    for offset in range(4):
        back = 3 - offset
        if back == 0:
            window = raw
        else:
            rolled = pltpu.roll(raw, back, 0)
            top = jnp.where(top_row < back, pltpu.roll(prev, back, 0), rolled[:8])
            window = jnp.concatenate([top, rolled[8:]], 0) * info[:, 1 + back : 2 + back]
        summed = summed + taps[offset : offset + 1, :] * window
    return jax.nn.silu(summed).astype(jnp.bfloat16)


def state_kernel(head_width, x_ref, tail_ref, wconv_ref, bias_ref, own_ref, other_ref, ownx_ref,
                 otherx_ref, dt_ref, rate_ref, info_ref, state_ref, l_ref, dtt_ref,
                 decay_ref, total_ref, xc_ref, bo_ref, co_ref, sent_ref, prefix_ref, ltile_ref,
                 prev_ref, bcprev_ref, small_ref):
    blk = pl.program_id(0)

    @pl.when(blk == 0)
    def _():
        state_ref[...] = jnp.zeros(state_ref.shape, jnp.float32)
        total_ref[...] = jnp.ones(total_ref.shape, jnp.float32)
        prev_ref[...] = tail_ref[:, : x_ref.shape[1]].astype(jnp.float32)
        small_ref[...] = jnp.ones(small_ref.shape, jnp.float32)
        bcprev_ref[0] = ownx_ref[:, 0:8, :]
        bcprev_ref[1] = otherx_ref[:, 0:8, :]

    info = info_ref[...]
    raw = x_ref[...].astype(jnp.float32)
    xc = causal_conv(raw, prev_ref[...], wconv_ref[...].astype(jnp.float32), bias_ref[...], info)
    prev_ref[...] = raw[BLOCK - 8 :]
    xc_ref[...] = xc
    lower = info_ref[0:1, 5:6] > 0.5
    convolved = []
    for which in range(2):
        halves = []
        for side, (raw_ref, extra_ref) in enumerate(((own_ref, ownx_ref), (other_ref, otherx_ref))):
            raw_bc = raw_ref[which].astype(jnp.float32)
            extra = extra_ref[which]
            halves.append(
                causal_conv(raw_bc, bcprev_ref[side, which], extra[8:12], extra[12:13], info)
            )
            bcprev_ref[side, which] = raw_bc[BLOCK - 8 :]
        convolved.append(jnp.where(
            lower, jnp.concatenate(halves, 1), jnp.concatenate(halves[::-1], 1)
        ))
    b_mat, c_mat = convolved
    bo_ref[...] = b_mat
    co_ref[...] = c_mat

    rows = lax.broadcasted_iota(jnp.int32, (2 * BLOCK, BLOCK), 0)
    cols = lax.broadcasted_iota(jnp.int32, (2 * BLOCK, BLOCK), 1)
    picker = jnp.where(
        ((rows < BLOCK) & (rows >= cols)) | (rows - BLOCK == cols), 1.0, 0.0
    ).astype(jnp.bfloat16)
    rest = dt_ref[...]
    cum = None
    for _ in range(3):
        piece = rest.astype(jnp.bfloat16)
        part = lax.dot_general(
            picker, piece, (((1,), (1,)), ((), ())), preferred_element_type=jnp.float32
        )
        cum = part if cum is None else cum + part
        rest = rest - piece.astype(jnp.float32)
    l_small = -cum[:BLOCK] * rate_ref[...]
    dt_small = cum[BLOCK:]
    l_ref[...] = l_small
    dtt_ref[...] = dt_small
    seg_col = info[:, 0:1]
    end_col = (seg_col == seg_col[BLOCK - 1 : BLOCK, :]).astype(jnp.float32)
    decay_x = expand_heads(
        jnp.exp(l_small[BLOCK - 1 : BLOCK, :]) * info[BLOCK - 1 : BLOCK, 1:2], head_width
    )
    decay_ref[0] = decay_x
    prefix_ref[0] = total_ref[...]
    total_ref[...] = total_ref[...] * decay_x
    carry = (jnp.exp(l_small) * info[:, 1:2]) * small_ref[...]
    small_ref[...] = small_ref[...] * (
        jnp.exp(l_small[BLOCK - 1 : BLOCK, :]) * info[BLOCK - 1 : BLOCK, 1:2]
    )
    tile_heads = ltile_ref.shape[2]
    for tile in range(ltile_ref.shape[0]):
        ltile_ref[tile] = carry[:, tile * tile_heads : (tile + 1) * tile_heads]
    ending = expand_heads(
        jnp.exp(l_small[BLOCK - 1 : BLOCK, :] - l_small) * dt_small * end_col, head_width
    )
    weighted = (xc.astype(jnp.float32) * ending).astype(jnp.bfloat16)
    new_state = decay_x * state_ref[...] + lax.dot_general(
        b_mat, weighted, (((0,), (0,)), ((), ())), preferred_element_type=jnp.float32
    )
    state_ref[...] = new_state

    @pl.when(blk == pl.num_programs(0) - 1)
    def _():
        sent_ref[...] = new_state.astype(jnp.bfloat16)


def run_state(x, tails, wconv, bias_row, own_raw, other_raw, own_extra, other_extra,
              step_size, rate_row, info):
    rows, width = x.shape
    head_count = step_size.shape[0]
    half = own_raw.shape[2]
    n_size = 2 * half
    block_count = rows // BLOCK
    tiles = width // CORRECT_TILE
    tile_heads = head_count // tiles
    row_block = lambda cols: pl.BlockSpec((BLOCK, cols), lambda b: (b, 0))
    whole = lambda shape: pl.BlockSpec(shape, lambda b: (0,) * len(shape))
    return pl.pallas_call(
        functools.partial(state_kernel, width // head_count),
        grid=(block_count,),
        in_specs=[row_block(width), whole(tails.shape), whole((4, width)), whole((1, width)),
                  pl.BlockSpec((2, BLOCK, half), lambda b: (0, b, 0)),
                  pl.BlockSpec((2, BLOCK, half), lambda b: (0, b, 0)),
                  whole(own_extra.shape), whole(own_extra.shape),
                  pl.BlockSpec((head_count, BLOCK), lambda b: (0, b)),
                  whole((1, head_count)), row_block(info.shape[1])],
        out_specs=[whole((n_size, width)), row_block(head_count), row_block(head_count),
                   pl.BlockSpec((1, 1, width), lambda b: (b, 0, 0)), whole((1, width)),
                   row_block(width), row_block(n_size), row_block(n_size),
                   whole((n_size, width)), pl.BlockSpec((1, 1, width), lambda b: (b, 0, 0)),
                   pl.BlockSpec((tiles, BLOCK, tile_heads), lambda b: (0, b, 0))],
        out_shape=[jax.ShapeDtypeStruct((n_size, width), jnp.float32),
                   jax.ShapeDtypeStruct((rows, head_count), jnp.float32),
                   jax.ShapeDtypeStruct((rows, head_count), jnp.float32),
                   jax.ShapeDtypeStruct((block_count, 1, width), jnp.float32),
                   jax.ShapeDtypeStruct((1, width), jnp.float32),
                   jax.ShapeDtypeStruct((rows, width), jnp.bfloat16),
                   jax.ShapeDtypeStruct((rows, n_size), jnp.bfloat16),
                   jax.ShapeDtypeStruct((rows, n_size), jnp.bfloat16),
                   jax.ShapeDtypeStruct((n_size, width), jnp.bfloat16),
                   jax.ShapeDtypeStruct((block_count, 1, width), jnp.float32),
                   jax.ShapeDtypeStruct((tiles, rows, tile_heads), jnp.float32)],
        scratch_shapes=[pltpu.VMEM((8, width), jnp.float32),
                        pltpu.VMEM((2, 2, 8, half), jnp.float32),
                        pltpu.VMEM((1, head_count), jnp.float32)],
        compiler_params=pltpu.CompilerParams(dimension_semantics=("arbitrary",)),
    )(x, tails, wconv, bias_row, own_raw, other_raw, own_extra, other_extra, step_size,
      rate_row, info)


def partial_kernel(head_width, from_zero, *refs):
    if from_zero:
        (x_ref, b_ref, c_ref, l_ref, dt_ref, segr_ref, info_ref, decay_ref, skip_ref, out_ref,
         end_ref, state_ref) = refs
    else:
        (x_ref, b_ref, c_ref, l_ref, dt_ref, segr_ref, info_ref, decay_ref, skip_ref, init_ref,
         after_ref, out_ref, end_ref, state_ref) = refs
    blk = pl.program_id(0)

    @pl.when(blk == 0)
    def _():
        if from_zero:
            state_ref[...] = jnp.zeros(state_ref.shape, jnp.float32)
        else:
            state_ref[...] = init_ref[...]

    info = info_ref[...]
    seg_col = info[:, 0:1]
    end_col = (seg_col == seg_col[BLOCK - 1 : BLOCK, :]).astype(jnp.float32)
    l_small = l_ref[...]
    dt_small = dt_ref[...]
    x = x_ref[...].astype(jnp.float32)
    state = state_ref[...]
    c_mat = c_ref[...]
    b_mat = b_ref[...]
    scores = lax.dot_general(
        c_mat, b_mat, (((1,), (1,)), ((), ())), preferred_element_type=jnp.float32
    )
    rows = lax.broadcasted_iota(jnp.int32, (BLOCK, BLOCK), 0)
    cols = lax.broadcasted_iota(jnp.int32, (BLOCK, BLOCK), 1)
    allowed = (rows >= cols) & (seg_col == segr_ref[...])
    masked = jnp.where(allowed, scores, 0.0).astype(jnp.bfloat16)
    rising = expand_heads(jnp.exp(l_small), head_width)
    falling = expand_heads(jnp.exp(-l_small) * dt_small, head_width)
    intra = split_dot(masked, x * falling) * rising
    inter = split_dot(c_mat, state) * (rising * info[:, 1:2])
    out_ref[...] = intra + inter + skip_ref[...] * x
    ending = expand_heads(
        jnp.exp(l_small[BLOCK - 1 : BLOCK, :] - l_small) * dt_small * end_col, head_width
    )
    weighted = (x * ending).astype(jnp.bfloat16)
    new_state = decay_ref[0] * state + lax.dot_general(
        b_mat, weighted, (((0,), (0,)), ((), ())), preferred_element_type=jnp.float32
    )
    state_ref[...] = new_state

    @pl.when(blk == pl.num_programs(0) - 1)
    def _():
        end_ref[...] = new_state


def run_partial(first, count, x, b_full, c_full, l_t, dt_t, seg_row, info, decay_x, skip_x,
                init=None, after=None):
    rows, width = x.shape
    head_count = l_t.shape[1]
    n_size = b_full.shape[1]
    row_block = lambda cols: pl.BlockSpec((BLOCK, cols), lambda b: (b + first, 0))
    whole = lambda shape: pl.BlockSpec(shape, lambda b: (0,) * len(shape))
    from_zero = init is None
    in_specs = [row_block(width), row_block(n_size), row_block(n_size), row_block(head_count),
                row_block(head_count), pl.BlockSpec((1, BLOCK), lambda b: (0, b + first)),
                row_block(info.shape[1]), pl.BlockSpec((1, 1, width), lambda b: (b + first, 0, 0)),
                whole((1, width))]
    args = [x, b_full, c_full, l_t, dt_t, seg_row, info, decay_x, skip_x]
    if not from_zero:
        in_specs += [whole((n_size, width)), pl.BlockSpec(memory_space=pl.ANY)]
        args += [init, after]
    return pl.pallas_call(
        functools.partial(partial_kernel, width // head_count, from_zero),
        grid=(count,),
        in_specs=in_specs,
        out_specs=[pl.BlockSpec((BLOCK, width), lambda b: (b, 0)), whole((n_size, width))],
        out_shape=[jax.ShapeDtypeStruct((count * BLOCK, width), jnp.float32),
                   jax.ShapeDtypeStruct((n_size, width), jnp.float32)],
        scratch_shapes=[pltpu.VMEM((n_size, width), jnp.float32)],
        compiler_params=pltpu.CompilerParams(dimension_semantics=("arbitrary",)),
    )(*args)


def correct_kernel(head_width, y_ref, z_ref, c_ref, g_ref, ein_ref, out_ref):
    factor = expand_heads(g_ref[0], head_width)
    carried = jnp.dot(c_ref[...], ein_ref[...], preferred_element_type=jnp.float32)
    partial = jnp.concatenate([y_ref[...], z_ref[...]], 0)
    out_ref[...] = (partial + carried * factor).astype(jnp.bfloat16)


def run_correct(first, second, c_full, g_tiles, entering):
    rows = first.shape[0] + second.shape[0]
    width = first.shape[1]
    tiles, _, heads_per = g_tiles.shape
    tile = CORRECT_TILE
    head_width = tile // heads_per
    n_size = c_full.shape[1]
    return pl.pallas_call(
        functools.partial(correct_kernel, head_width),
        grid=(tiles,),
        in_specs=[pl.BlockSpec((first.shape[0], tile), lambda j: (0, j)),
                  pl.BlockSpec((second.shape[0], tile), lambda j: (0, j)),
                  pl.BlockSpec((rows, n_size), lambda j: (0, 0)),
                  pl.BlockSpec((1, rows, heads_per), lambda j: (j, 0, 0)),
                  pl.BlockSpec((n_size, tile), lambda j: (0, j))],
        out_specs=pl.BlockSpec((rows, tile), lambda j: (0, j)),
        out_shape=jax.ShapeDtypeStruct((rows, width), jnp.bfloat16),
        compiler_params=pltpu.CompilerParams(dimension_semantics=("arbitrary",)),
    )(first, second, c_full, g_tiles, entering)


def run_blocks(with_y, x, b_full, c_full, l_t, dt_t, seg_row, seg_col, entry_col, decay_x,
               skip_x, entering):
    rows, width = x.shape
    head_count = l_t.shape[1]
    head_width = width // head_count
    n_size = b_full.shape[1]
    block_count = rows // BLOCK
    row_block = lambda cols: pl.BlockSpec((BLOCK, cols), lambda b: (b, 0))
    bt_spec = pl.BlockSpec((n_size, BLOCK), lambda b: (0, b))
    decay_spec = pl.BlockSpec((1, 1, width), lambda b: (b, 0, 0))
    state_spec = pl.BlockSpec((n_size, width), lambda b: (0, 0))
    state_shape = jax.ShapeDtypeStruct((n_size, width), jnp.float32)
    kernel = functools.partial(block_kernel, with_y, head_width)
    params = pltpu.CompilerParams(dimension_semantics=("arbitrary",))
    if with_y:
        return pl.pallas_call(
            kernel,
            grid=(block_count,),
            in_specs=[row_block(width), row_block(n_size), row_block(n_size),
                      row_block(head_count), row_block(head_count),
                      pl.BlockSpec((1, BLOCK), lambda b: (0, b)), row_block(seg_col.shape[1]),
                      decay_spec, pl.BlockSpec((1, width), lambda b: (0, 0)), state_spec],
            out_specs=row_block(width),
            out_shape=jax.ShapeDtypeStruct((rows, width), jnp.bfloat16),
            scratch_shapes=[pltpu.VMEM((n_size, width), jnp.float32)],
            compiler_params=params,
        )(x, b_full, c_full, l_t, dt_t, seg_row, seg_col, decay_x, skip_x, entering)
    return pl.pallas_call(
        kernel,
        grid=(block_count,),
        in_specs=[row_block(width), bt_spec, row_block(head_count), row_block(head_count),
                  row_block(1), decay_spec],
        out_specs=state_spec,
        out_shape=state_shape,
        compiler_params=params,
    )(x, b_t, l_t, dt_t, seg_col, decay_x)


def body(
    inner_input,
    state_input,
    conv_inner,
    bias_inner,
    conv_state,
    bias_state,
    step_size,
    decay_rate,
    skip_gain,
    lengths,
):
    own_rows = inner_input.shape[0]
    head_count = decay_rate.shape[0]
    group_half = state_input.shape[2]
    block_count = own_rows // BLOCK
    positions = lax.axis_index("seq") * own_rows + jnp.arange(own_rows + 3, dtype=jnp.int32) - 3
    seg_ext = segment_of(lengths, positions)
    width = inner_input.shape[1]
    tails = jnp.concatenate(
        [inner_input[-8:], jnp.transpose(state_input[:, -8:], (1, 0, 2)).reshape(8, -1)], 1
    )
    tails = shifted(tails, "seq", 1)
    state_tail = tails[:, width:].reshape(8, 2, group_half)
    extra = jnp.concatenate(
        [jnp.transpose(state_tail, (1, 0, 2)).astype(jnp.float32),
         conv_state.astype(jnp.float32), bias_state[:, None, :]],
        1,
    )
    partner_raw, partner_extra = from_partner((state_input, extra), "head", 0)
    lower_half = (lax.axis_index("head") % 2 == 0).astype(jnp.float32)
    head_width = inner_input.shape[1] // head_count
    spread = lambda v: jnp.repeat(v, head_width, axis=-1)
    skip_x = spread(skip_gain).reshape(1, -1)
    seg_own = seg_ext[3:].reshape(block_count, BLOCK)
    seg_prev = seg_ext[2 : 2 + own_rows].reshape(block_count, BLOCK)[:, 0]
    seg_row = seg_ext[3:].reshape(1, own_rows).astype(jnp.float32)
    own_seg = seg_ext[3:]
    entry_col = (seg_own == seg_prev[:, None]).reshape(own_rows)
    keeps = [(seg_ext[3 - back : 3 - back + own_rows] == own_seg) for back in (1, 2, 3)]
    info = jnp.stack(
        [own_seg.astype(jnp.float32), entry_col.astype(jnp.float32)]
        + [keep.astype(jnp.float32) for keep in keeps]
        + [jnp.zeros((own_rows,), jnp.float32), jnp.full((own_rows,), lower_half, jnp.float32),
           jnp.zeros((own_rows,), jnp.float32)],
        1,
    )

    (local_end, l_t, dt_t, decay_x, total_decay, inner_conv, b_full, c_full, end_sent,
     prefix_x, g_tiles) = run_state(
        inner_input, tails, conv_inner, bias_inner.reshape(1, -1), state_input, partner_raw,
        extra, partner_extra,
        step_size, decay_rate.reshape(1, -1), info
    )

    def relay(step_num, incoming):
        return shifted(
            (total_decay * incoming.astype(jnp.float32) + local_end).astype(jnp.bfloat16), "seq", 1
        )

    part_rows = own_rows * lax.axis_size("seq")
    hops = min(lax.axis_size("seq") - 1, -(-(part_rows // 2) // own_rows))
    half_blocks = block_count // 2
    operands = (inner_conv, b_full, c_full, l_t, dt_t, seg_row, info, decay_x, skip_x)
    incoming = shifted(end_sent, "seq", 1)
    partial, middle = run_partial(0, half_blocks, *operands)
    incoming, partial, middle = lax.optimization_barrier((incoming, partial, middle))
    first_hop = incoming
    for step_num in range(1, hops):
        incoming = relay(step_num, incoming)
    second, _ = run_partial(
        half_blocks, block_count - half_blocks, *operands, init=middle, after=first_hop
    )
    return run_correct(partial, second, c_full, g_tiles, incoming)


def solution(mesh):
    return jax.shard_map(
        body,
        mesh=mesh,
        in_specs=(
            P(("grp", "seq"), "head"),
            P(None, ("grp", "seq"), "head"),
            P(None, "head"),
            P("head"),
            P(None, None, "head"),
            P(None, "head"),
            P("head", ("grp", "seq")),
            P("head"),
            P("head"),
            P("grp"),
        ),
        out_specs=P(("grp", "seq"), "head"),
        check_vma=False,
    )
```

```python
import functools

import jax
import jax.numpy as jnp
from jax import lax
from jax.experimental import pallas as pl
from jax.experimental.pallas import tpu as pltpu
from jax.sharding import PartitionSpec as P

BLOCK = 128
CORRECT_TILE = 256


def shifted(value, axis, steps):
    count = lax.axis_size(axis)
    initial, last = (max(0, -steps), min(count, count - steps))
    return lax.ppermute(value, axis, [(source, source + steps) for source in range(initial, last)])


def from_partner(block, axis, stride):
    count = lax.axis_size(axis)
    route = []
    for low in range(count):
        high = low | 1 << stride
        if high != low and high < count:
            route += [(low, high), (high, low)]
    return lax.ppermute(block, axis, route)


def segment_of(lengths, positions):
    starts = jnp.cumsum(lengths, dtype=jnp.int32) - lengths
    covered = (starts[None, :] <= positions[:, None]).astype(jnp.int32)
    return jnp.sum(covered, axis=1, dtype=jnp.int32) - 1


def convolve(extended, weight, bias_row, seg_ext, row_count):
    own_seg = seg_ext[3:]
    summed = (
        jnp.zeros(extended.shape[:-2] + (row_count, extended.shape[-1]), jnp.float32) + bias_row
    )
    for offset in range(4):
        kept_mask = (seg_ext[offset : offset + row_count] == own_seg).astype(jnp.float32)[:, None]
        window = extended[..., offset : offset + row_count, :].astype(jnp.float32)
        summed = summed + weight[offset].astype(jnp.float32) * window * kept_mask
    return jax.nn.silu(summed).astype(jnp.bfloat16)


def split_dot(lhs, value):
    high = value.astype(jnp.bfloat16)
    low = (value - high.astype(jnp.float32)).astype(jnp.bfloat16)
    return jnp.dot(lhs, high, preferred_element_type=jnp.float32) + jnp.dot(
        lhs, low, preferred_element_type=jnp.float32
    )


def expand_heads(small, head_width):
    rows, heads = small.shape
    per_tile = 128 // head_width
    lane = lax.broadcasted_iota(jnp.int32, (rows, 128), 1) // head_width
    tiles = []
    for tile in range(heads // per_tile):
        picked = jnp.broadcast_to(small[:, tile * per_tile : tile * per_tile + 1], (rows, 128))
        for k in range(1, per_tile):
            column = small[:, tile * per_tile + k : tile * per_tile + k + 1]
            picked = jnp.where(lane == k, jnp.broadcast_to(column, (rows, 128)), picked)
        tiles.append(picked)
    return jnp.concatenate(tiles, axis=1)


def block_kernel(with_y, head_width, *refs):
    if with_y:
        (x_ref, b_ref, c_ref, l_ref, dt_ref, segr_ref, info_ref, decay_ref,
         skip_ref, ein_ref, out_ref, state_ref) = refs
    else:
        (x_ref, b_ref, l_ref, dt_ref, segc_ref, decay_ref, state_ref) = refs
    blk = pl.program_id(0)

    @pl.when(blk == 0)
    def _():
        if with_y:
            state_ref[...] = ein_ref[...].astype(jnp.float32)
        else:
            state_ref[...] = jnp.zeros(state_ref.shape, jnp.float32)

    info = info_ref[...]
    seg_col = info[:, 0:1]
    end_col = (seg_col == seg_col[BLOCK - 1 : BLOCK, :]).astype(jnp.float32)
    l_small = l_ref[...]
    dt_small = dt_ref[...]
    x = x_ref[...].astype(jnp.float32)
    state = state_ref[...]
    if with_y:
        c_mat = c_ref[...]
        seg_row = segr_ref[...]
        scores = lax.dot_general(
            c_mat, b_ref[...], (((1,), (1,)), ((), ())), preferred_element_type=jnp.float32
        )
        rows = lax.broadcasted_iota(jnp.int32, (BLOCK, BLOCK), 0)
        cols = lax.broadcasted_iota(jnp.int32, (BLOCK, BLOCK), 1)
        allowed = (rows >= cols) & (seg_col == seg_row)
        masked = jnp.where(allowed, scores, 0.0).astype(jnp.bfloat16)
        rising = expand_heads(jnp.exp(l_small), head_width)
        falling = expand_heads(jnp.exp(-l_small) * dt_small, head_width)
        intra = split_dot(masked, x * falling) * rising
        inter = split_dot(c_mat, state) * (rising * info[:, 1:2])
        out_ref[...] = (intra + inter + skip_ref[...] * x).astype(jnp.bfloat16)
    ending = expand_heads(
        jnp.exp(l_small[BLOCK - 1 : BLOCK, :] - l_small) * dt_small * end_col, head_width
    )
    weighted = (x * ending).astype(jnp.bfloat16)
    state_ref[...] = decay_ref[0] * state + lax.dot_general(
        b_ref[...], weighted, (((0,), (0,)), ((), ())), preferred_element_type=jnp.float32
    )


def causal_conv(raw, prev, taps, bias, info):
    top_row = lax.broadcasted_iota(jnp.int32, prev.shape, 0)
    summed = jnp.zeros(raw.shape, jnp.float32) + bias
    for offset in range(4):
        back = 3 - offset
        if back == 0:
            window = raw
        else:
            rolled = pltpu.roll(raw, back, 0)
            top = jnp.where(top_row < back, pltpu.roll(prev, back, 0), rolled[:8])
            window = jnp.concatenate([top, rolled[8:]], 0) * info[:, 1 + back : 2 + back]
        summed = summed + taps[offset : offset + 1, :] * window
    return jax.nn.silu(summed).astype(jnp.bfloat16)


def state_kernel(head_width, x_ref, tail_ref, wconv_ref, bias_ref, own_ref, other_ref, ownx_ref,
                 otherx_ref, dt_ref, rate_ref, info_ref, state_ref, l_ref, dtt_ref,
                 decay_ref, total_ref, xc_ref, bo_ref, co_ref, sent_ref, prefix_ref, ltile_ref,
                 prev_ref, bcprev_ref, small_ref):
    blk = pl.program_id(0)

    @pl.when(blk == 0)
    def _():
        state_ref[...] = jnp.zeros(state_ref.shape, jnp.float32)
        total_ref[...] = jnp.ones(total_ref.shape, jnp.float32)
        prev_ref[...] = tail_ref[:, : x_ref.shape[1]].astype(jnp.float32)
        small_ref[...] = jnp.ones(small_ref.shape, jnp.float32)
        bcprev_ref[0] = ownx_ref[:, 0:8, :]
        bcprev_ref[1] = otherx_ref[:, 0:8, :]

    info = info_ref[...]
    raw = x_ref[...].astype(jnp.float32)
    xc = causal_conv(raw, prev_ref[...], wconv_ref[...].astype(jnp.float32), bias_ref[...], info)
    prev_ref[...] = raw[BLOCK - 8 :]
    xc_ref[...] = xc
    lower = info_ref[0:1, 5:6] > 0.5
    convolved = []
    for which in range(2):
        halves = []
        for side, (raw_ref, extra_ref) in enumerate(((own_ref, ownx_ref), (other_ref, otherx_ref))):
            raw_bc = raw_ref[which].astype(jnp.float32)
            extra = extra_ref[which]
            halves.append(
                causal_conv(raw_bc, bcprev_ref[side, which], extra[8:12], extra[12:13], info)
            )
            bcprev_ref[side, which] = raw_bc[BLOCK - 8 :]
        convolved.append(jnp.where(
            lower, jnp.concatenate(halves, 1), jnp.concatenate(halves[::-1], 1)
        ))
    b_mat, c_mat = convolved
    bo_ref[...] = b_mat
    co_ref[...] = c_mat

    rows = lax.broadcasted_iota(jnp.int32, (2 * BLOCK, BLOCK), 0)
    cols = lax.broadcasted_iota(jnp.int32, (2 * BLOCK, BLOCK), 1)
    picker = jnp.where(
        ((rows < BLOCK) & (rows >= cols)) | (rows - BLOCK == cols), 1.0, 0.0
    ).astype(jnp.bfloat16)
    rest = dt_ref[...]
    cum = None
    for _ in range(3):
        piece = rest.astype(jnp.bfloat16)
        part = lax.dot_general(
            picker, piece, (((1,), (1,)), ((), ())), preferred_element_type=jnp.float32
        )
        cum = part if cum is None else cum + part
        rest = rest - piece.astype(jnp.float32)
    l_small = -cum[:BLOCK] * rate_ref[...]
    dt_small = cum[BLOCK:]
    l_ref[...] = l_small
    dtt_ref[...] = dt_small
    seg_col = info[:, 0:1]
    end_col = (seg_col == seg_col[BLOCK - 1 : BLOCK, :]).astype(jnp.float32)
    decay_x = expand_heads(
        jnp.exp(l_small[BLOCK - 1 : BLOCK, :]) * info[BLOCK - 1 : BLOCK, 1:2], head_width
    )
    decay_ref[0] = decay_x
    prefix_ref[0] = total_ref[...]
    total_ref[...] = total_ref[...] * decay_x
    carry = (jnp.exp(l_small) * info[:, 1:2]) * small_ref[...]
    small_ref[...] = small_ref[...] * (
        jnp.exp(l_small[BLOCK - 1 : BLOCK, :]) * info[BLOCK - 1 : BLOCK, 1:2]
    )
    tile_heads = ltile_ref.shape[2]
    for tile in range(ltile_ref.shape[0]):
        ltile_ref[tile] = carry[:, tile * tile_heads : (tile + 1) * tile_heads]
    ending = expand_heads(
        jnp.exp(l_small[BLOCK - 1 : BLOCK, :] - l_small) * dt_small * end_col, head_width
    )
    weighted = (xc.astype(jnp.float32) * ending).astype(jnp.bfloat16)
    new_state = decay_x * state_ref[...] + lax.dot_general(
        b_mat, weighted, (((0,), (0,)), ((), ())), preferred_element_type=jnp.float32
    )
    state_ref[...] = new_state

    @pl.when(blk == pl.num_programs(0) - 1)
    def _():
        sent_ref[...] = new_state.astype(jnp.bfloat16)


def run_state(x, tails, wconv, bias_row, own_raw, other_raw, own_extra, other_extra,
              step_size, rate_row, info):
    rows, width = x.shape
    head_count = step_size.shape[0]
    half = own_raw.shape[2]
    n_size = 2 * half
    block_count = rows // BLOCK
    tiles = width // CORRECT_TILE
    tile_heads = head_count // tiles
    row_block = lambda cols: pl.BlockSpec((BLOCK, cols), lambda b: (b, 0))
    whole = lambda shape: pl.BlockSpec(shape, lambda b: (0,) * len(shape))
    return pl.pallas_call(
        functools.partial(state_kernel, width // head_count),
        grid=(block_count,),
        in_specs=[row_block(width), whole(tails.shape), whole((4, width)), whole((1, width)),
                  pl.BlockSpec((2, BLOCK, half), lambda b: (0, b, 0)),
                  pl.BlockSpec((2, BLOCK, half), lambda b: (0, b, 0)),
                  whole(own_extra.shape), whole(own_extra.shape),
                  pl.BlockSpec((head_count, BLOCK), lambda b: (0, b)),
                  whole((1, head_count)), row_block(info.shape[1])],
        out_specs=[whole((n_size, width)), row_block(head_count), row_block(head_count),
                   pl.BlockSpec((1, 1, width), lambda b: (b, 0, 0)), whole((1, width)),
                   row_block(width), row_block(n_size), row_block(n_size),
                   whole((n_size, width)), pl.BlockSpec((1, 1, width), lambda b: (b, 0, 0)),
                   pl.BlockSpec((tiles, BLOCK, tile_heads), lambda b: (0, b, 0))],
        out_shape=[jax.ShapeDtypeStruct((n_size, width), jnp.float32),
                   jax.ShapeDtypeStruct((rows, head_count), jnp.float32),
                   jax.ShapeDtypeStruct((rows, head_count), jnp.float32),
                   jax.ShapeDtypeStruct((block_count, 1, width), jnp.float32),
                   jax.ShapeDtypeStruct((1, width), jnp.float32),
                   jax.ShapeDtypeStruct((rows, width), jnp.bfloat16),
                   jax.ShapeDtypeStruct((rows, n_size), jnp.bfloat16),
                   jax.ShapeDtypeStruct((rows, n_size), jnp.bfloat16),
                   jax.ShapeDtypeStruct((n_size, width), jnp.bfloat16),
                   jax.ShapeDtypeStruct((block_count, 1, width), jnp.float32),
                   jax.ShapeDtypeStruct((tiles, rows, tile_heads), jnp.float32)],
        scratch_shapes=[pltpu.VMEM((8, width), jnp.float32),
                        pltpu.VMEM((2, 2, 8, half), jnp.float32),
                        pltpu.VMEM((1, head_count), jnp.float32)],
        compiler_params=pltpu.CompilerParams(dimension_semantics=("arbitrary",)),
    )(x, tails, wconv, bias_row, own_raw, other_raw, own_extra, other_extra, step_size,
      rate_row, info)


def partial_kernel(head_width, from_zero, *refs):
    if from_zero:
        (x_ref, b_ref, c_ref, l_ref, dt_ref, segr_ref, info_ref, decay_ref, skip_ref, out_ref,
         end_ref, state_ref) = refs
    else:
        (x_ref, b_ref, c_ref, l_ref, dt_ref, segr_ref, info_ref, decay_ref, skip_ref, init_ref,
         after_ref, out_ref, state_ref) = refs
    blk = pl.program_id(0)

    @pl.when(blk == 0)
    def _():
        if from_zero:
            state_ref[...] = jnp.zeros(state_ref.shape, jnp.float32)
        else:
            state_ref[...] = init_ref[...]

    info = info_ref[...]
    seg_col = info[:, 0:1]
    end_col = (seg_col == seg_col[BLOCK - 1 : BLOCK, :]).astype(jnp.float32)
    l_small = l_ref[...]
    dt_small = dt_ref[...]
    x = x_ref[...].astype(jnp.float32)
    state = state_ref[...]
    c_mat = c_ref[...]
    b_mat = b_ref[...]
    scores = lax.dot_general(
        c_mat, b_mat, (((1,), (1,)), ((), ())), preferred_element_type=jnp.float32
    )
    rows = lax.broadcasted_iota(jnp.int32, (BLOCK, BLOCK), 0)
    cols = lax.broadcasted_iota(jnp.int32, (BLOCK, BLOCK), 1)
    allowed = (rows >= cols) & (seg_col == segr_ref[...])
    masked = jnp.where(allowed, scores, 0.0).astype(jnp.bfloat16)
    rising = expand_heads(jnp.exp(l_small), head_width)
    falling = expand_heads(jnp.exp(-l_small) * dt_small, head_width)
    intra = split_dot(masked, x * falling) * rising
    inter = split_dot(c_mat, state) * (rising * info[:, 1:2])
    out_ref[...] = intra + inter + skip_ref[...] * x
    last = blk == pl.num_programs(0) - 1

    @pl.when(jnp.logical_or(jnp.logical_not(last), from_zero))
    def _():
        ending = expand_heads(
            jnp.exp(l_small[BLOCK - 1 : BLOCK, :] - l_small) * dt_small * end_col, head_width
        )
        weighted = (x * ending).astype(jnp.bfloat16)
        new_state = decay_ref[0] * state + lax.dot_general(
            b_mat, weighted, (((0,), (0,)), ((), ())), preferred_element_type=jnp.float32
        )
        state_ref[...] = new_state
        if from_zero:

            @pl.when(last)
            def _():
                end_ref[...] = new_state


def run_partial(first, count, x, b_full, c_full, l_t, dt_t, seg_row, info, decay_x, skip_x,
                init=None, after=None):
    rows, width = x.shape
    head_count = l_t.shape[1]
    n_size = b_full.shape[1]
    row_block = lambda cols: pl.BlockSpec((BLOCK, cols), lambda b: (b + first, 0))
    whole = lambda shape: pl.BlockSpec(shape, lambda b: (0,) * len(shape))
    from_zero = init is None
    in_specs = [row_block(width), row_block(n_size), row_block(n_size), row_block(head_count),
                row_block(head_count), pl.BlockSpec((1, BLOCK), lambda b: (0, b + first)),
                row_block(info.shape[1]), pl.BlockSpec((1, 1, width), lambda b: (b + first, 0, 0)),
                whole((1, width))]
    args = [x, b_full, c_full, l_t, dt_t, seg_row, info, decay_x, skip_x]
    if not from_zero:
        in_specs += [whole((n_size, width)), pl.BlockSpec(memory_space=pl.ANY)]
        args += [init, after]
    out_specs = [pl.BlockSpec((BLOCK, width), lambda b: (b, 0))]
    out_shape = [jax.ShapeDtypeStruct((count * BLOCK, width), jnp.float32)]
    if from_zero:
        out_specs.append(whole((n_size, width)))
        out_shape.append(jax.ShapeDtypeStruct((n_size, width), jnp.float32))
    return pl.pallas_call(
        functools.partial(partial_kernel, width // head_count, from_zero),
        grid=(count,),
        in_specs=in_specs,
        out_specs=out_specs,
        out_shape=out_shape,
        scratch_shapes=[pltpu.VMEM((n_size, width), jnp.float32)],
        compiler_params=pltpu.CompilerParams(dimension_semantics=("arbitrary",)),
    )(*args)


def correct_kernel(head_width, y_ref, z_ref, c_ref, g_ref, ein_ref, out_ref):
    factor = expand_heads(g_ref[0], head_width)
    carried = jnp.dot(c_ref[...], ein_ref[...], preferred_element_type=jnp.float32)
    split = y_ref.shape[0]
    out_ref[:split] = (y_ref[...] + carried[:split] * factor[:split]).astype(jnp.bfloat16)
    out_ref[split:] = (z_ref[...] + carried[split:] * factor[split:]).astype(jnp.bfloat16)


def run_correct(first, second, c_full, g_tiles, entering):
    rows = first.shape[0] + second.shape[0]
    width = first.shape[1]
    tiles, _, heads_per = g_tiles.shape
    tile = CORRECT_TILE
    head_width = tile // heads_per
    n_size = c_full.shape[1]
    return pl.pallas_call(
        functools.partial(correct_kernel, head_width),
        grid=(tiles,),
        in_specs=[pl.BlockSpec((first.shape[0], tile), lambda j: (0, j)),
                  pl.BlockSpec((second.shape[0], tile), lambda j: (0, j)),
                  pl.BlockSpec((rows, n_size), lambda j: (0, 0)),
                  pl.BlockSpec((1, rows, heads_per), lambda j: (j, 0, 0)),
                  pl.BlockSpec((n_size, tile), lambda j: (0, j))],
        out_specs=pl.BlockSpec((rows, tile), lambda j: (0, j)),
        out_shape=jax.ShapeDtypeStruct((rows, width), jnp.bfloat16),
        compiler_params=pltpu.CompilerParams(dimension_semantics=("arbitrary",)),
    )(first, second, c_full, g_tiles, entering)


def run_blocks(with_y, x, b_full, c_full, l_t, dt_t, seg_row, seg_col, entry_col, decay_x,
               skip_x, entering):
    rows, width = x.shape
    head_count = l_t.shape[1]
    head_width = width // head_count
    n_size = b_full.shape[1]
    block_count = rows // BLOCK
    row_block = lambda cols: pl.BlockSpec((BLOCK, cols), lambda b: (b, 0))
    bt_spec = pl.BlockSpec((n_size, BLOCK), lambda b: (0, b))
    decay_spec = pl.BlockSpec((1, 1, width), lambda b: (b, 0, 0))
    state_spec = pl.BlockSpec((n_size, width), lambda b: (0, 0))
    state_shape = jax.ShapeDtypeStruct((n_size, width), jnp.float32)
    kernel = functools.partial(block_kernel, with_y, head_width)
    params = pltpu.CompilerParams(dimension_semantics=("arbitrary",))
    if with_y:
        return pl.pallas_call(
            kernel,
            grid=(block_count,),
            in_specs=[row_block(width), row_block(n_size), row_block(n_size),
                      row_block(head_count), row_block(head_count),
                      pl.BlockSpec((1, BLOCK), lambda b: (0, b)), row_block(seg_col.shape[1]),
                      decay_spec, pl.BlockSpec((1, width), lambda b: (0, 0)), state_spec],
            out_specs=row_block(width),
            out_shape=jax.ShapeDtypeStruct((rows, width), jnp.bfloat16),
            scratch_shapes=[pltpu.VMEM((n_size, width), jnp.float32)],
            compiler_params=params,
        )(x, b_full, c_full, l_t, dt_t, seg_row, seg_col, decay_x, skip_x, entering)
    return pl.pallas_call(
        kernel,
        grid=(block_count,),
        in_specs=[row_block(width), bt_spec, row_block(head_count), row_block(head_count),
                  row_block(1), decay_spec],
        out_specs=state_spec,
        out_shape=state_shape,
        compiler_params=params,
    )(x, b_t, l_t, dt_t, seg_col, decay_x)


def body(
    inner_input,
    state_input,
    conv_inner,
    bias_inner,
    conv_state,
    bias_state,
    step_size,
    decay_rate,
    skip_gain,
    lengths,
):
    own_rows = inner_input.shape[0]
    head_count = decay_rate.shape[0]
    group_half = state_input.shape[2]
    block_count = own_rows // BLOCK
    positions = lax.axis_index("seq") * own_rows + jnp.arange(own_rows + 3, dtype=jnp.int32) - 3
    seg_ext = segment_of(lengths, positions)
    width = inner_input.shape[1]
    tails = jnp.concatenate(
        [inner_input[-8:], jnp.transpose(state_input[:, -8:], (1, 0, 2)).reshape(8, -1)], 1
    )
    tails = shifted(tails, "seq", 1)
    state_tail = tails[:, width:].reshape(8, 2, group_half)
    extra = jnp.concatenate(
        [jnp.transpose(state_tail, (1, 0, 2)).astype(jnp.float32),
         conv_state.astype(jnp.float32), bias_state[:, None, :]],
        1,
    )
    partner_raw, partner_extra = from_partner((state_input, extra), "head", 0)
    lower_half = (lax.axis_index("head") % 2 == 0).astype(jnp.float32)
    head_width = inner_input.shape[1] // head_count
    spread = lambda v: jnp.repeat(v, head_width, axis=-1)
    skip_x = spread(skip_gain).reshape(1, -1)
    seg_own = seg_ext[3:].reshape(block_count, BLOCK)
    seg_prev = seg_ext[2 : 2 + own_rows].reshape(block_count, BLOCK)[:, 0]
    seg_row = seg_ext[3:].reshape(1, own_rows).astype(jnp.float32)
    own_seg = seg_ext[3:]
    entry_col = (seg_own == seg_prev[:, None]).reshape(own_rows)
    keeps = [(seg_ext[3 - back : 3 - back + own_rows] == own_seg) for back in (1, 2, 3)]
    info = jnp.stack(
        [own_seg.astype(jnp.float32), entry_col.astype(jnp.float32)]
        + [keep.astype(jnp.float32) for keep in keeps]
        + [jnp.zeros((own_rows,), jnp.float32), jnp.full((own_rows,), lower_half, jnp.float32),
           jnp.zeros((own_rows,), jnp.float32)],
        1,
    )

    (local_end, l_t, dt_t, decay_x, total_decay, inner_conv, b_full, c_full, end_sent,
     prefix_x, g_tiles) = run_state(
        inner_input, tails, conv_inner, bias_inner.reshape(1, -1), state_input, partner_raw,
        extra, partner_extra,
        step_size, decay_rate.reshape(1, -1), info
    )

    def relay(step_num, incoming):
        return shifted(
            (total_decay * incoming.astype(jnp.float32) + local_end).astype(jnp.bfloat16), "seq", 1
        )

    part_rows = own_rows * lax.axis_size("seq")
    hops = min(lax.axis_size("seq") - 1, -(-(part_rows // 2) // own_rows))
    half_blocks = block_count // 2
    operands = (inner_conv, b_full, c_full, l_t, dt_t, seg_row, info, decay_x, skip_x)
    incoming = shifted(end_sent, "seq", 1)
    partial, middle = run_partial(0, half_blocks, *operands)
    incoming, partial, middle = lax.optimization_barrier((incoming, partial, middle))
    first_hop = incoming
    for step_num in range(1, hops):
        incoming = relay(step_num, incoming)
    (second,) = run_partial(
        half_blocks, block_count - half_blocks, *operands, init=middle, after=first_hop
    )
    return run_correct(partial, second, c_full, g_tiles, incoming)


def solution(mesh):
    return jax.shard_map(
        body,
        mesh=mesh,
        in_specs=(
            P(("grp", "seq"), "head"),
            P(None, ("grp", "seq"), "head"),
            P(None, "head"),
            P("head"),
            P(None, None, "head"),
            P(None, "head"),
            P("head", ("grp", "seq")),
            P("head"),
            P("head"),
            P("grp"),
        ),
        out_specs=P(("grp", "seq"), "head"),
        check_vma=False,
    )
```

```python
import functools

import jax
import jax.numpy as jnp
from jax import lax
from jax.experimental import pallas as pl
from jax.experimental.pallas import tpu as pltpu
from jax.sharding import PartitionSpec as P

BLOCK = 128
CORRECT_TILE = 256


def shifted(value, axis, steps):
    count = lax.axis_size(axis)
    initial, last = (max(0, -steps), min(count, count - steps))
    return lax.ppermute(value, axis, [(source, source + steps) for source in range(initial, last)])


def from_partner(block, axis, stride):
    count = lax.axis_size(axis)
    route = []
    for low in range(count):
        high = low | 1 << stride
        if high != low and high < count:
            route += [(low, high), (high, low)]
    return lax.ppermute(block, axis, route)


def segment_of(lengths, positions):
    starts = jnp.cumsum(lengths, dtype=jnp.int32) - lengths
    covered = (starts[None, :] <= positions[:, None]).astype(jnp.int32)
    return jnp.sum(covered, axis=1, dtype=jnp.int32) - 1


def convolve(extended, weight, bias_row, seg_ext, row_count):
    own_seg = seg_ext[3:]
    summed = (
        jnp.zeros(extended.shape[:-2] + (row_count, extended.shape[-1]), jnp.float32) + bias_row
    )
    for offset in range(4):
        kept_mask = (seg_ext[offset : offset + row_count] == own_seg).astype(jnp.float32)[:, None]
        window = extended[..., offset : offset + row_count, :].astype(jnp.float32)
        summed = summed + weight[offset].astype(jnp.float32) * window * kept_mask
    return jax.nn.silu(summed).astype(jnp.bfloat16)


def split_dot(lhs, value):
    high = value.astype(jnp.bfloat16)
    low = (value - high.astype(jnp.float32)).astype(jnp.bfloat16)
    return jnp.dot(lhs, high, preferred_element_type=jnp.float32) + jnp.dot(
        lhs, low, preferred_element_type=jnp.float32
    )


def expand_heads(small, head_width):
    rows, heads = small.shape
    per_tile = 128 // head_width
    lane = lax.broadcasted_iota(jnp.int32, (rows, 128), 1) // head_width
    tiles = []
    for tile in range(heads // per_tile):
        picked = jnp.broadcast_to(small[:, tile * per_tile : tile * per_tile + 1], (rows, 128))
        for k in range(1, per_tile):
            column = small[:, tile * per_tile + k : tile * per_tile + k + 1]
            picked = jnp.where(lane == k, jnp.broadcast_to(column, (rows, 128)), picked)
        tiles.append(picked)
    return jnp.concatenate(tiles, axis=1)


def block_kernel(with_y, head_width, *refs):
    if with_y:
        (x_ref, b_ref, c_ref, l_ref, dt_ref, segr_ref, info_ref, decay_ref,
         skip_ref, ein_ref, out_ref, state_ref) = refs
    else:
        (x_ref, b_ref, l_ref, dt_ref, segc_ref, decay_ref, state_ref) = refs
    blk = pl.program_id(0)

    @pl.when(blk == 0)
    def _():
        if with_y:
            state_ref[...] = ein_ref[...].astype(jnp.float32)
        else:
            state_ref[...] = jnp.zeros(state_ref.shape, jnp.float32)

    info = info_ref[...]
    seg_col = info[:, 0:1]
    end_col = (seg_col == seg_col[BLOCK - 1 : BLOCK, :]).astype(jnp.float32)
    l_small = l_ref[...]
    dt_small = dt_ref[...]
    x = x_ref[...].astype(jnp.float32)
    state = state_ref[...]
    if with_y:
        c_mat = c_ref[...]
        seg_row = segr_ref[...]
        scores = lax.dot_general(
            c_mat, b_ref[...], (((1,), (1,)), ((), ())), preferred_element_type=jnp.float32
        )
        rows = lax.broadcasted_iota(jnp.int32, (BLOCK, BLOCK), 0)
        cols = lax.broadcasted_iota(jnp.int32, (BLOCK, BLOCK), 1)
        allowed = (rows >= cols) & (seg_col == seg_row)
        masked = jnp.where(allowed, scores, 0.0).astype(jnp.bfloat16)
        rising = expand_heads(jnp.exp(l_small), head_width)
        falling = expand_heads(jnp.exp(-l_small) * dt_small, head_width)
        intra = split_dot(masked, x * falling) * rising
        inter = split_dot(c_mat, state) * (rising * info[:, 1:2])
        out_ref[...] = (intra + inter + skip_ref[...] * x).astype(jnp.bfloat16)
    ending = expand_heads(
        jnp.exp(l_small[BLOCK - 1 : BLOCK, :] - l_small) * dt_small * end_col, head_width
    )
    weighted = (x * ending).astype(jnp.bfloat16)
    state_ref[...] = decay_ref[0] * state + lax.dot_general(
        b_ref[...], weighted, (((0,), (0,)), ((), ())), preferred_element_type=jnp.float32
    )


def causal_conv(raw, prev, taps, bias, info):
    top_row = lax.broadcasted_iota(jnp.int32, prev.shape, 0)
    summed = jnp.zeros(raw.shape, jnp.float32) + bias
    for offset in range(4):
        back = 3 - offset
        if back == 0:
            window = raw
        else:
            rolled = pltpu.roll(raw, back, 0)
            top = jnp.where(top_row < back, pltpu.roll(prev, back, 0), rolled[:8])
            window = jnp.concatenate([top, rolled[8:]], 0) * info[:, 1 + back : 2 + back]
        summed = summed + taps[offset : offset + 1, :] * window
    return (summed * (0.5 + 0.5 * jnp.tanh(0.5 * summed))).astype(jnp.bfloat16)


def state_kernel(head_width, x_ref, tail_ref, wconv_ref, bias_ref, own_ref, other_ref, ownx_ref,
                 otherx_ref, dt_ref, rate_ref, info_ref, state_ref, l_ref, dtt_ref,
                 decay_ref, total_ref, xc_ref, bo_ref, co_ref, sent_ref, prefix_ref, ltile_ref,
                 prev_ref, bcprev_ref, small_ref):
    blk = pl.program_id(0)

    @pl.when(blk == 0)
    def _():
        state_ref[...] = jnp.zeros(state_ref.shape, jnp.float32)
        total_ref[...] = jnp.ones(total_ref.shape, jnp.float32)
        prev_ref[...] = tail_ref[:, : x_ref.shape[1]].astype(jnp.float32)
        small_ref[...] = jnp.ones(small_ref.shape, jnp.float32)
        bcprev_ref[0] = ownx_ref[:, 0:8, :]
        bcprev_ref[1] = otherx_ref[:, 0:8, :]

    info = info_ref[...]
    raw = x_ref[...].astype(jnp.float32)
    xc = causal_conv(raw, prev_ref[...], wconv_ref[...].astype(jnp.float32), bias_ref[...], info)
    prev_ref[...] = raw[BLOCK - 8 :]
    xc_ref[...] = xc
    lower = info_ref[0:1, 5:6] > 0.5
    convolved = []
    for which in range(2):
        halves = []
        for side, (raw_ref, extra_ref) in enumerate(((own_ref, ownx_ref), (other_ref, otherx_ref))):
            raw_bc = raw_ref[which].astype(jnp.float32)
            extra = extra_ref[which]
            halves.append(
                causal_conv(raw_bc, bcprev_ref[side, which], extra[8:12], extra[12:13], info)
            )
            bcprev_ref[side, which] = raw_bc[BLOCK - 8 :]
        convolved.append(jnp.where(
            lower, jnp.concatenate(halves, 1), jnp.concatenate(halves[::-1], 1)
        ))
    b_mat, c_mat = convolved
    bo_ref[...] = b_mat
    co_ref[...] = c_mat

    rows = lax.broadcasted_iota(jnp.int32, (2 * BLOCK, BLOCK), 0)
    cols = lax.broadcasted_iota(jnp.int32, (2 * BLOCK, BLOCK), 1)
    picker = jnp.where(
        ((rows < BLOCK) & (rows >= cols)) | (rows - BLOCK == cols), 1.0, 0.0
    ).astype(jnp.bfloat16)
    rest = dt_ref[...]
    cum = None
    for _ in range(3):
        piece = rest.astype(jnp.bfloat16)
        part = lax.dot_general(
            picker, piece, (((1,), (1,)), ((), ())), preferred_element_type=jnp.float32
        )
        cum = part if cum is None else cum + part
        rest = rest - piece.astype(jnp.float32)
    l_small = -cum[:BLOCK] * rate_ref[...]
    dt_small = cum[BLOCK:]
    l_ref[...] = l_small
    dtt_ref[...] = dt_small
    seg_col = info[:, 0:1]
    end_col = (seg_col == seg_col[BLOCK - 1 : BLOCK, :]).astype(jnp.float32)
    decay_x = expand_heads(
        jnp.exp(l_small[BLOCK - 1 : BLOCK, :]) * info[BLOCK - 1 : BLOCK, 1:2], head_width
    )
    decay_ref[0] = decay_x
    prefix_ref[0] = total_ref[...]
    total_ref[...] = total_ref[...] * decay_x
    carry = (jnp.exp(l_small) * info[:, 1:2]) * small_ref[...]
    small_ref[...] = small_ref[...] * (
        jnp.exp(l_small[BLOCK - 1 : BLOCK, :]) * info[BLOCK - 1 : BLOCK, 1:2]
    )
    tile_heads = ltile_ref.shape[2]
    for tile in range(ltile_ref.shape[0]):
        ltile_ref[tile] = carry[:, tile * tile_heads : (tile + 1) * tile_heads]
    ending = expand_heads(
        jnp.exp(l_small[BLOCK - 1 : BLOCK, :] - l_small) * dt_small * end_col, head_width
    )
    weighted = (xc.astype(jnp.float32) * ending).astype(jnp.bfloat16)
    new_state = decay_x * state_ref[...] + lax.dot_general(
        b_mat, weighted, (((0,), (0,)), ((), ())), preferred_element_type=jnp.float32
    )
    state_ref[...] = new_state

    @pl.when(blk == pl.num_programs(0) - 1)
    def _():
        sent_ref[...] = new_state.astype(jnp.bfloat16)


def run_state(x, tails, wconv, bias_row, own_raw, other_raw, own_extra, other_extra,
              step_size, rate_row, info):
    rows, width = x.shape
    head_count = step_size.shape[0]
    half = own_raw.shape[2]
    n_size = 2 * half
    block_count = rows // BLOCK
    tiles = width // CORRECT_TILE
    tile_heads = head_count // tiles
    row_block = lambda cols: pl.BlockSpec((BLOCK, cols), lambda b: (b, 0))
    whole = lambda shape: pl.BlockSpec(shape, lambda b: (0,) * len(shape))
    return pl.pallas_call(
        functools.partial(state_kernel, width // head_count),
        grid=(block_count,),
        in_specs=[row_block(width), whole(tails.shape), whole((4, width)), whole((1, width)),
                  pl.BlockSpec((2, BLOCK, half), lambda b: (0, b, 0)),
                  pl.BlockSpec((2, BLOCK, half), lambda b: (0, b, 0)),
                  whole(own_extra.shape), whole(own_extra.shape),
                  pl.BlockSpec((head_count, BLOCK), lambda b: (0, b)),
                  whole((1, head_count)), row_block(info.shape[1])],
        out_specs=[whole((n_size, width)), row_block(head_count), row_block(head_count),
                   pl.BlockSpec((1, 1, width), lambda b: (b, 0, 0)), whole((1, width)),
                   row_block(width), row_block(n_size), row_block(n_size),
                   whole((n_size, width)), pl.BlockSpec((1, 1, width), lambda b: (b, 0, 0)),
                   pl.BlockSpec((tiles, BLOCK, tile_heads), lambda b: (0, b, 0))],
        out_shape=[jax.ShapeDtypeStruct((n_size, width), jnp.float32),
                   jax.ShapeDtypeStruct((rows, head_count), jnp.float32),
                   jax.ShapeDtypeStruct((rows, head_count), jnp.float32),
                   jax.ShapeDtypeStruct((block_count, 1, width), jnp.float32),
                   jax.ShapeDtypeStruct((1, width), jnp.float32),
                   jax.ShapeDtypeStruct((rows, width), jnp.bfloat16),
                   jax.ShapeDtypeStruct((rows, n_size), jnp.bfloat16),
                   jax.ShapeDtypeStruct((rows, n_size), jnp.bfloat16),
                   jax.ShapeDtypeStruct((n_size, width), jnp.bfloat16),
                   jax.ShapeDtypeStruct((block_count, 1, width), jnp.float32),
                   jax.ShapeDtypeStruct((tiles, rows, tile_heads), jnp.float32)],
        scratch_shapes=[pltpu.VMEM((8, width), jnp.float32),
                        pltpu.VMEM((2, 2, 8, half), jnp.float32),
                        pltpu.VMEM((1, head_count), jnp.float32)],
        compiler_params=pltpu.CompilerParams(dimension_semantics=("arbitrary",)),
    )(x, tails, wconv, bias_row, own_raw, other_raw, own_extra, other_extra, step_size,
      rate_row, info)


def partial_kernel(head_width, from_zero, *refs):
    if from_zero:
        (x_ref, b_ref, c_ref, l_ref, dt_ref, segr_ref, info_ref, decay_ref, skip_ref, out_ref,
         end_ref, state_ref) = refs
    else:
        (x_ref, b_ref, c_ref, l_ref, dt_ref, segr_ref, info_ref, decay_ref, skip_ref, init_ref,
         after_ref, out_ref, state_ref) = refs
    blk = pl.program_id(0)

    @pl.when(blk == 0)
    def _():
        if from_zero:
            state_ref[...] = jnp.zeros(state_ref.shape, jnp.float32)
        else:
            state_ref[...] = init_ref[...]

    info = info_ref[...]
    seg_col = info[:, 0:1]
    end_col = (seg_col == seg_col[BLOCK - 1 : BLOCK, :]).astype(jnp.float32)
    l_small = l_ref[...]
    dt_small = dt_ref[...]
    x = x_ref[...].astype(jnp.float32)
    state = state_ref[...]
    c_mat = c_ref[...]
    b_mat = b_ref[...]
    scores = lax.dot_general(
        c_mat, b_mat, (((1,), (1,)), ((), ())), preferred_element_type=jnp.float32
    )
    rows = lax.broadcasted_iota(jnp.int32, (BLOCK, BLOCK), 0)
    cols = lax.broadcasted_iota(jnp.int32, (BLOCK, BLOCK), 1)
    allowed = (rows >= cols) & (seg_col == segr_ref[...])
    masked = jnp.where(allowed, scores, 0.0).astype(jnp.bfloat16)
    rising = expand_heads(jnp.exp(l_small), head_width)
    falling = expand_heads(jnp.exp(-l_small) * dt_small, head_width)
    intra = split_dot(masked, x * falling) * rising
    inter = split_dot(c_mat, state) * (rising * info[:, 1:2])
    out_ref[...] = intra + inter + skip_ref[...] * x
    last = blk == pl.num_programs(0) - 1

    @pl.when(jnp.logical_or(jnp.logical_not(last), from_zero))
    def _():
        ending = expand_heads(
            jnp.exp(l_small[BLOCK - 1 : BLOCK, :] - l_small) * dt_small * end_col, head_width
        )
        weighted = (x * ending).astype(jnp.bfloat16)
        new_state = decay_ref[0] * state + lax.dot_general(
            b_mat, weighted, (((0,), (0,)), ((), ())), preferred_element_type=jnp.float32
        )
        state_ref[...] = new_state
        if from_zero:

            @pl.when(last)
            def _():
                end_ref[...] = new_state


def run_partial(first, count, x, b_full, c_full, l_t, dt_t, seg_row, info, decay_x, skip_x,
                init=None, after=None):
    rows, width = x.shape
    head_count = l_t.shape[1]
    n_size = b_full.shape[1]
    row_block = lambda cols: pl.BlockSpec((BLOCK, cols), lambda b: (b + first, 0))
    whole = lambda shape: pl.BlockSpec(shape, lambda b: (0,) * len(shape))
    from_zero = init is None
    in_specs = [row_block(width), row_block(n_size), row_block(n_size), row_block(head_count),
                row_block(head_count), pl.BlockSpec((1, BLOCK), lambda b: (0, b + first)),
                row_block(info.shape[1]), pl.BlockSpec((1, 1, width), lambda b: (b + first, 0, 0)),
                whole((1, width))]
    args = [x, b_full, c_full, l_t, dt_t, seg_row, info, decay_x, skip_x]
    if not from_zero:
        in_specs += [whole((n_size, width)), pl.BlockSpec(memory_space=pl.ANY)]
        args += [init, after]
    out_specs = [pl.BlockSpec((BLOCK, width), lambda b: (b, 0))]
    out_shape = [jax.ShapeDtypeStruct((count * BLOCK, width), jnp.float32)]
    if from_zero:
        out_specs.append(whole((n_size, width)))
        out_shape.append(jax.ShapeDtypeStruct((n_size, width), jnp.float32))
    return pl.pallas_call(
        functools.partial(partial_kernel, width // head_count, from_zero),
        grid=(count,),
        in_specs=in_specs,
        out_specs=out_specs,
        out_shape=out_shape,
        scratch_shapes=[pltpu.VMEM((n_size, width), jnp.float32)],
        compiler_params=pltpu.CompilerParams(dimension_semantics=("arbitrary",)),
    )(*args)


def correct_kernel(head_width, y_ref, z_ref, c_ref, g_ref, ein_ref, out_ref):
    factor = expand_heads(g_ref[0], head_width)
    carried = jnp.dot(c_ref[...], ein_ref[...], preferred_element_type=jnp.float32)
    split = y_ref.shape[0]
    out_ref[:split] = (y_ref[...] + carried[:split] * factor[:split]).astype(jnp.bfloat16)
    out_ref[split:] = (z_ref[...] + carried[split:] * factor[split:]).astype(jnp.bfloat16)


def run_correct(first, second, c_full, g_tiles, entering):
    rows = first.shape[0] + second.shape[0]
    width = first.shape[1]
    tiles, _, heads_per = g_tiles.shape
    tile = CORRECT_TILE
    head_width = tile // heads_per
    n_size = c_full.shape[1]
    return pl.pallas_call(
        functools.partial(correct_kernel, head_width),
        grid=(tiles,),
        in_specs=[pl.BlockSpec((first.shape[0], tile), lambda j: (0, j)),
                  pl.BlockSpec((second.shape[0], tile), lambda j: (0, j)),
                  pl.BlockSpec((rows, n_size), lambda j: (0, 0)),
                  pl.BlockSpec((1, rows, heads_per), lambda j: (j, 0, 0)),
                  pl.BlockSpec((n_size, tile), lambda j: (0, j))],
        out_specs=pl.BlockSpec((rows, tile), lambda j: (0, j)),
        out_shape=jax.ShapeDtypeStruct((rows, width), jnp.bfloat16),
        compiler_params=pltpu.CompilerParams(dimension_semantics=("arbitrary",)),
    )(first, second, c_full, g_tiles, entering)


def run_blocks(with_y, x, b_full, c_full, l_t, dt_t, seg_row, seg_col, entry_col, decay_x,
               skip_x, entering):
    rows, width = x.shape
    head_count = l_t.shape[1]
    head_width = width // head_count
    n_size = b_full.shape[1]
    block_count = rows // BLOCK
    row_block = lambda cols: pl.BlockSpec((BLOCK, cols), lambda b: (b, 0))
    bt_spec = pl.BlockSpec((n_size, BLOCK), lambda b: (0, b))
    decay_spec = pl.BlockSpec((1, 1, width), lambda b: (b, 0, 0))
    state_spec = pl.BlockSpec((n_size, width), lambda b: (0, 0))
    state_shape = jax.ShapeDtypeStruct((n_size, width), jnp.float32)
    kernel = functools.partial(block_kernel, with_y, head_width)
    params = pltpu.CompilerParams(dimension_semantics=("arbitrary",))
    if with_y:
        return pl.pallas_call(
            kernel,
            grid=(block_count,),
            in_specs=[row_block(width), row_block(n_size), row_block(n_size),
                      row_block(head_count), row_block(head_count),
                      pl.BlockSpec((1, BLOCK), lambda b: (0, b)), row_block(seg_col.shape[1]),
                      decay_spec, pl.BlockSpec((1, width), lambda b: (0, 0)), state_spec],
            out_specs=row_block(width),
            out_shape=jax.ShapeDtypeStruct((rows, width), jnp.bfloat16),
            scratch_shapes=[pltpu.VMEM((n_size, width), jnp.float32)],
            compiler_params=params,
        )(x, b_full, c_full, l_t, dt_t, seg_row, seg_col, decay_x, skip_x, entering)
    return pl.pallas_call(
        kernel,
        grid=(block_count,),
        in_specs=[row_block(width), bt_spec, row_block(head_count), row_block(head_count),
                  row_block(1), decay_spec],
        out_specs=state_spec,
        out_shape=state_shape,
        compiler_params=params,
    )(x, b_t, l_t, dt_t, seg_col, decay_x)


def body(
    inner_input,
    state_input,
    conv_inner,
    bias_inner,
    conv_state,
    bias_state,
    step_size,
    decay_rate,
    skip_gain,
    lengths,
):
    own_rows = inner_input.shape[0]
    head_count = decay_rate.shape[0]
    group_half = state_input.shape[2]
    block_count = own_rows // BLOCK
    positions = lax.axis_index("seq") * own_rows + jnp.arange(own_rows + 3, dtype=jnp.int32) - 3
    seg_ext = segment_of(lengths, positions)
    width = inner_input.shape[1]
    tails = jnp.concatenate(
        [inner_input[-8:], jnp.transpose(state_input[:, -8:], (1, 0, 2)).reshape(8, -1)], 1
    )
    tails = shifted(tails, "seq", 1)
    state_tail = tails[:, width:].reshape(8, 2, group_half)
    extra = jnp.concatenate(
        [jnp.transpose(state_tail, (1, 0, 2)).astype(jnp.float32),
         conv_state.astype(jnp.float32), bias_state[:, None, :]],
        1,
    )
    partner_raw, partner_extra = from_partner((state_input, extra), "head", 0)
    lower_half = (lax.axis_index("head") % 2 == 0).astype(jnp.float32)
    head_width = inner_input.shape[1] // head_count
    spread = lambda v: jnp.repeat(v, head_width, axis=-1)
    skip_x = spread(skip_gain).reshape(1, -1)
    seg_own = seg_ext[3:].reshape(block_count, BLOCK)
    seg_prev = seg_ext[2 : 2 + own_rows].reshape(block_count, BLOCK)[:, 0]
    seg_row = seg_ext[3:].reshape(1, own_rows).astype(jnp.float32)
    own_seg = seg_ext[3:]
    entry_col = (seg_own == seg_prev[:, None]).reshape(own_rows)
    keeps = [(seg_ext[3 - back : 3 - back + own_rows] == own_seg) for back in (1, 2, 3)]
    info = jnp.stack(
        [own_seg.astype(jnp.float32), entry_col.astype(jnp.float32)]
        + [keep.astype(jnp.float32) for keep in keeps]
        + [jnp.zeros((own_rows,), jnp.float32), jnp.full((own_rows,), lower_half, jnp.float32),
           jnp.zeros((own_rows,), jnp.float32)],
        1,
    )

    (local_end, l_t, dt_t, decay_x, total_decay, inner_conv, b_full, c_full, end_sent,
     prefix_x, g_tiles) = run_state(
        inner_input, tails, conv_inner, bias_inner.reshape(1, -1), state_input, partner_raw,
        extra, partner_extra,
        step_size, decay_rate.reshape(1, -1), info
    )

    def relay(step_num, incoming):
        return shifted(
            (total_decay * incoming.astype(jnp.float32) + local_end).astype(jnp.bfloat16), "seq", 1
        )

    part_rows = own_rows * lax.axis_size("seq")
    hops = min(lax.axis_size("seq") - 1, -(-(part_rows // 2) // own_rows))
    half_blocks = block_count // 2
    operands = (inner_conv, b_full, c_full, l_t, dt_t, seg_row, info, decay_x, skip_x)
    incoming = shifted(end_sent, "seq", 1)
    partial, middle = run_partial(0, half_blocks, *operands)
    incoming, partial, middle = lax.optimization_barrier((incoming, partial, middle))
    first_hop = incoming
    for step_num in range(1, hops):
        incoming = relay(step_num, incoming)
    (second,) = run_partial(
        half_blocks, block_count - half_blocks, *operands, init=middle, after=first_hop
    )
    return run_correct(partial, second, c_full, g_tiles, incoming)


def solution(mesh):
    return jax.shard_map(
        body,
        mesh=mesh,
        in_specs=(
            P(("grp", "seq"), "head"),
            P(None, ("grp", "seq"), "head"),
            P(None, "head"),
            P("head"),
            P(None, None, "head"),
            P(None, "head"),
            P("head", ("grp", "seq")),
            P("head"),
            P("head"),
            P("grp"),
        ),
        out_specs=P(("grp", "seq"), "head"),
        check_vma=False,
    )
```

```python
import functools

import jax
import jax.numpy as jnp
from jax import lax
from jax.experimental import pallas as pl
from jax.experimental.pallas import tpu as pltpu
from jax.sharding import PartitionSpec as P

BLOCK = 128
CORRECT_TILE = 256


def shifted(value, axis, steps):
    count = lax.axis_size(axis)
    initial, last = (max(0, -steps), min(count, count - steps))
    return lax.ppermute(value, axis, [(source, source + steps) for source in range(initial, last)])


def from_partner(block, axis, stride):
    count = lax.axis_size(axis)
    route = []
    for low in range(count):
        high = low | 1 << stride
        if high != low and high < count:
            route += [(low, high), (high, low)]
    return lax.ppermute(block, axis, route)


def segment_of(lengths, positions):
    start = jnp.zeros((), jnp.int32)
    count = jnp.full(positions.shape, -1, jnp.int32)
    for req in range(lengths.shape[0]):
        count = count + (start <= positions).astype(jnp.int32)
        start = start + lengths[req]
    return count


def convolve(extended, weight, bias_row, seg_ext, row_count):
    own_seg = seg_ext[3:]
    summed = (
        jnp.zeros(extended.shape[:-2] + (row_count, extended.shape[-1]), jnp.float32) + bias_row
    )
    for offset in range(4):
        kept_mask = (seg_ext[offset : offset + row_count] == own_seg).astype(jnp.float32)[:, None]
        window = extended[..., offset : offset + row_count, :].astype(jnp.float32)
        summed = summed + weight[offset].astype(jnp.float32) * window * kept_mask
    return jax.nn.silu(summed).astype(jnp.bfloat16)


def split_dot(lhs, value):
    high = value.astype(jnp.bfloat16)
    low = (value - high.astype(jnp.float32)).astype(jnp.bfloat16)
    return jnp.dot(lhs, high, preferred_element_type=jnp.float32) + jnp.dot(
        lhs, low, preferred_element_type=jnp.float32
    )


def expand_heads(small, head_width):
    rows, heads = small.shape
    per_tile = 128 // head_width
    lane = lax.broadcasted_iota(jnp.int32, (rows, 128), 1) // head_width
    tiles = []
    for tile in range(heads // per_tile):
        picked = jnp.broadcast_to(small[:, tile * per_tile : tile * per_tile + 1], (rows, 128))
        for k in range(1, per_tile):
            column = small[:, tile * per_tile + k : tile * per_tile + k + 1]
            picked = jnp.where(lane == k, jnp.broadcast_to(column, (rows, 128)), picked)
        tiles.append(picked)
    return jnp.concatenate(tiles, axis=1)


def block_kernel(with_y, head_width, *refs):
    if with_y:
        (x_ref, b_ref, c_ref, l_ref, dt_ref, segr_ref, info_ref, decay_ref,
         skip_ref, ein_ref, out_ref, state_ref) = refs
    else:
        (x_ref, b_ref, l_ref, dt_ref, segc_ref, decay_ref, state_ref) = refs
    blk = pl.program_id(0)

    @pl.when(blk == 0)
    def _():
        if with_y:
            state_ref[...] = ein_ref[...].astype(jnp.float32)
        else:
            state_ref[...] = jnp.zeros(state_ref.shape, jnp.float32)

    info = info_ref[...]
    seg_col = info[:, 0:1]
    end_col = (seg_col == seg_col[BLOCK - 1 : BLOCK, :]).astype(jnp.float32)
    l_small = l_ref[...]
    dt_small = dt_ref[...]
    x = x_ref[...].astype(jnp.float32)
    state = state_ref[...]
    if with_y:
        c_mat = c_ref[...]
        seg_row = segr_ref[...]
        scores = lax.dot_general(
            c_mat, b_ref[...], (((1,), (1,)), ((), ())), preferred_element_type=jnp.float32
        )
        rows = lax.broadcasted_iota(jnp.int32, (BLOCK, BLOCK), 0)
        cols = lax.broadcasted_iota(jnp.int32, (BLOCK, BLOCK), 1)
        allowed = (rows >= cols) & (seg_col == seg_row)
        masked = jnp.where(allowed, scores, 0.0).astype(jnp.bfloat16)
        rising = expand_heads(jnp.exp(l_small), head_width)
        falling = expand_heads(jnp.exp(-l_small) * dt_small, head_width)
        intra = split_dot(masked, x * falling) * rising
        inter = split_dot(c_mat, state) * (rising * info[:, 1:2])
        out_ref[...] = (intra + inter + skip_ref[...] * x).astype(jnp.bfloat16)
    ending = expand_heads(
        jnp.exp(l_small[BLOCK - 1 : BLOCK, :] - l_small) * dt_small * end_col, head_width
    )
    weighted = (x * ending).astype(jnp.bfloat16)
    state_ref[...] = decay_ref[0] * state + lax.dot_general(
        b_ref[...], weighted, (((0,), (0,)), ((), ())), preferred_element_type=jnp.float32
    )


def causal_conv(raw, prev, taps, bias, info):
    top_row = lax.broadcasted_iota(jnp.int32, prev.shape, 0)
    summed = jnp.zeros(raw.shape, jnp.float32) + bias
    for offset in range(4):
        back = 3 - offset
        if back == 0:
            window = raw
        else:
            rolled = pltpu.roll(raw, back, 0)
            top = jnp.where(top_row < back, pltpu.roll(prev, back, 0), rolled[:8])
            window = jnp.concatenate([top, rolled[8:]], 0) * info[:, 1 + back : 2 + back]
        summed = summed + taps[offset : offset + 1, :] * window
    return jax.nn.silu(summed).astype(jnp.bfloat16)


def state_kernel(head_width, x_ref, tail_ref, wconv_ref, bias_ref, own_ref, other_ref, ownx_ref,
                 otherx_ref, dt_ref, rate_ref, info_ref, state_ref, l_ref, dtt_ref,
                 decay_ref, total_ref, xc_ref, bo_ref, co_ref, sent_ref, prefix_ref, ltile_ref,
                 prev_ref, bcprev_ref, small_ref):
    blk = pl.program_id(0)

    @pl.when(blk == 0)
    def _():
        state_ref[...] = jnp.zeros(state_ref.shape, jnp.float32)
        total_ref[...] = jnp.ones(total_ref.shape, jnp.float32)
        prev_ref[...] = tail_ref[:, : x_ref.shape[1]].astype(jnp.float32)
        small_ref[...] = jnp.ones(small_ref.shape, jnp.float32)
        bcprev_ref[0] = ownx_ref[:, 0:8, :]
        bcprev_ref[1] = otherx_ref[:, 0:8, :]

    info = info_ref[...]
    raw = x_ref[...].astype(jnp.float32)
    xc = causal_conv(raw, prev_ref[...], wconv_ref[...].astype(jnp.float32), bias_ref[...], info)
    prev_ref[...] = raw[BLOCK - 8 :]
    xc_ref[...] = xc
    lower = info_ref[0:1, 5:6] > 0.5
    convolved = []
    for which in range(2):
        halves = []
        for side, (raw_ref, extra_ref) in enumerate(((own_ref, ownx_ref), (other_ref, otherx_ref))):
            raw_bc = raw_ref[which].astype(jnp.float32)
            extra = extra_ref[which]
            halves.append(
                causal_conv(raw_bc, bcprev_ref[side, which], extra[8:12], extra[12:13], info)
            )
            bcprev_ref[side, which] = raw_bc[BLOCK - 8 :]
        convolved.append(jnp.where(
            lower, jnp.concatenate(halves, 1), jnp.concatenate(halves[::-1], 1)
        ))
    b_mat, c_mat = convolved
    bo_ref[...] = b_mat
    co_ref[...] = c_mat

    rows = lax.broadcasted_iota(jnp.int32, (2 * BLOCK, BLOCK), 0)
    cols = lax.broadcasted_iota(jnp.int32, (2 * BLOCK, BLOCK), 1)
    picker = jnp.where(
        ((rows < BLOCK) & (rows >= cols)) | (rows - BLOCK == cols), 1.0, 0.0
    ).astype(jnp.bfloat16)
    rest = dt_ref[...]
    cum = None
    for _ in range(3):
        piece = rest.astype(jnp.bfloat16)
        part = lax.dot_general(
            picker, piece, (((1,), (1,)), ((), ())), preferred_element_type=jnp.float32
        )
        cum = part if cum is None else cum + part
        rest = rest - piece.astype(jnp.float32)
    l_small = -cum[:BLOCK] * rate_ref[...]
    dt_small = cum[BLOCK:]
    l_ref[...] = l_small
    dtt_ref[...] = dt_small
    seg_col = info[:, 0:1]
    end_col = (seg_col == seg_col[BLOCK - 1 : BLOCK, :]).astype(jnp.float32)
    decay_x = expand_heads(
        jnp.exp(l_small[BLOCK - 1 : BLOCK, :]) * info[BLOCK - 1 : BLOCK, 1:2], head_width
    )
    decay_ref[0] = decay_x
    prefix_ref[0] = total_ref[...]
    total_ref[...] = total_ref[...] * decay_x
    carry = (jnp.exp(l_small) * info[:, 1:2]) * small_ref[...]
    small_ref[...] = small_ref[...] * (
        jnp.exp(l_small[BLOCK - 1 : BLOCK, :]) * info[BLOCK - 1 : BLOCK, 1:2]
    )
    tile_heads = ltile_ref.shape[2]
    for tile in range(ltile_ref.shape[0]):
        ltile_ref[tile] = carry[:, tile * tile_heads : (tile + 1) * tile_heads]
    ending = expand_heads(
        jnp.exp(l_small[BLOCK - 1 : BLOCK, :] - l_small) * dt_small * end_col, head_width
    )
    weighted = (xc.astype(jnp.float32) * ending).astype(jnp.bfloat16)
    new_state = decay_x * state_ref[...] + lax.dot_general(
        b_mat, weighted, (((0,), (0,)), ((), ())), preferred_element_type=jnp.float32
    )
    state_ref[...] = new_state

    @pl.when(blk == pl.num_programs(0) - 1)
    def _():
        sent_ref[...] = new_state.astype(jnp.bfloat16)


def run_state(x, tails, wconv, bias_row, own_raw, other_raw, own_extra, other_extra,
              step_size, rate_row, info):
    rows, width = x.shape
    head_count = step_size.shape[0]
    half = own_raw.shape[2]
    n_size = 2 * half
    block_count = rows // BLOCK
    tiles = width // CORRECT_TILE
    tile_heads = head_count // tiles
    row_block = lambda cols: pl.BlockSpec((BLOCK, cols), lambda b: (b, 0))
    whole = lambda shape: pl.BlockSpec(shape, lambda b: (0,) * len(shape))
    return pl.pallas_call(
        functools.partial(state_kernel, width // head_count),
        grid=(block_count,),
        in_specs=[row_block(width), whole(tails.shape), whole((4, width)), whole((1, width)),
                  pl.BlockSpec((2, BLOCK, half), lambda b: (0, b, 0)),
                  pl.BlockSpec((2, BLOCK, half), lambda b: (0, b, 0)),
                  whole(own_extra.shape), whole(own_extra.shape),
                  pl.BlockSpec((head_count, BLOCK), lambda b: (0, b)),
                  whole((1, head_count)), row_block(info.shape[1])],
        out_specs=[whole((n_size, width)), row_block(head_count), row_block(head_count),
                   pl.BlockSpec((1, 1, width), lambda b: (b, 0, 0)), whole((1, width)),
                   row_block(width), row_block(n_size), row_block(n_size),
                   whole((n_size, width)), pl.BlockSpec((1, 1, width), lambda b: (b, 0, 0)),
                   pl.BlockSpec((tiles, BLOCK, tile_heads), lambda b: (0, b, 0))],
        out_shape=[jax.ShapeDtypeStruct((n_size, width), jnp.float32),
                   jax.ShapeDtypeStruct((rows, head_count), jnp.float32),
                   jax.ShapeDtypeStruct((rows, head_count), jnp.float32),
                   jax.ShapeDtypeStruct((block_count, 1, width), jnp.float32),
                   jax.ShapeDtypeStruct((1, width), jnp.float32),
                   jax.ShapeDtypeStruct((rows, width), jnp.bfloat16),
                   jax.ShapeDtypeStruct((rows, n_size), jnp.bfloat16),
                   jax.ShapeDtypeStruct((rows, n_size), jnp.bfloat16),
                   jax.ShapeDtypeStruct((n_size, width), jnp.bfloat16),
                   jax.ShapeDtypeStruct((block_count, 1, width), jnp.float32),
                   jax.ShapeDtypeStruct((tiles, rows, tile_heads), jnp.float32)],
        scratch_shapes=[pltpu.VMEM((8, width), jnp.float32),
                        pltpu.VMEM((2, 2, 8, half), jnp.float32),
                        pltpu.VMEM((1, head_count), jnp.float32)],
        compiler_params=pltpu.CompilerParams(dimension_semantics=("arbitrary",)),
    )(x, tails, wconv, bias_row, own_raw, other_raw, own_extra, other_extra, step_size,
      rate_row, info)


def partial_kernel(head_width, from_zero, *refs):
    if from_zero:
        (x_ref, b_ref, c_ref, l_ref, dt_ref, segr_ref, info_ref, decay_ref, skip_ref, out_ref,
         end_ref, state_ref) = refs
    else:
        (x_ref, b_ref, c_ref, l_ref, dt_ref, segr_ref, info_ref, decay_ref, skip_ref, init_ref,
         after_ref, out_ref, state_ref) = refs
    blk = pl.program_id(0)

    @pl.when(blk == 0)
    def _():
        if from_zero:
            state_ref[...] = jnp.zeros(state_ref.shape, jnp.float32)
        else:
            state_ref[...] = init_ref[...]

    info = info_ref[...]
    seg_col = info[:, 0:1]
    end_col = (seg_col == seg_col[BLOCK - 1 : BLOCK, :]).astype(jnp.float32)
    l_small = l_ref[...]
    dt_small = dt_ref[...]
    x = x_ref[...].astype(jnp.float32)
    state = state_ref[...]
    c_mat = c_ref[...]
    b_mat = b_ref[...]
    scores = lax.dot_general(
        c_mat, b_mat, (((1,), (1,)), ((), ())), preferred_element_type=jnp.float32
    )
    rows = lax.broadcasted_iota(jnp.int32, (BLOCK, BLOCK), 0)
    cols = lax.broadcasted_iota(jnp.int32, (BLOCK, BLOCK), 1)
    allowed = (rows >= cols) & (seg_col == segr_ref[...])
    masked = jnp.where(allowed, scores, 0.0).astype(jnp.bfloat16)
    rising = expand_heads(jnp.exp(l_small), head_width)
    falling = expand_heads(jnp.exp(-l_small) * dt_small, head_width)
    intra = split_dot(masked, x * falling) * rising
    inter = split_dot(c_mat, state) * (rising * info[:, 1:2])
    out_ref[...] = intra + inter + skip_ref[...] * x
    last = blk == pl.num_programs(0) - 1

    @pl.when(jnp.logical_or(jnp.logical_not(last), from_zero))
    def _():
        ending = expand_heads(
            jnp.exp(l_small[BLOCK - 1 : BLOCK, :] - l_small) * dt_small * end_col, head_width
        )
        weighted = (x * ending).astype(jnp.bfloat16)
        new_state = decay_ref[0] * state + lax.dot_general(
            b_mat, weighted, (((0,), (0,)), ((), ())), preferred_element_type=jnp.float32
        )
        state_ref[...] = new_state
        if from_zero:

            @pl.when(last)
            def _():
                end_ref[...] = new_state


def run_partial(first, count, x, b_full, c_full, l_t, dt_t, seg_row, info, decay_x, skip_x,
                init=None, after=None):
    rows, width = x.shape
    head_count = l_t.shape[1]
    n_size = b_full.shape[1]
    row_block = lambda cols: pl.BlockSpec((BLOCK, cols), lambda b: (b + first, 0))
    whole = lambda shape: pl.BlockSpec(shape, lambda b: (0,) * len(shape))
    from_zero = init is None
    in_specs = [row_block(width), row_block(n_size), row_block(n_size), row_block(head_count),
                row_block(head_count), pl.BlockSpec((1, BLOCK), lambda b: (0, b + first)),
                row_block(info.shape[1]), pl.BlockSpec((1, 1, width), lambda b: (b + first, 0, 0)),
                whole((1, width))]
    args = [x, b_full, c_full, l_t, dt_t, seg_row, info, decay_x, skip_x]
    if not from_zero:
        in_specs += [whole((n_size, width)), pl.BlockSpec(memory_space=pl.ANY)]
        args += [init, after]
    out_specs = [pl.BlockSpec((BLOCK, width), lambda b: (b, 0))]
    out_shape = [jax.ShapeDtypeStruct((count * BLOCK, width), jnp.float32)]
    if from_zero:
        out_specs.append(whole((n_size, width)))
        out_shape.append(jax.ShapeDtypeStruct((n_size, width), jnp.float32))
    return pl.pallas_call(
        functools.partial(partial_kernel, width // head_count, from_zero),
        grid=(count,),
        in_specs=in_specs,
        out_specs=out_specs,
        out_shape=out_shape,
        scratch_shapes=[pltpu.VMEM((n_size, width), jnp.float32)],
        compiler_params=pltpu.CompilerParams(dimension_semantics=("arbitrary",)),
    )(*args)


def correct_kernel(head_width, y_ref, z_ref, c_ref, g_ref, ein_ref, out_ref):
    factor = expand_heads(g_ref[0], head_width)
    carried = jnp.dot(c_ref[...], ein_ref[...], preferred_element_type=jnp.float32)
    split = y_ref.shape[0]
    out_ref[:split] = (y_ref[...] + carried[:split] * factor[:split]).astype(jnp.bfloat16)
    out_ref[split:] = (z_ref[...] + carried[split:] * factor[split:]).astype(jnp.bfloat16)


def run_correct(first, second, c_full, g_tiles, entering):
    rows = first.shape[0] + second.shape[0]
    width = first.shape[1]
    tiles, _, heads_per = g_tiles.shape
    tile = CORRECT_TILE
    head_width = tile // heads_per
    n_size = c_full.shape[1]
    return pl.pallas_call(
        functools.partial(correct_kernel, head_width),
        grid=(tiles,),
        in_specs=[pl.BlockSpec((first.shape[0], tile), lambda j: (0, j)),
                  pl.BlockSpec((second.shape[0], tile), lambda j: (0, j)),
                  pl.BlockSpec((rows, n_size), lambda j: (0, 0)),
                  pl.BlockSpec((1, rows, heads_per), lambda j: (j, 0, 0)),
                  pl.BlockSpec((n_size, tile), lambda j: (0, j))],
        out_specs=pl.BlockSpec((rows, tile), lambda j: (0, j)),
        out_shape=jax.ShapeDtypeStruct((rows, width), jnp.bfloat16),
        compiler_params=pltpu.CompilerParams(dimension_semantics=("arbitrary",)),
    )(first, second, c_full, g_tiles, entering)


def run_blocks(with_y, x, b_full, c_full, l_t, dt_t, seg_row, seg_col, entry_col, decay_x,
               skip_x, entering):
    rows, width = x.shape
    head_count = l_t.shape[1]
    head_width = width // head_count
    n_size = b_full.shape[1]
    block_count = rows // BLOCK
    row_block = lambda cols: pl.BlockSpec((BLOCK, cols), lambda b: (b, 0))
    bt_spec = pl.BlockSpec((n_size, BLOCK), lambda b: (0, b))
    decay_spec = pl.BlockSpec((1, 1, width), lambda b: (b, 0, 0))
    state_spec = pl.BlockSpec((n_size, width), lambda b: (0, 0))
    state_shape = jax.ShapeDtypeStruct((n_size, width), jnp.float32)
    kernel = functools.partial(block_kernel, with_y, head_width)
    params = pltpu.CompilerParams(dimension_semantics=("arbitrary",))
    if with_y:
        return pl.pallas_call(
            kernel,
            grid=(block_count,),
            in_specs=[row_block(width), row_block(n_size), row_block(n_size),
                      row_block(head_count), row_block(head_count),
                      pl.BlockSpec((1, BLOCK), lambda b: (0, b)), row_block(seg_col.shape[1]),
                      decay_spec, pl.BlockSpec((1, width), lambda b: (0, 0)), state_spec],
            out_specs=row_block(width),
            out_shape=jax.ShapeDtypeStruct((rows, width), jnp.bfloat16),
            scratch_shapes=[pltpu.VMEM((n_size, width), jnp.float32)],
            compiler_params=params,
        )(x, b_full, c_full, l_t, dt_t, seg_row, seg_col, decay_x, skip_x, entering)
    return pl.pallas_call(
        kernel,
        grid=(block_count,),
        in_specs=[row_block(width), bt_spec, row_block(head_count), row_block(head_count),
                  row_block(1), decay_spec],
        out_specs=state_spec,
        out_shape=state_shape,
        compiler_params=params,
    )(x, b_t, l_t, dt_t, seg_col, decay_x)


def body(
    inner_input,
    state_input,
    conv_inner,
    bias_inner,
    conv_state,
    bias_state,
    step_size,
    decay_rate,
    skip_gain,
    lengths,
):
    own_rows = inner_input.shape[0]
    head_count = decay_rate.shape[0]
    group_half = state_input.shape[2]
    block_count = own_rows // BLOCK
    positions = lax.axis_index("seq") * own_rows + jnp.arange(own_rows + 3, dtype=jnp.int32) - 3
    seg_ext = segment_of(lengths, positions)
    width = inner_input.shape[1]
    tails = jnp.concatenate(
        [inner_input[-8:], jnp.transpose(state_input[:, -8:], (1, 0, 2)).reshape(8, -1)], 1
    )
    tails = shifted(tails, "seq", 1)
    state_tail = tails[:, width:].reshape(8, 2, group_half)
    extra = jnp.concatenate(
        [jnp.transpose(state_tail, (1, 0, 2)).astype(jnp.float32),
         conv_state.astype(jnp.float32), bias_state[:, None, :]],
        1,
    )
    partner_raw, partner_extra = from_partner((state_input, extra), "head", 0)
    lower_half = (lax.axis_index("head") % 2 == 0).astype(jnp.float32)
    head_width = inner_input.shape[1] // head_count
    spread = lambda v: jnp.repeat(v, head_width, axis=-1)
    skip_x = spread(skip_gain).reshape(1, -1)
    seg_own = seg_ext[3:].reshape(block_count, BLOCK)
    seg_prev = seg_ext[2 : 2 + own_rows].reshape(block_count, BLOCK)[:, 0]
    seg_row = seg_ext[3:].reshape(1, own_rows).astype(jnp.float32)
    own_seg = seg_ext[3:]
    entry_col = (seg_own == seg_prev[:, None]).reshape(own_rows)
    keeps = [(seg_ext[3 - back : 3 - back + own_rows] == own_seg) for back in (1, 2, 3)]
    columns = [own_seg.astype(jnp.float32), entry_col.astype(jnp.float32)]
    columns += [keep.astype(jnp.float32) for keep in keeps]
    columns += [jnp.zeros((own_rows,), jnp.float32), jnp.full((own_rows,), lower_half, jnp.float32)]
    column_id = lax.broadcasted_iota(jnp.int32, (own_rows, 8), 1)
    info = jnp.zeros((own_rows, 8), jnp.float32)
    for place, column in enumerate(columns):
        info = jnp.where(column_id == place, column[:, None], info)

    (local_end, l_t, dt_t, decay_x, total_decay, inner_conv, b_full, c_full, end_sent,
     prefix_x, g_tiles) = run_state(
        inner_input, tails, conv_inner, bias_inner.reshape(1, -1), state_input, partner_raw,
        extra, partner_extra,
        step_size, decay_rate.reshape(1, -1), info
    )

    def relay(step_num, incoming):
        return shifted(
            (total_decay * incoming.astype(jnp.float32) + local_end).astype(jnp.bfloat16), "seq", 1
        )

    part_rows = own_rows * lax.axis_size("seq")
    hops = min(lax.axis_size("seq") - 1, -(-(part_rows // 2) // own_rows))
    half_blocks = block_count // 2
    operands = (inner_conv, b_full, c_full, l_t, dt_t, seg_row, info, decay_x, skip_x)
    incoming = shifted(end_sent, "seq", 1)
    partial, middle = run_partial(0, half_blocks, *operands)
    incoming, partial, middle = lax.optimization_barrier((incoming, partial, middle))
    first_hop = incoming
    for step_num in range(1, hops):
        incoming = relay(step_num, incoming)
    (second,) = run_partial(
        half_blocks, block_count - half_blocks, *operands, init=middle, after=first_hop
    )
    return run_correct(partial, second, c_full, g_tiles, incoming)


def solution(mesh):
    return jax.shard_map(
        body,
        mesh=mesh,
        in_specs=(
            P(("grp", "seq"), "head"),
            P(None, ("grp", "seq"), "head"),
            P(None, "head"),
            P("head"),
            P(None, None, "head"),
            P(None, "head"),
            P("head", ("grp", "seq")),
            P("head"),
            P("head"),
            P("grp"),
        ),
        out_specs=P(("grp", "seq"), "head"),
        check_vma=False,
    )
```

```python
import functools

import jax
import jax.numpy as jnp
from jax import lax
from jax.experimental import pallas as pl
from jax.experimental.pallas import tpu as pltpu
from jax.sharding import PartitionSpec as P

BLOCK = 128
CORRECT_TILE = 256


def shifted(value, axis, steps):
    count = lax.axis_size(axis)
    initial, last = (max(0, -steps), min(count, count - steps))
    return lax.ppermute(value, axis, [(source, source + steps) for source in range(initial, last)])


def from_partner(block, axis, stride):
    count = lax.axis_size(axis)
    route = []
    for low in range(count):
        high = low | 1 << stride
        if high != low and high < count:
            route += [(low, high), (high, low)]
    return lax.ppermute(block, axis, route)


def segment_of(lengths, positions):
    starts = jnp.cumsum(lengths, dtype=jnp.int32) - lengths
    covered = (starts[None, :] <= positions[:, None]).astype(jnp.int32)
    return jnp.sum(covered, axis=1, dtype=jnp.int32) - 1


def convolve(extended, weight, bias_row, seg_ext, row_count):
    own_seg = seg_ext[3:]
    summed = (
        jnp.zeros(extended.shape[:-2] + (row_count, extended.shape[-1]), jnp.float32) + bias_row
    )
    for offset in range(4):
        kept_mask = (seg_ext[offset : offset + row_count] == own_seg).astype(jnp.float32)[:, None]
        window = extended[..., offset : offset + row_count, :].astype(jnp.float32)
        summed = summed + weight[offset].astype(jnp.float32) * window * kept_mask
    return jax.nn.silu(summed).astype(jnp.bfloat16)


def split_dot(lhs, value):
    high = value.astype(jnp.bfloat16)
    low = (value - high.astype(jnp.float32)).astype(jnp.bfloat16)
    return jnp.dot(lhs, high, preferred_element_type=jnp.float32) + jnp.dot(
        lhs, low, preferred_element_type=jnp.float32
    )


def expand_heads(small, head_width):
    rows, heads = small.shape
    width = heads * head_width
    owner = lax.broadcasted_iota(jnp.int32, (heads, width), 1) // head_width
    spread = (owner == lax.broadcasted_iota(jnp.int32, (heads, width), 0)).astype(jnp.float32)
    spread = spread.astype(jnp.bfloat16)
    rest = small
    out = None
    for _ in range(3):
        piece = rest.astype(jnp.bfloat16)
        part = jnp.dot(piece, spread, preferred_element_type=jnp.float32)
        out = part if out is None else out + part
        rest = rest - piece.astype(jnp.float32)
    return out


def block_kernel(with_y, head_width, *refs):
    if with_y:
        (x_ref, b_ref, c_ref, l_ref, dt_ref, segr_ref, info_ref, decay_ref,
         skip_ref, ein_ref, out_ref, state_ref) = refs
    else:
        (x_ref, b_ref, l_ref, dt_ref, segc_ref, decay_ref, state_ref) = refs
    blk = pl.program_id(0)

    @pl.when(blk == 0)
    def _():
        if with_y:
            state_ref[...] = ein_ref[...].astype(jnp.float32)
        else:
            state_ref[...] = jnp.zeros(state_ref.shape, jnp.float32)

    info = info_ref[...]
    seg_col = info[:, 0:1]
    end_col = (seg_col == seg_col[BLOCK - 1 : BLOCK, :]).astype(jnp.float32)
    l_small = l_ref[...]
    dt_small = dt_ref[...]
    x = x_ref[...].astype(jnp.float32)
    state = state_ref[...]
    if with_y:
        c_mat = c_ref[...]
        seg_row = segr_ref[...]
        scores = lax.dot_general(
            c_mat, b_ref[...], (((1,), (1,)), ((), ())), preferred_element_type=jnp.float32
        )
        rows = lax.broadcasted_iota(jnp.int32, (BLOCK, BLOCK), 0)
        cols = lax.broadcasted_iota(jnp.int32, (BLOCK, BLOCK), 1)
        allowed = (rows >= cols) & (seg_col == seg_row)
        masked = jnp.where(allowed, scores, 0.0).astype(jnp.bfloat16)
        rising = expand_heads(jnp.exp(l_small), head_width)
        falling = expand_heads(jnp.exp(-l_small) * dt_small, head_width)
        intra = split_dot(masked, x * falling) * rising
        inter = split_dot(c_mat, state) * (rising * info[:, 1:2])
        out_ref[...] = (intra + inter + skip_ref[...] * x).astype(jnp.bfloat16)
    ending = expand_heads(
        jnp.exp(l_small[BLOCK - 1 : BLOCK, :] - l_small) * dt_small * end_col, head_width
    )
    weighted = (x * ending).astype(jnp.bfloat16)
    state_ref[...] = decay_ref[0] * state + lax.dot_general(
        b_ref[...], weighted, (((0,), (0,)), ((), ())), preferred_element_type=jnp.float32
    )


def causal_conv(raw, prev, taps, bias, info):
    top_row = lax.broadcasted_iota(jnp.int32, prev.shape, 0)
    summed = jnp.zeros(raw.shape, jnp.float32) + bias
    for offset in range(4):
        back = 3 - offset
        if back == 0:
            window = raw
        else:
            rolled = pltpu.roll(raw, back, 0)
            top = jnp.where(top_row < back, pltpu.roll(prev, back, 0), rolled[:8])
            window = jnp.concatenate([top, rolled[8:]], 0) * info[:, 1 + back : 2 + back]
        summed = summed + taps[offset : offset + 1, :] * window
    return jax.nn.silu(summed).astype(jnp.bfloat16)


def state_kernel(head_width, x_ref, tail_ref, wconv_ref, bias_ref, own_ref, other_ref, ownx_ref,
                 otherx_ref, dt_ref, rate_ref, info_ref, state_ref, l_ref, dtt_ref,
                 decay_ref, total_ref, xc_ref, bo_ref, co_ref, sent_ref, prefix_ref, ltile_ref,
                 prev_ref, bcprev_ref, small_ref):
    blk = pl.program_id(0)

    @pl.when(blk == 0)
    def _():
        state_ref[...] = jnp.zeros(state_ref.shape, jnp.float32)
        total_ref[...] = jnp.ones(total_ref.shape, jnp.float32)
        prev_ref[...] = tail_ref[:, : x_ref.shape[1]].astype(jnp.float32)
        small_ref[...] = jnp.ones(small_ref.shape, jnp.float32)
        bcprev_ref[0] = ownx_ref[:, 0:8, :]
        bcprev_ref[1] = otherx_ref[:, 0:8, :]

    info = info_ref[...]
    raw = x_ref[...].astype(jnp.float32)
    xc = causal_conv(raw, prev_ref[...], wconv_ref[...].astype(jnp.float32), bias_ref[...], info)
    prev_ref[...] = raw[BLOCK - 8 :]
    xc_ref[...] = xc
    lower = info_ref[0:1, 5:6] > 0.5
    convolved = []
    for which in range(2):
        halves = []
        for side, (raw_ref, extra_ref) in enumerate(((own_ref, ownx_ref), (other_ref, otherx_ref))):
            raw_bc = raw_ref[which].astype(jnp.float32)
            extra = extra_ref[which]
            halves.append(
                causal_conv(raw_bc, bcprev_ref[side, which], extra[8:12], extra[12:13], info)
            )
            bcprev_ref[side, which] = raw_bc[BLOCK - 8 :]
        convolved.append(jnp.where(
            lower, jnp.concatenate(halves, 1), jnp.concatenate(halves[::-1], 1)
        ))
    b_mat, c_mat = convolved
    bo_ref[...] = b_mat
    co_ref[...] = c_mat

    rows = lax.broadcasted_iota(jnp.int32, (2 * BLOCK, BLOCK), 0)
    cols = lax.broadcasted_iota(jnp.int32, (2 * BLOCK, BLOCK), 1)
    picker = jnp.where(
        ((rows < BLOCK) & (rows >= cols)) | (rows - BLOCK == cols), 1.0, 0.0
    ).astype(jnp.bfloat16)
    rest = dt_ref[...]
    cum = None
    for _ in range(3):
        piece = rest.astype(jnp.bfloat16)
        part = lax.dot_general(
            picker, piece, (((1,), (1,)), ((), ())), preferred_element_type=jnp.float32
        )
        cum = part if cum is None else cum + part
        rest = rest - piece.astype(jnp.float32)
    l_small = -cum[:BLOCK] * rate_ref[...]
    dt_small = cum[BLOCK:]
    l_ref[...] = l_small
    dtt_ref[...] = dt_small
    seg_col = info[:, 0:1]
    end_col = (seg_col == seg_col[BLOCK - 1 : BLOCK, :]).astype(jnp.float32)
    decay_x = expand_heads(
        jnp.exp(l_small[BLOCK - 1 : BLOCK, :]) * info[BLOCK - 1 : BLOCK, 1:2], head_width
    )
    decay_ref[0] = decay_x
    prefix_ref[0] = total_ref[...]
    total_ref[...] = total_ref[...] * decay_x
    carry = (jnp.exp(l_small) * info[:, 1:2]) * small_ref[...]
    small_ref[...] = small_ref[...] * (
        jnp.exp(l_small[BLOCK - 1 : BLOCK, :]) * info[BLOCK - 1 : BLOCK, 1:2]
    )
    tile_heads = ltile_ref.shape[2]
    for tile in range(ltile_ref.shape[0]):
        ltile_ref[tile] = carry[:, tile * tile_heads : (tile + 1) * tile_heads]
    ending = expand_heads(
        jnp.exp(l_small[BLOCK - 1 : BLOCK, :] - l_small) * dt_small * end_col, head_width
    )
    weighted = (xc.astype(jnp.float32) * ending).astype(jnp.bfloat16)
    new_state = decay_x * state_ref[...] + lax.dot_general(
        b_mat, weighted, (((0,), (0,)), ((), ())), preferred_element_type=jnp.float32
    )
    state_ref[...] = new_state

    @pl.when(blk == pl.num_programs(0) - 1)
    def _():
        sent_ref[...] = new_state.astype(jnp.bfloat16)


def run_state(x, tails, wconv, bias_row, own_raw, other_raw, own_extra, other_extra,
              step_size, rate_row, info):
    rows, width = x.shape
    head_count = step_size.shape[0]
    half = own_raw.shape[2]
    n_size = 2 * half
    block_count = rows // BLOCK
    tiles = width // CORRECT_TILE
    tile_heads = head_count // tiles
    row_block = lambda cols: pl.BlockSpec((BLOCK, cols), lambda b: (b, 0))
    whole = lambda shape: pl.BlockSpec(shape, lambda b: (0,) * len(shape))
    return pl.pallas_call(
        functools.partial(state_kernel, width // head_count),
        grid=(block_count,),
        in_specs=[row_block(width), whole(tails.shape), whole((4, width)), whole((1, width)),
                  pl.BlockSpec((2, BLOCK, half), lambda b: (0, b, 0)),
                  pl.BlockSpec((2, BLOCK, half), lambda b: (0, b, 0)),
                  whole(own_extra.shape), whole(own_extra.shape),
                  pl.BlockSpec((head_count, BLOCK), lambda b: (0, b)),
                  whole((1, head_count)), row_block(info.shape[1])],
        out_specs=[whole((n_size, width)), row_block(head_count), row_block(head_count),
                   pl.BlockSpec((1, 1, width), lambda b: (b, 0, 0)), whole((1, width)),
                   row_block(width), row_block(n_size), row_block(n_size),
                   whole((n_size, width)), pl.BlockSpec((1, 1, width), lambda b: (b, 0, 0)),
                   pl.BlockSpec((tiles, BLOCK, tile_heads), lambda b: (0, b, 0))],
        out_shape=[jax.ShapeDtypeStruct((n_size, width), jnp.float32),
                   jax.ShapeDtypeStruct((rows, head_count), jnp.float32),
                   jax.ShapeDtypeStruct((rows, head_count), jnp.float32),
                   jax.ShapeDtypeStruct((block_count, 1, width), jnp.float32),
                   jax.ShapeDtypeStruct((1, width), jnp.float32),
                   jax.ShapeDtypeStruct((rows, width), jnp.bfloat16),
                   jax.ShapeDtypeStruct((rows, n_size), jnp.bfloat16),
                   jax.ShapeDtypeStruct((rows, n_size), jnp.bfloat16),
                   jax.ShapeDtypeStruct((n_size, width), jnp.bfloat16),
                   jax.ShapeDtypeStruct((block_count, 1, width), jnp.float32),
                   jax.ShapeDtypeStruct((tiles, rows, tile_heads), jnp.float32)],
        scratch_shapes=[pltpu.VMEM((8, width), jnp.float32),
                        pltpu.VMEM((2, 2, 8, half), jnp.float32),
                        pltpu.VMEM((1, head_count), jnp.float32)],
        compiler_params=pltpu.CompilerParams(dimension_semantics=("arbitrary",)),
    )(x, tails, wconv, bias_row, own_raw, other_raw, own_extra, other_extra, step_size,
      rate_row, info)


def partial_kernel(head_width, from_zero, *refs):
    if from_zero:
        (x_ref, b_ref, c_ref, l_ref, dt_ref, segr_ref, info_ref, decay_ref, skip_ref, out_ref,
         end_ref, state_ref) = refs
    else:
        (x_ref, b_ref, c_ref, l_ref, dt_ref, segr_ref, info_ref, decay_ref, skip_ref, init_ref,
         after_ref, out_ref, state_ref) = refs
    blk = pl.program_id(0)

    @pl.when(blk == 0)
    def _():
        if from_zero:
            state_ref[...] = jnp.zeros(state_ref.shape, jnp.float32)
        else:
            state_ref[...] = init_ref[...]

    info = info_ref[...]
    seg_col = info[:, 0:1]
    end_col = (seg_col == seg_col[BLOCK - 1 : BLOCK, :]).astype(jnp.float32)
    l_small = l_ref[...]
    dt_small = dt_ref[...]
    x = x_ref[...].astype(jnp.float32)
    state = state_ref[...]
    c_mat = c_ref[...]
    b_mat = b_ref[...]
    scores = lax.dot_general(
        c_mat, b_mat, (((1,), (1,)), ((), ())), preferred_element_type=jnp.float32
    )
    rows = lax.broadcasted_iota(jnp.int32, (BLOCK, BLOCK), 0)
    cols = lax.broadcasted_iota(jnp.int32, (BLOCK, BLOCK), 1)
    allowed = (rows >= cols) & (seg_col == segr_ref[...])
    masked = jnp.where(allowed, scores, 0.0).astype(jnp.bfloat16)
    rising = expand_heads(jnp.exp(l_small), head_width)
    falling = expand_heads(jnp.exp(-l_small) * dt_small, head_width)
    intra = split_dot(masked, x * falling) * rising
    inter = split_dot(c_mat, state) * (rising * info[:, 1:2])
    out_ref[...] = intra + inter + skip_ref[...] * x
    last = blk == pl.num_programs(0) - 1

    @pl.when(jnp.logical_or(jnp.logical_not(last), from_zero))
    def _():
        ending = expand_heads(
            jnp.exp(l_small[BLOCK - 1 : BLOCK, :] - l_small) * dt_small * end_col, head_width
        )
        weighted = (x * ending).astype(jnp.bfloat16)
        new_state = decay_ref[0] * state + lax.dot_general(
            b_mat, weighted, (((0,), (0,)), ((), ())), preferred_element_type=jnp.float32
        )
        state_ref[...] = new_state
        if from_zero:

            @pl.when(last)
            def _():
                end_ref[...] = new_state


def run_partial(first, count, x, b_full, c_full, l_t, dt_t, seg_row, info, decay_x, skip_x,
                init=None, after=None):
    rows, width = x.shape
    head_count = l_t.shape[1]
    n_size = b_full.shape[1]
    row_block = lambda cols: pl.BlockSpec((BLOCK, cols), lambda b: (b + first, 0))
    whole = lambda shape: pl.BlockSpec(shape, lambda b: (0,) * len(shape))
    from_zero = init is None
    in_specs = [row_block(width), row_block(n_size), row_block(n_size), row_block(head_count),
                row_block(head_count), pl.BlockSpec((1, BLOCK), lambda b: (0, b + first)),
                row_block(info.shape[1]), pl.BlockSpec((1, 1, width), lambda b: (b + first, 0, 0)),
                whole((1, width))]
    args = [x, b_full, c_full, l_t, dt_t, seg_row, info, decay_x, skip_x]
    if not from_zero:
        in_specs += [whole((n_size, width)), pl.BlockSpec(memory_space=pl.ANY)]
        args += [init, after]
    out_specs = [pl.BlockSpec((BLOCK, width), lambda b: (b, 0))]
    out_shape = [jax.ShapeDtypeStruct((count * BLOCK, width), jnp.float32)]
    if from_zero:
        out_specs.append(whole((n_size, width)))
        out_shape.append(jax.ShapeDtypeStruct((n_size, width), jnp.float32))
    return pl.pallas_call(
        functools.partial(partial_kernel, width // head_count, from_zero),
        grid=(count,),
        in_specs=in_specs,
        out_specs=out_specs,
        out_shape=out_shape,
        scratch_shapes=[pltpu.VMEM((n_size, width), jnp.float32)],
        compiler_params=pltpu.CompilerParams(dimension_semantics=("arbitrary",)),
    )(*args)


def correct_kernel(head_width, y_ref, z_ref, c_ref, g_ref, ein_ref, out_ref):
    factor = expand_heads(g_ref[0], head_width)
    carried = jnp.dot(c_ref[...], ein_ref[...], preferred_element_type=jnp.float32)
    split = y_ref.shape[0]
    out_ref[:split] = (y_ref[...] + carried[:split] * factor[:split]).astype(jnp.bfloat16)
    out_ref[split:] = (z_ref[...] + carried[split:] * factor[split:]).astype(jnp.bfloat16)


def run_correct(first, second, c_full, g_tiles, entering):
    rows = first.shape[0] + second.shape[0]
    width = first.shape[1]
    tiles, _, heads_per = g_tiles.shape
    tile = CORRECT_TILE
    head_width = tile // heads_per
    n_size = c_full.shape[1]
    return pl.pallas_call(
        functools.partial(correct_kernel, head_width),
        grid=(tiles,),
        in_specs=[pl.BlockSpec((first.shape[0], tile), lambda j: (0, j)),
                  pl.BlockSpec((second.shape[0], tile), lambda j: (0, j)),
                  pl.BlockSpec((rows, n_size), lambda j: (0, 0)),
                  pl.BlockSpec((1, rows, heads_per), lambda j: (j, 0, 0)),
                  pl.BlockSpec((n_size, tile), lambda j: (0, j))],
        out_specs=pl.BlockSpec((rows, tile), lambda j: (0, j)),
        out_shape=jax.ShapeDtypeStruct((rows, width), jnp.bfloat16),
        compiler_params=pltpu.CompilerParams(dimension_semantics=("arbitrary",)),
    )(first, second, c_full, g_tiles, entering)


def run_blocks(with_y, x, b_full, c_full, l_t, dt_t, seg_row, seg_col, entry_col, decay_x,
               skip_x, entering):
    rows, width = x.shape
    head_count = l_t.shape[1]
    head_width = width // head_count
    n_size = b_full.shape[1]
    block_count = rows // BLOCK
    row_block = lambda cols: pl.BlockSpec((BLOCK, cols), lambda b: (b, 0))
    bt_spec = pl.BlockSpec((n_size, BLOCK), lambda b: (0, b))
    decay_spec = pl.BlockSpec((1, 1, width), lambda b: (b, 0, 0))
    state_spec = pl.BlockSpec((n_size, width), lambda b: (0, 0))
    state_shape = jax.ShapeDtypeStruct((n_size, width), jnp.float32)
    kernel = functools.partial(block_kernel, with_y, head_width)
    params = pltpu.CompilerParams(dimension_semantics=("arbitrary",))
    if with_y:
        return pl.pallas_call(
            kernel,
            grid=(block_count,),
            in_specs=[row_block(width), row_block(n_size), row_block(n_size),
                      row_block(head_count), row_block(head_count),
                      pl.BlockSpec((1, BLOCK), lambda b: (0, b)), row_block(seg_col.shape[1]),
                      decay_spec, pl.BlockSpec((1, width), lambda b: (0, 0)), state_spec],
            out_specs=row_block(width),
            out_shape=jax.ShapeDtypeStruct((rows, width), jnp.bfloat16),
            scratch_shapes=[pltpu.VMEM((n_size, width), jnp.float32)],
            compiler_params=params,
        )(x, b_full, c_full, l_t, dt_t, seg_row, seg_col, decay_x, skip_x, entering)
    return pl.pallas_call(
        kernel,
        grid=(block_count,),
        in_specs=[row_block(width), bt_spec, row_block(head_count), row_block(head_count),
                  row_block(1), decay_spec],
        out_specs=state_spec,
        out_shape=state_shape,
        compiler_params=params,
    )(x, b_t, l_t, dt_t, seg_col, decay_x)


def body(
    inner_input,
    state_input,
    conv_inner,
    bias_inner,
    conv_state,
    bias_state,
    step_size,
    decay_rate,
    skip_gain,
    lengths,
):
    own_rows = inner_input.shape[0]
    head_count = decay_rate.shape[0]
    group_half = state_input.shape[2]
    block_count = own_rows // BLOCK
    positions = lax.axis_index("seq") * own_rows + jnp.arange(own_rows + 3, dtype=jnp.int32) - 3
    seg_ext = segment_of(lengths, positions)
    width = inner_input.shape[1]
    tails = jnp.concatenate(
        [inner_input[-8:], jnp.transpose(state_input[:, -8:], (1, 0, 2)).reshape(8, -1)], 1
    )
    tails = shifted(tails, "seq", 1)
    state_tail = tails[:, width:].reshape(8, 2, group_half)
    extra = jnp.concatenate(
        [jnp.transpose(state_tail, (1, 0, 2)).astype(jnp.float32),
         conv_state.astype(jnp.float32), bias_state[:, None, :]],
        1,
    )
    partner_raw, partner_extra = from_partner((state_input, extra), "head", 0)
    lower_half = (lax.axis_index("head") % 2 == 0).astype(jnp.float32)
    head_width = inner_input.shape[1] // head_count
    spread = lambda v: jnp.repeat(v, head_width, axis=-1)
    skip_x = spread(skip_gain).reshape(1, -1)
    seg_own = seg_ext[3:].reshape(block_count, BLOCK)
    seg_prev = seg_ext[2 : 2 + own_rows].reshape(block_count, BLOCK)[:, 0]
    seg_row = seg_ext[3:].reshape(1, own_rows).astype(jnp.float32)
    own_seg = seg_ext[3:]
    entry_col = (seg_own == seg_prev[:, None]).reshape(own_rows)
    keeps = [(seg_ext[3 - back : 3 - back + own_rows] == own_seg) for back in (1, 2, 3)]
    info = jnp.stack(
        [own_seg.astype(jnp.float32), entry_col.astype(jnp.float32)]
        + [keep.astype(jnp.float32) for keep in keeps]
        + [jnp.zeros((own_rows,), jnp.float32), jnp.full((own_rows,), lower_half, jnp.float32),
           jnp.zeros((own_rows,), jnp.float32)],
        1,
    )

    (local_end, l_t, dt_t, decay_x, total_decay, inner_conv, b_full, c_full, end_sent,
     prefix_x, g_tiles) = run_state(
        inner_input, tails, conv_inner, bias_inner.reshape(1, -1), state_input, partner_raw,
        extra, partner_extra,
        step_size, decay_rate.reshape(1, -1), info
    )

    def relay(step_num, incoming):
        return shifted(
            (total_decay * incoming.astype(jnp.float32) + local_end).astype(jnp.bfloat16), "seq", 1
        )

    part_rows = own_rows * lax.axis_size("seq")
    hops = min(lax.axis_size("seq") - 1, -(-(part_rows // 2) // own_rows))
    half_blocks = block_count // 2
    operands = (inner_conv, b_full, c_full, l_t, dt_t, seg_row, info, decay_x, skip_x)
    incoming = shifted(end_sent, "seq", 1)
    partial, middle = run_partial(0, half_blocks, *operands)
    incoming, partial, middle = lax.optimization_barrier((incoming, partial, middle))
    first_hop = incoming
    for step_num in range(1, hops):
        incoming = relay(step_num, incoming)
    (second,) = run_partial(
        half_blocks, block_count - half_blocks, *operands, init=middle, after=first_hop
    )
    return run_correct(partial, second, c_full, g_tiles, incoming)


def solution(mesh):
    return jax.shard_map(
        body,
        mesh=mesh,
        in_specs=(
            P(("grp", "seq"), "head"),
            P(None, ("grp", "seq"), "head"),
            P(None, "head"),
            P("head"),
            P(None, None, "head"),
            P(None, "head"),
            P("head", ("grp", "seq")),
            P("head"),
            P("head"),
            P("grp"),
        ),
        out_specs=P(("grp", "seq"), "head"),
        check_vma=False,
    )
```

```python
import functools

import jax
import jax.numpy as jnp
from jax import lax
from jax.experimental import pallas as pl
from jax.experimental.pallas import tpu as pltpu
from jax.sharding import PartitionSpec as P

BLOCK = 128
CORRECT_TILE = 256


def shifted(value, axis, steps):
    count = lax.axis_size(axis)
    initial, last = (max(0, -steps), min(count, count - steps))
    return lax.ppermute(value, axis, [(source, source + steps) for source in range(initial, last)])


def from_partner(block, axis, stride):
    count = lax.axis_size(axis)
    route = []
    for low in range(count):
        high = low | 1 << stride
        if high != low and high < count:
            route += [(low, high), (high, low)]
    return lax.ppermute(block, axis, route)


def segment_of(lengths, positions):
    starts = jnp.cumsum(lengths, dtype=jnp.int32) - lengths
    covered = (starts[None, :] <= positions[:, None]).astype(jnp.int32)
    return jnp.sum(covered, axis=1, dtype=jnp.int32) - 1


def convolve(extended, weight, bias_row, seg_ext, row_count):
    own_seg = seg_ext[3:]
    summed = (
        jnp.zeros(extended.shape[:-2] + (row_count, extended.shape[-1]), jnp.float32) + bias_row
    )
    for offset in range(4):
        kept_mask = (seg_ext[offset : offset + row_count] == own_seg).astype(jnp.float32)[:, None]
        window = extended[..., offset : offset + row_count, :].astype(jnp.float32)
        summed = summed + weight[offset].astype(jnp.float32) * window * kept_mask
    return jax.nn.silu(summed).astype(jnp.bfloat16)


def split_dot(lhs, value):
    high = value.astype(jnp.bfloat16)
    low = (value - high.astype(jnp.float32)).astype(jnp.bfloat16)
    return jnp.dot(lhs, high, preferred_element_type=jnp.float32) + jnp.dot(
        lhs, low, preferred_element_type=jnp.float32
    )


def expand_heads(small, head_width):
    rows, heads = small.shape
    per_tile = 128 // head_width
    lane = lax.broadcasted_iota(jnp.int32, (rows, 128), 1) // head_width
    tiles = []
    for tile in range(heads // per_tile):
        picked = jnp.broadcast_to(small[:, tile * per_tile : tile * per_tile + 1], (rows, 128))
        for k in range(1, per_tile):
            column = small[:, tile * per_tile + k : tile * per_tile + k + 1]
            picked = jnp.where(lane == k, jnp.broadcast_to(column, (rows, 128)), picked)
        tiles.append(picked)
    return jnp.concatenate(tiles, axis=1)


def block_kernel(with_y, head_width, *refs):
    if with_y:
        (x_ref, b_ref, c_ref, l_ref, dt_ref, segr_ref, info_ref, decay_ref,
         skip_ref, ein_ref, out_ref, state_ref) = refs
    else:
        (x_ref, b_ref, l_ref, dt_ref, segc_ref, decay_ref, state_ref) = refs
    blk = pl.program_id(0)

    @pl.when(blk == 0)
    def _():
        if with_y:
            state_ref[...] = ein_ref[...].astype(jnp.float32)
        else:
            state_ref[...] = jnp.zeros(state_ref.shape, jnp.float32)

    info = info_ref[...]
    seg_col = info[:, 0:1]
    end_col = (seg_col == seg_col[BLOCK - 1 : BLOCK, :]).astype(jnp.float32)
    l_small = l_ref[...]
    dt_small = dt_ref[...]
    x = x_ref[...].astype(jnp.float32)
    state = state_ref[...]
    if with_y:
        c_mat = c_ref[...]
        seg_row = segr_ref[...]
        scores = lax.dot_general(
            c_mat, b_ref[...], (((1,), (1,)), ((), ())), preferred_element_type=jnp.float32
        )
        rows = lax.broadcasted_iota(jnp.int32, (BLOCK, BLOCK), 0)
        cols = lax.broadcasted_iota(jnp.int32, (BLOCK, BLOCK), 1)
        allowed = (rows >= cols) & (seg_col == seg_row)
        masked = jnp.where(allowed, scores, 0.0).astype(jnp.bfloat16)
        rising = expand_heads(jnp.exp(l_small), head_width)
        falling = expand_heads(jnp.exp(-l_small) * dt_small, head_width)
        intra = split_dot(masked, x * falling) * rising
        inter = split_dot(c_mat, state) * (rising * info[:, 1:2])
        out_ref[...] = (intra + inter + skip_ref[...] * x).astype(jnp.bfloat16)
    ending = expand_heads(
        jnp.exp(l_small[BLOCK - 1 : BLOCK, :] - l_small) * dt_small * end_col, head_width
    )
    weighted = (x * ending).astype(jnp.bfloat16)
    state_ref[...] = decay_ref[0] * state + lax.dot_general(
        b_ref[...], weighted, (((0,), (0,)), ((), ())), preferred_element_type=jnp.float32
    )


def causal_conv(raw, prev, taps, bias, info, masked):
    top_row = lax.broadcasted_iota(jnp.int32, prev.shape, 0)
    summed = jnp.zeros(raw.shape, jnp.float32) + bias
    for offset in range(4):
        back = 3 - offset
        if back == 0:
            window = raw
        else:
            rolled = pltpu.roll(raw, back, 0)
            top = jnp.where(top_row < back, pltpu.roll(prev, back, 0), rolled[:8])
            window = jnp.concatenate([top, rolled[8:]], 0)
            if masked:
                window = window * info[:, 1 + back : 2 + back]
        summed = summed + taps[offset : offset + 1, :] * window
    return jax.nn.silu(summed).astype(jnp.bfloat16)


def state_kernel(head_width, starts_ref, x_ref, tail_ref, wconv_ref, bias_ref, own_ref, other_ref,
                 ownx_ref, otherx_ref, dt_ref, rate_ref, info_ref, state_ref, l_ref, dtt_ref,
                 decay_ref, total_ref, xc_ref, bo_ref, co_ref, sent_ref, prefix_ref, ltile_ref,
                 prev_ref, bcprev_ref, small_ref):
    blk = pl.program_id(0)

    @pl.when(blk == 0)
    def _():
        state_ref[...] = jnp.zeros(state_ref.shape, jnp.float32)
        total_ref[...] = jnp.ones(total_ref.shape, jnp.float32)
        prev_ref[...] = tail_ref[:, : x_ref.shape[1]].astype(jnp.float32)
        small_ref[...] = jnp.ones(small_ref.shape, jnp.float32)
        bcprev_ref[0] = ownx_ref[:, 0:8, :]
        bcprev_ref[1] = otherx_ref[:, 0:8, :]

    info = info_ref[...]
    lower = info_ref[0:1, 5:6] > 0.5

    def convolve_block(masked):
        raw = x_ref[...].astype(jnp.float32)
        xc_ref[...] = causal_conv(
            raw, prev_ref[...], wconv_ref[...].astype(jnp.float32), bias_ref[...], info, masked
        )
        prev_ref[...] = raw[BLOCK - 8 :]
        outs = (bo_ref, co_ref)
        for which in range(2):
            halves = []
            pairs = ((own_ref, ownx_ref), (other_ref, otherx_ref))
            for side, (raw_ref, extra_ref) in enumerate(pairs):
                raw_bc = raw_ref[which].astype(jnp.float32)
                extra = extra_ref[which]
                halves.append(causal_conv(
                    raw_bc, bcprev_ref[side, which], extra[8:12], extra[12:13], info, masked
                ))
                bcprev_ref[side, which] = raw_bc[BLOCK - 8 :]
            outs[which][...] = jnp.where(
                lower, jnp.concatenate(halves, 1), jnp.concatenate(halves[::-1], 1)
            )

    @pl.when(starts_ref[blk] != 0)
    def _():
        convolve_block(True)

    @pl.when(starts_ref[blk] == 0)
    def _():
        convolve_block(False)

    xc = xc_ref[...]
    convolved = [bo_ref[...], co_ref[...]]
    b_mat, c_mat = convolved
    bo_ref[...] = b_mat
    co_ref[...] = c_mat

    rows = lax.broadcasted_iota(jnp.int32, (2 * BLOCK, BLOCK), 0)
    cols = lax.broadcasted_iota(jnp.int32, (2 * BLOCK, BLOCK), 1)
    picker = jnp.where(
        ((rows < BLOCK) & (rows >= cols)) | (rows - BLOCK == cols), 1.0, 0.0
    ).astype(jnp.bfloat16)
    rest = dt_ref[...]
    cum = None
    for _ in range(3):
        piece = rest.astype(jnp.bfloat16)
        part = lax.dot_general(
            picker, piece, (((1,), (1,)), ((), ())), preferred_element_type=jnp.float32
        )
        cum = part if cum is None else cum + part
        rest = rest - piece.astype(jnp.float32)
    l_small = -cum[:BLOCK] * rate_ref[...]
    dt_small = cum[BLOCK:]
    l_ref[...] = l_small
    dtt_ref[...] = dt_small
    seg_col = info[:, 0:1]
    end_col = (seg_col == seg_col[BLOCK - 1 : BLOCK, :]).astype(jnp.float32)
    decay_x = expand_heads(
        jnp.exp(l_small[BLOCK - 1 : BLOCK, :]) * info[BLOCK - 1 : BLOCK, 1:2], head_width
    )
    decay_ref[0] = decay_x
    prefix_ref[0] = total_ref[...]
    total_ref[...] = total_ref[...] * decay_x
    carry = (jnp.exp(l_small) * info[:, 1:2]) * small_ref[...]
    small_ref[...] = small_ref[...] * (
        jnp.exp(l_small[BLOCK - 1 : BLOCK, :]) * info[BLOCK - 1 : BLOCK, 1:2]
    )
    tile_heads = ltile_ref.shape[2]
    for tile in range(ltile_ref.shape[0]):
        ltile_ref[tile] = carry[:, tile * tile_heads : (tile + 1) * tile_heads]
    ending = expand_heads(
        jnp.exp(l_small[BLOCK - 1 : BLOCK, :] - l_small) * dt_small * end_col, head_width
    )
    weighted = (xc.astype(jnp.float32) * ending).astype(jnp.bfloat16)
    new_state = decay_x * state_ref[...] + lax.dot_general(
        b_mat, weighted, (((0,), (0,)), ((), ())), preferred_element_type=jnp.float32
    )
    state_ref[...] = new_state

    @pl.when(blk == pl.num_programs(0) - 1)
    def _():
        sent_ref[...] = new_state.astype(jnp.bfloat16)


def run_state(starts, x, tails, wconv, bias_row, own_raw, other_raw, own_extra, other_extra,
              step_size, rate_row, info):
    rows, width = x.shape
    head_count = step_size.shape[0]
    half = own_raw.shape[2]
    n_size = 2 * half
    block_count = rows // BLOCK
    tiles = width // CORRECT_TILE
    tile_heads = head_count // tiles
    row_block = lambda cols: pl.BlockSpec((BLOCK, cols), lambda b: (b, 0))
    whole = lambda shape: pl.BlockSpec(shape, lambda b: (0,) * len(shape))
    return pl.pallas_call(
        functools.partial(state_kernel, width // head_count),
        grid=(block_count,),
        in_specs=[pl.BlockSpec(memory_space=pltpu.SMEM),
                  row_block(width), whole(tails.shape), whole((4, width)), whole((1, width)),
                  pl.BlockSpec((2, BLOCK, half), lambda b: (0, b, 0)),
                  pl.BlockSpec((2, BLOCK, half), lambda b: (0, b, 0)),
                  whole(own_extra.shape), whole(own_extra.shape),
                  pl.BlockSpec((head_count, BLOCK), lambda b: (0, b)),
                  whole((1, head_count)), row_block(info.shape[1])],
        out_specs=[whole((n_size, width)), row_block(head_count), row_block(head_count),
                   pl.BlockSpec((1, 1, width), lambda b: (b, 0, 0)), whole((1, width)),
                   row_block(width), row_block(n_size), row_block(n_size),
                   whole((n_size, width)), pl.BlockSpec((1, 1, width), lambda b: (b, 0, 0)),
                   pl.BlockSpec((tiles, BLOCK, tile_heads), lambda b: (0, b, 0))],
        out_shape=[jax.ShapeDtypeStruct((n_size, width), jnp.float32),
                   jax.ShapeDtypeStruct((rows, head_count), jnp.float32),
                   jax.ShapeDtypeStruct((rows, head_count), jnp.float32),
                   jax.ShapeDtypeStruct((block_count, 1, width), jnp.float32),
                   jax.ShapeDtypeStruct((1, width), jnp.float32),
                   jax.ShapeDtypeStruct((rows, width), jnp.bfloat16),
                   jax.ShapeDtypeStruct((rows, n_size), jnp.bfloat16),
                   jax.ShapeDtypeStruct((rows, n_size), jnp.bfloat16),
                   jax.ShapeDtypeStruct((n_size, width), jnp.bfloat16),
                   jax.ShapeDtypeStruct((block_count, 1, width), jnp.float32),
                   jax.ShapeDtypeStruct((tiles, rows, tile_heads), jnp.float32)],
        scratch_shapes=[pltpu.VMEM((8, width), jnp.float32),
                        pltpu.VMEM((2, 2, 8, half), jnp.float32),
                        pltpu.VMEM((1, head_count), jnp.float32)],
        compiler_params=pltpu.CompilerParams(dimension_semantics=("arbitrary",)),
    )(starts, x, tails, wconv, bias_row, own_raw, other_raw, own_extra, other_extra, step_size,
      rate_row, info)


def partial_kernel(head_width, from_zero, *refs):
    if from_zero:
        (x_ref, b_ref, c_ref, l_ref, dt_ref, segr_ref, info_ref, decay_ref, skip_ref, out_ref,
         end_ref, state_ref) = refs
    else:
        (x_ref, b_ref, c_ref, l_ref, dt_ref, segr_ref, info_ref, decay_ref, skip_ref, init_ref,
         after_ref, out_ref, state_ref) = refs
    blk = pl.program_id(0)

    @pl.when(blk == 0)
    def _():
        if from_zero:
            state_ref[...] = jnp.zeros(state_ref.shape, jnp.float32)
        else:
            state_ref[...] = init_ref[...]

    info = info_ref[...]
    seg_col = info[:, 0:1]
    end_col = (seg_col == seg_col[BLOCK - 1 : BLOCK, :]).astype(jnp.float32)
    l_small = l_ref[...]
    dt_small = dt_ref[...]
    x = x_ref[...].astype(jnp.float32)
    state = state_ref[...]
    c_mat = c_ref[...]
    b_mat = b_ref[...]
    scores = lax.dot_general(
        c_mat, b_mat, (((1,), (1,)), ((), ())), preferred_element_type=jnp.float32
    )
    rows = lax.broadcasted_iota(jnp.int32, (BLOCK, BLOCK), 0)
    cols = lax.broadcasted_iota(jnp.int32, (BLOCK, BLOCK), 1)
    allowed = (rows >= cols) & (seg_col == segr_ref[...])
    masked = jnp.where(allowed, scores, 0.0).astype(jnp.bfloat16)
    rising = expand_heads(jnp.exp(l_small), head_width)
    falling = expand_heads(jnp.exp(-l_small) * dt_small, head_width)
    intra = split_dot(masked, x * falling) * rising
    inter = split_dot(c_mat, state) * (rising * info[:, 1:2])
    out_ref[...] = intra + inter + skip_ref[...] * x
    last = blk == pl.num_programs(0) - 1

    @pl.when(jnp.logical_or(jnp.logical_not(last), from_zero))
    def _():
        ending = expand_heads(
            jnp.exp(l_small[BLOCK - 1 : BLOCK, :] - l_small) * dt_small * end_col, head_width
        )
        weighted = (x * ending).astype(jnp.bfloat16)
        new_state = decay_ref[0] * state + lax.dot_general(
            b_mat, weighted, (((0,), (0,)), ((), ())), preferred_element_type=jnp.float32
        )
        state_ref[...] = new_state
        if from_zero:

            @pl.when(last)
            def _():
                end_ref[...] = new_state


def run_partial(first, count, x, b_full, c_full, l_t, dt_t, seg_row, info, decay_x, skip_x,
                init=None, after=None):
    rows, width = x.shape
    head_count = l_t.shape[1]
    n_size = b_full.shape[1]
    row_block = lambda cols: pl.BlockSpec((BLOCK, cols), lambda b: (b + first, 0))
    whole = lambda shape: pl.BlockSpec(shape, lambda b: (0,) * len(shape))
    from_zero = init is None
    in_specs = [row_block(width), row_block(n_size), row_block(n_size), row_block(head_count),
                row_block(head_count), pl.BlockSpec((1, BLOCK), lambda b: (0, b + first)),
                row_block(info.shape[1]), pl.BlockSpec((1, 1, width), lambda b: (b + first, 0, 0)),
                whole((1, width))]
    args = [x, b_full, c_full, l_t, dt_t, seg_row, info, decay_x, skip_x]
    if not from_zero:
        in_specs += [whole((n_size, width)), pl.BlockSpec(memory_space=pl.ANY)]
        args += [init, after]
    out_specs = [pl.BlockSpec((BLOCK, width), lambda b: (b, 0))]
    out_shape = [jax.ShapeDtypeStruct((count * BLOCK, width), jnp.float32)]
    if from_zero:
        out_specs.append(whole((n_size, width)))
        out_shape.append(jax.ShapeDtypeStruct((n_size, width), jnp.float32))
    return pl.pallas_call(
        functools.partial(partial_kernel, width // head_count, from_zero),
        grid=(count,),
        in_specs=in_specs,
        out_specs=out_specs,
        out_shape=out_shape,
        scratch_shapes=[pltpu.VMEM((n_size, width), jnp.float32)],
        compiler_params=pltpu.CompilerParams(dimension_semantics=("arbitrary",)),
    )(*args)


def correct_kernel(head_width, y_ref, z_ref, c_ref, g_ref, ein_ref, out_ref):
    factor = expand_heads(g_ref[0], head_width)
    carried = jnp.dot(c_ref[...], ein_ref[...], preferred_element_type=jnp.float32)
    split = y_ref.shape[0]
    out_ref[:split] = (y_ref[...] + carried[:split] * factor[:split]).astype(jnp.bfloat16)
    out_ref[split:] = (z_ref[...] + carried[split:] * factor[split:]).astype(jnp.bfloat16)


def run_correct(first, second, c_full, g_tiles, entering):
    rows = first.shape[0] + second.shape[0]
    width = first.shape[1]
    tiles, _, heads_per = g_tiles.shape
    tile = CORRECT_TILE
    head_width = tile // heads_per
    n_size = c_full.shape[1]
    return pl.pallas_call(
        functools.partial(correct_kernel, head_width),
        grid=(tiles,),
        in_specs=[pl.BlockSpec((first.shape[0], tile), lambda j: (0, j)),
                  pl.BlockSpec((second.shape[0], tile), lambda j: (0, j)),
                  pl.BlockSpec((rows, n_size), lambda j: (0, 0)),
                  pl.BlockSpec((1, rows, heads_per), lambda j: (j, 0, 0)),
                  pl.BlockSpec((n_size, tile), lambda j: (0, j))],
        out_specs=pl.BlockSpec((rows, tile), lambda j: (0, j)),
        out_shape=jax.ShapeDtypeStruct((rows, width), jnp.bfloat16),
        compiler_params=pltpu.CompilerParams(dimension_semantics=("arbitrary",)),
    )(first, second, c_full, g_tiles, entering)


def run_blocks(with_y, x, b_full, c_full, l_t, dt_t, seg_row, seg_col, entry_col, decay_x,
               skip_x, entering):
    rows, width = x.shape
    head_count = l_t.shape[1]
    head_width = width // head_count
    n_size = b_full.shape[1]
    block_count = rows // BLOCK
    row_block = lambda cols: pl.BlockSpec((BLOCK, cols), lambda b: (b, 0))
    bt_spec = pl.BlockSpec((n_size, BLOCK), lambda b: (0, b))
    decay_spec = pl.BlockSpec((1, 1, width), lambda b: (b, 0, 0))
    state_spec = pl.BlockSpec((n_size, width), lambda b: (0, 0))
    state_shape = jax.ShapeDtypeStruct((n_size, width), jnp.float32)
    kernel = functools.partial(block_kernel, with_y, head_width)
    params = pltpu.CompilerParams(dimension_semantics=("arbitrary",))
    if with_y:
        return pl.pallas_call(
            kernel,
            grid=(block_count,),
            in_specs=[row_block(width), row_block(n_size), row_block(n_size),
                      row_block(head_count), row_block(head_count),
                      pl.BlockSpec((1, BLOCK), lambda b: (0, b)), row_block(seg_col.shape[1]),
                      decay_spec, pl.BlockSpec((1, width), lambda b: (0, 0)), state_spec],
            out_specs=row_block(width),
            out_shape=jax.ShapeDtypeStruct((rows, width), jnp.bfloat16),
            scratch_shapes=[pltpu.VMEM((n_size, width), jnp.float32)],
            compiler_params=params,
        )(x, b_full, c_full, l_t, dt_t, seg_row, seg_col, decay_x, skip_x, entering)
    return pl.pallas_call(
        kernel,
        grid=(block_count,),
        in_specs=[row_block(width), bt_spec, row_block(head_count), row_block(head_count),
                  row_block(1), decay_spec],
        out_specs=state_spec,
        out_shape=state_shape,
        compiler_params=params,
    )(x, b_t, l_t, dt_t, seg_col, decay_x)


def body(
    inner_input,
    state_input,
    conv_inner,
    bias_inner,
    conv_state,
    bias_state,
    step_size,
    decay_rate,
    skip_gain,
    lengths,
):
    own_rows = inner_input.shape[0]
    head_count = decay_rate.shape[0]
    group_half = state_input.shape[2]
    block_count = own_rows // BLOCK
    positions = lax.axis_index("seq") * own_rows + jnp.arange(own_rows + 3, dtype=jnp.int32) - 3
    seg_ext = segment_of(lengths, positions)
    width = inner_input.shape[1]
    tails = jnp.concatenate(
        [inner_input[-8:], jnp.transpose(state_input[:, -8:], (1, 0, 2)).reshape(8, -1)], 1
    )
    tails = shifted(tails, "seq", 1)
    state_tail = tails[:, width:].reshape(8, 2, group_half)
    extra = jnp.concatenate(
        [jnp.transpose(state_tail, (1, 0, 2)).astype(jnp.float32),
         conv_state.astype(jnp.float32), bias_state[:, None, :]],
        1,
    )
    partner_raw, partner_extra = from_partner((state_input, extra), "head", 0)
    lower_half = (lax.axis_index("head") % 2 == 0).astype(jnp.float32)
    head_width = inner_input.shape[1] // head_count
    spread = lambda v: jnp.repeat(v, head_width, axis=-1)
    skip_x = spread(skip_gain).reshape(1, -1)
    seg_own = seg_ext[3:].reshape(block_count, BLOCK)
    seg_prev = seg_ext[2 : 2 + own_rows].reshape(block_count, BLOCK)[:, 0]
    seg_row = seg_ext[3:].reshape(1, own_rows).astype(jnp.float32)
    own_seg = seg_ext[3:]
    entry_col = (seg_own == seg_prev[:, None]).reshape(own_rows)
    keeps = [(seg_ext[3 - back : 3 - back + own_rows] == own_seg) for back in (1, 2, 3)]
    cut = jnp.logical_not(keeps[0] & keeps[1] & keeps[2])
    block_starts = jnp.any(cut.reshape(block_count, BLOCK), axis=1).astype(jnp.int32)
    info = jnp.stack(
        [own_seg.astype(jnp.float32), entry_col.astype(jnp.float32)]
        + [keep.astype(jnp.float32) for keep in keeps]
        + [jnp.zeros((own_rows,), jnp.float32), jnp.full((own_rows,), lower_half, jnp.float32),
           jnp.zeros((own_rows,), jnp.float32)],
        1,
    )

    (local_end, l_t, dt_t, decay_x, total_decay, inner_conv, b_full, c_full, end_sent,
     prefix_x, g_tiles) = run_state(
        block_starts,
        inner_input, tails, conv_inner, bias_inner.reshape(1, -1), state_input, partner_raw,
        extra, partner_extra,
        step_size, decay_rate.reshape(1, -1), info
    )

    def relay(step_num, incoming):
        return shifted(
            (total_decay * incoming.astype(jnp.float32) + local_end).astype(jnp.bfloat16), "seq", 1
        )

    part_rows = own_rows * lax.axis_size("seq")
    hops = min(lax.axis_size("seq") - 1, -(-(part_rows // 2) // own_rows))
    half_blocks = block_count // 2
    operands = (inner_conv, b_full, c_full, l_t, dt_t, seg_row, info, decay_x, skip_x)
    incoming = shifted(end_sent, "seq", 1)
    partial, middle = run_partial(0, half_blocks, *operands)
    incoming, partial, middle = lax.optimization_barrier((incoming, partial, middle))
    first_hop = incoming
    for step_num in range(1, hops):
        incoming = relay(step_num, incoming)
    (second,) = run_partial(
        half_blocks, block_count - half_blocks, *operands, init=middle, after=first_hop
    )
    return run_correct(partial, second, c_full, g_tiles, incoming)


def solution(mesh):
    return jax.shard_map(
        body,
        mesh=mesh,
        in_specs=(
            P(("grp", "seq"), "head"),
            P(None, ("grp", "seq"), "head"),
            P(None, "head"),
            P("head"),
            P(None, None, "head"),
            P(None, "head"),
            P("head", ("grp", "seq")),
            P("head"),
            P("head"),
            P("grp"),
        ),
        out_specs=P(("grp", "seq"), "head"),
        check_vma=False,
    )
```

```python
import functools

import jax
import jax.numpy as jnp
from jax import lax
from jax.experimental import pallas as pl
from jax.experimental.pallas import tpu as pltpu
from jax.sharding import PartitionSpec as P

BLOCK = 128
CORRECT_TILE = 256


def shifted(value, axis, steps):
    count = lax.axis_size(axis)
    initial, last = (max(0, -steps), min(count, count - steps))
    return lax.ppermute(value, axis, [(source, source + steps) for source in range(initial, last)])


def from_partner(block, axis, stride):
    count = lax.axis_size(axis)
    route = []
    for low in range(count):
        high = low | 1 << stride
        if high != low and high < count:
            route += [(low, high), (high, low)]
    return lax.ppermute(block, axis, route)


def segment_of(lengths, positions):
    starts = jnp.cumsum(lengths, dtype=jnp.int32) - lengths
    covered = (starts[None, :] <= positions[:, None]).astype(jnp.int32)
    return jnp.sum(covered, axis=1, dtype=jnp.int32) - 1


def convolve(extended, weight, bias_row, seg_ext, row_count):
    own_seg = seg_ext[3:]
    summed = (
        jnp.zeros(extended.shape[:-2] + (row_count, extended.shape[-1]), jnp.float32) + bias_row
    )
    for offset in range(4):
        kept_mask = (seg_ext[offset : offset + row_count] == own_seg).astype(jnp.float32)[:, None]
        window = extended[..., offset : offset + row_count, :].astype(jnp.float32)
        summed = summed + weight[offset].astype(jnp.float32) * window * kept_mask
    return jax.nn.silu(summed).astype(jnp.bfloat16)


def split_dot(lhs, value):
    high = value.astype(jnp.bfloat16)
    low = (value - high.astype(jnp.float32)).astype(jnp.bfloat16)
    return jnp.dot(lhs, high, preferred_element_type=jnp.float32) + jnp.dot(
        lhs, low, preferred_element_type=jnp.float32
    )


def expand_heads(small, head_width):
    rows, heads = small.shape
    per_tile = 128 // head_width
    lane = lax.broadcasted_iota(jnp.int32, (rows, 128), 1) // head_width
    tiles = []
    for tile in range(heads // per_tile):
        picked = jnp.broadcast_to(small[:, tile * per_tile : tile * per_tile + 1], (rows, 128))
        for k in range(1, per_tile):
            column = small[:, tile * per_tile + k : tile * per_tile + k + 1]
            picked = jnp.where(lane == k, jnp.broadcast_to(column, (rows, 128)), picked)
        tiles.append(picked)
    return jnp.concatenate(tiles, axis=1)


def block_kernel(with_y, head_width, *refs):
    if with_y:
        (x_ref, b_ref, c_ref, l_ref, dt_ref, segr_ref, info_ref, decay_ref,
         skip_ref, ein_ref, out_ref, state_ref) = refs
    else:
        (x_ref, b_ref, l_ref, dt_ref, segc_ref, decay_ref, state_ref) = refs
    blk = pl.program_id(0)

    @pl.when(blk == 0)
    def _():
        if with_y:
            state_ref[...] = ein_ref[...].astype(jnp.float32)
        else:
            state_ref[...] = jnp.zeros(state_ref.shape, jnp.float32)

    info = info_ref[...]
    seg_col = info[:, 0:1]
    end_col = (seg_col == seg_col[BLOCK - 1 : BLOCK, :]).astype(jnp.float32)
    l_small = l_ref[...]
    dt_small = dt_ref[...]
    x = x_ref[...].astype(jnp.float32)
    state = state_ref[...]
    if with_y:
        c_mat = c_ref[...]
        seg_row = segr_ref[...]
        scores = lax.dot_general(
            c_mat, b_ref[...], (((1,), (1,)), ((), ())), preferred_element_type=jnp.float32
        )
        rows = lax.broadcasted_iota(jnp.int32, (BLOCK, BLOCK), 0)
        cols = lax.broadcasted_iota(jnp.int32, (BLOCK, BLOCK), 1)
        allowed = (rows >= cols) & (seg_col == seg_row)
        masked = jnp.where(allowed, scores, 0.0).astype(jnp.bfloat16)
        rising = expand_heads(jnp.exp(l_small), head_width)
        falling = expand_heads(jnp.exp(-l_small) * dt_small, head_width)
        intra = split_dot(masked, x * falling) * rising
        inter = split_dot(c_mat, state) * (rising * info[:, 1:2])
        out_ref[...] = (intra + inter + skip_ref[...] * x).astype(jnp.bfloat16)
    ending = expand_heads(
        jnp.exp(l_small[BLOCK - 1 : BLOCK, :] - l_small) * dt_small * end_col, head_width
    )
    weighted = (x * ending).astype(jnp.bfloat16)
    state_ref[...] = decay_ref[0] * state + lax.dot_general(
        b_ref[...], weighted, (((0,), (0,)), ((), ())), preferred_element_type=jnp.float32
    )


def causal_conv(raw, prev, taps, bias, info):
    top_row = lax.broadcasted_iota(jnp.int32, prev.shape, 0)
    summed = jnp.zeros(raw.shape, jnp.float32) + bias
    for offset in range(4):
        back = 3 - offset
        if back == 0:
            window = raw
        else:
            rolled = pltpu.roll(raw, back, 0)
            top = jnp.where(top_row < back, pltpu.roll(prev, back, 0), rolled[:8])
            window = jnp.concatenate([top, rolled[8:]], 0) * info[:, 1 + back : 2 + back]
        summed = summed + taps[offset : offset + 1, :] * window
    return jax.nn.silu(summed).astype(jnp.bfloat16)


def state_kernel(head_width, x_ref, tail_ref, wconv_ref, bias_ref, own_ref, other_ref, ownx_ref,
                 otherx_ref, dt_ref, rate_ref, info_ref, state_ref, l_ref, dtt_ref,
                 decay_ref, total_ref, xc_ref, bo_ref, sent_ref, prefix_ref, ltile_ref,
                 prev_ref, bcprev_ref, small_ref):
    blk = pl.program_id(0)

    @pl.when(blk == 0)
    def _():
        state_ref[...] = jnp.zeros(state_ref.shape, jnp.float32)
        total_ref[...] = jnp.ones(total_ref.shape, jnp.float32)
        prev_ref[...] = tail_ref[:, : x_ref.shape[1]].astype(jnp.float32)
        small_ref[...] = jnp.ones(small_ref.shape, jnp.float32)
        bcprev_ref[0] = ownx_ref[:, 0:8, :]
        bcprev_ref[1] = otherx_ref[:, 0:8, :]

    info = info_ref[...]
    raw = x_ref[...].astype(jnp.float32)
    xc = causal_conv(raw, prev_ref[...], wconv_ref[...].astype(jnp.float32), bias_ref[...], info)
    prev_ref[...] = raw[BLOCK - 8 :]
    xc_ref[...] = xc
    lower = info_ref[0:1, 5:6] > 0.5
    convolved = []
    for which in range(1):
        halves = []
        for side, (raw_ref, extra_ref) in enumerate(((own_ref, ownx_ref), (other_ref, otherx_ref))):
            raw_bc = raw_ref[which].astype(jnp.float32)
            extra = extra_ref[which]
            halves.append(
                causal_conv(raw_bc, bcprev_ref[side, which], extra[8:12], extra[12:13], info)
            )
            bcprev_ref[side, which] = raw_bc[BLOCK - 8 :]
        convolved.append(jnp.where(
            lower, jnp.concatenate(halves, 1), jnp.concatenate(halves[::-1], 1)
        ))
    b_mat = convolved[0]
    bo_ref[...] = b_mat

    rows = lax.broadcasted_iota(jnp.int32, (2 * BLOCK, BLOCK), 0)
    cols = lax.broadcasted_iota(jnp.int32, (2 * BLOCK, BLOCK), 1)
    picker = jnp.where(
        ((rows < BLOCK) & (rows >= cols)) | (rows - BLOCK == cols), 1.0, 0.0
    ).astype(jnp.bfloat16)
    rest = dt_ref[...]
    cum = None
    for _ in range(3):
        piece = rest.astype(jnp.bfloat16)
        part = lax.dot_general(
            picker, piece, (((1,), (1,)), ((), ())), preferred_element_type=jnp.float32
        )
        cum = part if cum is None else cum + part
        rest = rest - piece.astype(jnp.float32)
    l_small = -cum[:BLOCK] * rate_ref[...]
    dt_small = cum[BLOCK:]
    l_ref[...] = l_small
    dtt_ref[...] = dt_small
    seg_col = info[:, 0:1]
    end_col = (seg_col == seg_col[BLOCK - 1 : BLOCK, :]).astype(jnp.float32)
    decay_x = expand_heads(
        jnp.exp(l_small[BLOCK - 1 : BLOCK, :]) * info[BLOCK - 1 : BLOCK, 1:2], head_width
    )
    decay_ref[0] = decay_x
    prefix_ref[0] = total_ref[...]
    total_ref[...] = total_ref[...] * decay_x
    carry = (jnp.exp(l_small) * info[:, 1:2]) * small_ref[...]
    small_ref[...] = small_ref[...] * (
        jnp.exp(l_small[BLOCK - 1 : BLOCK, :]) * info[BLOCK - 1 : BLOCK, 1:2]
    )
    tile_heads = ltile_ref.shape[2]
    for tile in range(ltile_ref.shape[0]):
        ltile_ref[tile] = carry[:, tile * tile_heads : (tile + 1) * tile_heads]
    ending = expand_heads(
        jnp.exp(l_small[BLOCK - 1 : BLOCK, :] - l_small) * dt_small * end_col, head_width
    )
    weighted = (xc.astype(jnp.float32) * ending).astype(jnp.bfloat16)
    new_state = decay_x * state_ref[...] + lax.dot_general(
        b_mat, weighted, (((0,), (0,)), ((), ())), preferred_element_type=jnp.float32
    )
    state_ref[...] = new_state

    @pl.when(blk == pl.num_programs(0) - 1)
    def _():
        sent_ref[...] = new_state.astype(jnp.bfloat16)


def run_state(x, tails, wconv, bias_row, own_raw, other_raw, own_extra, other_extra,
              step_size, rate_row, info):
    rows, width = x.shape
    head_count = step_size.shape[0]
    half = own_raw.shape[2]
    n_size = 2 * half
    block_count = rows // BLOCK
    tiles = width // CORRECT_TILE
    tile_heads = head_count // tiles
    row_block = lambda cols: pl.BlockSpec((BLOCK, cols), lambda b: (b, 0))
    whole = lambda shape: pl.BlockSpec(shape, lambda b: (0,) * len(shape))
    return pl.pallas_call(
        functools.partial(state_kernel, width // head_count),
        grid=(block_count,),
        in_specs=[row_block(width), whole(tails.shape), whole((4, width)), whole((1, width)),
                  pl.BlockSpec((2, BLOCK, half), lambda b: (0, b, 0)),
                  pl.BlockSpec((2, BLOCK, half), lambda b: (0, b, 0)),
                  whole(own_extra.shape), whole(own_extra.shape),
                  pl.BlockSpec((head_count, BLOCK), lambda b: (0, b)),
                  whole((1, head_count)), row_block(info.shape[1])],
        out_specs=[whole((n_size, width)), row_block(head_count), row_block(head_count),
                   pl.BlockSpec((1, 1, width), lambda b: (b, 0, 0)), whole((1, width)),
                   row_block(width), row_block(n_size),
                   whole((n_size, width)), pl.BlockSpec((1, 1, width), lambda b: (b, 0, 0)),
                   pl.BlockSpec((tiles, BLOCK, tile_heads), lambda b: (0, b, 0))],
        out_shape=[jax.ShapeDtypeStruct((n_size, width), jnp.float32),
                   jax.ShapeDtypeStruct((rows, head_count), jnp.float32),
                   jax.ShapeDtypeStruct((rows, head_count), jnp.float32),
                   jax.ShapeDtypeStruct((block_count, 1, width), jnp.float32),
                   jax.ShapeDtypeStruct((1, width), jnp.float32),
                   jax.ShapeDtypeStruct((rows, width), jnp.bfloat16),
                   jax.ShapeDtypeStruct((rows, n_size), jnp.bfloat16),
                   jax.ShapeDtypeStruct((n_size, width), jnp.bfloat16),
                   jax.ShapeDtypeStruct((block_count, 1, width), jnp.float32),
                   jax.ShapeDtypeStruct((tiles, rows, tile_heads), jnp.float32)],
        scratch_shapes=[pltpu.VMEM((8, width), jnp.float32),
                        pltpu.VMEM((2, 2, 8, half), jnp.float32),
                        pltpu.VMEM((1, head_count), jnp.float32)],
        compiler_params=pltpu.CompilerParams(dimension_semantics=("arbitrary",)),
    )(x, tails, wconv, bias_row, own_raw, other_raw, own_extra, other_extra, step_size,
      rate_row, info)


def partial_kernel(head_width, from_zero, *refs):
    if from_zero:
        (x_ref, b_ref, cown_ref, cother_ref, ownx_ref, otherx_ref, l_ref, dt_ref, segr_ref,
         info_ref, decay_ref, skip_ref, out_ref, cout_ref, end_ref, state_ref, cprev_ref) = refs
    else:
        (x_ref, b_ref, cown_ref, cother_ref, ownx_ref, otherx_ref, l_ref, dt_ref, segr_ref,
         info_ref, decay_ref, skip_ref, init_ref, after_ref, pown_ref, pother_ref, out_ref,
         cout_ref, state_ref, cprev_ref) = refs
    blk = pl.program_id(0)

    @pl.when(blk == 0)
    def _():
        if from_zero:
            state_ref[...] = jnp.zeros(state_ref.shape, jnp.float32)
            cprev_ref[0] = ownx_ref[1, 0:8, :]
            cprev_ref[1] = otherx_ref[1, 0:8, :]
        else:
            state_ref[...] = init_ref[...]
            cprev_ref[0] = pown_ref[0, 8:16, :].astype(jnp.float32)
            cprev_ref[1] = pother_ref[0, 8:16, :].astype(jnp.float32)

    info = info_ref[...]
    seg_col = info[:, 0:1]
    end_col = (seg_col == seg_col[BLOCK - 1 : BLOCK, :]).astype(jnp.float32)
    l_small = l_ref[...]
    dt_small = dt_ref[...]
    x = x_ref[...].astype(jnp.float32)
    state = state_ref[...]
    halves = []
    for side, (raw_ref, extra_ref) in enumerate(((cown_ref, ownx_ref), (cother_ref, otherx_ref))):
        raw_c = raw_ref[0].astype(jnp.float32)
        extra = extra_ref[1]
        halves.append(causal_conv(raw_c, cprev_ref[side], extra[8:12], extra[12:13], info))
        cprev_ref[side] = raw_c[BLOCK - 8 :]
    lower = info_ref[0:1, 5:6] > 0.5
    c_mat = jnp.where(lower, jnp.concatenate(halves, 1), jnp.concatenate(halves[::-1], 1))
    cout_ref[...] = c_mat
    b_mat = b_ref[...]
    scores = lax.dot_general(
        c_mat, b_mat, (((1,), (1,)), ((), ())), preferred_element_type=jnp.float32
    )
    rows = lax.broadcasted_iota(jnp.int32, (BLOCK, BLOCK), 0)
    cols = lax.broadcasted_iota(jnp.int32, (BLOCK, BLOCK), 1)
    allowed = (rows >= cols) & (seg_col == segr_ref[...])
    masked = jnp.where(allowed, scores, 0.0).astype(jnp.bfloat16)
    rising = expand_heads(jnp.exp(l_small), head_width)
    falling = expand_heads(jnp.exp(-l_small) * dt_small, head_width)
    intra = split_dot(masked, x * falling) * rising
    inter = split_dot(c_mat, state) * (rising * info[:, 1:2])
    out_ref[...] = intra + inter + skip_ref[...] * x
    last = blk == pl.num_programs(0) - 1

    @pl.when(jnp.logical_or(jnp.logical_not(last), from_zero))
    def _():
        ending = expand_heads(
            jnp.exp(l_small[BLOCK - 1 : BLOCK, :] - l_small) * dt_small * end_col, head_width
        )
        weighted = (x * ending).astype(jnp.bfloat16)
        new_state = decay_ref[0] * state + lax.dot_general(
            b_mat, weighted, (((0,), (0,)), ((), ())), preferred_element_type=jnp.float32
        )
        state_ref[...] = new_state
        if from_zero:

            @pl.when(last)
            def _():
                end_ref[...] = new_state


def run_partial(first, count, x, b_full, c_raws, l_t, dt_t, seg_row, info, decay_x, skip_x,
                init=None, after=None):
    rows, width = x.shape
    head_count = l_t.shape[1]
    n_size = b_full.shape[1]
    own_raw, other_raw, own_extra, other_extra = c_raws
    half = own_raw.shape[2]
    row_block = lambda cols: pl.BlockSpec((BLOCK, cols), lambda b: (b + first, 0))
    whole = lambda shape: pl.BlockSpec(shape, lambda b: (0,) * len(shape))
    from_zero = init is None
    plane = pl.BlockSpec((1, BLOCK, half), lambda b: (1, b + first, 0))
    in_specs = [row_block(width), row_block(n_size), plane, plane, whole(own_extra.shape),
                whole(own_extra.shape), row_block(head_count),
                row_block(head_count), pl.BlockSpec((1, BLOCK), lambda b: (0, b + first)),
                row_block(info.shape[1]), pl.BlockSpec((1, 1, width), lambda b: (b + first, 0, 0)),
                whole((1, width))]
    args = [x, b_full, own_raw, other_raw, own_extra, other_extra, l_t, dt_t, seg_row, info,
            decay_x, skip_x]
    if not from_zero:
        before = pl.BlockSpec((1, 16, half), lambda b: (1, first * (BLOCK // 16) - 1, 0))
        in_specs += [whole((n_size, width)), pl.BlockSpec(memory_space=pl.ANY), before, before]
        args += [init, after, own_raw, other_raw]
    out_specs = [pl.BlockSpec((BLOCK, width), lambda b: (b, 0)),
                 pl.BlockSpec((BLOCK, n_size), lambda b: (b, 0))]
    out_shape = [jax.ShapeDtypeStruct((count * BLOCK, width), jnp.float32),
                 jax.ShapeDtypeStruct((count * BLOCK, n_size), jnp.bfloat16)]
    if from_zero:
        out_specs.append(whole((n_size, width)))
        out_shape.append(jax.ShapeDtypeStruct((n_size, width), jnp.float32))
    return pl.pallas_call(
        functools.partial(partial_kernel, width // head_count, from_zero),
        grid=(count,),
        in_specs=in_specs,
        out_specs=out_specs,
        out_shape=out_shape,
        scratch_shapes=[pltpu.VMEM((n_size, width), jnp.float32),
                        pltpu.VMEM((2, 8, half), jnp.float32)],
        compiler_params=pltpu.CompilerParams(dimension_semantics=("arbitrary",)),
    )(*args)


def correct_kernel(head_width, y_ref, z_ref, c_ref, d_ref, g_ref, ein_ref, out_ref):
    factor = expand_heads(g_ref[0], head_width)
    ein = ein_ref[...]
    split = y_ref.shape[0]
    carried = jnp.dot(c_ref[...], ein, preferred_element_type=jnp.float32)
    out_ref[:split] = (y_ref[...] + carried * factor[:split]).astype(jnp.bfloat16)
    carried = jnp.dot(d_ref[...], ein, preferred_element_type=jnp.float32)
    out_ref[split:] = (z_ref[...] + carried * factor[split:]).astype(jnp.bfloat16)


def run_correct(first, second, c_first, c_second, g_tiles, entering):
    rows = first.shape[0] + second.shape[0]
    width = first.shape[1]
    tiles, _, heads_per = g_tiles.shape
    tile = CORRECT_TILE
    head_width = tile // heads_per
    n_size = c_first.shape[1]
    return pl.pallas_call(
        functools.partial(correct_kernel, head_width),
        grid=(tiles,),
        in_specs=[pl.BlockSpec((first.shape[0], tile), lambda j: (0, j)),
                  pl.BlockSpec((second.shape[0], tile), lambda j: (0, j)),
                  pl.BlockSpec((first.shape[0], n_size), lambda j: (0, 0)),
                  pl.BlockSpec((second.shape[0], n_size), lambda j: (0, 0)),
                  pl.BlockSpec((1, rows, heads_per), lambda j: (j, 0, 0)),
                  pl.BlockSpec((n_size, tile), lambda j: (0, j))],
        out_specs=pl.BlockSpec((rows, tile), lambda j: (0, j)),
        out_shape=jax.ShapeDtypeStruct((rows, width), jnp.bfloat16),
        compiler_params=pltpu.CompilerParams(dimension_semantics=("arbitrary",)),
    )(first, second, c_first, c_second, g_tiles, entering)


def run_blocks(with_y, x, b_full, c_full, l_t, dt_t, seg_row, seg_col, entry_col, decay_x,
               skip_x, entering):
    rows, width = x.shape
    head_count = l_t.shape[1]
    head_width = width // head_count
    n_size = b_full.shape[1]
    block_count = rows // BLOCK
    row_block = lambda cols: pl.BlockSpec((BLOCK, cols), lambda b: (b, 0))
    bt_spec = pl.BlockSpec((n_size, BLOCK), lambda b: (0, b))
    decay_spec = pl.BlockSpec((1, 1, width), lambda b: (b, 0, 0))
    state_spec = pl.BlockSpec((n_size, width), lambda b: (0, 0))
    state_shape = jax.ShapeDtypeStruct((n_size, width), jnp.float32)
    kernel = functools.partial(block_kernel, with_y, head_width)
    params = pltpu.CompilerParams(dimension_semantics=("arbitrary",))
    if with_y:
        return pl.pallas_call(
            kernel,
            grid=(block_count,),
            in_specs=[row_block(width), row_block(n_size), row_block(n_size),
                      row_block(head_count), row_block(head_count),
                      pl.BlockSpec((1, BLOCK), lambda b: (0, b)), row_block(seg_col.shape[1]),
                      decay_spec, pl.BlockSpec((1, width), lambda b: (0, 0)), state_spec],
            out_specs=row_block(width),
            out_shape=jax.ShapeDtypeStruct((rows, width), jnp.bfloat16),
            scratch_shapes=[pltpu.VMEM((n_size, width), jnp.float32)],
            compiler_params=params,
        )(x, b_full, c_full, l_t, dt_t, seg_row, seg_col, decay_x, skip_x, entering)
    return pl.pallas_call(
        kernel,
        grid=(block_count,),
        in_specs=[row_block(width), bt_spec, row_block(head_count), row_block(head_count),
                  row_block(1), decay_spec],
        out_specs=state_spec,
        out_shape=state_shape,
        compiler_params=params,
    )(x, b_t, l_t, dt_t, seg_col, decay_x)


def body(
    inner_input,
    state_input,
    conv_inner,
    bias_inner,
    conv_state,
    bias_state,
    step_size,
    decay_rate,
    skip_gain,
    lengths,
):
    own_rows = inner_input.shape[0]
    head_count = decay_rate.shape[0]
    group_half = state_input.shape[2]
    block_count = own_rows // BLOCK
    positions = lax.axis_index("seq") * own_rows + jnp.arange(own_rows + 3, dtype=jnp.int32) - 3
    seg_ext = segment_of(lengths, positions)
    width = inner_input.shape[1]
    tails = jnp.concatenate(
        [inner_input[-8:], jnp.transpose(state_input[:, -8:], (1, 0, 2)).reshape(8, -1)], 1
    )
    tails = shifted(tails, "seq", 1)
    state_tail = tails[:, width:].reshape(8, 2, group_half)
    extra = jnp.concatenate(
        [jnp.transpose(state_tail, (1, 0, 2)).astype(jnp.float32),
         conv_state.astype(jnp.float32), bias_state[:, None, :]],
        1,
    )
    partner_raw, partner_extra = from_partner((state_input, extra), "head", 0)
    lower_half = (lax.axis_index("head") % 2 == 0).astype(jnp.float32)
    head_width = inner_input.shape[1] // head_count
    spread = lambda v: jnp.repeat(v, head_width, axis=-1)
    skip_x = spread(skip_gain).reshape(1, -1)
    seg_own = seg_ext[3:].reshape(block_count, BLOCK)
    seg_prev = seg_ext[2 : 2 + own_rows].reshape(block_count, BLOCK)[:, 0]
    seg_row = seg_ext[3:].reshape(1, own_rows).astype(jnp.float32)
    own_seg = seg_ext[3:]
    entry_col = (seg_own == seg_prev[:, None]).reshape(own_rows)
    keeps = [(seg_ext[3 - back : 3 - back + own_rows] == own_seg) for back in (1, 2, 3)]
    info = jnp.stack(
        [own_seg.astype(jnp.float32), entry_col.astype(jnp.float32)]
        + [keep.astype(jnp.float32) for keep in keeps]
        + [jnp.zeros((own_rows,), jnp.float32), jnp.full((own_rows,), lower_half, jnp.float32),
           jnp.zeros((own_rows,), jnp.float32)],
        1,
    )

    (local_end, l_t, dt_t, decay_x, total_decay, inner_conv, b_full, end_sent,
     prefix_x, g_tiles) = run_state(
        inner_input, tails, conv_inner, bias_inner.reshape(1, -1), state_input, partner_raw,
        extra, partner_extra,
        step_size, decay_rate.reshape(1, -1), info
    )

    def relay(step_num, incoming):
        return shifted(
            (total_decay * incoming.astype(jnp.float32) + local_end).astype(jnp.bfloat16), "seq", 1
        )

    part_rows = own_rows * lax.axis_size("seq")
    hops = min(lax.axis_size("seq") - 1, -(-(part_rows // 2) // own_rows))
    half_blocks = block_count // 2
    c_raws = (state_input, partner_raw, extra, partner_extra)
    operands = (inner_conv, b_full, c_raws, l_t, dt_t, seg_row, info, decay_x, skip_x)
    incoming = shifted(end_sent, "seq", 1)
    partial, c_first, middle = run_partial(0, half_blocks, *operands)
    incoming, partial, c_first, middle = lax.optimization_barrier(
        (incoming, partial, c_first, middle)
    )
    first_hop = incoming
    for step_num in range(1, hops):
        incoming = relay(step_num, incoming)
    second, c_second = run_partial(
        half_blocks, block_count - half_blocks, *operands, init=middle, after=first_hop
    )
    return run_correct(partial, second, c_first, c_second, g_tiles, incoming)


def solution(mesh):
    return jax.shard_map(
        body,
        mesh=mesh,
        in_specs=(
            P(("grp", "seq"), "head"),
            P(None, ("grp", "seq"), "head"),
            P(None, "head"),
            P("head"),
            P(None, None, "head"),
            P(None, "head"),
            P("head", ("grp", "seq")),
            P("head"),
            P("head"),
            P("grp"),
        ),
        out_specs=P(("grp", "seq"), "head"),
        check_vma=False,
    )
```

```python
import functools

import jax
import jax.numpy as jnp
from jax import lax
from jax.experimental import pallas as pl
from jax.experimental.pallas import tpu as pltpu
from jax.sharding import PartitionSpec as P

BLOCK = 128
CORRECT_TILE = 512


def shifted(value, axis, steps):
    count = lax.axis_size(axis)
    initial, last = (max(0, -steps), min(count, count - steps))
    return lax.ppermute(value, axis, [(source, source + steps) for source in range(initial, last)])


def from_partner(block, axis, stride):
    count = lax.axis_size(axis)
    route = []
    for low in range(count):
        high = low | 1 << stride
        if high != low and high < count:
            route += [(low, high), (high, low)]
    return lax.ppermute(block, axis, route)


def segment_of(lengths, positions):
    starts = jnp.cumsum(lengths, dtype=jnp.int32) - lengths
    covered = (starts[None, :] <= positions[:, None]).astype(jnp.int32)
    return jnp.sum(covered, axis=1, dtype=jnp.int32) - 1


def convolve(extended, weight, bias_row, seg_ext, row_count):
    own_seg = seg_ext[3:]
    summed = (
        jnp.zeros(extended.shape[:-2] + (row_count, extended.shape[-1]), jnp.float32) + bias_row
    )
    for offset in range(4):
        kept_mask = (seg_ext[offset : offset + row_count] == own_seg).astype(jnp.float32)[:, None]
        window = extended[..., offset : offset + row_count, :].astype(jnp.float32)
        summed = summed + weight[offset].astype(jnp.float32) * window * kept_mask
    return jax.nn.silu(summed).astype(jnp.bfloat16)


def split_dot(lhs, value):
    high = value.astype(jnp.bfloat16)
    low = (value - high.astype(jnp.float32)).astype(jnp.bfloat16)
    return jnp.dot(lhs, high, preferred_element_type=jnp.float32) + jnp.dot(
        lhs, low, preferred_element_type=jnp.float32
    )


def expand_heads(small, head_width):
    rows, heads = small.shape
    per_tile = 128 // head_width
    lane = lax.broadcasted_iota(jnp.int32, (rows, 128), 1) // head_width
    tiles = []
    for tile in range(heads // per_tile):
        picked = jnp.broadcast_to(small[:, tile * per_tile : tile * per_tile + 1], (rows, 128))
        for k in range(1, per_tile):
            column = small[:, tile * per_tile + k : tile * per_tile + k + 1]
            picked = jnp.where(lane == k, jnp.broadcast_to(column, (rows, 128)), picked)
        tiles.append(picked)
    return jnp.concatenate(tiles, axis=1)


def block_kernel(with_y, head_width, *refs):
    if with_y:
        (x_ref, b_ref, c_ref, l_ref, dt_ref, segr_ref, info_ref, decay_ref,
         skip_ref, ein_ref, out_ref, state_ref) = refs
    else:
        (x_ref, b_ref, l_ref, dt_ref, segc_ref, decay_ref, state_ref) = refs
    blk = pl.program_id(0)

    @pl.when(blk == 0)
    def _():
        if with_y:
            state_ref[...] = ein_ref[...].astype(jnp.float32)
        else:
            state_ref[...] = jnp.zeros(state_ref.shape, jnp.float32)

    info = info_ref[...]
    seg_col = info[:, 0:1]
    end_col = (seg_col == seg_col[BLOCK - 1 : BLOCK, :]).astype(jnp.float32)
    l_small = l_ref[...]
    dt_small = dt_ref[...]
    x = x_ref[...].astype(jnp.float32)
    state = state_ref[...]
    if with_y:
        c_mat = c_ref[...]
        seg_row = segr_ref[...]
        scores = lax.dot_general(
            c_mat, b_ref[...], (((1,), (1,)), ((), ())), preferred_element_type=jnp.float32
        )
        rows = lax.broadcasted_iota(jnp.int32, (BLOCK, BLOCK), 0)
        cols = lax.broadcasted_iota(jnp.int32, (BLOCK, BLOCK), 1)
        allowed = (rows >= cols) & (seg_col == seg_row)
        masked = jnp.where(allowed, scores, 0.0).astype(jnp.bfloat16)
        rising = expand_heads(jnp.exp(l_small), head_width)
        falling = expand_heads(jnp.exp(-l_small) * dt_small, head_width)
        intra = split_dot(masked, x * falling) * rising
        inter = split_dot(c_mat, state) * (rising * info[:, 1:2])
        out_ref[...] = (intra + inter + skip_ref[...] * x).astype(jnp.bfloat16)
    ending = expand_heads(
        jnp.exp(l_small[BLOCK - 1 : BLOCK, :] - l_small) * dt_small * end_col, head_width
    )
    weighted = (x * ending).astype(jnp.bfloat16)
    state_ref[...] = decay_ref[0] * state + lax.dot_general(
        b_ref[...], weighted, (((0,), (0,)), ((), ())), preferred_element_type=jnp.float32
    )


def causal_conv(raw, prev, taps, bias, info):
    top_row = lax.broadcasted_iota(jnp.int32, prev.shape, 0)
    summed = jnp.zeros(raw.shape, jnp.float32) + bias
    for offset in range(4):
        back = 3 - offset
        if back == 0:
            window = raw
        else:
            rolled = pltpu.roll(raw, back, 0)
            top = jnp.where(top_row < back, pltpu.roll(prev, back, 0), rolled[:8])
            window = jnp.concatenate([top, rolled[8:]], 0) * info[:, 1 + back : 2 + back]
        summed = summed + taps[offset : offset + 1, :] * window
    return jax.nn.silu(summed).astype(jnp.bfloat16)


def state_kernel(head_width, x_ref, tail_ref, wconv_ref, bias_ref, own_ref, other_ref, ownx_ref,
                 otherx_ref, dt_ref, rate_ref, info_ref, state_ref, l_ref, dtt_ref,
                 decay_ref, total_ref, xc_ref, bo_ref, sent_ref, prefix_ref, ltile_ref,
                 prev_ref, bcprev_ref, small_ref):
    blk = pl.program_id(0)

    @pl.when(blk == 0)
    def _():
        state_ref[...] = jnp.zeros(state_ref.shape, jnp.float32)
        total_ref[...] = jnp.ones(total_ref.shape, jnp.float32)
        prev_ref[...] = tail_ref[:, : x_ref.shape[1]].astype(jnp.float32)
        small_ref[...] = jnp.ones(small_ref.shape, jnp.float32)
        bcprev_ref[0] = ownx_ref[:, 0:8, :]
        bcprev_ref[1] = otherx_ref[:, 0:8, :]

    info = info_ref[...]
    raw = x_ref[...].astype(jnp.float32)
    xc = causal_conv(raw, prev_ref[...], wconv_ref[...].astype(jnp.float32), bias_ref[...], info)
    prev_ref[...] = raw[BLOCK - 8 :]
    xc_ref[...] = xc
    lower = info_ref[0:1, 5:6] > 0.5
    convolved = []
    for which in range(1):
        halves = []
        for side, (raw_ref, extra_ref) in enumerate(((own_ref, ownx_ref), (other_ref, otherx_ref))):
            raw_bc = raw_ref[which].astype(jnp.float32)
            extra = extra_ref[which]
            halves.append(
                causal_conv(raw_bc, bcprev_ref[side, which], extra[8:12], extra[12:13], info)
            )
            bcprev_ref[side, which] = raw_bc[BLOCK - 8 :]
        convolved.append(jnp.where(
            lower, jnp.concatenate(halves, 1), jnp.concatenate(halves[::-1], 1)
        ))
    b_mat = convolved[0]
    bo_ref[...] = b_mat

    rows = lax.broadcasted_iota(jnp.int32, (2 * BLOCK, BLOCK), 0)
    cols = lax.broadcasted_iota(jnp.int32, (2 * BLOCK, BLOCK), 1)
    picker = jnp.where(
        ((rows < BLOCK) & (rows >= cols)) | (rows - BLOCK == cols), 1.0, 0.0
    ).astype(jnp.bfloat16)
    rest = dt_ref[...]
    cum = None
    for _ in range(3):
        piece = rest.astype(jnp.bfloat16)
        part = lax.dot_general(
            picker, piece, (((1,), (1,)), ((), ())), preferred_element_type=jnp.float32
        )
        cum = part if cum is None else cum + part
        rest = rest - piece.astype(jnp.float32)
    l_small = -cum[:BLOCK] * rate_ref[...]
    dt_small = cum[BLOCK:]
    l_ref[...] = l_small
    dtt_ref[...] = dt_small
    seg_col = info[:, 0:1]
    end_col = (seg_col == seg_col[BLOCK - 1 : BLOCK, :]).astype(jnp.float32)
    decay_x = expand_heads(
        jnp.exp(l_small[BLOCK - 1 : BLOCK, :]) * info[BLOCK - 1 : BLOCK, 1:2], head_width
    )
    decay_ref[0] = decay_x
    prefix_ref[0] = total_ref[...]
    total_ref[...] = total_ref[...] * decay_x
    carry = (jnp.exp(l_small) * info[:, 1:2]) * small_ref[...]
    small_ref[...] = small_ref[...] * (
        jnp.exp(l_small[BLOCK - 1 : BLOCK, :]) * info[BLOCK - 1 : BLOCK, 1:2]
    )
    tile_heads = ltile_ref.shape[2]
    for tile in range(ltile_ref.shape[0]):
        ltile_ref[tile] = carry[:, tile * tile_heads : (tile + 1) * tile_heads]
    ending = expand_heads(
        jnp.exp(l_small[BLOCK - 1 : BLOCK, :] - l_small) * dt_small * end_col, head_width
    )
    weighted = (xc.astype(jnp.float32) * ending).astype(jnp.bfloat16)
    new_state = decay_x * state_ref[...] + lax.dot_general(
        b_mat, weighted, (((0,), (0,)), ((), ())), preferred_element_type=jnp.float32
    )
    state_ref[...] = new_state

    @pl.when(blk == pl.num_programs(0) - 1)
    def _():
        sent_ref[...] = new_state.astype(jnp.bfloat16)


def run_state(x, tails, wconv, bias_row, own_raw, other_raw, own_extra, other_extra,
              step_size, rate_row, info):
    rows, width = x.shape
    head_count = step_size.shape[0]
    half = own_raw.shape[2]
    n_size = 2 * half
    block_count = rows // BLOCK
    tiles = width // CORRECT_TILE
    tile_heads = head_count // tiles
    row_block = lambda cols: pl.BlockSpec((BLOCK, cols), lambda b: (b, 0))
    whole = lambda shape: pl.BlockSpec(shape, lambda b: (0,) * len(shape))
    return pl.pallas_call(
        functools.partial(state_kernel, width // head_count),
        grid=(block_count,),
        in_specs=[row_block(width), whole(tails.shape), whole((4, width)), whole((1, width)),
                  pl.BlockSpec((2, BLOCK, half), lambda b: (0, b, 0)),
                  pl.BlockSpec((2, BLOCK, half), lambda b: (0, b, 0)),
                  whole(own_extra.shape), whole(own_extra.shape),
                  pl.BlockSpec((head_count, BLOCK), lambda b: (0, b)),
                  whole((1, head_count)), row_block(info.shape[1])],
        out_specs=[whole((n_size, width)), row_block(head_count), row_block(head_count),
                   pl.BlockSpec((1, 1, width), lambda b: (b, 0, 0)), whole((1, width)),
                   row_block(width), row_block(n_size),
                   whole((n_size, width)), pl.BlockSpec((1, 1, width), lambda b: (b, 0, 0)),
                   pl.BlockSpec((tiles, BLOCK, tile_heads), lambda b: (0, b, 0))],
        out_shape=[jax.ShapeDtypeStruct((n_size, width), jnp.float32),
                   jax.ShapeDtypeStruct((rows, head_count), jnp.float32),
                   jax.ShapeDtypeStruct((rows, head_count), jnp.float32),
                   jax.ShapeDtypeStruct((block_count, 1, width), jnp.float32),
                   jax.ShapeDtypeStruct((1, width), jnp.float32),
                   jax.ShapeDtypeStruct((rows, width), jnp.bfloat16),
                   jax.ShapeDtypeStruct((rows, n_size), jnp.bfloat16),
                   jax.ShapeDtypeStruct((n_size, width), jnp.bfloat16),
                   jax.ShapeDtypeStruct((block_count, 1, width), jnp.float32),
                   jax.ShapeDtypeStruct((tiles, rows, tile_heads), jnp.float32)],
        scratch_shapes=[pltpu.VMEM((8, width), jnp.float32),
                        pltpu.VMEM((2, 2, 8, half), jnp.float32),
                        pltpu.VMEM((1, head_count), jnp.float32)],
        compiler_params=pltpu.CompilerParams(dimension_semantics=("arbitrary",)),
    )(x, tails, wconv, bias_row, own_raw, other_raw, own_extra, other_extra, step_size,
      rate_row, info)


def partial_kernel(head_width, from_zero, *refs):
    if from_zero:
        (x_ref, b_ref, cown_ref, cother_ref, ownx_ref, otherx_ref, l_ref, dt_ref, segr_ref,
         info_ref, decay_ref, skip_ref, out_ref, cout_ref, end_ref, state_ref, cprev_ref) = refs
    else:
        (x_ref, b_ref, cown_ref, cother_ref, ownx_ref, otherx_ref, l_ref, dt_ref, segr_ref,
         info_ref, decay_ref, skip_ref, init_ref, after_ref, pown_ref, pother_ref, out_ref,
         cout_ref, state_ref, cprev_ref) = refs
    blk = pl.program_id(0)

    @pl.when(blk == 0)
    def _():
        if from_zero:
            state_ref[...] = jnp.zeros(state_ref.shape, jnp.float32)
            cprev_ref[0] = ownx_ref[1, 0:8, :]
            cprev_ref[1] = otherx_ref[1, 0:8, :]
        else:
            state_ref[...] = init_ref[...]
            cprev_ref[0] = pown_ref[0, 8:16, :].astype(jnp.float32)
            cprev_ref[1] = pother_ref[0, 8:16, :].astype(jnp.float32)

    info = info_ref[...]
    seg_col = info[:, 0:1]
    end_col = (seg_col == seg_col[BLOCK - 1 : BLOCK, :]).astype(jnp.float32)
    l_small = l_ref[...]
    dt_small = dt_ref[...]
    x = x_ref[...].astype(jnp.float32)
    state = state_ref[...]
    halves = []
    for side, (raw_ref, extra_ref) in enumerate(((cown_ref, ownx_ref), (cother_ref, otherx_ref))):
        raw_c = raw_ref[0].astype(jnp.float32)
        extra = extra_ref[1]
        halves.append(causal_conv(raw_c, cprev_ref[side], extra[8:12], extra[12:13], info))
        cprev_ref[side] = raw_c[BLOCK - 8 :]
    lower = info_ref[0:1, 5:6] > 0.5
    c_mat = jnp.where(lower, jnp.concatenate(halves, 1), jnp.concatenate(halves[::-1], 1))
    cout_ref[...] = c_mat
    b_mat = b_ref[...]
    scores = lax.dot_general(
        c_mat, b_mat, (((1,), (1,)), ((), ())), preferred_element_type=jnp.float32
    )
    rows = lax.broadcasted_iota(jnp.int32, (BLOCK, BLOCK), 0)
    cols = lax.broadcasted_iota(jnp.int32, (BLOCK, BLOCK), 1)
    allowed = (rows >= cols) & (seg_col == segr_ref[...])
    masked = jnp.where(allowed, scores, 0.0).astype(jnp.bfloat16)
    rising = expand_heads(jnp.exp(l_small), head_width)
    falling = expand_heads(jnp.exp(-l_small) * dt_small, head_width)
    intra = split_dot(masked, x * falling) * rising
    inter = split_dot(c_mat, state) * (rising * info[:, 1:2])
    out_ref[...] = intra + inter + skip_ref[...] * x
    last = blk == pl.num_programs(0) - 1

    @pl.when(jnp.logical_or(jnp.logical_not(last), from_zero))
    def _():
        ending = expand_heads(
            jnp.exp(l_small[BLOCK - 1 : BLOCK, :] - l_small) * dt_small * end_col, head_width
        )
        weighted = (x * ending).astype(jnp.bfloat16)
        new_state = decay_ref[0] * state + lax.dot_general(
            b_mat, weighted, (((0,), (0,)), ((), ())), preferred_element_type=jnp.float32
        )
        state_ref[...] = new_state
        if from_zero:

            @pl.when(last)
            def _():
                end_ref[...] = new_state


def run_partial(first, count, x, b_full, c_raws, l_t, dt_t, seg_row, info, decay_x, skip_x,
                init=None, after=None):
    rows, width = x.shape
    head_count = l_t.shape[1]
    n_size = b_full.shape[1]
    own_raw, other_raw, own_extra, other_extra = c_raws
    half = own_raw.shape[2]
    row_block = lambda cols: pl.BlockSpec((BLOCK, cols), lambda b: (b + first, 0))
    whole = lambda shape: pl.BlockSpec(shape, lambda b: (0,) * len(shape))
    from_zero = init is None
    plane = pl.BlockSpec((1, BLOCK, half), lambda b: (1, b + first, 0))
    in_specs = [row_block(width), row_block(n_size), plane, plane, whole(own_extra.shape),
                whole(own_extra.shape), row_block(head_count),
                row_block(head_count), pl.BlockSpec((1, BLOCK), lambda b: (0, b + first)),
                row_block(info.shape[1]), pl.BlockSpec((1, 1, width), lambda b: (b + first, 0, 0)),
                whole((1, width))]
    args = [x, b_full, own_raw, other_raw, own_extra, other_extra, l_t, dt_t, seg_row, info,
            decay_x, skip_x]
    if not from_zero:
        before = pl.BlockSpec((1, 16, half), lambda b: (1, first * (BLOCK // 16) - 1, 0))
        in_specs += [whole((n_size, width)), pl.BlockSpec(memory_space=pl.ANY), before, before]
        args += [init, after, own_raw, other_raw]
    out_specs = [pl.BlockSpec((BLOCK, width), lambda b: (b, 0)),
                 pl.BlockSpec((BLOCK, n_size), lambda b: (b, 0))]
    out_shape = [jax.ShapeDtypeStruct((count * BLOCK, width), jnp.float32),
                 jax.ShapeDtypeStruct((count * BLOCK, n_size), jnp.bfloat16)]
    if from_zero:
        out_specs.append(whole((n_size, width)))
        out_shape.append(jax.ShapeDtypeStruct((n_size, width), jnp.float32))
    return pl.pallas_call(
        functools.partial(partial_kernel, width // head_count, from_zero),
        grid=(count,),
        in_specs=in_specs,
        out_specs=out_specs,
        out_shape=out_shape,
        scratch_shapes=[pltpu.VMEM((n_size, width), jnp.float32),
                        pltpu.VMEM((2, 8, half), jnp.float32)],
        compiler_params=pltpu.CompilerParams(dimension_semantics=("arbitrary",)),
    )(*args)


def correct_kernel(head_width, y_ref, z_ref, c_ref, d_ref, g_ref, ein_ref, out_ref):
    factor = expand_heads(g_ref[0], head_width)
    ein = ein_ref[...]
    split = y_ref.shape[0]
    carried = jnp.dot(c_ref[...], ein, preferred_element_type=jnp.float32)
    out_ref[:split] = (y_ref[...] + carried * factor[:split]).astype(jnp.bfloat16)
    carried = jnp.dot(d_ref[...], ein, preferred_element_type=jnp.float32)
    out_ref[split:] = (z_ref[...] + carried * factor[split:]).astype(jnp.bfloat16)


def run_correct(first, second, c_first, c_second, g_tiles, entering):
    rows = first.shape[0] + second.shape[0]
    width = first.shape[1]
    tiles, _, heads_per = g_tiles.shape
    tile = CORRECT_TILE
    head_width = tile // heads_per
    n_size = c_first.shape[1]
    return pl.pallas_call(
        functools.partial(correct_kernel, head_width),
        grid=(tiles,),
        in_specs=[pl.BlockSpec((first.shape[0], tile), lambda j: (0, j)),
                  pl.BlockSpec((second.shape[0], tile), lambda j: (0, j)),
                  pl.BlockSpec((first.shape[0], n_size), lambda j: (0, 0)),
                  pl.BlockSpec((second.shape[0], n_size), lambda j: (0, 0)),
                  pl.BlockSpec((1, rows, heads_per), lambda j: (j, 0, 0)),
                  pl.BlockSpec((n_size, tile), lambda j: (0, j))],
        out_specs=pl.BlockSpec((rows, tile), lambda j: (0, j)),
        out_shape=jax.ShapeDtypeStruct((rows, width), jnp.bfloat16),
        compiler_params=pltpu.CompilerParams(dimension_semantics=("arbitrary",)),
    )(first, second, c_first, c_second, g_tiles, entering)


def run_blocks(with_y, x, b_full, c_full, l_t, dt_t, seg_row, seg_col, entry_col, decay_x,
               skip_x, entering):
    rows, width = x.shape
    head_count = l_t.shape[1]
    head_width = width // head_count
    n_size = b_full.shape[1]
    block_count = rows // BLOCK
    row_block = lambda cols: pl.BlockSpec((BLOCK, cols), lambda b: (b, 0))
    bt_spec = pl.BlockSpec((n_size, BLOCK), lambda b: (0, b))
    decay_spec = pl.BlockSpec((1, 1, width), lambda b: (b, 0, 0))
    state_spec = pl.BlockSpec((n_size, width), lambda b: (0, 0))
    state_shape = jax.ShapeDtypeStruct((n_size, width), jnp.float32)
    kernel = functools.partial(block_kernel, with_y, head_width)
    params = pltpu.CompilerParams(dimension_semantics=("arbitrary",))
    if with_y:
        return pl.pallas_call(
            kernel,
            grid=(block_count,),
            in_specs=[row_block(width), row_block(n_size), row_block(n_size),
                      row_block(head_count), row_block(head_count),
                      pl.BlockSpec((1, BLOCK), lambda b: (0, b)), row_block(seg_col.shape[1]),
                      decay_spec, pl.BlockSpec((1, width), lambda b: (0, 0)), state_spec],
            out_specs=row_block(width),
            out_shape=jax.ShapeDtypeStruct((rows, width), jnp.bfloat16),
            scratch_shapes=[pltpu.VMEM((n_size, width), jnp.float32)],
            compiler_params=params,
        )(x, b_full, c_full, l_t, dt_t, seg_row, seg_col, decay_x, skip_x, entering)
    return pl.pallas_call(
        kernel,
        grid=(block_count,),
        in_specs=[row_block(width), bt_spec, row_block(head_count), row_block(head_count),
                  row_block(1), decay_spec],
        out_specs=state_spec,
        out_shape=state_shape,
        compiler_params=params,
    )(x, b_t, l_t, dt_t, seg_col, decay_x)


def body(
    inner_input,
    state_input,
    conv_inner,
    bias_inner,
    conv_state,
    bias_state,
    step_size,
    decay_rate,
    skip_gain,
    lengths,
):
    own_rows = inner_input.shape[0]
    head_count = decay_rate.shape[0]
    group_half = state_input.shape[2]
    block_count = own_rows // BLOCK
    positions = lax.axis_index("seq") * own_rows + jnp.arange(own_rows + 3, dtype=jnp.int32) - 3
    seg_ext = segment_of(lengths, positions)
    width = inner_input.shape[1]
    tails = jnp.concatenate(
        [inner_input[-8:], jnp.transpose(state_input[:, -8:], (1, 0, 2)).reshape(8, -1)], 1
    )
    tails = shifted(tails, "seq", 1)
    state_tail = tails[:, width:].reshape(8, 2, group_half)
    extra = jnp.concatenate(
        [jnp.transpose(state_tail, (1, 0, 2)).astype(jnp.float32),
         conv_state.astype(jnp.float32), bias_state[:, None, :]],
        1,
    )
    partner_raw, partner_extra = from_partner((state_input, extra), "head", 0)
    lower_half = (lax.axis_index("head") % 2 == 0).astype(jnp.float32)
    head_width = inner_input.shape[1] // head_count
    spread = lambda v: jnp.repeat(v, head_width, axis=-1)
    skip_x = spread(skip_gain).reshape(1, -1)
    seg_own = seg_ext[3:].reshape(block_count, BLOCK)
    seg_prev = seg_ext[2 : 2 + own_rows].reshape(block_count, BLOCK)[:, 0]
    seg_row = seg_ext[3:].reshape(1, own_rows).astype(jnp.float32)
    own_seg = seg_ext[3:]
    entry_col = (seg_own == seg_prev[:, None]).reshape(own_rows)
    keeps = [(seg_ext[3 - back : 3 - back + own_rows] == own_seg) for back in (1, 2, 3)]
    info = jnp.stack(
        [own_seg.astype(jnp.float32), entry_col.astype(jnp.float32)]
        + [keep.astype(jnp.float32) for keep in keeps]
        + [jnp.zeros((own_rows,), jnp.float32), jnp.full((own_rows,), lower_half, jnp.float32),
           jnp.zeros((own_rows,), jnp.float32)],
        1,
    )

    (local_end, l_t, dt_t, decay_x, total_decay, inner_conv, b_full, end_sent,
     prefix_x, g_tiles) = run_state(
        inner_input, tails, conv_inner, bias_inner.reshape(1, -1), state_input, partner_raw,
        extra, partner_extra,
        step_size, decay_rate.reshape(1, -1), info
    )

    def relay(step_num, incoming):
        return shifted(
            (total_decay * incoming.astype(jnp.float32) + local_end).astype(jnp.bfloat16), "seq", 1
        )

    part_rows = own_rows * lax.axis_size("seq")
    hops = min(lax.axis_size("seq") - 1, -(-(part_rows // 2) // own_rows))
    half_blocks = block_count // 2
    c_raws = (state_input, partner_raw, extra, partner_extra)
    operands = (inner_conv, b_full, c_raws, l_t, dt_t, seg_row, info, decay_x, skip_x)
    incoming = shifted(end_sent, "seq", 1)
    partial, c_first, middle = run_partial(0, half_blocks, *operands)
    incoming, partial, c_first, middle = lax.optimization_barrier(
        (incoming, partial, c_first, middle)
    )
    first_hop = incoming
    for step_num in range(1, hops):
        incoming = relay(step_num, incoming)
    second, c_second = run_partial(
        half_blocks, block_count - half_blocks, *operands, init=middle, after=first_hop
    )
    return run_correct(partial, second, c_first, c_second, g_tiles, incoming)


def solution(mesh):
    return jax.shard_map(
        body,
        mesh=mesh,
        in_specs=(
            P(("grp", "seq"), "head"),
            P(None, ("grp", "seq"), "head"),
            P(None, "head"),
            P("head"),
            P(None, None, "head"),
            P(None, "head"),
            P("head", ("grp", "seq")),
            P("head"),
            P("head"),
            P("grp"),
        ),
        out_specs=P(("grp", "seq"), "head"),
        check_vma=False,
    )
```

```python
import functools

import jax
import jax.numpy as jnp
from jax import lax
from jax.experimental import pallas as pl
from jax.experimental.pallas import tpu as pltpu
from jax.sharding import PartitionSpec as P

BLOCK = 128
CORRECT_TILE = 512


def shifted(value, axis, steps):
    count = lax.axis_size(axis)
    initial, last = (max(0, -steps), min(count, count - steps))
    return lax.ppermute(value, axis, [(source, source + steps) for source in range(initial, last)])


def from_partner(block, axis, stride):
    count = lax.axis_size(axis)
    route = []
    for low in range(count):
        high = low | 1 << stride
        if high != low and high < count:
            route += [(low, high), (high, low)]
    return lax.ppermute(block, axis, route)


def segment_of(lengths, positions):
    starts = jnp.cumsum(lengths, dtype=jnp.int32) - lengths
    covered = (starts[None, :] <= positions[:, None]).astype(jnp.int32)
    return jnp.sum(covered, axis=1, dtype=jnp.int32) - 1


def convolve(extended, weight, bias_row, seg_ext, row_count):
    own_seg = seg_ext[3:]
    summed = (
        jnp.zeros(extended.shape[:-2] + (row_count, extended.shape[-1]), jnp.float32) + bias_row
    )
    for offset in range(4):
        kept_mask = (seg_ext[offset : offset + row_count] == own_seg).astype(jnp.float32)[:, None]
        window = extended[..., offset : offset + row_count, :].astype(jnp.float32)
        summed = summed + weight[offset].astype(jnp.float32) * window * kept_mask
    return jax.nn.silu(summed).astype(jnp.bfloat16)


def split_dot(lhs, value):
    high = value.astype(jnp.bfloat16)
    low = (value - high.astype(jnp.float32)).astype(jnp.bfloat16)
    return jnp.dot(lhs, high, preferred_element_type=jnp.float32) + jnp.dot(
        lhs, low, preferred_element_type=jnp.float32
    )


def expand_heads(small, head_width):
    rows, heads = small.shape
    per_tile = 128 // head_width
    lane = lax.broadcasted_iota(jnp.int32, (rows, 128), 1) // head_width
    tiles = []
    for tile in range(heads // per_tile):
        picked = jnp.broadcast_to(small[:, tile * per_tile : tile * per_tile + 1], (rows, 128))
        for k in range(1, per_tile):
            column = small[:, tile * per_tile + k : tile * per_tile + k + 1]
            picked = jnp.where(lane == k, jnp.broadcast_to(column, (rows, 128)), picked)
        tiles.append(picked)
    return jnp.concatenate(tiles, axis=1)


def block_kernel(with_y, head_width, *refs):
    if with_y:
        (x_ref, b_ref, c_ref, l_ref, dt_ref, segr_ref, info_ref, decay_ref,
         skip_ref, ein_ref, out_ref, state_ref) = refs
    else:
        (x_ref, b_ref, l_ref, dt_ref, segc_ref, decay_ref, state_ref) = refs
    blk = pl.program_id(0)

    @pl.when(blk == 0)
    def _():
        if with_y:
            state_ref[...] = ein_ref[...].astype(jnp.float32)
        else:
            state_ref[...] = jnp.zeros(state_ref.shape, jnp.float32)

    info = info_ref[...]
    seg_col = info[:, 0:1]
    end_col = (seg_col == seg_col[BLOCK - 1 : BLOCK, :]).astype(jnp.float32)
    l_small = l_ref[...]
    dt_small = dt_ref[...]
    x = x_ref[...].astype(jnp.float32)
    state = state_ref[...]
    if with_y:
        c_mat = c_ref[...]
        seg_row = segr_ref[...]
        scores = lax.dot_general(
            c_mat, b_ref[...], (((1,), (1,)), ((), ())), preferred_element_type=jnp.float32
        )
        rows = lax.broadcasted_iota(jnp.int32, (BLOCK, BLOCK), 0)
        cols = lax.broadcasted_iota(jnp.int32, (BLOCK, BLOCK), 1)
        allowed = (rows >= cols) & (seg_col == seg_row)
        masked = jnp.where(allowed, scores, 0.0).astype(jnp.bfloat16)
        rising = expand_heads(jnp.exp(l_small), head_width)
        falling = expand_heads(jnp.exp(-l_small) * dt_small, head_width)
        intra = split_dot(masked, x * falling) * rising
        inter = split_dot(c_mat, state) * (rising * info[:, 1:2])
        out_ref[...] = (intra + inter + skip_ref[...] * x).astype(jnp.bfloat16)
    ending = expand_heads(
        jnp.exp(l_small[BLOCK - 1 : BLOCK, :] - l_small) * dt_small * end_col, head_width
    )
    weighted = (x * ending).astype(jnp.bfloat16)
    state_ref[...] = decay_ref[0] * state + lax.dot_general(
        b_ref[...], weighted, (((0,), (0,)), ((), ())), preferred_element_type=jnp.float32
    )


def causal_conv(raw, prev, taps, bias, info):
    top_row = lax.broadcasted_iota(jnp.int32, prev.shape, 0)
    summed = jnp.zeros(raw.shape, jnp.float32) + bias
    for offset in range(4):
        back = 3 - offset
        if back == 0:
            window = raw
        else:
            rolled = pltpu.roll(raw, back, 0)
            top = jnp.where(top_row < back, pltpu.roll(prev, back, 0), rolled[:8])
            window = jnp.concatenate([top, rolled[8:]], 0) * info[:, 1 + back : 2 + back]
        summed = summed + taps[offset : offset + 1, :] * window
    return jax.nn.silu(summed).astype(jnp.bfloat16)


def state_block(head_width, x_ref, tail_ref, wconv_ref, bias_ref, own_ref, other_ref, ownx_ref,
                 otherx_ref, dt_ref, rate_ref, info_ref, state_ref, l_ref, dtt_ref,
                 decay_ref, total_ref, xc_ref, bo_ref, sent_ref, prefix_ref, ltile_ref,
                 prev_ref, bcprev_ref, small_ref):
    info = info_ref[...]
    raw = x_ref[...].astype(jnp.float32)
    xc = causal_conv(raw, prev_ref[...], wconv_ref[...].astype(jnp.float32), bias_ref[...], info)
    prev_ref[...] = raw[BLOCK - 8 :]
    xc_ref[...] = xc
    lower = info_ref[0:1, 5:6] > 0.5
    convolved = []
    for which in range(1):
        halves = []
        for side, (raw_ref, extra_ref) in enumerate(((own_ref, ownx_ref), (other_ref, otherx_ref))):
            raw_bc = raw_ref[which].astype(jnp.float32)
            extra = extra_ref[which]
            halves.append(
                causal_conv(raw_bc, bcprev_ref[side, which], extra[8:12], extra[12:13], info)
            )
            bcprev_ref[side, which] = raw_bc[BLOCK - 8 :]
        convolved.append(jnp.where(
            lower, jnp.concatenate(halves, 1), jnp.concatenate(halves[::-1], 1)
        ))
    b_mat = convolved[0]
    bo_ref[...] = b_mat

    rows = lax.broadcasted_iota(jnp.int32, (2 * BLOCK, BLOCK), 0)
    cols = lax.broadcasted_iota(jnp.int32, (2 * BLOCK, BLOCK), 1)
    picker = jnp.where(
        ((rows < BLOCK) & (rows >= cols)) | (rows - BLOCK == cols), 1.0, 0.0
    ).astype(jnp.bfloat16)
    rest = dt_ref[...]
    cum = None
    for _ in range(3):
        piece = rest.astype(jnp.bfloat16)
        part = lax.dot_general(
            picker, piece, (((1,), (1,)), ((), ())), preferred_element_type=jnp.float32
        )
        cum = part if cum is None else cum + part
        rest = rest - piece.astype(jnp.float32)
    l_small = -cum[:BLOCK] * rate_ref[...]
    dt_small = cum[BLOCK:]
    l_ref[...] = l_small
    dtt_ref[...] = dt_small
    seg_col = info[:, 0:1]
    end_col = (seg_col == seg_col[BLOCK - 1 : BLOCK, :]).astype(jnp.float32)
    decay_x = expand_heads(
        jnp.exp(l_small[BLOCK - 1 : BLOCK, :]) * info[BLOCK - 1 : BLOCK, 1:2], head_width
    )
    decay_ref[0] = decay_x
    prefix_ref[0] = total_ref[...]
    total_ref[...] = total_ref[...] * decay_x
    carry = (jnp.exp(l_small) * info[:, 1:2]) * small_ref[...]
    small_ref[...] = small_ref[...] * (
        jnp.exp(l_small[BLOCK - 1 : BLOCK, :]) * info[BLOCK - 1 : BLOCK, 1:2]
    )
    tile_heads = ltile_ref.shape[2]
    for tile in range(ltile_ref.shape[0]):
        ltile_ref[tile] = carry[:, tile * tile_heads : (tile + 1) * tile_heads]
    ending = expand_heads(
        jnp.exp(l_small[BLOCK - 1 : BLOCK, :] - l_small) * dt_small * end_col, head_width
    )
    weighted = (xc.astype(jnp.float32) * ending).astype(jnp.bfloat16)
    new_state = decay_x * state_ref[...] + lax.dot_general(
        b_mat, weighted, (((0,), (0,)), ((), ())), preferred_element_type=jnp.float32
    )
    state_ref[...] = new_state


def state_kernel(head_width, per_step, x_ref, tail_ref, wconv_ref, bias_ref, own_ref, other_ref,
                 ownx_ref, otherx_ref, dt_ref, rate_ref, info_ref, state_ref, l_ref, dtt_ref,
                 decay_ref, total_ref, xc_ref, bo_ref, sent_ref, prefix_ref, ltile_ref,
                 prev_ref, bcprev_ref, small_ref):
    blk = pl.program_id(0)

    @pl.when(blk == 0)
    def _():
        state_ref[...] = jnp.zeros(state_ref.shape, jnp.float32)
        total_ref[...] = jnp.ones(total_ref.shape, jnp.float32)
        prev_ref[...] = tail_ref[:, : x_ref.shape[1]].astype(jnp.float32)
        small_ref[...] = jnp.ones(small_ref.shape, jnp.float32)
        bcprev_ref[0] = ownx_ref[:, 0:8, :]
        bcprev_ref[1] = otherx_ref[:, 0:8, :]

    for sub in range(per_step):
        rows = pl.ds(sub * BLOCK, BLOCK)
        state_block(
            head_width, x_ref.at[rows, :], tail_ref, wconv_ref, bias_ref, own_ref.at[:, rows, :],
            other_ref.at[:, rows, :], ownx_ref, otherx_ref, dt_ref.at[:, rows], rate_ref,
            info_ref.at[rows, :], state_ref, l_ref.at[rows, :], dtt_ref.at[rows, :],
            decay_ref.at[pl.ds(sub, 1)], total_ref, xc_ref.at[rows, :], bo_ref.at[rows, :],
            sent_ref, prefix_ref.at[pl.ds(sub, 1)], ltile_ref.at[:, rows, :], prev_ref,
            bcprev_ref, small_ref,
        )

    @pl.when(blk == pl.num_programs(0) - 1)
    def _():
        sent_ref[...] = state_ref[...].astype(jnp.bfloat16)


def run_state(x, tails, wconv, bias_row, own_raw, other_raw, own_extra, other_extra,
              step_size, rate_row, info):
    rows, width = x.shape
    head_count = step_size.shape[0]
    half = own_raw.shape[2]
    n_size = 2 * half
    block_count = rows // BLOCK
    tiles = width // CORRECT_TILE
    tile_heads = head_count // tiles
    per_step = 2 if block_count % 2 == 0 else 1
    step_rows = per_step * BLOCK
    row_block = lambda cols: pl.BlockSpec((step_rows, cols), lambda b: (b, 0))
    whole = lambda shape: pl.BlockSpec(shape, lambda b: (0,) * len(shape))
    return pl.pallas_call(
        functools.partial(state_kernel, width // head_count, per_step),
        grid=(block_count // per_step,),
        in_specs=[row_block(width), whole(tails.shape), whole((4, width)), whole((1, width)),
                  pl.BlockSpec((2, step_rows, half), lambda b: (0, b, 0)),
                  pl.BlockSpec((2, step_rows, half), lambda b: (0, b, 0)),
                  whole(own_extra.shape), whole(own_extra.shape),
                  pl.BlockSpec((head_count, step_rows), lambda b: (0, b)),
                  whole((1, head_count)), row_block(info.shape[1])],
        out_specs=[whole((n_size, width)), row_block(head_count), row_block(head_count),
                   pl.BlockSpec((per_step, 1, width), lambda b: (b, 0, 0)), whole((1, width)),
                   row_block(width), row_block(n_size),
                   whole((n_size, width)), pl.BlockSpec((per_step, 1, width), lambda b: (b, 0, 0)),
                   pl.BlockSpec((tiles, step_rows, tile_heads), lambda b: (0, b, 0))],
        out_shape=[jax.ShapeDtypeStruct((n_size, width), jnp.float32),
                   jax.ShapeDtypeStruct((rows, head_count), jnp.float32),
                   jax.ShapeDtypeStruct((rows, head_count), jnp.float32),
                   jax.ShapeDtypeStruct((block_count, 1, width), jnp.float32),
                   jax.ShapeDtypeStruct((1, width), jnp.float32),
                   jax.ShapeDtypeStruct((rows, width), jnp.bfloat16),
                   jax.ShapeDtypeStruct((rows, n_size), jnp.bfloat16),
                   jax.ShapeDtypeStruct((n_size, width), jnp.bfloat16),
                   jax.ShapeDtypeStruct((block_count, 1, width), jnp.float32),
                   jax.ShapeDtypeStruct((tiles, rows, tile_heads), jnp.float32)],
        scratch_shapes=[pltpu.VMEM((8, width), jnp.float32),
                        pltpu.VMEM((2, 2, 8, half), jnp.float32),
                        pltpu.VMEM((1, head_count), jnp.float32)],
        compiler_params=pltpu.CompilerParams(dimension_semantics=("arbitrary",)),
    )(x, tails, wconv, bias_row, own_raw, other_raw, own_extra, other_extra, step_size,
      rate_row, info)


def partial_kernel(head_width, from_zero, *refs):
    if from_zero:
        (x_ref, b_ref, cown_ref, cother_ref, ownx_ref, otherx_ref, l_ref, dt_ref, segr_ref,
         info_ref, decay_ref, skip_ref, out_ref, cout_ref, end_ref, state_ref, cprev_ref) = refs
    else:
        (x_ref, b_ref, cown_ref, cother_ref, ownx_ref, otherx_ref, l_ref, dt_ref, segr_ref,
         info_ref, decay_ref, skip_ref, init_ref, after_ref, pown_ref, pother_ref, out_ref,
         cout_ref, state_ref, cprev_ref) = refs
    blk = pl.program_id(0)

    @pl.when(blk == 0)
    def _():
        if from_zero:
            state_ref[...] = jnp.zeros(state_ref.shape, jnp.float32)
            cprev_ref[0] = ownx_ref[1, 0:8, :]
            cprev_ref[1] = otherx_ref[1, 0:8, :]
        else:
            state_ref[...] = init_ref[...]
            cprev_ref[0] = pown_ref[0, 8:16, :].astype(jnp.float32)
            cprev_ref[1] = pother_ref[0, 8:16, :].astype(jnp.float32)

    info = info_ref[...]
    seg_col = info[:, 0:1]
    end_col = (seg_col == seg_col[BLOCK - 1 : BLOCK, :]).astype(jnp.float32)
    l_small = l_ref[...]
    dt_small = dt_ref[...]
    x = x_ref[...].astype(jnp.float32)
    state = state_ref[...]
    halves = []
    for side, (raw_ref, extra_ref) in enumerate(((cown_ref, ownx_ref), (cother_ref, otherx_ref))):
        raw_c = raw_ref[0].astype(jnp.float32)
        extra = extra_ref[1]
        halves.append(causal_conv(raw_c, cprev_ref[side], extra[8:12], extra[12:13], info))
        cprev_ref[side] = raw_c[BLOCK - 8 :]
    lower = info_ref[0:1, 5:6] > 0.5
    c_mat = jnp.where(lower, jnp.concatenate(halves, 1), jnp.concatenate(halves[::-1], 1))
    cout_ref[...] = c_mat
    b_mat = b_ref[...]
    scores = lax.dot_general(
        c_mat, b_mat, (((1,), (1,)), ((), ())), preferred_element_type=jnp.float32
    )
    rows = lax.broadcasted_iota(jnp.int32, (BLOCK, BLOCK), 0)
    cols = lax.broadcasted_iota(jnp.int32, (BLOCK, BLOCK), 1)
    allowed = (rows >= cols) & (seg_col == segr_ref[...])
    masked = jnp.where(allowed, scores, 0.0).astype(jnp.bfloat16)
    rising = expand_heads(jnp.exp(l_small), head_width)
    falling = expand_heads(jnp.exp(-l_small) * dt_small, head_width)
    intra = split_dot(masked, x * falling) * rising
    inter = split_dot(c_mat, state) * (rising * info[:, 1:2])
    out_ref[...] = intra + inter + skip_ref[...] * x
    last = blk == pl.num_programs(0) - 1

    @pl.when(jnp.logical_or(jnp.logical_not(last), from_zero))
    def _():
        ending = expand_heads(
            jnp.exp(l_small[BLOCK - 1 : BLOCK, :] - l_small) * dt_small * end_col, head_width
        )
        weighted = (x * ending).astype(jnp.bfloat16)
        new_state = decay_ref[0] * state + lax.dot_general(
            b_mat, weighted, (((0,), (0,)), ((), ())), preferred_element_type=jnp.float32
        )
        state_ref[...] = new_state
        if from_zero:

            @pl.when(last)
            def _():
                end_ref[...] = new_state


def run_partial(first, count, x, b_full, c_raws, l_t, dt_t, seg_row, info, decay_x, skip_x,
                init=None, after=None):
    rows, width = x.shape
    head_count = l_t.shape[1]
    n_size = b_full.shape[1]
    own_raw, other_raw, own_extra, other_extra = c_raws
    half = own_raw.shape[2]
    row_block = lambda cols: pl.BlockSpec((BLOCK, cols), lambda b: (b + first, 0))
    whole = lambda shape: pl.BlockSpec(shape, lambda b: (0,) * len(shape))
    from_zero = init is None
    plane = pl.BlockSpec((1, BLOCK, half), lambda b: (1, b + first, 0))
    in_specs = [row_block(width), row_block(n_size), plane, plane, whole(own_extra.shape),
                whole(own_extra.shape), row_block(head_count),
                row_block(head_count), pl.BlockSpec((1, BLOCK), lambda b: (0, b + first)),
                row_block(info.shape[1]), pl.BlockSpec((1, 1, width), lambda b: (b + first, 0, 0)),
                whole((1, width))]
    args = [x, b_full, own_raw, other_raw, own_extra, other_extra, l_t, dt_t, seg_row, info,
            decay_x, skip_x]
    if not from_zero:
        before = pl.BlockSpec((1, 16, half), lambda b: (1, first * (BLOCK // 16) - 1, 0))
        in_specs += [whole((n_size, width)), pl.BlockSpec(memory_space=pl.ANY), before, before]
        args += [init, after, own_raw, other_raw]
    out_specs = [pl.BlockSpec((BLOCK, width), lambda b: (b, 0)),
                 pl.BlockSpec((BLOCK, n_size), lambda b: (b, 0))]
    out_shape = [jax.ShapeDtypeStruct((count * BLOCK, width), jnp.float32),
                 jax.ShapeDtypeStruct((count * BLOCK, n_size), jnp.bfloat16)]
    if from_zero:
        out_specs.append(whole((n_size, width)))
        out_shape.append(jax.ShapeDtypeStruct((n_size, width), jnp.float32))
    return pl.pallas_call(
        functools.partial(partial_kernel, width // head_count, from_zero),
        grid=(count,),
        in_specs=in_specs,
        out_specs=out_specs,
        out_shape=out_shape,
        scratch_shapes=[pltpu.VMEM((n_size, width), jnp.float32),
                        pltpu.VMEM((2, 8, half), jnp.float32)],
        compiler_params=pltpu.CompilerParams(dimension_semantics=("arbitrary",)),
    )(*args)


def correct_kernel(head_width, y_ref, z_ref, c_ref, d_ref, g_ref, ein_ref, out_ref):
    factor = expand_heads(g_ref[0], head_width)
    ein = ein_ref[...]
    split = y_ref.shape[0]
    carried = jnp.dot(c_ref[...], ein, preferred_element_type=jnp.float32)
    out_ref[:split] = (y_ref[...] + carried * factor[:split]).astype(jnp.bfloat16)
    carried = jnp.dot(d_ref[...], ein, preferred_element_type=jnp.float32)
    out_ref[split:] = (z_ref[...] + carried * factor[split:]).astype(jnp.bfloat16)


def run_correct(first, second, c_first, c_second, g_tiles, entering):
    rows = first.shape[0] + second.shape[0]
    width = first.shape[1]
    tiles, _, heads_per = g_tiles.shape
    tile = CORRECT_TILE
    head_width = tile // heads_per
    n_size = c_first.shape[1]
    return pl.pallas_call(
        functools.partial(correct_kernel, head_width),
        grid=(tiles,),
        in_specs=[pl.BlockSpec((first.shape[0], tile), lambda j: (0, j)),
                  pl.BlockSpec((second.shape[0], tile), lambda j: (0, j)),
                  pl.BlockSpec((first.shape[0], n_size), lambda j: (0, 0)),
                  pl.BlockSpec((second.shape[0], n_size), lambda j: (0, 0)),
                  pl.BlockSpec((1, rows, heads_per), lambda j: (j, 0, 0)),
                  pl.BlockSpec((n_size, tile), lambda j: (0, j))],
        out_specs=pl.BlockSpec((rows, tile), lambda j: (0, j)),
        out_shape=jax.ShapeDtypeStruct((rows, width), jnp.bfloat16),
        compiler_params=pltpu.CompilerParams(dimension_semantics=("arbitrary",)),
    )(first, second, c_first, c_second, g_tiles, entering)


def run_blocks(with_y, x, b_full, c_full, l_t, dt_t, seg_row, seg_col, entry_col, decay_x,
               skip_x, entering):
    rows, width = x.shape
    head_count = l_t.shape[1]
    head_width = width // head_count
    n_size = b_full.shape[1]
    block_count = rows // BLOCK
    row_block = lambda cols: pl.BlockSpec((BLOCK, cols), lambda b: (b, 0))
    bt_spec = pl.BlockSpec((n_size, BLOCK), lambda b: (0, b))
    decay_spec = pl.BlockSpec((1, 1, width), lambda b: (b, 0, 0))
    state_spec = pl.BlockSpec((n_size, width), lambda b: (0, 0))
    state_shape = jax.ShapeDtypeStruct((n_size, width), jnp.float32)
    kernel = functools.partial(block_kernel, with_y, head_width)
    params = pltpu.CompilerParams(dimension_semantics=("arbitrary",))
    if with_y:
        return pl.pallas_call(
            kernel,
            grid=(block_count,),
            in_specs=[row_block(width), row_block(n_size), row_block(n_size),
                      row_block(head_count), row_block(head_count),
                      pl.BlockSpec((1, BLOCK), lambda b: (0, b)), row_block(seg_col.shape[1]),
                      decay_spec, pl.BlockSpec((1, width), lambda b: (0, 0)), state_spec],
            out_specs=row_block(width),
            out_shape=jax.ShapeDtypeStruct((rows, width), jnp.bfloat16),
            scratch_shapes=[pltpu.VMEM((n_size, width), jnp.float32)],
            compiler_params=params,
        )(x, b_full, c_full, l_t, dt_t, seg_row, seg_col, decay_x, skip_x, entering)
    return pl.pallas_call(
        kernel,
        grid=(block_count,),
        in_specs=[row_block(width), bt_spec, row_block(head_count), row_block(head_count),
                  row_block(1), decay_spec],
        out_specs=state_spec,
        out_shape=state_shape,
        compiler_params=params,
    )(x, b_t, l_t, dt_t, seg_col, decay_x)


def body(
    inner_input,
    state_input,
    conv_inner,
    bias_inner,
    conv_state,
    bias_state,
    step_size,
    decay_rate,
    skip_gain,
    lengths,
):
    own_rows = inner_input.shape[0]
    head_count = decay_rate.shape[0]
    group_half = state_input.shape[2]
    block_count = own_rows // BLOCK
    positions = lax.axis_index("seq") * own_rows + jnp.arange(own_rows + 3, dtype=jnp.int32) - 3
    seg_ext = segment_of(lengths, positions)
    width = inner_input.shape[1]
    tails = jnp.concatenate(
        [inner_input[-8:], jnp.transpose(state_input[:, -8:], (1, 0, 2)).reshape(8, -1)], 1
    )
    tails = shifted(tails, "seq", 1)
    state_tail = tails[:, width:].reshape(8, 2, group_half)
    extra = jnp.concatenate(
        [jnp.transpose(state_tail, (1, 0, 2)).astype(jnp.float32),
         conv_state.astype(jnp.float32), bias_state[:, None, :]],
        1,
    )
    partner_raw, partner_extra = from_partner((state_input, extra), "head", 0)
    lower_half = (lax.axis_index("head") % 2 == 0).astype(jnp.float32)
    head_width = inner_input.shape[1] // head_count
    spread = lambda v: jnp.repeat(v, head_width, axis=-1)
    skip_x = spread(skip_gain).reshape(1, -1)
    seg_own = seg_ext[3:].reshape(block_count, BLOCK)
    seg_prev = seg_ext[2 : 2 + own_rows].reshape(block_count, BLOCK)[:, 0]
    seg_row = seg_ext[3:].reshape(1, own_rows).astype(jnp.float32)
    own_seg = seg_ext[3:]
    entry_col = (seg_own == seg_prev[:, None]).reshape(own_rows)
    keeps = [(seg_ext[3 - back : 3 - back + own_rows] == own_seg) for back in (1, 2, 3)]
    info = jnp.stack(
        [own_seg.astype(jnp.float32), entry_col.astype(jnp.float32)]
        + [keep.astype(jnp.float32) for keep in keeps]
        + [jnp.zeros((own_rows,), jnp.float32), jnp.full((own_rows,), lower_half, jnp.float32),
           jnp.zeros((own_rows,), jnp.float32)],
        1,
    )

    (local_end, l_t, dt_t, decay_x, total_decay, inner_conv, b_full, end_sent,
     prefix_x, g_tiles) = run_state(
        inner_input, tails, conv_inner, bias_inner.reshape(1, -1), state_input, partner_raw,
        extra, partner_extra,
        step_size, decay_rate.reshape(1, -1), info
    )

    def relay(step_num, incoming):
        return shifted(
            (total_decay * incoming.astype(jnp.float32) + local_end).astype(jnp.bfloat16), "seq", 1
        )

    part_rows = own_rows * lax.axis_size("seq")
    hops = min(lax.axis_size("seq") - 1, -(-(part_rows // 2) // own_rows))
    half_blocks = block_count // 2
    c_raws = (state_input, partner_raw, extra, partner_extra)
    operands = (inner_conv, b_full, c_raws, l_t, dt_t, seg_row, info, decay_x, skip_x)
    incoming = shifted(end_sent, "seq", 1)
    partial, c_first, middle = run_partial(0, half_blocks, *operands)
    incoming, partial, c_first, middle = lax.optimization_barrier(
        (incoming, partial, c_first, middle)
    )
    first_hop = incoming
    for step_num in range(1, hops):
        incoming = relay(step_num, incoming)
    second, c_second = run_partial(
        half_blocks, block_count - half_blocks, *operands, init=middle, after=first_hop
    )
    return run_correct(partial, second, c_first, c_second, g_tiles, incoming)


def solution(mesh):
    return jax.shard_map(
        body,
        mesh=mesh,
        in_specs=(
            P(("grp", "seq"), "head"),
            P(None, ("grp", "seq"), "head"),
            P(None, "head"),
            P("head"),
            P(None, None, "head"),
            P(None, "head"),
            P("head", ("grp", "seq")),
            P("head"),
            P("head"),
            P("grp"),
        ),
        out_specs=P(("grp", "seq"), "head"),
        check_vma=False,
    )
```

```python
import functools

import jax
import jax.numpy as jnp
from jax import lax
from jax.experimental import pallas as pl
from jax.experimental.pallas import tpu as pltpu
from jax.sharding import PartitionSpec as P

BLOCK = 128
CORRECT_TILE = 512


def shifted(value, axis, steps):
    count = lax.axis_size(axis)
    initial, last = (max(0, -steps), min(count, count - steps))
    return lax.ppermute(value, axis, [(source, source + steps) for source in range(initial, last)])


def from_partner(block, axis, stride):
    count = lax.axis_size(axis)
    route = []
    for low in range(count):
        high = low | 1 << stride
        if high != low and high < count:
            route += [(low, high), (high, low)]
    return lax.ppermute(block, axis, route)


def segment_of(lengths, positions):
    starts = jnp.cumsum(lengths, dtype=jnp.int32) - lengths
    covered = (starts[None, :] <= positions[:, None]).astype(jnp.int32)
    return jnp.sum(covered, axis=1, dtype=jnp.int32) - 1


def convolve(extended, weight, bias_row, seg_ext, row_count):
    own_seg = seg_ext[3:]
    summed = (
        jnp.zeros(extended.shape[:-2] + (row_count, extended.shape[-1]), jnp.float32) + bias_row
    )
    for offset in range(4):
        kept_mask = (seg_ext[offset : offset + row_count] == own_seg).astype(jnp.float32)[:, None]
        window = extended[..., offset : offset + row_count, :].astype(jnp.float32)
        summed = summed + weight[offset].astype(jnp.float32) * window * kept_mask
    return jax.nn.silu(summed).astype(jnp.bfloat16)


def split_dot(lhs, value):
    high = value.astype(jnp.bfloat16)
    low = (value - high.astype(jnp.float32)).astype(jnp.bfloat16)
    return jnp.dot(lhs, high, preferred_element_type=jnp.float32) + jnp.dot(
        lhs, low, preferred_element_type=jnp.float32
    )


def expand_heads(small, head_width):
    rows, heads = small.shape
    per_tile = 128 // head_width
    lane = lax.broadcasted_iota(jnp.int32, (rows, 128), 1) // head_width
    tiles = []
    for tile in range(heads // per_tile):
        picked = jnp.broadcast_to(small[:, tile * per_tile : tile * per_tile + 1], (rows, 128))
        for k in range(1, per_tile):
            column = small[:, tile * per_tile + k : tile * per_tile + k + 1]
            picked = jnp.where(lane == k, jnp.broadcast_to(column, (rows, 128)), picked)
        tiles.append(picked)
    return jnp.concatenate(tiles, axis=1)


def block_kernel(with_y, head_width, *refs):
    if with_y:
        (x_ref, b_ref, c_ref, l_ref, dt_ref, segr_ref, info_ref, decay_ref,
         skip_ref, ein_ref, out_ref, state_ref) = refs
    else:
        (x_ref, b_ref, l_ref, dt_ref, segc_ref, decay_ref, state_ref) = refs
    blk = pl.program_id(0)

    @pl.when(blk == 0)
    def _():
        if with_y:
            state_ref[...] = ein_ref[...].astype(jnp.float32)
        else:
            state_ref[...] = jnp.zeros(state_ref.shape, jnp.float32)

    info = info_ref[...]
    seg_col = info[:, 0:1]
    end_col = (seg_col == seg_col[BLOCK - 1 : BLOCK, :]).astype(jnp.float32)
    l_small = l_ref[...]
    dt_small = dt_ref[...]
    x = x_ref[...].astype(jnp.float32)
    state = state_ref[...]
    if with_y:
        c_mat = c_ref[...]
        seg_row = segr_ref[...]
        scores = lax.dot_general(
            c_mat, b_ref[...], (((1,), (1,)), ((), ())), preferred_element_type=jnp.float32
        )
        rows = lax.broadcasted_iota(jnp.int32, (BLOCK, BLOCK), 0)
        cols = lax.broadcasted_iota(jnp.int32, (BLOCK, BLOCK), 1)
        allowed = (rows >= cols) & (seg_col == seg_row)
        masked = jnp.where(allowed, scores, 0.0).astype(jnp.bfloat16)
        rising = expand_heads(jnp.exp(l_small), head_width)
        falling = expand_heads(jnp.exp(-l_small) * dt_small, head_width)
        intra = split_dot(masked, x * falling) * rising
        inter = split_dot(c_mat, state) * (rising * info[:, 1:2])
        out_ref[...] = (intra + inter + skip_ref[...] * x).astype(jnp.bfloat16)
    ending = expand_heads(
        jnp.exp(l_small[BLOCK - 1 : BLOCK, :] - l_small) * dt_small * end_col, head_width
    )
    weighted = (x * ending).astype(jnp.bfloat16)
    state_ref[...] = decay_ref[0] * state + lax.dot_general(
        b_ref[...], weighted, (((0,), (0,)), ((), ())), preferred_element_type=jnp.float32
    )


def causal_conv(raw, prev, taps, bias, info):
    top_row = lax.broadcasted_iota(jnp.int32, prev.shape, 0)
    summed = jnp.zeros(raw.shape, jnp.float32) + bias
    for offset in range(4):
        back = 3 - offset
        if back == 0:
            window = raw
        else:
            rolled = pltpu.roll(raw, back, 0)
            top = jnp.where(top_row < back, pltpu.roll(prev, back, 0), rolled[:8])
            window = jnp.concatenate([top, rolled[8:]], 0) * info[:, 1 + back : 2 + back]
        summed = summed + taps[offset : offset + 1, :] * window
    return jax.nn.silu(summed).astype(jnp.bfloat16)


def state_block(head_width, x_ref, tail_ref, wconv_ref, bias_ref, own_ref, other_ref, ownx_ref,
                 otherx_ref, dt_ref, rate_ref, info_ref, state_ref, l_ref, dtt_ref,
                 decay_ref, total_ref, xc_ref, bo_ref, sent_ref, prefix_ref, ltile_ref,
                 prev_ref, bcprev_ref, small_ref):
    info = info_ref[...]
    raw = x_ref[...].astype(jnp.float32)
    xc = causal_conv(raw, prev_ref[...], wconv_ref[...].astype(jnp.float32), bias_ref[...], info)
    prev_ref[...] = raw[BLOCK - 8 :]
    xc_ref[...] = xc
    lower = info_ref[0:1, 5:6] > 0.5
    convolved = []
    for which in range(1):
        halves = []
        for side, (raw_ref, extra_ref) in enumerate(((own_ref, ownx_ref), (other_ref, otherx_ref))):
            raw_bc = raw_ref[which].astype(jnp.float32)
            extra = extra_ref[which]
            halves.append(
                causal_conv(raw_bc, bcprev_ref[side, which], extra[8:12], extra[12:13], info)
            )
            bcprev_ref[side, which] = raw_bc[BLOCK - 8 :]
        convolved.append(jnp.where(
            lower, jnp.concatenate(halves, 1), jnp.concatenate(halves[::-1], 1)
        ))
    b_mat = convolved[0]
    bo_ref[...] = b_mat

    rows = lax.broadcasted_iota(jnp.int32, (2 * BLOCK, BLOCK), 0)
    cols = lax.broadcasted_iota(jnp.int32, (2 * BLOCK, BLOCK), 1)
    picker = jnp.where(
        ((rows < BLOCK) & (rows >= cols)) | (rows - BLOCK == cols), 1.0, 0.0
    ).astype(jnp.bfloat16)
    rest = dt_ref[...]
    cum = None
    for _ in range(3):
        piece = rest.astype(jnp.bfloat16)
        part = lax.dot_general(
            picker, piece, (((1,), (1,)), ((), ())), preferred_element_type=jnp.float32
        )
        cum = part if cum is None else cum + part
        rest = rest - piece.astype(jnp.float32)
    l_small = -cum[:BLOCK] * rate_ref[...]
    dt_small = cum[BLOCK:]
    l_ref[...] = l_small
    dtt_ref[...] = dt_small
    seg_col = info[:, 0:1]
    end_col = (seg_col == seg_col[BLOCK - 1 : BLOCK, :]).astype(jnp.float32)
    decay_x = expand_heads(
        jnp.exp(l_small[BLOCK - 1 : BLOCK, :]) * info[BLOCK - 1 : BLOCK, 1:2], head_width
    )
    decay_ref[0] = decay_x
    prefix_ref[0] = total_ref[...]
    total_ref[...] = total_ref[...] * decay_x
    carry = (jnp.exp(l_small) * info[:, 1:2]) * small_ref[...]
    small_ref[...] = small_ref[...] * (
        jnp.exp(l_small[BLOCK - 1 : BLOCK, :]) * info[BLOCK - 1 : BLOCK, 1:2]
    )
    tile_heads = ltile_ref.shape[2]
    for tile in range(ltile_ref.shape[0]):
        ltile_ref[tile] = carry[:, tile * tile_heads : (tile + 1) * tile_heads]
    ending = expand_heads(
        jnp.exp(l_small[BLOCK - 1 : BLOCK, :] - l_small) * dt_small * end_col, head_width
    )
    weighted = (xc.astype(jnp.float32) * ending).astype(jnp.bfloat16)
    new_state = decay_x * state_ref[...] + lax.dot_general(
        b_mat, weighted, (((0,), (0,)), ((), ())), preferred_element_type=jnp.float32
    )
    state_ref[...] = new_state


def state_kernel(head_width, per_step, x_ref, tail_ref, wconv_ref, bias_ref, own_ref, other_ref,
                 ownx_ref, otherx_ref, dt_ref, rate_ref, info_ref, state_ref, l_ref, dtt_ref,
                 decay_ref, total_ref, xc_ref, bo_ref, sent_ref, prefix_ref, ltile_ref,
                 prev_ref, bcprev_ref, small_ref):
    blk = pl.program_id(0)

    @pl.when(blk == 0)
    def _():
        state_ref[...] = jnp.zeros(state_ref.shape, jnp.float32)
        total_ref[...] = jnp.ones(total_ref.shape, jnp.float32)
        prev_ref[...] = tail_ref[:, : x_ref.shape[1]].astype(jnp.float32)
        small_ref[...] = jnp.ones(small_ref.shape, jnp.float32)
        bcprev_ref[0] = ownx_ref[:, 0:8, :]
        bcprev_ref[1] = otherx_ref[:, 0:8, :]

    for sub in range(per_step):
        rows = pl.ds(sub * BLOCK, BLOCK)
        state_block(
            head_width, x_ref.at[rows, :], tail_ref, wconv_ref, bias_ref, own_ref.at[:, rows, :],
            other_ref.at[:, rows, :], ownx_ref, otherx_ref, dt_ref.at[:, rows], rate_ref,
            info_ref.at[rows, :], state_ref, l_ref.at[rows, :], dtt_ref.at[rows, :],
            decay_ref.at[pl.ds(sub, 1)], total_ref, xc_ref.at[rows, :], bo_ref.at[rows, :],
            sent_ref, prefix_ref.at[pl.ds(sub, 1)], ltile_ref.at[:, rows, :], prev_ref,
            bcprev_ref, small_ref,
        )

    @pl.when(blk == pl.num_programs(0) - 1)
    def _():
        sent_ref[...] = state_ref[...].astype(jnp.bfloat16)


def run_state(x, tails, wconv, bias_row, own_raw, other_raw, own_extra, other_extra,
              step_size, rate_row, info):
    rows, width = x.shape
    head_count = step_size.shape[0]
    half = own_raw.shape[2]
    n_size = 2 * half
    block_count = rows // BLOCK
    tiles = width // CORRECT_TILE
    tile_heads = head_count // tiles
    per_step = 4 if block_count % 4 == 0 else 1
    step_rows = per_step * BLOCK
    row_block = lambda cols: pl.BlockSpec((step_rows, cols), lambda b: (b, 0))
    whole = lambda shape: pl.BlockSpec(shape, lambda b: (0,) * len(shape))
    return pl.pallas_call(
        functools.partial(state_kernel, width // head_count, per_step),
        grid=(block_count // per_step,),
        in_specs=[row_block(width), whole(tails.shape), whole((4, width)), whole((1, width)),
                  pl.BlockSpec((2, step_rows, half), lambda b: (0, b, 0)),
                  pl.BlockSpec((2, step_rows, half), lambda b: (0, b, 0)),
                  whole(own_extra.shape), whole(own_extra.shape),
                  pl.BlockSpec((head_count, step_rows), lambda b: (0, b)),
                  whole((1, head_count)), row_block(info.shape[1])],
        out_specs=[whole((n_size, width)), row_block(head_count), row_block(head_count),
                   pl.BlockSpec((per_step, 1, width), lambda b: (b, 0, 0)), whole((1, width)),
                   row_block(width), row_block(n_size),
                   whole((n_size, width)), pl.BlockSpec((per_step, 1, width), lambda b: (b, 0, 0)),
                   pl.BlockSpec((tiles, step_rows, tile_heads), lambda b: (0, b, 0))],
        out_shape=[jax.ShapeDtypeStruct((n_size, width), jnp.float32),
                   jax.ShapeDtypeStruct((rows, head_count), jnp.float32),
                   jax.ShapeDtypeStruct((rows, head_count), jnp.float32),
                   jax.ShapeDtypeStruct((block_count, 1, width), jnp.float32),
                   jax.ShapeDtypeStruct((1, width), jnp.float32),
                   jax.ShapeDtypeStruct((rows, width), jnp.bfloat16),
                   jax.ShapeDtypeStruct((rows, n_size), jnp.bfloat16),
                   jax.ShapeDtypeStruct((n_size, width), jnp.bfloat16),
                   jax.ShapeDtypeStruct((block_count, 1, width), jnp.float32),
                   jax.ShapeDtypeStruct((tiles, rows, tile_heads), jnp.float32)],
        scratch_shapes=[pltpu.VMEM((8, width), jnp.float32),
                        pltpu.VMEM((2, 2, 8, half), jnp.float32),
                        pltpu.VMEM((1, head_count), jnp.float32)],
        compiler_params=pltpu.CompilerParams(dimension_semantics=("arbitrary",)),
    )(x, tails, wconv, bias_row, own_raw, other_raw, own_extra, other_extra, step_size,
      rate_row, info)


def partial_kernel(head_width, from_zero, *refs):
    if from_zero:
        (x_ref, b_ref, cown_ref, cother_ref, ownx_ref, otherx_ref, l_ref, dt_ref, segr_ref,
         info_ref, decay_ref, skip_ref, out_ref, cout_ref, end_ref, state_ref, cprev_ref) = refs
    else:
        (x_ref, b_ref, cown_ref, cother_ref, ownx_ref, otherx_ref, l_ref, dt_ref, segr_ref,
         info_ref, decay_ref, skip_ref, init_ref, after_ref, pown_ref, pother_ref, out_ref,
         cout_ref, state_ref, cprev_ref) = refs
    blk = pl.program_id(0)

    @pl.when(blk == 0)
    def _():
        if from_zero:
            state_ref[...] = jnp.zeros(state_ref.shape, jnp.float32)
            cprev_ref[0] = ownx_ref[1, 0:8, :]
            cprev_ref[1] = otherx_ref[1, 0:8, :]
        else:
            state_ref[...] = init_ref[...]
            cprev_ref[0] = pown_ref[0, 8:16, :].astype(jnp.float32)
            cprev_ref[1] = pother_ref[0, 8:16, :].astype(jnp.float32)

    info = info_ref[...]
    seg_col = info[:, 0:1]
    end_col = (seg_col == seg_col[BLOCK - 1 : BLOCK, :]).astype(jnp.float32)
    l_small = l_ref[...]
    dt_small = dt_ref[...]
    x = x_ref[...].astype(jnp.float32)
    state = state_ref[...]
    halves = []
    for side, (raw_ref, extra_ref) in enumerate(((cown_ref, ownx_ref), (cother_ref, otherx_ref))):
        raw_c = raw_ref[0].astype(jnp.float32)
        extra = extra_ref[1]
        halves.append(causal_conv(raw_c, cprev_ref[side], extra[8:12], extra[12:13], info))
        cprev_ref[side] = raw_c[BLOCK - 8 :]
    lower = info_ref[0:1, 5:6] > 0.5
    c_mat = jnp.where(lower, jnp.concatenate(halves, 1), jnp.concatenate(halves[::-1], 1))
    cout_ref[...] = c_mat
    b_mat = b_ref[...]
    scores = lax.dot_general(
        c_mat, b_mat, (((1,), (1,)), ((), ())), preferred_element_type=jnp.float32
    )
    rows = lax.broadcasted_iota(jnp.int32, (BLOCK, BLOCK), 0)
    cols = lax.broadcasted_iota(jnp.int32, (BLOCK, BLOCK), 1)
    allowed = (rows >= cols) & (seg_col == segr_ref[...])
    masked = jnp.where(allowed, scores, 0.0).astype(jnp.bfloat16)
    rising = expand_heads(jnp.exp(l_small), head_width)
    falling = expand_heads(jnp.exp(-l_small) * dt_small, head_width)
    intra = split_dot(masked, x * falling) * rising
    inter = split_dot(c_mat, state) * (rising * info[:, 1:2])
    out_ref[...] = intra + inter + skip_ref[...] * x
    last = blk == pl.num_programs(0) - 1

    @pl.when(jnp.logical_or(jnp.logical_not(last), from_zero))
    def _():
        ending = expand_heads(
            jnp.exp(l_small[BLOCK - 1 : BLOCK, :] - l_small) * dt_small * end_col, head_width
        )
        weighted = (x * ending).astype(jnp.bfloat16)
        new_state = decay_ref[0] * state + lax.dot_general(
            b_mat, weighted, (((0,), (0,)), ((), ())), preferred_element_type=jnp.float32
        )
        state_ref[...] = new_state
        if from_zero:

            @pl.when(last)
            def _():
                end_ref[...] = new_state


def run_partial(first, count, x, b_full, c_raws, l_t, dt_t, seg_row, info, decay_x, skip_x,
                init=None, after=None):
    rows, width = x.shape
    head_count = l_t.shape[1]
    n_size = b_full.shape[1]
    own_raw, other_raw, own_extra, other_extra = c_raws
    half = own_raw.shape[2]
    row_block = lambda cols: pl.BlockSpec((BLOCK, cols), lambda b: (b + first, 0))
    whole = lambda shape: pl.BlockSpec(shape, lambda b: (0,) * len(shape))
    from_zero = init is None
    plane = pl.BlockSpec((1, BLOCK, half), lambda b: (1, b + first, 0))
    in_specs = [row_block(width), row_block(n_size), plane, plane, whole(own_extra.shape),
                whole(own_extra.shape), row_block(head_count),
                row_block(head_count), pl.BlockSpec((1, BLOCK), lambda b: (0, b + first)),
                row_block(info.shape[1]), pl.BlockSpec((1, 1, width), lambda b: (b + first, 0, 0)),
                whole((1, width))]
    args = [x, b_full, own_raw, other_raw, own_extra, other_extra, l_t, dt_t, seg_row, info,
            decay_x, skip_x]
    if not from_zero:
        before = pl.BlockSpec((1, 16, half), lambda b: (1, first * (BLOCK // 16) - 1, 0))
        in_specs += [whole((n_size, width)), pl.BlockSpec(memory_space=pl.ANY), before, before]
        args += [init, after, own_raw, other_raw]
    out_specs = [pl.BlockSpec((BLOCK, width), lambda b: (b, 0)),
                 pl.BlockSpec((BLOCK, n_size), lambda b: (b, 0))]
    out_shape = [jax.ShapeDtypeStruct((count * BLOCK, width), jnp.float32),
                 jax.ShapeDtypeStruct((count * BLOCK, n_size), jnp.bfloat16)]
    if from_zero:
        out_specs.append(whole((n_size, width)))
        out_shape.append(jax.ShapeDtypeStruct((n_size, width), jnp.float32))
    return pl.pallas_call(
        functools.partial(partial_kernel, width // head_count, from_zero),
        grid=(count,),
        in_specs=in_specs,
        out_specs=out_specs,
        out_shape=out_shape,
        scratch_shapes=[pltpu.VMEM((n_size, width), jnp.float32),
                        pltpu.VMEM((2, 8, half), jnp.float32)],
        compiler_params=pltpu.CompilerParams(dimension_semantics=("arbitrary",)),
    )(*args)


def correct_kernel(head_width, y_ref, z_ref, c_ref, d_ref, g_ref, ein_ref, out_ref):
    factor = expand_heads(g_ref[0], head_width)
    ein = ein_ref[...]
    split = y_ref.shape[0]
    carried = jnp.dot(c_ref[...], ein, preferred_element_type=jnp.float32)
    out_ref[:split] = (y_ref[...] + carried * factor[:split]).astype(jnp.bfloat16)
    carried = jnp.dot(d_ref[...], ein, preferred_element_type=jnp.float32)
    out_ref[split:] = (z_ref[...] + carried * factor[split:]).astype(jnp.bfloat16)


def run_correct(first, second, c_first, c_second, g_tiles, entering):
    rows = first.shape[0] + second.shape[0]
    width = first.shape[1]
    tiles, _, heads_per = g_tiles.shape
    tile = CORRECT_TILE
    head_width = tile // heads_per
    n_size = c_first.shape[1]
    return pl.pallas_call(
        functools.partial(correct_kernel, head_width),
        grid=(tiles,),
        in_specs=[pl.BlockSpec((first.shape[0], tile), lambda j: (0, j)),
                  pl.BlockSpec((second.shape[0], tile), lambda j: (0, j)),
                  pl.BlockSpec((first.shape[0], n_size), lambda j: (0, 0)),
                  pl.BlockSpec((second.shape[0], n_size), lambda j: (0, 0)),
                  pl.BlockSpec((1, rows, heads_per), lambda j: (j, 0, 0)),
                  pl.BlockSpec((n_size, tile), lambda j: (0, j))],
        out_specs=pl.BlockSpec((rows, tile), lambda j: (0, j)),
        out_shape=jax.ShapeDtypeStruct((rows, width), jnp.bfloat16),
        compiler_params=pltpu.CompilerParams(dimension_semantics=("arbitrary",)),
    )(first, second, c_first, c_second, g_tiles, entering)


def run_blocks(with_y, x, b_full, c_full, l_t, dt_t, seg_row, seg_col, entry_col, decay_x,
               skip_x, entering):
    rows, width = x.shape
    head_count = l_t.shape[1]
    head_width = width // head_count
    n_size = b_full.shape[1]
    block_count = rows // BLOCK
    row_block = lambda cols: pl.BlockSpec((BLOCK, cols), lambda b: (b, 0))
    bt_spec = pl.BlockSpec((n_size, BLOCK), lambda b: (0, b))
    decay_spec = pl.BlockSpec((1, 1, width), lambda b: (b, 0, 0))
    state_spec = pl.BlockSpec((n_size, width), lambda b: (0, 0))
    state_shape = jax.ShapeDtypeStruct((n_size, width), jnp.float32)
    kernel = functools.partial(block_kernel, with_y, head_width)
    params = pltpu.CompilerParams(dimension_semantics=("arbitrary",))
    if with_y:
        return pl.pallas_call(
            kernel,
            grid=(block_count,),
            in_specs=[row_block(width), row_block(n_size), row_block(n_size),
                      row_block(head_count), row_block(head_count),
                      pl.BlockSpec((1, BLOCK), lambda b: (0, b)), row_block(seg_col.shape[1]),
                      decay_spec, pl.BlockSpec((1, width), lambda b: (0, 0)), state_spec],
            out_specs=row_block(width),
            out_shape=jax.ShapeDtypeStruct((rows, width), jnp.bfloat16),
            scratch_shapes=[pltpu.VMEM((n_size, width), jnp.float32)],
            compiler_params=params,
        )(x, b_full, c_full, l_t, dt_t, seg_row, seg_col, decay_x, skip_x, entering)
    return pl.pallas_call(
        kernel,
        grid=(block_count,),
        in_specs=[row_block(width), bt_spec, row_block(head_count), row_block(head_count),
                  row_block(1), decay_spec],
        out_specs=state_spec,
        out_shape=state_shape,
        compiler_params=params,
    )(x, b_t, l_t, dt_t, seg_col, decay_x)


def body(
    inner_input,
    state_input,
    conv_inner,
    bias_inner,
    conv_state,
    bias_state,
    step_size,
    decay_rate,
    skip_gain,
    lengths,
):
    own_rows = inner_input.shape[0]
    head_count = decay_rate.shape[0]
    group_half = state_input.shape[2]
    block_count = own_rows // BLOCK
    positions = lax.axis_index("seq") * own_rows + jnp.arange(own_rows + 3, dtype=jnp.int32) - 3
    seg_ext = segment_of(lengths, positions)
    width = inner_input.shape[1]
    tails = jnp.concatenate(
        [inner_input[-8:], jnp.transpose(state_input[:, -8:], (1, 0, 2)).reshape(8, -1)], 1
    )
    tails = shifted(tails, "seq", 1)
    state_tail = tails[:, width:].reshape(8, 2, group_half)
    extra = jnp.concatenate(
        [jnp.transpose(state_tail, (1, 0, 2)).astype(jnp.float32),
         conv_state.astype(jnp.float32), bias_state[:, None, :]],
        1,
    )
    partner_raw, partner_extra = from_partner((state_input, extra), "head", 0)
    lower_half = (lax.axis_index("head") % 2 == 0).astype(jnp.float32)
    head_width = inner_input.shape[1] // head_count
    spread = lambda v: jnp.repeat(v, head_width, axis=-1)
    skip_x = spread(skip_gain).reshape(1, -1)
    seg_own = seg_ext[3:].reshape(block_count, BLOCK)
    seg_prev = seg_ext[2 : 2 + own_rows].reshape(block_count, BLOCK)[:, 0]
    seg_row = seg_ext[3:].reshape(1, own_rows).astype(jnp.float32)
    own_seg = seg_ext[3:]
    entry_col = (seg_own == seg_prev[:, None]).reshape(own_rows)
    keeps = [(seg_ext[3 - back : 3 - back + own_rows] == own_seg) for back in (1, 2, 3)]
    info = jnp.stack(
        [own_seg.astype(jnp.float32), entry_col.astype(jnp.float32)]
        + [keep.astype(jnp.float32) for keep in keeps]
        + [jnp.zeros((own_rows,), jnp.float32), jnp.full((own_rows,), lower_half, jnp.float32),
           jnp.zeros((own_rows,), jnp.float32)],
        1,
    )

    (local_end, l_t, dt_t, decay_x, total_decay, inner_conv, b_full, end_sent,
     prefix_x, g_tiles) = run_state(
        inner_input, tails, conv_inner, bias_inner.reshape(1, -1), state_input, partner_raw,
        extra, partner_extra,
        step_size, decay_rate.reshape(1, -1), info
    )

    def relay(step_num, incoming):
        return shifted(
            (total_decay * incoming.astype(jnp.float32) + local_end).astype(jnp.bfloat16), "seq", 1
        )

    part_rows = own_rows * lax.axis_size("seq")
    hops = min(lax.axis_size("seq") - 1, -(-(part_rows // 2) // own_rows))
    half_blocks = block_count // 2
    c_raws = (state_input, partner_raw, extra, partner_extra)
    operands = (inner_conv, b_full, c_raws, l_t, dt_t, seg_row, info, decay_x, skip_x)
    incoming = shifted(end_sent, "seq", 1)
    partial, c_first, middle = run_partial(0, half_blocks, *operands)
    incoming, partial, c_first, middle = lax.optimization_barrier(
        (incoming, partial, c_first, middle)
    )
    first_hop = incoming
    for step_num in range(1, hops):
        incoming = relay(step_num, incoming)
    second, c_second = run_partial(
        half_blocks, block_count - half_blocks, *operands, init=middle, after=first_hop
    )
    return run_correct(partial, second, c_first, c_second, g_tiles, incoming)


def solution(mesh):
    return jax.shard_map(
        body,
        mesh=mesh,
        in_specs=(
            P(("grp", "seq"), "head"),
            P(None, ("grp", "seq"), "head"),
            P(None, "head"),
            P("head"),
            P(None, None, "head"),
            P(None, "head"),
            P("head", ("grp", "seq")),
            P("head"),
            P("head"),
            P("grp"),
        ),
        out_specs=P(("grp", "seq"), "head"),
        check_vma=False,
    )
```

```python
import functools

import jax
import jax.numpy as jnp
from jax import lax
from jax.experimental import pallas as pl
from jax.experimental.pallas import tpu as pltpu
from jax.sharding import PartitionSpec as P

BLOCK = 128
CORRECT_TILE = 1024


def shifted(value, axis, steps):
    count = lax.axis_size(axis)
    initial, last = (max(0, -steps), min(count, count - steps))
    return lax.ppermute(value, axis, [(source, source + steps) for source in range(initial, last)])


def from_partner(block, axis, stride):
    count = lax.axis_size(axis)
    route = []
    for low in range(count):
        high = low | 1 << stride
        if high != low and high < count:
            route += [(low, high), (high, low)]
    return lax.ppermute(block, axis, route)


def segment_of(lengths, positions):
    starts = jnp.cumsum(lengths, dtype=jnp.int32) - lengths
    covered = (starts[None, :] <= positions[:, None]).astype(jnp.int32)
    return jnp.sum(covered, axis=1, dtype=jnp.int32) - 1


def convolve(extended, weight, bias_row, seg_ext, row_count):
    own_seg = seg_ext[3:]
    summed = (
        jnp.zeros(extended.shape[:-2] + (row_count, extended.shape[-1]), jnp.float32) + bias_row
    )
    for offset in range(4):
        kept_mask = (seg_ext[offset : offset + row_count] == own_seg).astype(jnp.float32)[:, None]
        window = extended[..., offset : offset + row_count, :].astype(jnp.float32)
        summed = summed + weight[offset].astype(jnp.float32) * window * kept_mask
    return jax.nn.silu(summed).astype(jnp.bfloat16)


def split_dot(lhs, value):
    high = value.astype(jnp.bfloat16)
    low = (value - high.astype(jnp.float32)).astype(jnp.bfloat16)
    return jnp.dot(lhs, high, preferred_element_type=jnp.float32) + jnp.dot(
        lhs, low, preferred_element_type=jnp.float32
    )


def expand_heads(small, head_width):
    rows, heads = small.shape
    per_tile = 128 // head_width
    lane = lax.broadcasted_iota(jnp.int32, (rows, 128), 1) // head_width
    tiles = []
    for tile in range(heads // per_tile):
        picked = jnp.broadcast_to(small[:, tile * per_tile : tile * per_tile + 1], (rows, 128))
        for k in range(1, per_tile):
            column = small[:, tile * per_tile + k : tile * per_tile + k + 1]
            picked = jnp.where(lane == k, jnp.broadcast_to(column, (rows, 128)), picked)
        tiles.append(picked)
    return jnp.concatenate(tiles, axis=1)


def block_kernel(with_y, head_width, *refs):
    if with_y:
        (x_ref, b_ref, c_ref, l_ref, dt_ref, segr_ref, info_ref, decay_ref,
         skip_ref, ein_ref, out_ref, state_ref) = refs
    else:
        (x_ref, b_ref, l_ref, dt_ref, segc_ref, decay_ref, state_ref) = refs
    blk = pl.program_id(0)

    @pl.when(blk == 0)
    def _():
        if with_y:
            state_ref[...] = ein_ref[...].astype(jnp.float32)
        else:
            state_ref[...] = jnp.zeros(state_ref.shape, jnp.float32)

    info = info_ref[...]
    seg_col = info[:, 0:1]
    end_col = (seg_col == seg_col[BLOCK - 1 : BLOCK, :]).astype(jnp.float32)
    l_small = l_ref[...]
    dt_small = dt_ref[...]
    x = x_ref[...].astype(jnp.float32)
    state = state_ref[...]
    if with_y:
        c_mat = c_ref[...]
        seg_row = segr_ref[...]
        scores = lax.dot_general(
            c_mat, b_ref[...], (((1,), (1,)), ((), ())), preferred_element_type=jnp.float32
        )
        rows = lax.broadcasted_iota(jnp.int32, (BLOCK, BLOCK), 0)
        cols = lax.broadcasted_iota(jnp.int32, (BLOCK, BLOCK), 1)
        allowed = (rows >= cols) & (seg_col == seg_row)
        masked = jnp.where(allowed, scores, 0.0).astype(jnp.bfloat16)
        rising = expand_heads(jnp.exp(l_small), head_width)
        falling = expand_heads(jnp.exp(-l_small) * dt_small, head_width)
        intra = split_dot(masked, x * falling) * rising
        inter = split_dot(c_mat, state) * (rising * info[:, 1:2])
        out_ref[...] = (intra + inter + skip_ref[...] * x).astype(jnp.bfloat16)
    ending = expand_heads(
        jnp.exp(l_small[BLOCK - 1 : BLOCK, :] - l_small) * dt_small * end_col, head_width
    )
    weighted = (x * ending).astype(jnp.bfloat16)
    state_ref[...] = decay_ref[0] * state + lax.dot_general(
        b_ref[...], weighted, (((0,), (0,)), ((), ())), preferred_element_type=jnp.float32
    )


def causal_conv(raw, prev, taps, bias, info):
    top_row = lax.broadcasted_iota(jnp.int32, prev.shape, 0)
    summed = jnp.zeros(raw.shape, jnp.float32) + bias
    for offset in range(4):
        back = 3 - offset
        if back == 0:
            window = raw
        else:
            rolled = pltpu.roll(raw, back, 0)
            top = jnp.where(top_row < back, pltpu.roll(prev, back, 0), rolled[:8])
            window = jnp.concatenate([top, rolled[8:]], 0) * info[:, 1 + back : 2 + back]
        summed = summed + taps[offset : offset + 1, :] * window
    return jax.nn.silu(summed).astype(jnp.bfloat16)


def state_block(head_width, x_ref, tail_ref, wconv_ref, bias_ref, own_ref, other_ref, ownx_ref,
                 otherx_ref, dt_ref, rate_ref, info_ref, state_ref, l_ref, dtt_ref,
                 decay_ref, total_ref, xc_ref, bo_ref, sent_ref, prefix_ref, ltile_ref,
                 prev_ref, bcprev_ref, small_ref):
    info = info_ref[...]
    raw = x_ref[...].astype(jnp.float32)
    xc = causal_conv(raw, prev_ref[...], wconv_ref[...].astype(jnp.float32), bias_ref[...], info)
    prev_ref[...] = raw[BLOCK - 8 :]
    xc_ref[...] = xc
    lower = info_ref[0:1, 5:6] > 0.5
    convolved = []
    for which in range(1):
        halves = []
        for side, (raw_ref, extra_ref) in enumerate(((own_ref, ownx_ref), (other_ref, otherx_ref))):
            raw_bc = raw_ref[which].astype(jnp.float32)
            extra = extra_ref[which]
            halves.append(
                causal_conv(raw_bc, bcprev_ref[side, which], extra[8:12], extra[12:13], info)
            )
            bcprev_ref[side, which] = raw_bc[BLOCK - 8 :]
        convolved.append(jnp.where(
            lower, jnp.concatenate(halves, 1), jnp.concatenate(halves[::-1], 1)
        ))
    b_mat = convolved[0]
    bo_ref[...] = b_mat

    rows = lax.broadcasted_iota(jnp.int32, (2 * BLOCK, BLOCK), 0)
    cols = lax.broadcasted_iota(jnp.int32, (2 * BLOCK, BLOCK), 1)
    picker = jnp.where(
        ((rows < BLOCK) & (rows >= cols)) | (rows - BLOCK == cols), 1.0, 0.0
    ).astype(jnp.bfloat16)
    rest = dt_ref[...]
    cum = None
    for _ in range(3):
        piece = rest.astype(jnp.bfloat16)
        part = lax.dot_general(
            picker, piece, (((1,), (1,)), ((), ())), preferred_element_type=jnp.float32
        )
        cum = part if cum is None else cum + part
        rest = rest - piece.astype(jnp.float32)
    l_small = -cum[:BLOCK] * rate_ref[...]
    dt_small = cum[BLOCK:]
    l_ref[...] = l_small
    dtt_ref[...] = dt_small
    seg_col = info[:, 0:1]
    end_col = (seg_col == seg_col[BLOCK - 1 : BLOCK, :]).astype(jnp.float32)
    decay_x = expand_heads(
        jnp.exp(l_small[BLOCK - 1 : BLOCK, :]) * info[BLOCK - 1 : BLOCK, 1:2], head_width
    )
    decay_ref[0] = decay_x
    prefix_ref[0] = total_ref[...]
    total_ref[...] = total_ref[...] * decay_x
    carry = (jnp.exp(l_small) * info[:, 1:2]) * small_ref[...]
    small_ref[...] = small_ref[...] * (
        jnp.exp(l_small[BLOCK - 1 : BLOCK, :]) * info[BLOCK - 1 : BLOCK, 1:2]
    )
    tile_heads = ltile_ref.shape[2]
    for tile in range(ltile_ref.shape[0]):
        ltile_ref[tile] = carry[:, tile * tile_heads : (tile + 1) * tile_heads]
    ending = expand_heads(
        jnp.exp(l_small[BLOCK - 1 : BLOCK, :] - l_small) * dt_small * end_col, head_width
    )
    weighted = (xc.astype(jnp.float32) * ending).astype(jnp.bfloat16)
    new_state = decay_x * state_ref[...] + lax.dot_general(
        b_mat, weighted, (((0,), (0,)), ((), ())), preferred_element_type=jnp.float32
    )
    state_ref[...] = new_state


def state_kernel(head_width, per_step, x_ref, tail_ref, wconv_ref, bias_ref, own_ref, other_ref,
                 ownx_ref, otherx_ref, dt_ref, rate_ref, info_ref, state_ref, l_ref, dtt_ref,
                 decay_ref, total_ref, xc_ref, bo_ref, sent_ref, prefix_ref, ltile_ref,
                 prev_ref, bcprev_ref, small_ref):
    blk = pl.program_id(0)

    @pl.when(blk == 0)
    def _():
        state_ref[...] = jnp.zeros(state_ref.shape, jnp.float32)
        total_ref[...] = jnp.ones(total_ref.shape, jnp.float32)
        prev_ref[...] = tail_ref[:, : x_ref.shape[1]].astype(jnp.float32)
        small_ref[...] = jnp.ones(small_ref.shape, jnp.float32)
        bcprev_ref[0] = ownx_ref[:, 0:8, :]
        bcprev_ref[1] = otherx_ref[:, 0:8, :]

    for sub in range(per_step):
        rows = pl.ds(sub * BLOCK, BLOCK)
        state_block(
            head_width, x_ref.at[rows, :], tail_ref, wconv_ref, bias_ref, own_ref.at[:, rows, :],
            other_ref.at[:, rows, :], ownx_ref, otherx_ref, dt_ref.at[:, rows], rate_ref,
            info_ref.at[rows, :], state_ref, l_ref.at[rows, :], dtt_ref.at[rows, :],
            decay_ref.at[pl.ds(sub, 1)], total_ref, xc_ref.at[rows, :], bo_ref.at[rows, :],
            sent_ref, prefix_ref.at[pl.ds(sub, 1)], ltile_ref.at[:, rows, :], prev_ref,
            bcprev_ref, small_ref,
        )

    @pl.when(blk == pl.num_programs(0) - 1)
    def _():
        sent_ref[...] = state_ref[...].astype(jnp.bfloat16)


def run_state(x, tails, wconv, bias_row, own_raw, other_raw, own_extra, other_extra,
              step_size, rate_row, info):
    rows, width = x.shape
    head_count = step_size.shape[0]
    half = own_raw.shape[2]
    n_size = 2 * half
    block_count = rows // BLOCK
    tiles = width // CORRECT_TILE
    tile_heads = head_count // tiles
    per_step = 2 if block_count % 2 == 0 else 1
    step_rows = per_step * BLOCK
    row_block = lambda cols: pl.BlockSpec((step_rows, cols), lambda b: (b, 0))
    whole = lambda shape: pl.BlockSpec(shape, lambda b: (0,) * len(shape))
    return pl.pallas_call(
        functools.partial(state_kernel, width // head_count, per_step),
        grid=(block_count // per_step,),
        in_specs=[row_block(width), whole(tails.shape), whole((4, width)), whole((1, width)),
                  pl.BlockSpec((2, step_rows, half), lambda b: (0, b, 0)),
                  pl.BlockSpec((2, step_rows, half), lambda b: (0, b, 0)),
                  whole(own_extra.shape), whole(own_extra.shape),
                  pl.BlockSpec((head_count, step_rows), lambda b: (0, b)),
                  whole((1, head_count)), row_block(info.shape[1])],
        out_specs=[whole((n_size, width)), row_block(head_count), row_block(head_count),
                   pl.BlockSpec((per_step, 1, width), lambda b: (b, 0, 0)), whole((1, width)),
                   row_block(width), row_block(n_size),
                   whole((n_size, width)), pl.BlockSpec((per_step, 1, width), lambda b: (b, 0, 0)),
                   pl.BlockSpec((tiles, step_rows, tile_heads), lambda b: (0, b, 0))],
        out_shape=[jax.ShapeDtypeStruct((n_size, width), jnp.float32),
                   jax.ShapeDtypeStruct((rows, head_count), jnp.float32),
                   jax.ShapeDtypeStruct((rows, head_count), jnp.float32),
                   jax.ShapeDtypeStruct((block_count, 1, width), jnp.float32),
                   jax.ShapeDtypeStruct((1, width), jnp.float32),
                   jax.ShapeDtypeStruct((rows, width), jnp.bfloat16),
                   jax.ShapeDtypeStruct((rows, n_size), jnp.bfloat16),
                   jax.ShapeDtypeStruct((n_size, width), jnp.bfloat16),
                   jax.ShapeDtypeStruct((block_count, 1, width), jnp.float32),
                   jax.ShapeDtypeStruct((tiles, rows, tile_heads), jnp.float32)],
        scratch_shapes=[pltpu.VMEM((8, width), jnp.float32),
                        pltpu.VMEM((2, 2, 8, half), jnp.float32),
                        pltpu.VMEM((1, head_count), jnp.float32)],
        compiler_params=pltpu.CompilerParams(dimension_semantics=("arbitrary",)),
    )(x, tails, wconv, bias_row, own_raw, other_raw, own_extra, other_extra, step_size,
      rate_row, info)


def partial_kernel(head_width, from_zero, *refs):
    if from_zero:
        (x_ref, b_ref, cown_ref, cother_ref, ownx_ref, otherx_ref, l_ref, dt_ref, segr_ref,
         info_ref, decay_ref, skip_ref, out_ref, cout_ref, end_ref, state_ref, cprev_ref) = refs
    else:
        (x_ref, b_ref, cown_ref, cother_ref, ownx_ref, otherx_ref, l_ref, dt_ref, segr_ref,
         info_ref, decay_ref, skip_ref, init_ref, after_ref, pown_ref, pother_ref, out_ref,
         cout_ref, state_ref, cprev_ref) = refs
    blk = pl.program_id(0)

    @pl.when(blk == 0)
    def _():
        if from_zero:
            state_ref[...] = jnp.zeros(state_ref.shape, jnp.float32)
            cprev_ref[0] = ownx_ref[1, 0:8, :]
            cprev_ref[1] = otherx_ref[1, 0:8, :]
        else:
            state_ref[...] = init_ref[...]
            cprev_ref[0] = pown_ref[0, 8:16, :].astype(jnp.float32)
            cprev_ref[1] = pother_ref[0, 8:16, :].astype(jnp.float32)

    info = info_ref[...]
    seg_col = info[:, 0:1]
    end_col = (seg_col == seg_col[BLOCK - 1 : BLOCK, :]).astype(jnp.float32)
    l_small = l_ref[...]
    dt_small = dt_ref[...]
    x = x_ref[...].astype(jnp.float32)
    state = state_ref[...]
    halves = []
    for side, (raw_ref, extra_ref) in enumerate(((cown_ref, ownx_ref), (cother_ref, otherx_ref))):
        raw_c = raw_ref[0].astype(jnp.float32)
        extra = extra_ref[1]
        halves.append(causal_conv(raw_c, cprev_ref[side], extra[8:12], extra[12:13], info))
        cprev_ref[side] = raw_c[BLOCK - 8 :]
    lower = info_ref[0:1, 5:6] > 0.5
    c_mat = jnp.where(lower, jnp.concatenate(halves, 1), jnp.concatenate(halves[::-1], 1))
    cout_ref[...] = c_mat
    b_mat = b_ref[...]
    scores = lax.dot_general(
        c_mat, b_mat, (((1,), (1,)), ((), ())), preferred_element_type=jnp.float32
    )
    rows = lax.broadcasted_iota(jnp.int32, (BLOCK, BLOCK), 0)
    cols = lax.broadcasted_iota(jnp.int32, (BLOCK, BLOCK), 1)
    allowed = (rows >= cols) & (seg_col == segr_ref[...])
    masked = jnp.where(allowed, scores, 0.0).astype(jnp.bfloat16)
    rising = expand_heads(jnp.exp(l_small), head_width)
    falling = expand_heads(jnp.exp(-l_small) * dt_small, head_width)
    intra = split_dot(masked, x * falling) * rising
    inter = split_dot(c_mat, state) * (rising * info[:, 1:2])
    out_ref[...] = intra + inter + skip_ref[...] * x
    last = blk == pl.num_programs(0) - 1

    @pl.when(jnp.logical_or(jnp.logical_not(last), from_zero))
    def _():
        ending = expand_heads(
            jnp.exp(l_small[BLOCK - 1 : BLOCK, :] - l_small) * dt_small * end_col, head_width
        )
        weighted = (x * ending).astype(jnp.bfloat16)
        new_state = decay_ref[0] * state + lax.dot_general(
            b_mat, weighted, (((0,), (0,)), ((), ())), preferred_element_type=jnp.float32
        )
        state_ref[...] = new_state
        if from_zero:

            @pl.when(last)
            def _():
                end_ref[...] = new_state


def run_partial(first, count, x, b_full, c_raws, l_t, dt_t, seg_row, info, decay_x, skip_x,
                init=None, after=None):
    rows, width = x.shape
    head_count = l_t.shape[1]
    n_size = b_full.shape[1]
    own_raw, other_raw, own_extra, other_extra = c_raws
    half = own_raw.shape[2]
    row_block = lambda cols: pl.BlockSpec((BLOCK, cols), lambda b: (b + first, 0))
    whole = lambda shape: pl.BlockSpec(shape, lambda b: (0,) * len(shape))
    from_zero = init is None
    plane = pl.BlockSpec((1, BLOCK, half), lambda b: (1, b + first, 0))
    in_specs = [row_block(width), row_block(n_size), plane, plane, whole(own_extra.shape),
                whole(own_extra.shape), row_block(head_count),
                row_block(head_count), pl.BlockSpec((1, BLOCK), lambda b: (0, b + first)),
                row_block(info.shape[1]), pl.BlockSpec((1, 1, width), lambda b: (b + first, 0, 0)),
                whole((1, width))]
    args = [x, b_full, own_raw, other_raw, own_extra, other_extra, l_t, dt_t, seg_row, info,
            decay_x, skip_x]
    if not from_zero:
        before = pl.BlockSpec((1, 16, half), lambda b: (1, first * (BLOCK // 16) - 1, 0))
        in_specs += [whole((n_size, width)), pl.BlockSpec(memory_space=pl.ANY), before, before]
        args += [init, after, own_raw, other_raw]
    out_specs = [pl.BlockSpec((BLOCK, width), lambda b: (b, 0)),
                 pl.BlockSpec((BLOCK, n_size), lambda b: (b, 0))]
    out_shape = [jax.ShapeDtypeStruct((count * BLOCK, width), jnp.float32),
                 jax.ShapeDtypeStruct((count * BLOCK, n_size), jnp.bfloat16)]
    if from_zero:
        out_specs.append(whole((n_size, width)))
        out_shape.append(jax.ShapeDtypeStruct((n_size, width), jnp.float32))
    return pl.pallas_call(
        functools.partial(partial_kernel, width // head_count, from_zero),
        grid=(count,),
        in_specs=in_specs,
        out_specs=out_specs,
        out_shape=out_shape,
        scratch_shapes=[pltpu.VMEM((n_size, width), jnp.float32),
                        pltpu.VMEM((2, 8, half), jnp.float32)],
        compiler_params=pltpu.CompilerParams(dimension_semantics=("arbitrary",)),
    )(*args)


def correct_kernel(head_width, y_ref, z_ref, c_ref, d_ref, g_ref, ein_ref, out_ref):
    factor = expand_heads(g_ref[0], head_width)
    ein = ein_ref[...]
    split = y_ref.shape[0]
    carried = jnp.dot(c_ref[...], ein, preferred_element_type=jnp.float32)
    out_ref[:split] = (y_ref[...] + carried * factor[:split]).astype(jnp.bfloat16)
    carried = jnp.dot(d_ref[...], ein, preferred_element_type=jnp.float32)
    out_ref[split:] = (z_ref[...] + carried * factor[split:]).astype(jnp.bfloat16)


def run_correct(first, second, c_first, c_second, g_tiles, entering):
    rows = first.shape[0] + second.shape[0]
    width = first.shape[1]
    tiles, _, heads_per = g_tiles.shape
    tile = CORRECT_TILE
    head_width = tile // heads_per
    n_size = c_first.shape[1]
    return pl.pallas_call(
        functools.partial(correct_kernel, head_width),
        grid=(tiles,),
        in_specs=[pl.BlockSpec((first.shape[0], tile), lambda j: (0, j)),
                  pl.BlockSpec((second.shape[0], tile), lambda j: (0, j)),
                  pl.BlockSpec((first.shape[0], n_size), lambda j: (0, 0)),
                  pl.BlockSpec((second.shape[0], n_size), lambda j: (0, 0)),
                  pl.BlockSpec((1, rows, heads_per), lambda j: (j, 0, 0)),
                  pl.BlockSpec((n_size, tile), lambda j: (0, j))],
        out_specs=pl.BlockSpec((rows, tile), lambda j: (0, j)),
        out_shape=jax.ShapeDtypeStruct((rows, width), jnp.bfloat16),
        compiler_params=pltpu.CompilerParams(dimension_semantics=("arbitrary",)),
    )(first, second, c_first, c_second, g_tiles, entering)


def run_blocks(with_y, x, b_full, c_full, l_t, dt_t, seg_row, seg_col, entry_col, decay_x,
               skip_x, entering):
    rows, width = x.shape
    head_count = l_t.shape[1]
    head_width = width // head_count
    n_size = b_full.shape[1]
    block_count = rows // BLOCK
    row_block = lambda cols: pl.BlockSpec((BLOCK, cols), lambda b: (b, 0))
    bt_spec = pl.BlockSpec((n_size, BLOCK), lambda b: (0, b))
    decay_spec = pl.BlockSpec((1, 1, width), lambda b: (b, 0, 0))
    state_spec = pl.BlockSpec((n_size, width), lambda b: (0, 0))
    state_shape = jax.ShapeDtypeStruct((n_size, width), jnp.float32)
    kernel = functools.partial(block_kernel, with_y, head_width)
    params = pltpu.CompilerParams(dimension_semantics=("arbitrary",))
    if with_y:
        return pl.pallas_call(
            kernel,
            grid=(block_count,),
            in_specs=[row_block(width), row_block(n_size), row_block(n_size),
                      row_block(head_count), row_block(head_count),
                      pl.BlockSpec((1, BLOCK), lambda b: (0, b)), row_block(seg_col.shape[1]),
                      decay_spec, pl.BlockSpec((1, width), lambda b: (0, 0)), state_spec],
            out_specs=row_block(width),
            out_shape=jax.ShapeDtypeStruct((rows, width), jnp.bfloat16),
            scratch_shapes=[pltpu.VMEM((n_size, width), jnp.float32)],
            compiler_params=params,
        )(x, b_full, c_full, l_t, dt_t, seg_row, seg_col, decay_x, skip_x, entering)
    return pl.pallas_call(
        kernel,
        grid=(block_count,),
        in_specs=[row_block(width), bt_spec, row_block(head_count), row_block(head_count),
                  row_block(1), decay_spec],
        out_specs=state_spec,
        out_shape=state_shape,
        compiler_params=params,
    )(x, b_t, l_t, dt_t, seg_col, decay_x)


def body(
    inner_input,
    state_input,
    conv_inner,
    bias_inner,
    conv_state,
    bias_state,
    step_size,
    decay_rate,
    skip_gain,
    lengths,
):
    own_rows = inner_input.shape[0]
    head_count = decay_rate.shape[0]
    group_half = state_input.shape[2]
    block_count = own_rows // BLOCK
    positions = lax.axis_index("seq") * own_rows + jnp.arange(own_rows + 3, dtype=jnp.int32) - 3
    seg_ext = segment_of(lengths, positions)
    width = inner_input.shape[1]
    tails = jnp.concatenate(
        [inner_input[-8:], jnp.transpose(state_input[:, -8:], (1, 0, 2)).reshape(8, -1)], 1
    )
    tails = shifted(tails, "seq", 1)
    state_tail = tails[:, width:].reshape(8, 2, group_half)
    extra = jnp.concatenate(
        [jnp.transpose(state_tail, (1, 0, 2)).astype(jnp.float32),
         conv_state.astype(jnp.float32), bias_state[:, None, :]],
        1,
    )
    partner_raw, partner_extra = from_partner((state_input, extra), "head", 0)
    lower_half = (lax.axis_index("head") % 2 == 0).astype(jnp.float32)
    head_width = inner_input.shape[1] // head_count
    spread = lambda v: jnp.repeat(v, head_width, axis=-1)
    skip_x = spread(skip_gain).reshape(1, -1)
    seg_own = seg_ext[3:].reshape(block_count, BLOCK)
    seg_prev = seg_ext[2 : 2 + own_rows].reshape(block_count, BLOCK)[:, 0]
    seg_row = seg_ext[3:].reshape(1, own_rows).astype(jnp.float32)
    own_seg = seg_ext[3:]
    entry_col = (seg_own == seg_prev[:, None]).reshape(own_rows)
    keeps = [(seg_ext[3 - back : 3 - back + own_rows] == own_seg) for back in (1, 2, 3)]
    info = jnp.stack(
        [own_seg.astype(jnp.float32), entry_col.astype(jnp.float32)]
        + [keep.astype(jnp.float32) for keep in keeps]
        + [jnp.zeros((own_rows,), jnp.float32), jnp.full((own_rows,), lower_half, jnp.float32),
           jnp.zeros((own_rows,), jnp.float32)],
        1,
    )

    (local_end, l_t, dt_t, decay_x, total_decay, inner_conv, b_full, end_sent,
     prefix_x, g_tiles) = run_state(
        inner_input, tails, conv_inner, bias_inner.reshape(1, -1), state_input, partner_raw,
        extra, partner_extra,
        step_size, decay_rate.reshape(1, -1), info
    )

    def relay(step_num, incoming):
        return shifted(
            (total_decay * incoming.astype(jnp.float32) + local_end).astype(jnp.bfloat16), "seq", 1
        )

    part_rows = own_rows * lax.axis_size("seq")
    hops = min(lax.axis_size("seq") - 1, -(-(part_rows // 2) // own_rows))
    half_blocks = block_count // 2
    c_raws = (state_input, partner_raw, extra, partner_extra)
    operands = (inner_conv, b_full, c_raws, l_t, dt_t, seg_row, info, decay_x, skip_x)
    incoming = shifted(end_sent, "seq", 1)
    partial, c_first, middle = run_partial(0, half_blocks, *operands)
    incoming, partial, c_first, middle = lax.optimization_barrier(
        (incoming, partial, c_first, middle)
    )
    first_hop = incoming
    for step_num in range(1, hops):
        incoming = relay(step_num, incoming)
    second, c_second = run_partial(
        half_blocks, block_count - half_blocks, *operands, init=middle, after=first_hop
    )
    return run_correct(partial, second, c_first, c_second, g_tiles, incoming)


def solution(mesh):
    return jax.shard_map(
        body,
        mesh=mesh,
        in_specs=(
            P(("grp", "seq"), "head"),
            P(None, ("grp", "seq"), "head"),
            P(None, "head"),
            P("head"),
            P(None, None, "head"),
            P(None, "head"),
            P("head", ("grp", "seq")),
            P("head"),
            P("head"),
            P("grp"),
        ),
        out_specs=P(("grp", "seq"), "head"),
        check_vma=False,
    )
```
